128 devices in a mesh: flow: 32 (over y, z, core), grp: 4 (over x).
Axes of the slice: x: 4, y: 4, z: 4, core: 2. Of those that a mesh axis runs over, the one named last changes fastest.
Arguments:
- velocity: float32 [3, 256, 128, 256], P(None, 'flow', 'grp'), may hold values from -6 to 6
- eddy_visc: float32 [256, 128, 256], P('flow', 'grp'), may hold values from 0.05 to 0.4
- projection: bfloat16 [125, 512], replicated, may hold values from -0.25 to 0.25
- acoustic_state: float32 [4, 125, 16384], P(None, None, ('flow', 'grp')), may hold values from -6 to 6
- route_send: int32 [128, 128, 2], P(('flow', 'grp')), may hold values from -1 to 127, as said below
- route_place: int32 [128, 128], P(('flow', 'grp')), may hold values from 0 to 255, as said below
Outputs:
- velocity_out: float32 [3, 256, 128, 256], P(None, 'flow', 'grp')
- acoustic_out: float32 [4, 125, 16384], P(None, None, ('flow', 'grp'))
The draws below stay inside these ranges and needn't reach their ends.
Inputs may be any that keep to these rules, and one draw needn't show every extreme that they name: `route_send`: row h lists, for each owner o, the local indices of home h's elements that o holds in 2 slots, -1 in an empty slot; every local element of h stands exactly once in row h; an owner holds elements of 64 home devices, all 2 slots of each filled. `route_place`: row o is a permutation of the filled slots h * 2 + k of owner o; position j of owner o holds home h's element route_send[h, o, k].
All inputs are finite; a program needn't handle non-finite values.
Results may differ from the reference program's by a relative error of at most 0.0003.
Values sent between devices are 32-bit elements; how exact they have to be, the bound alone decides.
No kernel may reach another device: no remote copies, remote signals or barrier semaphores. Data moves between devices by JAX's collectives and lax.ppermute only.
A program may use at most 64 MiB of HBM per device.

```python
import math
import jax
import jax.numpy as jnp
import numpy as np
from jax import lax

CX = 8
CY = 32
CZ = 256
ELEM_NODES = 125
ELEM_CELLS = 512
LES_SECTIONS = 2
AC_SECTIONS = 2
NX = 256
NY = 128
DEVS = 128
ELEM_DEV = 128
ELEMS = 16384
CAP = 2
N_FLOW = 32
N_GRP = 4


def routing_tables(key):
    group_count = ELEM_DEV // CAP
    values = jnp.arange(DEVS, dtype=jnp.int32)
    ranks = jax.random.permutation(jax.random.fold_in(key, 11), DEVS).astype(jnp.int32)
    priority = jnp.where(values == 1, -3, jnp.where(values == DEVS // 2, -2, jnp.where(values == DEVS - 1, -1, ranks)))
    shifts = jnp.argsort(priority, stable=True)[:group_count].astype(jnp.int32)
    homes = jnp.arange(DEVS, dtype=jnp.int32)
    block_key = jax.random.fold_in(key, 12)
    blocks = jax.vmap(lambda home: jax.random.permutation(jax.random.fold_in(block_key, home), ELEM_DEV))(homes)
    blocks = blocks.astype(jnp.int32).reshape(DEVS, group_count, CAP)
    owners = (homes[:, None] + shifts[None, :]) % DEVS
    sending = jnp.full((DEVS, DEVS, CAP), -1, jnp.int32).at[homes[:, None], owners].set(blocks)
    sources = (homes[:, None] - shifts[None, :]) % DEVS
    slot_ids = (sources[:, :, None] * CAP + jnp.arange(CAP, dtype=jnp.int32)[None, None, :]).reshape(DEVS, ELEM_DEV)
    place_key = jax.random.fold_in(key, 13)
    orders = jax.vmap(lambda owner: jax.random.permutation(jax.random.fold_in(place_key, owner), ELEM_DEV))(homes)
    placing = jnp.take_along_axis(slot_ids, orders.astype(jnp.int32), axis=1)
    return (sending, placing.astype(jnp.int32))


def draw_route_send(key, part):
    return routing_tables(key)[0]


def draw_route_place(key, part):
    return routing_tables(key)[1]


def shard_levels(rng, shape, split, least, high):
    loudness, own = 1.0, jax.random.fold_in(rng, 6)
    for axis_at, shards_of in split:
        heights = jnp.exp(jax.random.uniform(jax.random.fold_in(own, axis_at), (shards_of,), jnp.float32, least / len(split), high / len(split)))
        loudness = loudness * jnp.repeat(heights, shape[axis_at] // shards_of).reshape([-1 if axis == axis_at else 1 for axis in range(len(shape))])
    return loudness


def gaussian(stream_key, dims, spread, most, cuts=(), kind=jnp.bfloat16):
    drawn = jax.random.normal(stream_key, dims, jnp.float32) * spread
    if len(cuts) > 0:
        drawn = shard_levels(stream_key, dims, cuts, -0.22, 0.18) * drawn
    return jnp.clip(drawn, min=-most, max=most).astype(kind)


def setup_inputs(seed: int = 0) -> dict:
    key_list = jax.random.split(jax.random.key(seed), 7)
    velocity = gaussian(key_list[0], (3, NX, NY, CZ), 1.0, 6.0, ((1, 32), (2, 4)), jnp.float32)
    eddy_visc = jnp.clip(jnp.exp(math.log(0.4) - 2.0794415 * jax.random.uniform(key_list[1], (NX, NY, CZ), jnp.float32) ** shard_levels(key_list[1], (NX, NY, CZ), ((0, 32), (1, 4)), -0.2, 0.2)), 0.05, 0.4)
    projection = gaussian(key_list[2], (ELEM_NODES, ELEM_CELLS), ELEM_CELLS ** -0.5, 0.25)
    acoustic_state = gaussian(key_list[3], (4, ELEM_NODES, ELEMS), 1.0, 6.0, ((2, 128),), jnp.float32)
    route_send = draw_route_send(jax.random.fold_in(key_list[6], 71), 0)
    route_place = draw_route_place(jax.random.fold_in(key_list[6], 71), 0)
    return {"velocity": velocity, "eddy_visc": eddy_visc, "projection": projection, "acoustic_state": acoustic_state, "route_send": route_send, "route_place": route_place}


TIME_STEP_LES = 0.15
TIME_STEP_ACOUSTIC = 0.02
GEOMETRY = 2.0
LIFT_FACTOR = 20.0

def gll_derivative():
    gll_nodes = np.array([-1.0, -math.sqrt(3.0 / 7.0), 0.0, math.sqrt(3.0 / 7.0), 1.0])
    bary_weights = np.array([1.0 / np.prod([gll_nodes[first] - gll_nodes[other] for other in range(5) if other != first]) for first in range(5)])
    matrix = np.zeros((5, 5))
    for row_id in range(5):
        for col_id in range(5):
            if row_id != col_id:
                matrix[row_id, col_id] = bary_weights[col_id] / bary_weights[row_id] / (gll_nodes[row_id] - gll_nodes[col_id])
    for row_id in range(5):
        matrix[row_id, row_id] = -matrix[row_id].sum()
    return matrix

def neighbour_slice(field, axis_id, offset):
    length = field.shape[axis_id]
    pieces = [slice(1, -1)] * 3
    pieces[axis_id] = slice(1 + offset, length - 1 + offset)
    return field[tuple(pieces)]

def central(field, axis_id):
    return 0.5 * (neighbour_slice(field, axis_id, 1) - neighbour_slice(field, axis_id, -1))

def les_terms(padded_vel, padded_visc):
    comp_x, comp_y, comp_z = (padded_vel[0], padded_vel[1], padded_vel[2])
    vort_x = central(comp_z, 1) - central(comp_y, 2)
    vort_y = central(comp_x, 2) - central(comp_z, 0)
    vort_z = central(comp_y, 0) - central(comp_x, 1)
    centre = [neighbour_slice(padded_vel[comp], 0, 0) for comp in range(3)]
    lamb = jnp.stack([vort_y * centre[2] - vort_z * centre[1], vort_z * centre[0] - vort_x * centre[2], vort_x * centre[1] - vort_y * centre[0]])
    visc_centre = neighbour_slice(padded_visc, 0, 0)
    terms = []
    for comp in range(3):
        field = padded_vel[comp]
        middle = centre[comp]
        total = jnp.zeros_like(middle)
        for axis_id in range(3):
            upper = 0.5 * (visc_centre + neighbour_slice(padded_visc, axis_id, 1))
            lower = 0.5 * (visc_centre + neighbour_slice(padded_visc, axis_id, -1))
            total = total + upper * (neighbour_slice(field, axis_id, 1) - middle) - lower * (middle - neighbour_slice(field, axis_id, -1))
        terms.append(total)
    new_vel = jnp.stack(centre) + TIME_STEP_LES * (jnp.stack(terms) - lamb)
    return (new_vel, lamb)

def project(lamb, projection):
    size_x, size_y, size_z = (lamb.shape[1], lamb.shape[2], lamb.shape[3])
    blocks = lamb.astype(jnp.bfloat16).reshape(3, size_x // 8, 8, size_y // 8, 8, size_z // 8, 8)
    blocks = blocks.transpose(2, 4, 6, 0, 1, 3, 5).reshape(512, -1)
    source = jnp.dot(projection, blocks, preferred_element_type=jnp.float32)
    source = source.reshape(125, 3, size_x // 8, size_y // 8, size_z // 8).transpose(1, 0, 2, 3, 4)
    return source.reshape(3, 5, 5, 5, size_x // 8, size_y // 8, size_z // 8)

def face_sequence(state, axis_id):
    low_face = jnp.take(state, 0, axis=1 + axis_id)
    high_face = jnp.take(state, 4, axis=1 + axis_id)
    paired = jnp.stack([low_face, high_face], axis=4 + axis_id)
    shape = list(low_face.shape)
    shape[3 + axis_id] = shape[3 + axis_id] * 2
    return paired.reshape(shape)

def face_neighbours(extended, axis_pos, count):
    other_low = lax.slice_in_dim(extended, 0, 2 * count, 2, axis_pos)
    other_high = lax.slice_in_dim(extended, 3, 2 * count + 2, 2, axis_pos)
    return (other_low, other_high)

def along(field, axis_id):
    dmat = jnp.asarray(gll_derivative(), dtype=jnp.float32)
    moved = jnp.tensordot(dmat, field, axes=([1], [axis_id]), precision=lax.Precision.HIGHEST)
    return jnp.moveaxis(moved, 0, axis_id)

def dg_rate(state, source, neighbours):
    pressure = state[0]
    rate_p = -GEOMETRY * (along(state[1], 0) + along(state[2], 1) + along(state[3], 2))
    rate_u = [-GEOMETRY * along(pressure, comp) - source[comp] for comp in range(3)]
    rate = jnp.stack([rate_p] + rate_u)
    for axis_id in range(3):
        other_low, other_high = neighbours[axis_id]
        for normal_sign, node_at, other_face in ((-1.0, 0, other_low), (1.0, 4, other_high)):
            own_face = jnp.take(state, node_at, axis=1 + axis_id)
            corr_p = LIFT_FACTOR * 0.5 * (normal_sign * (own_face[1 + axis_id] - other_face[1 + axis_id]) + (other_face[0] - own_face[0]))
            corr_u = LIFT_FACTOR * 0.5 * (other_face[1:] - own_face[1:])
            corr_u = corr_u.at[axis_id].add(LIFT_FACTOR * 0.5 * normal_sign * (own_face[0] - other_face[0]))
            correction = jnp.concatenate([corr_p[None], corr_u], axis=0)
            rate = rate.at[(slice(None),) * (1 + axis_id) + (node_at,)].add(correction)
    return rate

def reference(velocity, eddy_visc, projection, acoustic_state, route_send, route_place):
    vel = velocity
    lamb = None
    for turn in range(LES_SECTIONS):
        padded_vel = jnp.pad(vel, ((0, 0), (1, 1), (1, 1), (1, 1)))
        padded_visc = jnp.pad(eddy_visc, 1)
        vel, lamb = les_terms(padded_vel, padded_visc)
    source = project(lamb, projection)
    block_x, block_y, block_z = (CX // 8, CY // 8, CZ // 8)
    positions = jnp.arange(ELEMS, dtype=jnp.int32)
    owners = positions // ELEM_DEV
    slot_ids = route_place.reshape(-1).astype(jnp.int32)
    homes = slot_ids // CAP
    within = slot_ids % CAP
    local_block = route_send[homes, owners, within]
    home_index = (homes * ELEM_DEV + local_block).astype(jnp.int32)
    flat = acoustic_state.reshape(500, ELEMS)
    home_flat = jnp.zeros_like(flat).at[:, home_index].set(flat)
    state = home_flat.reshape(500, N_FLOW, N_GRP, block_x, block_y, block_z).transpose(0, 1, 3, 2, 4, 5)
    state = state.reshape(4, 5, 5, 5, N_FLOW * block_x, N_GRP * block_y, block_z)
    for turn in range(AC_SECTIONS):
        neighbours = []
        for axis_id in range(3):
            sequence = face_sequence(state, axis_id)
            widths = [(0, 0)] * 6
            widths[3 + axis_id] = (1, 1)
            extended = jnp.pad(sequence, widths)
            neighbours.append(face_neighbours(extended, 3 + axis_id, state.shape[4 + axis_id]))
        state = state + TIME_STEP_ACOUSTIC * dg_rate(state, source, neighbours)
    back = state.reshape(500, N_FLOW, block_x, N_GRP, block_y, block_z).transpose(0, 1, 3, 2, 4, 5).reshape(500, ELEMS)
    acoustic_out = back[:, home_index].reshape(4, 125, ELEMS)
    return (vel, acoustic_out)
```

```python
import math

import jax
import jax.numpy as jnp
import numpy as np
from jax import lax
from jax.experimental import pallas as pl
from jax.experimental.pallas import tpu as pltpu
from jax.sharding import PartitionSpec as P

LES_SECTIONS = 2
AC_SECTIONS = 2


TIME_STEP_LES = 0.15
TIME_STEP_ACOUSTIC = 0.02
GEOMETRY = 2.0
LIFT_FACTOR = 20.0
HIGH = lax.Precision.HIGHEST


def gll_derivative():
    gll_nodes = np.array([-1.0, -math.sqrt(3.0 / 7.0), 0.0, math.sqrt(3.0 / 7.0), 1.0])
    bary_weights = np.array(
        [
            1.0
            / np.prod([gll_nodes[first] - gll_nodes[other] for other in range(5) if other != first])
            for first in range(5)
        ]
    )
    matrix = np.zeros((5, 5))
    for row_id in range(5):
        for col_id in range(5):
            if row_id != col_id:
                matrix[row_id, col_id] = (
                    bary_weights[col_id]
                    / bary_weights[row_id]
                    / (gll_nodes[row_id] - gll_nodes[col_id])
                )
    for row_id in range(5):
        matrix[row_id, row_id] = -matrix[row_id].sum()
    return matrix


def node_id(coords):
    return coords[0] * 25 + coords[1] * 5 + coords[2]


def face_nodes(dim, at):
    ids = []
    for first in range(5):
        for second in range(5):
            coords = [first, second]
            coords.insert(dim, at)
            ids.append(node_id(coords))
    return ids


def dg_matrices():
    dmat = gll_derivative()
    own = np.zeros((500, 500))
    for a in range(5):
        for b in range(5):
            for c in range(5):
                row = node_id((a, b, c))
                pos = (a, b, c)
                for dim in range(3):
                    for k in range(5):
                        col_pos = list(pos)
                        col_pos[dim] = k
                        col = node_id(col_pos)
                        weight = -GEOMETRY * dmat[pos[dim], k]
                        own[row, (1 + dim) * 125 + col] += weight
                        own[(1 + dim) * 125 + row, col] += weight
    half = LIFT_FACTOR * 0.5
    other = np.zeros((500, 600))
    face_order = []
    for dim in range(3):
        for sign, at in ((-1.0, 0), (1.0, 4)):
            face_order.append((dim, sign, at))
    for slot, (dim, sign, at) in enumerate(face_order):
        for t, node in enumerate(face_nodes(dim, at)):
            col = lambda comp: slot * 100 + comp * 25 + t
            own[node, (1 + dim) * 125 + node] += half * sign
            own[node, node] += -half
            other[node, col(1 + dim)] += -half * sign
            other[node, col(0)] += half
            for k in range(3):
                own[(1 + k) * 125 + node, (1 + k) * 125 + node] += -half
                other[(1 + k) * 125 + node, col(1 + k)] += half
            own[(1 + dim) * 125 + node, node] += half * sign
            other[(1 + dim) * 125 + node, col(0)] += -half * sign
    return own.astype(np.float32), other.astype(np.float32)


def face_rows(state, dim, at):
    elems = state.shape[-1]
    cube = state.reshape(4, 5, 5, 5, elems)
    face = lax.index_in_dim(cube, at, axis=1 + dim, keepdims=False)
    return face.reshape(100, elems)


def les_kernel(want_lamb, vel_ref, nu_ref, vxlo_ref, vxhi_ref, vylo_ref, vyhi_ref,
               nxlo_ref, nxhi_ref, nylo_ref, nyhi_ref, out_ref, *rest):
    size_x, size_y, size_z = vel_ref.shape[1], vel_ref.shape[2], vel_ref.shape[3]
    row = lax.broadcasted_iota(jnp.int32, (size_y, size_z), 0)
    lane = lax.broadcasted_iota(jnp.int32, (size_y, size_z), 1)

    def yp(f, halo):
        return jnp.where(row == size_y - 1, halo, pltpu.roll(f, size_y - 1, 0))

    def ym(f, halo):
        return jnp.where(row == 0, halo, pltpu.roll(f, 1, 0))

    def zp(f):
        return jnp.where(lane == size_z - 1, 0.0, pltpu.roll(f, size_z - 1, 1))

    def zm(f):
        return jnp.where(lane == 0, 0.0, pltpu.roll(f, 1, 1))

    def step(x, carry):
        lo = jnp.maximum(x - 1, 0)
        hi = jnp.minimum(x + 1, size_x - 1)
        u = [vel_ref[c, x] for c in range(3)]
        uxm = [jnp.where(x == 0, vxlo_ref[c], vel_ref[c, lo]) for c in range(3)]
        uxp = [jnp.where(x == size_x - 1, vxhi_ref[c], vel_ref[c, hi]) for c in range(3)]
        uym = [ym(u[c], vylo_ref[c, x]) for c in range(3)]
        uyp = [yp(u[c], vyhi_ref[c, x]) for c in range(3)]
        uzm = [zm(u[c]) for c in range(3)]
        uzp = [zp(u[c]) for c in range(3)]
        nu = nu_ref[x]
        nxm = jnp.where(x == 0, nxlo_ref[...], nu_ref[lo])
        nxp = jnp.where(x == size_x - 1, nxhi_ref[...], nu_ref[hi])
        nym = ym(nu, nylo_ref[x])
        nyp = yp(nu, nyhi_ref[x])
        nzm = zm(nu)
        nzp = zp(nu)
        plus = (uxp, uyp, uzp)
        minus = (uxm, uym, uzm)

        def d(c, axis):
            return 0.5 * (plus[axis][c] - minus[axis][c])

        wx = d(2, 1) - d(1, 2)
        wy = d(0, 2) - d(2, 0)
        wz = d(1, 0) - d(0, 1)
        lamb = (wy * u[2] - wz * u[1], wz * u[0] - wx * u[2], wx * u[1] - wy * u[0])
        ups = (0.5 * (nu + nxp), 0.5 * (nu + nyp), 0.5 * (nu + nzp))
        downs = (0.5 * (nu + nxm), 0.5 * (nu + nym), 0.5 * (nu + nzm))
        for c in range(3):
            total = None
            for axis in range(3):
                term = ups[axis] * (plus[axis][c] - u[c]) - downs[axis] * (u[c] - minus[axis][c])
                total = term if total is None else total + term
            out_ref[c, x] = u[c] + TIME_STEP_LES * (total - lamb[c])
            if want_lamb:
                rest[0][c, x] = lamb[c].astype(rest[0].dtype)
        return carry

    lax.fori_loop(0, size_x, step, 0)


def les_section(vel, nu, vhalo, nhalo, want_lamb):
    out_shape = [jax.ShapeDtypeStruct(vel.shape, jnp.float32)]
    if want_lamb:
        out_shape.append(jax.ShapeDtypeStruct(vel.shape, jnp.bfloat16))
    res = pl.pallas_call(
        lambda *refs: les_kernel(want_lamb, *refs),
        out_shape=tuple(out_shape),
    )(vel, nu, *vhalo, *nhalo)
    return res


def halos(field, lead):
    flow_n = lax.axis_size("flow")
    grp_n = lax.axis_size("grp")
    up_f = [(i, i + 1) for i in range(flow_n - 1)]
    down_f = [(i + 1, i) for i in range(flow_n - 1)]
    up_g = [(i, i + 1) for i in range(grp_n - 1)]
    down_g = [(i + 1, i) for i in range(grp_n - 1)]
    size_x, size_y = field.shape[lead], field.shape[lead + 1]
    xlo = lax.ppermute(lax.index_in_dim(field, size_x - 1, lead, keepdims=False), "flow", up_f)
    xhi = lax.ppermute(lax.index_in_dim(field, 0, lead, keepdims=False), "flow", down_f)
    ylo = lax.ppermute(lax.slice_in_dim(field, size_y - 1, size_y, axis=lead + 1), "grp", up_g)
    yhi = lax.ppermute(lax.slice_in_dim(field, 0, 1, axis=lead + 1), "grp", down_g)
    return xlo, xhi, ylo, yhi


def project(lamb, projection):
    size_x, size_y, size_z = (lamb.shape[1], lamb.shape[2], lamb.shape[3])
    blocks = lamb.reshape(3, size_x // 8, 8, size_y // 8, 8, size_z // 8, 8)
    blocks = blocks.transpose(2, 4, 6, 0, 1, 3, 5).reshape(512, -1)
    source = jnp.dot(projection, blocks, preferred_element_type=jnp.float32)
    source = source.reshape(125, 3, -1).transpose(1, 0, 2)
    return source.reshape(375, -1)


def body(velocity, eddy_visc, projection, acoustic_state, route_send, route_place):
    nhalo = halos(eddy_visc, 0)
    vel = velocity
    lamb = None
    for turn in range(LES_SECTIONS):
        vhalo = halos(vel, 1)
        last = turn == LES_SECTIONS - 1
        res = les_section(vel, eddy_visc, vhalo, nhalo, last)
        vel = res[0]
        if last:
            lamb = res[1]
    source = project(lamb, projection)
    flow_size = lax.axis_size("flow")
    grp_size = lax.axis_size("grp")
    slot_cap = route_send.shape[2]
    elem_count = acoustic_state.shape[2]
    total_slots = flow_size * grp_size * slot_cap
    placing = route_place.reshape(-1)
    outgoing = (
        jnp.zeros((500, total_slots), jnp.float32)
        .at[:, placing]
        .set(acoustic_state.reshape(500, elem_count))
    )
    arrived = lax.all_to_all(outgoing, ("flow", "grp"), split_axis=1, concat_axis=1, tiled=True)
    sending = route_send.reshape(-1)
    filled = sending >= 0
    target = jnp.where(filled, sending, elem_count)
    state = jnp.zeros((500, elem_count), jnp.float32).at[:, target].set(arrived, mode="drop")

    block_y = velocity.shape[2] // 8
    block_z = velocity.shape[3] // 8
    own_np, other_np = dg_matrices()
    own_mat = jnp.asarray(own_np)
    other_mat = jnp.asarray(other_np)
    src_full = jnp.concatenate([jnp.zeros((125, elem_count), jnp.float32), source], axis=0)
    lane = lax.broadcasted_iota(jnp.int32, (1, elem_count), 1)
    ez = lane % block_z
    flow_n = lax.axis_size("flow")
    grp_n = lax.axis_size("grp")
    up_f = [(i, i + 1) for i in range(flow_n - 1)]
    down_f = [(i + 1, i) for i in range(flow_n - 1)]
    up_g = [(i, i + 1) for i in range(grp_n - 1)]
    down_g = [(i + 1, i) for i in range(grp_n - 1)]
    row_len = block_z
    for turn in range(AC_SECTIONS):
        fx0 = face_rows(state, 0, 0)
        fx4 = face_rows(state, 0, 4)
        fy0 = face_rows(state, 1, 0)
        fy4 = face_rows(state, 1, 4)
        fz0 = face_rows(state, 2, 0)
        fz4 = face_rows(state, 2, 4)
        oxlo = lax.ppermute(fx4, "flow", up_f)
        oxhi = lax.ppermute(fx0, "flow", down_f)
        ylo_recv = lax.ppermute(fy4[:, elem_count - row_len:], "grp", up_g)
        yhi_recv = lax.ppermute(fy0[:, :row_len], "grp", down_g)
        oylo = jnp.concatenate([ylo_recv, fy4[:, : elem_count - row_len]], axis=1)
        oyhi = jnp.concatenate([fy0[:, row_len:], yhi_recv], axis=1)
        zero_col = jnp.zeros((100, 1), jnp.float32)
        ozlo = jnp.where(ez == 0, 0.0, jnp.concatenate([zero_col, fz4[:, :-1]], axis=1))
        ozhi = jnp.where(ez == block_z - 1, 0.0, jnp.concatenate([fz0[:, 1:], zero_col], axis=1))
        others = jnp.concatenate([oxlo, oxhi, oylo, oyhi, ozlo, ozhi], axis=0)
        rate = (
            jnp.dot(own_mat, state, precision=HIGH)
            + jnp.dot(other_mat, others, precision=HIGH)
            - src_full
        )
        state = state + TIME_STEP_ACOUSTIC * rate
    flat_state = state
    leaving = jnp.where(filled[None, :], flat_state[:, jnp.where(filled, sending, 0)], 0.0)
    returned = lax.all_to_all(leaving, ("flow", "grp"), split_axis=1, concat_axis=1, tiled=True)
    acoustic_out = returned[:, placing].reshape(4, 125, elem_count)
    return (vel, acoustic_out)


def solution(mesh):
    placed = (
        P(None, "flow", "grp", None),
        P("flow", "grp", None),
        P(),
        P(None, None, ("flow", "grp")),
        P(("flow", "grp"), None, None),
        P(("flow", "grp"), None),
    )
    return jax.shard_map(
        body,
        mesh=mesh,
        in_specs=placed,
        out_specs=(P(None, "flow", "grp", None), P(None, None, ("flow", "grp"))),
        check_vma=False,
    )
```

```python
import math

import jax
import jax.numpy as jnp
import numpy as np
from jax import lax
from jax.experimental import pallas as pl
from jax.experimental.pallas import tpu as pltpu
from jax.sharding import PartitionSpec as P

LES_SECTIONS = 2
AC_SECTIONS = 2


TIME_STEP_LES = 0.15
TIME_STEP_ACOUSTIC = 0.02
GEOMETRY = 2.0
LIFT_FACTOR = 20.0
HIGH = lax.Precision.HIGHEST


def gll_derivative():
    gll_nodes = np.array([-1.0, -math.sqrt(3.0 / 7.0), 0.0, math.sqrt(3.0 / 7.0), 1.0])
    bary_weights = np.array(
        [
            1.0
            / np.prod([gll_nodes[first] - gll_nodes[other] for other in range(5) if other != first])
            for first in range(5)
        ]
    )
    matrix = np.zeros((5, 5))
    for row_id in range(5):
        for col_id in range(5):
            if row_id != col_id:
                matrix[row_id, col_id] = (
                    bary_weights[col_id]
                    / bary_weights[row_id]
                    / (gll_nodes[row_id] - gll_nodes[col_id])
                )
    for row_id in range(5):
        matrix[row_id, row_id] = -matrix[row_id].sum()
    return matrix


def node_id(coords):
    return coords[0] * 25 + coords[1] * 5 + coords[2]


def face_nodes(dim, at):
    ids = []
    for first in range(5):
        for second in range(5):
            coords = [first, second]
            coords.insert(dim, at)
            ids.append(node_id(coords))
    return ids


def dg_matrices():
    dmat = gll_derivative()
    own = np.zeros((500, 500))
    for a in range(5):
        for b in range(5):
            for c in range(5):
                row = node_id((a, b, c))
                pos = (a, b, c)
                for dim in range(3):
                    for k in range(5):
                        col_pos = list(pos)
                        col_pos[dim] = k
                        col = node_id(col_pos)
                        weight = -GEOMETRY * dmat[pos[dim], k]
                        own[row, (1 + dim) * 125 + col] += weight
                        own[(1 + dim) * 125 + row, col] += weight
    half = LIFT_FACTOR * 0.5
    other = np.zeros((500, 600))
    face_order = []
    for dim in range(3):
        for sign, at in ((-1.0, 0), (1.0, 4)):
            face_order.append((dim, sign, at))
    for slot, (dim, sign, at) in enumerate(face_order):
        for t, node in enumerate(face_nodes(dim, at)):
            col = lambda comp: slot * 100 + comp * 25 + t
            own[node, (1 + dim) * 125 + node] += half * sign
            own[node, node] += -half
            other[node, col(1 + dim)] += -half * sign
            other[node, col(0)] += half
            for k in range(3):
                own[(1 + k) * 125 + node, (1 + k) * 125 + node] += -half
                other[(1 + k) * 125 + node, col(1 + k)] += half
            own[(1 + dim) * 125 + node, node] += half * sign
            other[(1 + dim) * 125 + node, col(0)] += -half * sign
    return own.astype(np.float32), other.astype(np.float32)


def face_rows(state, dim, at):
    elems = state.shape[-1]
    cube = state.reshape(4, 5, 5, 5, elems)
    face = lax.index_in_dim(cube, at, axis=1 + dim, keepdims=False)
    return face.reshape(100, elems)


def les_kernel(want_lamb, vel_ref, nu_ref, vxlo_ref, vxhi_ref, vylo_ref, vyhi_ref,
               nxlo_ref, nxhi_ref, nylo_ref, nyhi_ref, out_ref, *rest):
    size_x, size_y, size_z = vel_ref.shape[1], vel_ref.shape[2], vel_ref.shape[3]
    row = lax.broadcasted_iota(jnp.int32, (size_y, size_z), 0)
    lane = lax.broadcasted_iota(jnp.int32, (size_y, size_z), 1)

    def yp(f, halo):
        return jnp.where(row == size_y - 1, halo, pltpu.roll(f, size_y - 1, 0))

    def ym(f, halo):
        return jnp.where(row == 0, halo, pltpu.roll(f, 1, 0))

    def zp(f):
        return jnp.where(lane == size_z - 1, 0.0, pltpu.roll(f, size_z - 1, 1))

    def zm(f):
        return jnp.where(lane == 0, 0.0, pltpu.roll(f, 1, 1))

    def step(x, carry):
        lo = jnp.maximum(x - 1, 0)
        hi = jnp.minimum(x + 1, size_x - 1)
        u = [vel_ref[c, x] for c in range(3)]
        uxm = [jnp.where(x == 0, vxlo_ref[c], vel_ref[c, lo]) for c in range(3)]
        uxp = [jnp.where(x == size_x - 1, vxhi_ref[c], vel_ref[c, hi]) for c in range(3)]
        uym = [ym(u[c], vylo_ref[c, x]) for c in range(3)]
        uyp = [yp(u[c], vyhi_ref[c, x]) for c in range(3)]
        uzm = [zm(u[c]) for c in range(3)]
        uzp = [zp(u[c]) for c in range(3)]
        nu = nu_ref[x]
        nxm = jnp.where(x == 0, nxlo_ref[...], nu_ref[lo])
        nxp = jnp.where(x == size_x - 1, nxhi_ref[...], nu_ref[hi])
        nym = ym(nu, nylo_ref[x])
        nyp = yp(nu, nyhi_ref[x])
        nzm = zm(nu)
        nzp = zp(nu)
        plus = (uxp, uyp, uzp)
        minus = (uxm, uym, uzm)

        def d(c, axis):
            return 0.5 * (plus[axis][c] - minus[axis][c])

        wx = d(2, 1) - d(1, 2)
        wy = d(0, 2) - d(2, 0)
        wz = d(1, 0) - d(0, 1)
        lamb = (wy * u[2] - wz * u[1], wz * u[0] - wx * u[2], wx * u[1] - wy * u[0])
        ups = (0.5 * (nu + nxp), 0.5 * (nu + nyp), 0.5 * (nu + nzp))
        downs = (0.5 * (nu + nxm), 0.5 * (nu + nym), 0.5 * (nu + nzm))
        for c in range(3):
            total = None
            for axis in range(3):
                term = ups[axis] * (plus[axis][c] - u[c]) - downs[axis] * (u[c] - minus[axis][c])
                total = term if total is None else total + term
            out_ref[c, x] = u[c] + TIME_STEP_LES * (total - lamb[c])
            if want_lamb:
                rest[0][c, x] = lamb[c].astype(rest[0].dtype)
        return carry

    lax.fori_loop(0, size_x, step, 0)


def les_section(vel, nu, vhalo, nhalo, want_lamb):
    out_shape = [jax.ShapeDtypeStruct(vel.shape, jnp.float32)]
    if want_lamb:
        out_shape.append(jax.ShapeDtypeStruct(vel.shape, jnp.bfloat16))
    res = pl.pallas_call(
        lambda *refs: les_kernel(want_lamb, *refs),
        out_shape=tuple(out_shape),
    )(vel, nu, *vhalo, *nhalo)
    return res


def halos(field, lead):
    flow_n = lax.axis_size("flow")
    grp_n = lax.axis_size("grp")
    up_f = [(i, i + 1) for i in range(flow_n - 1)]
    down_f = [(i + 1, i) for i in range(flow_n - 1)]
    up_g = [(i, i + 1) for i in range(grp_n - 1)]
    down_g = [(i + 1, i) for i in range(grp_n - 1)]
    size_x, size_y = field.shape[lead], field.shape[lead + 1]
    xlo = lax.ppermute(lax.index_in_dim(field, size_x - 1, lead, keepdims=False), "flow", up_f)
    xhi = lax.ppermute(lax.index_in_dim(field, 0, lead, keepdims=False), "flow", down_f)
    ylo = lax.ppermute(lax.slice_in_dim(field, size_y - 1, size_y, axis=lead + 1), "grp", up_g)
    yhi = lax.ppermute(lax.slice_in_dim(field, 0, 1, axis=lead + 1), "grp", down_g)
    return xlo, xhi, ylo, yhi


def project(lamb, projection):
    size_x, size_y, size_z = (lamb.shape[1], lamb.shape[2], lamb.shape[3])
    blocks = lamb.reshape(3, size_x // 8, 8, size_y // 8, 8, size_z // 8, 8)
    blocks = blocks.transpose(2, 4, 6, 0, 1, 3, 5).reshape(512, -1)
    source = jnp.dot(projection, blocks, preferred_element_type=jnp.float32)
    source = source.reshape(125, 3, -1).transpose(1, 0, 2)
    return source.reshape(375, -1)


def two_stage_all_to_all(value, flow_size, grp_size):
    rows, cols = value.shape
    cube = value.reshape(rows, flow_size, grp_size, cols // (flow_size * grp_size))
    cube = lax.all_to_all(cube, "grp", split_axis=2, concat_axis=2, tiled=True)
    cube = lax.all_to_all(cube, "flow", split_axis=1, concat_axis=1, tiled=True)
    return cube.reshape(rows, cols)


def body(velocity, eddy_visc, projection, acoustic_state, route_send, route_place):
    vel = velocity
    lamb = None
    nhalo = None
    for turn in range(LES_SECTIONS):
        last = turn == LES_SECTIONS - 1
        if nhalo is None:
            joint = halos(jnp.concatenate([vel, eddy_visc[None]], axis=0), 1)
            vhalo = [part[:3] for part in joint]
            nhalo = [part[3] for part in joint]
        else:
            vhalo = halos(vel, 1)
        res = les_section(vel, eddy_visc, vhalo, nhalo, last)
        vel = res[0]
        if last:
            lamb = res[1]
    source = project(lamb, projection)
    flow_size = lax.axis_size("flow")
    grp_size = lax.axis_size("grp")
    slot_cap = route_send.shape[2]
    elem_count = acoustic_state.shape[2]
    total_slots = flow_size * grp_size * slot_cap
    placing = route_place.reshape(-1)
    outgoing = (
        jnp.zeros((500, total_slots), jnp.float32)
        .at[:, placing]
        .set(acoustic_state.reshape(500, elem_count))
    )
    arrived = two_stage_all_to_all(outgoing, flow_size, grp_size)
    sending = route_send.reshape(-1)
    filled = sending >= 0
    target = jnp.where(filled, sending, elem_count)
    state = jnp.zeros((500, elem_count), jnp.float32).at[:, target].set(arrived, mode="drop")

    block_y = velocity.shape[2] // 8
    block_z = velocity.shape[3] // 8
    own_np, other_np = dg_matrices()
    own_mat = jnp.asarray(own_np)
    other_mat = jnp.asarray(other_np)
    src_full = jnp.concatenate([jnp.zeros((125, elem_count), jnp.float32), source], axis=0)
    lane = lax.broadcasted_iota(jnp.int32, (1, elem_count), 1)
    ez = lane % block_z
    flow_n = lax.axis_size("flow")
    grp_n = lax.axis_size("grp")
    up_f = [(i, i + 1) for i in range(flow_n - 1)]
    down_f = [(i + 1, i) for i in range(flow_n - 1)]
    up_g = [(i, i + 1) for i in range(grp_n - 1)]
    down_g = [(i + 1, i) for i in range(grp_n - 1)]
    row_len = block_z
    for turn in range(AC_SECTIONS):
        fx0 = face_rows(state, 0, 0)
        fx4 = face_rows(state, 0, 4)
        fy0 = face_rows(state, 1, 0)
        fy4 = face_rows(state, 1, 4)
        fz0 = face_rows(state, 2, 0)
        fz4 = face_rows(state, 2, 4)
        oxlo = lax.ppermute(fx4, "flow", up_f)
        oxhi = lax.ppermute(fx0, "flow", down_f)
        ylo_recv = lax.ppermute(fy4[:, elem_count - row_len:], "grp", up_g)
        yhi_recv = lax.ppermute(fy0[:, :row_len], "grp", down_g)
        oylo = jnp.concatenate([ylo_recv, fy4[:, : elem_count - row_len]], axis=1)
        oyhi = jnp.concatenate([fy0[:, row_len:], yhi_recv], axis=1)
        zero_col = jnp.zeros((100, 1), jnp.float32)
        ozlo = jnp.where(ez == 0, 0.0, jnp.concatenate([zero_col, fz4[:, :-1]], axis=1))
        ozhi = jnp.where(ez == block_z - 1, 0.0, jnp.concatenate([fz0[:, 1:], zero_col], axis=1))
        others = jnp.concatenate([oxlo, oxhi, oylo, oyhi, ozlo, ozhi], axis=0)
        rate = (
            jnp.dot(own_mat, state, precision=HIGH)
            + jnp.dot(other_mat, others, precision=HIGH)
            - src_full
        )
        state = state + TIME_STEP_ACOUSTIC * rate
    flat_state = state
    leaving = jnp.where(filled[None, :], flat_state[:, jnp.where(filled, sending, 0)], 0.0)
    returned = two_stage_all_to_all(leaving, flow_size, grp_size)
    acoustic_out = returned[:, placing].reshape(4, 125, elem_count)
    return (vel, acoustic_out)


def solution(mesh):
    placed = (
        P(None, "flow", "grp", None),
        P("flow", "grp", None),
        P(),
        P(None, None, ("flow", "grp")),
        P(("flow", "grp"), None, None),
        P(("flow", "grp"), None),
    )
    return jax.shard_map(
        body,
        mesh=mesh,
        in_specs=placed,
        out_specs=(P(None, "flow", "grp", None), P(None, None, ("flow", "grp"))),
        check_vma=False,
    )
```

```python
import math

import jax
import jax.numpy as jnp
import numpy as np
from jax import lax
from jax.experimental import pallas as pl
from jax.experimental.pallas import tpu as pltpu
from jax.sharding import PartitionSpec as P

LES_SECTIONS = 2
AC_SECTIONS = 2


TIME_STEP_LES = 0.15
TIME_STEP_ACOUSTIC = 0.02
GEOMETRY = 2.0
LIFT_FACTOR = 20.0
HIGH = lax.Precision.HIGHEST


def gll_derivative():
    gll_nodes = np.array([-1.0, -math.sqrt(3.0 / 7.0), 0.0, math.sqrt(3.0 / 7.0), 1.0])
    bary_weights = np.array(
        [
            1.0
            / np.prod([gll_nodes[first] - gll_nodes[other] for other in range(5) if other != first])
            for first in range(5)
        ]
    )
    matrix = np.zeros((5, 5))
    for row_id in range(5):
        for col_id in range(5):
            if row_id != col_id:
                matrix[row_id, col_id] = (
                    bary_weights[col_id]
                    / bary_weights[row_id]
                    / (gll_nodes[row_id] - gll_nodes[col_id])
                )
    for row_id in range(5):
        matrix[row_id, row_id] = -matrix[row_id].sum()
    return matrix


def node_id(coords):
    return coords[0] * 25 + coords[1] * 5 + coords[2]


def face_nodes(dim, at):
    ids = []
    for first in range(5):
        for second in range(5):
            coords = [first, second]
            coords.insert(dim, at)
            ids.append(node_id(coords))
    return ids


def dg_matrices():
    dmat = gll_derivative()
    own = np.zeros((500, 500))
    for a in range(5):
        for b in range(5):
            for c in range(5):
                row = node_id((a, b, c))
                pos = (a, b, c)
                for dim in range(3):
                    for k in range(5):
                        col_pos = list(pos)
                        col_pos[dim] = k
                        col = node_id(col_pos)
                        weight = -GEOMETRY * dmat[pos[dim], k]
                        own[row, (1 + dim) * 125 + col] += weight
                        own[(1 + dim) * 125 + row, col] += weight
    half = LIFT_FACTOR * 0.5
    other = np.zeros((500, 600))
    face_order = []
    for dim in range(3):
        for sign, at in ((-1.0, 0), (1.0, 4)):
            face_order.append((dim, sign, at))
    for slot, (dim, sign, at) in enumerate(face_order):
        for t, node in enumerate(face_nodes(dim, at)):
            col = lambda comp: slot * 100 + comp * 25 + t
            own[node, (1 + dim) * 125 + node] += half * sign
            own[node, node] += -half
            other[node, col(1 + dim)] += -half * sign
            other[node, col(0)] += half
            for k in range(3):
                own[(1 + k) * 125 + node, (1 + k) * 125 + node] += -half
                other[(1 + k) * 125 + node, col(1 + k)] += half
            own[(1 + dim) * 125 + node, node] += half * sign
            other[(1 + dim) * 125 + node, col(0)] += -half * sign
    return own.astype(np.float32), other.astype(np.float32)


def face_rows(state, dim, at):
    elems = state.shape[-1]
    cube = state.reshape(4, 5, 5, 5, elems)
    face = lax.index_in_dim(cube, at, axis=1 + dim, keepdims=False)
    return face.reshape(100, elems)


def les_kernel(want_lamb, vel_ref, nu_ref, vxlo_ref, vxhi_ref, vylo_ref, vyhi_ref,
               nxlo_ref, nxhi_ref, nylo_ref, nyhi_ref, out_ref, *rest):
    size_x, size_y, size_z = vel_ref.shape[1], vel_ref.shape[2], vel_ref.shape[3]
    row = lax.broadcasted_iota(jnp.int32, (size_y, size_z), 0)
    lane = lax.broadcasted_iota(jnp.int32, (size_y, size_z), 1)

    def yp(f, halo):
        return jnp.where(row == size_y - 1, halo, pltpu.roll(f, size_y - 1, 0))

    def ym(f, halo):
        return jnp.where(row == 0, halo, pltpu.roll(f, 1, 0))

    def zp(f):
        return jnp.where(lane == size_z - 1, 0.0, pltpu.roll(f, size_z - 1, 1))

    def zm(f):
        return jnp.where(lane == 0, 0.0, pltpu.roll(f, 1, 1))

    def step(x, carry):
        lo = jnp.maximum(x - 1, 0)
        hi = jnp.minimum(x + 1, size_x - 1)
        u = [vel_ref[c, x] for c in range(3)]
        uxm = [jnp.where(x == 0, vxlo_ref[c], vel_ref[c, lo]) for c in range(3)]
        uxp = [jnp.where(x == size_x - 1, vxhi_ref[c], vel_ref[c, hi]) for c in range(3)]
        uym = [ym(u[c], vylo_ref[c, x]) for c in range(3)]
        uyp = [yp(u[c], vyhi_ref[c, x]) for c in range(3)]
        uzm = [zm(u[c]) for c in range(3)]
        uzp = [zp(u[c]) for c in range(3)]
        nu = nu_ref[x]
        nxm = jnp.where(x == 0, nxlo_ref[...], nu_ref[lo])
        nxp = jnp.where(x == size_x - 1, nxhi_ref[...], nu_ref[hi])
        nym = ym(nu, nylo_ref[x])
        nyp = yp(nu, nyhi_ref[x])
        nzm = zm(nu)
        nzp = zp(nu)
        plus = (uxp, uyp, uzp)
        minus = (uxm, uym, uzm)

        def d(c, axis):
            return 0.5 * (plus[axis][c] - minus[axis][c])

        wx = d(2, 1) - d(1, 2)
        wy = d(0, 2) - d(2, 0)
        wz = d(1, 0) - d(0, 1)
        lamb = (wy * u[2] - wz * u[1], wz * u[0] - wx * u[2], wx * u[1] - wy * u[0])
        ups = (0.5 * (nu + nxp), 0.5 * (nu + nyp), 0.5 * (nu + nzp))
        downs = (0.5 * (nu + nxm), 0.5 * (nu + nym), 0.5 * (nu + nzm))
        for c in range(3):
            total = None
            for axis in range(3):
                term = ups[axis] * (plus[axis][c] - u[c]) - downs[axis] * (u[c] - minus[axis][c])
                total = term if total is None else total + term
            out_ref[c, x] = u[c] + TIME_STEP_LES * (total - lamb[c])
            if want_lamb:
                rest[0][c, x] = lamb[c].astype(rest[0].dtype)
        return carry

    lax.fori_loop(0, size_x, step, 0)


def les_section(vel, nu, vhalo, nhalo, want_lamb):
    out_shape = [jax.ShapeDtypeStruct(vel.shape, jnp.float32)]
    if want_lamb:
        out_shape.append(jax.ShapeDtypeStruct(vel.shape, jnp.bfloat16))
    res = pl.pallas_call(
        lambda *refs: les_kernel(want_lamb, *refs),
        out_shape=tuple(out_shape),
    )(vel, nu, *vhalo, *nhalo)
    return res


def halos(field, lead):
    flow_n = lax.axis_size("flow")
    grp_n = lax.axis_size("grp")
    up_f = [(i, i + 1) for i in range(flow_n - 1)]
    down_f = [(i + 1, i) for i in range(flow_n - 1)]
    up_g = [(i, i + 1) for i in range(grp_n - 1)]
    down_g = [(i + 1, i) for i in range(grp_n - 1)]
    size_x, size_y = field.shape[lead], field.shape[lead + 1]
    xlo = lax.ppermute(lax.index_in_dim(field, size_x - 1, lead, keepdims=False), "flow", up_f)
    xhi = lax.ppermute(lax.index_in_dim(field, 0, lead, keepdims=False), "flow", down_f)
    ylo = lax.ppermute(lax.slice_in_dim(field, size_y - 1, size_y, axis=lead + 1), "grp", up_g)
    yhi = lax.ppermute(lax.slice_in_dim(field, 0, 1, axis=lead + 1), "grp", down_g)
    return xlo, xhi, ylo, yhi


def project(lamb, projection):
    size_x, size_y, size_z = (lamb.shape[1], lamb.shape[2], lamb.shape[3])
    bx, by, bz = size_x // 8, size_y // 8, size_z // 8
    perm = np.zeros((size_z, size_z), np.float32)
    for ez in range(bz):
        for cz in range(8):
            perm[ez * 8 + cz, cz * bz + ez] = 1.0
    rows = lamb.reshape(-1, size_z)
    moved = jnp.dot(rows, jnp.asarray(perm, jnp.bfloat16), preferred_element_type=jnp.float32)
    moved = moved.astype(jnp.bfloat16)
    blocks = moved.reshape(3, bx, 8, by, 8, 8, bz).transpose(2, 4, 5, 0, 1, 3, 6).reshape(512, -1)
    source = jnp.dot(projection, blocks, preferred_element_type=jnp.float32)
    source = source.reshape(125, 3, -1).transpose(1, 0, 2)
    return source.reshape(375, -1)


def body(velocity, eddy_visc, projection, acoustic_state, route_send, route_place):
    vel = velocity
    lamb = None
    nhalo = None
    for turn in range(LES_SECTIONS):
        last = turn == LES_SECTIONS - 1
        if nhalo is None:
            joint = halos(jnp.concatenate([vel, eddy_visc[None]], axis=0), 1)
            vhalo = [part[:3] for part in joint]
            nhalo = [part[3] for part in joint]
        else:
            vhalo = halos(vel, 1)
        res = les_section(vel, eddy_visc, vhalo, nhalo, last)
        vel = res[0]
        if last:
            lamb = res[1]
    source = project(lamb, projection)
    flow_size = lax.axis_size("flow")
    grp_size = lax.axis_size("grp")
    slot_cap = route_send.shape[2]
    elem_count = acoustic_state.shape[2]
    total_slots = flow_size * grp_size * slot_cap
    placing = route_place.reshape(-1)
    outgoing = (
        jnp.zeros((500, total_slots), jnp.float32)
        .at[:, placing]
        .set(acoustic_state.reshape(500, elem_count))
    )
    arrived = lax.all_to_all(outgoing, ("flow", "grp"), split_axis=1, concat_axis=1, tiled=True)
    sending = route_send.reshape(-1)
    filled = sending >= 0
    target = jnp.where(filled, sending, elem_count)
    state = jnp.zeros((500, elem_count), jnp.float32).at[:, target].set(arrived, mode="drop")

    block_y = velocity.shape[2] // 8
    block_z = velocity.shape[3] // 8
    own_np, other_np = dg_matrices()
    own_mat = jnp.asarray(own_np)
    other_mat = jnp.asarray(other_np)
    src_full = jnp.concatenate([jnp.zeros((125, elem_count), jnp.float32), source], axis=0)
    lane = lax.broadcasted_iota(jnp.int32, (1, elem_count), 1)
    ez = lane % block_z
    flow_n = lax.axis_size("flow")
    grp_n = lax.axis_size("grp")
    up_f = [(i, i + 1) for i in range(flow_n - 1)]
    down_f = [(i + 1, i) for i in range(flow_n - 1)]
    up_g = [(i, i + 1) for i in range(grp_n - 1)]
    down_g = [(i + 1, i) for i in range(grp_n - 1)]
    row_len = block_z
    for turn in range(AC_SECTIONS):
        fx0 = face_rows(state, 0, 0)
        fx4 = face_rows(state, 0, 4)
        fy0 = face_rows(state, 1, 0)
        fy4 = face_rows(state, 1, 4)
        fz0 = face_rows(state, 2, 0)
        fz4 = face_rows(state, 2, 4)
        oxlo = lax.ppermute(fx4, "flow", up_f)
        oxhi = lax.ppermute(fx0, "flow", down_f)
        ylo_recv = lax.ppermute(fy4[:, elem_count - row_len:], "grp", up_g)
        yhi_recv = lax.ppermute(fy0[:, :row_len], "grp", down_g)
        oylo = jnp.concatenate([ylo_recv, fy4[:, : elem_count - row_len]], axis=1)
        oyhi = jnp.concatenate([fy0[:, row_len:], yhi_recv], axis=1)
        zero_col = jnp.zeros((100, 1), jnp.float32)
        ozlo = jnp.where(ez == 0, 0.0, jnp.concatenate([zero_col, fz4[:, :-1]], axis=1))
        ozhi = jnp.where(ez == block_z - 1, 0.0, jnp.concatenate([fz0[:, 1:], zero_col], axis=1))
        others = jnp.concatenate([oxlo, oxhi, oylo, oyhi, ozlo, ozhi], axis=0)
        rate = (
            jnp.dot(own_mat, state, precision=HIGH)
            + jnp.dot(other_mat, others, precision=HIGH)
            - src_full
        )
        state = state + TIME_STEP_ACOUSTIC * rate
    flat_state = state
    leaving = jnp.where(filled[None, :], flat_state[:, jnp.where(filled, sending, 0)], 0.0)
    returned = lax.all_to_all(leaving, ("flow", "grp"), split_axis=1, concat_axis=1, tiled=True)
    acoustic_out = returned[:, placing].reshape(4, 125, elem_count)
    return (vel, acoustic_out)


def solution(mesh):
    placed = (
        P(None, "flow", "grp", None),
        P("flow", "grp", None),
        P(),
        P(None, None, ("flow", "grp")),
        P(("flow", "grp"), None, None),
        P(("flow", "grp"), None),
    )
    return jax.shard_map(
        body,
        mesh=mesh,
        in_specs=placed,
        out_specs=(P(None, "flow", "grp", None), P(None, None, ("flow", "grp"))),
        check_vma=False,
    )
```

```python
import math

import jax
import jax.numpy as jnp
import numpy as np
from jax import lax
from jax.experimental import pallas as pl
from jax.experimental.pallas import tpu as pltpu
from jax.sharding import PartitionSpec as P

LES_SECTIONS = 2
AC_SECTIONS = 2


TIME_STEP_LES = 0.15
TIME_STEP_ACOUSTIC = 0.02
GEOMETRY = 2.0
LIFT_FACTOR = 20.0
HIGH = lax.Precision.HIGHEST


def gll_derivative():
    gll_nodes = np.array([-1.0, -math.sqrt(3.0 / 7.0), 0.0, math.sqrt(3.0 / 7.0), 1.0])
    bary_weights = np.array(
        [
            1.0
            / np.prod([gll_nodes[first] - gll_nodes[other] for other in range(5) if other != first])
            for first in range(5)
        ]
    )
    matrix = np.zeros((5, 5))
    for row_id in range(5):
        for col_id in range(5):
            if row_id != col_id:
                matrix[row_id, col_id] = (
                    bary_weights[col_id]
                    / bary_weights[row_id]
                    / (gll_nodes[row_id] - gll_nodes[col_id])
                )
    for row_id in range(5):
        matrix[row_id, row_id] = -matrix[row_id].sum()
    return matrix


def node_id(coords):
    return coords[0] * 25 + coords[1] * 5 + coords[2]


def face_nodes(dim, at):
    ids = []
    for first in range(5):
        for second in range(5):
            coords = [first, second]
            coords.insert(dim, at)
            ids.append(node_id(coords))
    return ids


def dg_matrices():
    dmat = gll_derivative()
    own = np.zeros((500, 500))
    for a in range(5):
        for b in range(5):
            for c in range(5):
                row = node_id((a, b, c))
                pos = (a, b, c)
                for dim in range(3):
                    for k in range(5):
                        col_pos = list(pos)
                        col_pos[dim] = k
                        col = node_id(col_pos)
                        weight = -GEOMETRY * dmat[pos[dim], k]
                        own[row, (1 + dim) * 125 + col] += weight
                        own[(1 + dim) * 125 + row, col] += weight
    half = LIFT_FACTOR * 0.5
    other = np.zeros((500, 600))
    face_order = []
    for dim in range(3):
        for sign, at in ((-1.0, 0), (1.0, 4)):
            face_order.append((dim, sign, at))
    for slot, (dim, sign, at) in enumerate(face_order):
        for t, node in enumerate(face_nodes(dim, at)):
            col = lambda comp: slot * 100 + comp * 25 + t
            own[node, (1 + dim) * 125 + node] += half * sign
            own[node, node] += -half
            other[node, col(1 + dim)] += -half * sign
            other[node, col(0)] += half
            for k in range(3):
                own[(1 + k) * 125 + node, (1 + k) * 125 + node] += -half
                other[(1 + k) * 125 + node, col(1 + k)] += half
            own[(1 + dim) * 125 + node, node] += half * sign
            other[(1 + dim) * 125 + node, col(0)] += -half * sign
    own_pad = np.zeros((512, 512), np.float32)
    other_pad = np.zeros((512, 768), np.float32)
    for ci in range(4):
        for cj in range(4):
            own_pad[ci * 128:ci * 128 + 125, cj * 128:cj * 128 + 125] = own[ci * 125:(ci + 1) * 125, cj * 125:(cj + 1) * 125]
        for slot in range(6):
            other_pad[ci * 128:ci * 128 + 125, slot * 128:slot * 128 + 100] = other[ci * 125:(ci + 1) * 125, slot * 100:(slot + 1) * 100]
    return own_pad, other_pad


def face_rows(state, dim, at):
    elems = state.shape[-1]
    cube = state.reshape(4, 5, 5, 5, elems)
    face = lax.index_in_dim(cube, at, axis=1 + dim, keepdims=False)
    return face.reshape(100, elems)


def les_kernel(want_lamb, vel_ref, nu_ref, vxlo_ref, vxhi_ref, vylo_ref, vyhi_ref,
               nxlo_ref, nxhi_ref, nylo_ref, nyhi_ref, out_ref, *rest):
    size_x, size_y, size_z = vel_ref.shape[1], vel_ref.shape[2], vel_ref.shape[3]
    row = lax.broadcasted_iota(jnp.int32, (size_y, size_z), 0)
    lane = lax.broadcasted_iota(jnp.int32, (size_y, size_z), 1)

    def yp(f, halo):
        return jnp.where(row == size_y - 1, halo, pltpu.roll(f, size_y - 1, 0))

    def ym(f, halo):
        return jnp.where(row == 0, halo, pltpu.roll(f, 1, 0))

    def zp(f):
        return jnp.where(lane == size_z - 1, 0.0, pltpu.roll(f, size_z - 1, 1))

    def zm(f):
        return jnp.where(lane == 0, 0.0, pltpu.roll(f, 1, 1))

    def step(x, carry):
        lo = jnp.maximum(x - 1, 0)
        hi = jnp.minimum(x + 1, size_x - 1)
        u = [vel_ref[c, x] for c in range(3)]
        uxm = [jnp.where(x == 0, vxlo_ref[c], vel_ref[c, lo]) for c in range(3)]
        uxp = [jnp.where(x == size_x - 1, vxhi_ref[c], vel_ref[c, hi]) for c in range(3)]
        uym = [ym(u[c], vylo_ref[c, x]) for c in range(3)]
        uyp = [yp(u[c], vyhi_ref[c, x]) for c in range(3)]
        uzm = [zm(u[c]) for c in range(3)]
        uzp = [zp(u[c]) for c in range(3)]
        nu = nu_ref[x]
        nxm = jnp.where(x == 0, nxlo_ref[3], nu_ref[lo])
        nxp = jnp.where(x == size_x - 1, nxhi_ref[3], nu_ref[hi])
        nym = ym(nu, nylo_ref[3, x])
        nyp = yp(nu, nyhi_ref[3, x])
        nzm = zm(nu)
        nzp = zp(nu)
        plus = (uxp, uyp, uzp)
        minus = (uxm, uym, uzm)

        def d(c, axis):
            return 0.5 * (plus[axis][c] - minus[axis][c])

        wx = d(2, 1) - d(1, 2)
        wy = d(0, 2) - d(2, 0)
        wz = d(1, 0) - d(0, 1)
        lamb = (wy * u[2] - wz * u[1], wz * u[0] - wx * u[2], wx * u[1] - wy * u[0])
        ups = (0.5 * (nu + nxp), 0.5 * (nu + nyp), 0.5 * (nu + nzp))
        downs = (0.5 * (nu + nxm), 0.5 * (nu + nym), 0.5 * (nu + nzm))
        for c in range(3):
            total = None
            for axis in range(3):
                term = ups[axis] * (plus[axis][c] - u[c]) - downs[axis] * (u[c] - minus[axis][c])
                total = term if total is None else total + term
            out_ref[c, x] = u[c] + TIME_STEP_LES * (total - lamb[c])
            if want_lamb:
                rest[0][c, x] = lamb[c].astype(rest[0].dtype)
        return carry

    lax.fori_loop(0, size_x, step, 0)


def les_section(vel, nu, vhalo, nhalo, want_lamb):
    out_shape = [jax.ShapeDtypeStruct(vel.shape, jnp.float32)]
    if want_lamb:
        out_shape.append(jax.ShapeDtypeStruct(vel.shape, jnp.bfloat16))
    res = pl.pallas_call(
        lambda *refs: les_kernel(want_lamb, *refs),
        out_shape=tuple(out_shape),
    )(vel, nu, *vhalo, *nhalo)
    return res


def halos(field, lead):
    flow_n = lax.axis_size("flow")
    grp_n = lax.axis_size("grp")
    up_f = [(i, i + 1) for i in range(flow_n - 1)]
    down_f = [(i + 1, i) for i in range(flow_n - 1)]
    up_g = [(i, i + 1) for i in range(grp_n - 1)]
    down_g = [(i + 1, i) for i in range(grp_n - 1)]
    size_x, size_y = field.shape[lead], field.shape[lead + 1]
    xlo = lax.ppermute(lax.index_in_dim(field, size_x - 1, lead, keepdims=False), "flow", up_f)
    xhi = lax.ppermute(lax.index_in_dim(field, 0, lead, keepdims=False), "flow", down_f)
    ylo = lax.ppermute(lax.slice_in_dim(field, size_y - 1, size_y, axis=lead + 1), "grp", up_g)
    yhi = lax.ppermute(lax.slice_in_dim(field, 0, 1, axis=lead + 1), "grp", down_g)
    return xlo, xhi, ylo, yhi


def project(lamb, projection):
    size_x, size_y, size_z = (lamb.shape[1], lamb.shape[2], lamb.shape[3])
    bx, by, bz = size_x // 8, size_y // 8, size_z // 8
    perm = np.zeros((size_z, size_z), np.float32)
    for ez in range(bz):
        for cz in range(8):
            perm[ez * 8 + cz, cz * bz + ez] = 1.0
    rows = lamb.reshape(-1, size_z)
    moved = jnp.dot(rows, jnp.asarray(perm, jnp.bfloat16), preferred_element_type=jnp.float32)
    moved = moved.astype(jnp.bfloat16)
    blocks = moved.reshape(3, bx, 8, by, 8, 8, bz).transpose(2, 4, 5, 0, 1, 3, 6).reshape(512, -1)
    padded_proj = jnp.pad(projection, ((0, 3), (0, 0)))
    source = jnp.dot(padded_proj, blocks, preferred_element_type=jnp.float32)
    source = source.reshape(128, 3, -1).transpose(1, 0, 2)
    return source.reshape(384, -1)


FACE_ROWS = 104


def extract_faces(state_ref, face_ref):
    for dim in range(3):
        for side, at in ((0, 0), (1, 4)):
            f = 2 * dim + side
            for comp in range(4):
                base = comp * 128
                if dim == 0:
                    face_ref[f, pl.ds(comp * 25, 25), :] = state_ref[pl.ds(base + at * 25, 25), :]
                elif dim == 1:
                    for a in range(5):
                        face_ref[f, pl.ds(comp * 25 + a * 5, 5), :] = state_ref[pl.ds(base + a * 25 + at * 5, 5), :]
                else:
                    face_ref[f, pl.ds(comp * 25, 25), :] = state_ref[pl.ds(base + at, 25, stride=5), :]


def send_faces(face_ref, sx0_ref, sx4_ref, sy0_ref, sy4_ref, row_len):
    sx0_ref[...] = face_ref[0]
    sx4_ref[...] = face_ref[1]
    sy0_ref[...] = face_ref[2][:, :row_len]
    last = pltpu.roll(face_ref[3], row_len, 1)
    sy4_ref[...] = last[:, :row_len]


def dg_faces_kernel(state_ref, sx0_ref, sx4_ref, sy0_ref, sy4_ref, face_ref):
    face_ref[...] = jnp.zeros(face_ref.shape, jnp.float32)
    extract_faces(state_ref, face_ref)
    send_faces(face_ref, sx0_ref, sx4_ref, sy0_ref, sy4_ref, sy0_ref.shape[1])


def dg_step_kernel(want_faces, state_ref, src_ref, xlo_ref, xhi_ref, ylo_ref, yhi_ref, own_ref, other_ref,
                   out_ref, *rest):
    if want_faces:
        sx0_ref, sx4_ref, sy0_ref, sy4_ref, face_ref, oth_ref, pad_ref = rest
    else:
        face_ref, oth_ref, pad_ref = rest
    elems = state_ref.shape[1]
    row_len = ylo_ref.shape[1]
    lane = lax.broadcasted_iota(jnp.int32, (FACE_ROWS, elems), 1)
    ez = lane % row_len
    face_ref[...] = jnp.zeros(face_ref.shape, jnp.float32)
    oth_ref[...] = jnp.zeros(oth_ref.shape, jnp.float32)
    extract_faces(state_ref, face_ref)
    oth_ref[pl.ds(0, FACE_ROWS), :] = xlo_ref[...]
    oth_ref[pl.ds(128, FACE_ROWS), :] = xhi_ref[...]
    pad_ref[:, pl.ds(0, row_len)] = ylo_ref[...]
    oth_ref[pl.ds(256, FACE_ROWS), :] = jnp.where(
        lane < row_len, pad_ref[...], pltpu.roll(face_ref[3], row_len, 1))
    pad_ref[:, pl.ds(0, row_len)] = yhi_ref[...]
    oth_ref[pl.ds(384, FACE_ROWS), :] = jnp.where(
        lane >= elems - row_len, pltpu.roll(pad_ref[...], elems - row_len, 1),
        pltpu.roll(face_ref[2], elems - row_len, 1))
    oth_ref[pl.ds(512, FACE_ROWS), :] = jnp.where(ez == 0, 0.0, pltpu.roll(face_ref[5], 1, 1))
    oth_ref[pl.ds(640, FACE_ROWS), :] = jnp.where(
        ez == row_len - 1, 0.0, pltpu.roll(face_ref[4], elems - 1, 1))
    state = state_ref[...]
    rate = jnp.dot(own_ref[...], state, precision=HIGH, preferred_element_type=jnp.float32)
    rate = rate + jnp.dot(other_ref[...], oth_ref[...], precision=HIGH, preferred_element_type=jnp.float32)
    out_ref[pl.ds(0, 128), :] = state[:128] + TIME_STEP_ACOUSTIC * rate[:128]
    out_ref[pl.ds(128, 384), :] = state[128:] + TIME_STEP_ACOUSTIC * (rate[128:] - src_ref[...])
    if want_faces:
        extract_faces(out_ref, face_ref)
        send_faces(face_ref, sx0_ref, sx4_ref, sy0_ref, sy4_ref, row_len)


def face_shapes(elems, row_len):
    big = jax.ShapeDtypeStruct((FACE_ROWS, elems), jnp.float32)
    small = jax.ShapeDtypeStruct((FACE_ROWS, row_len), jnp.float32)
    return [big, big, small, small]


def dg_faces(state, row_len):
    elems = state.shape[1]
    return pl.pallas_call(
        dg_faces_kernel,
        out_shape=tuple(face_shapes(elems, row_len)),
        scratch_shapes=[pltpu.VMEM((6, FACE_ROWS, elems), jnp.float32)],
    )(state)


def dg_step(state, src, recv, own_mat, other_mat, want_faces):
    elems = state.shape[1]
    row_len = recv[2].shape[1]
    out_shape = [jax.ShapeDtypeStruct(state.shape, jnp.float32)]
    if want_faces:
        out_shape += face_shapes(elems, row_len)
    res = pl.pallas_call(
        lambda *refs: dg_step_kernel(want_faces, *refs),
        out_shape=tuple(out_shape),
        scratch_shapes=[
            pltpu.VMEM((6, FACE_ROWS, elems), jnp.float32),
            pltpu.VMEM((768, elems), jnp.float32),
            pltpu.VMEM((FACE_ROWS, elems), jnp.float32),
        ],
    )(state, src, *recv, own_mat, other_mat)
    return res


def exchange_faces(sent):
    sx0, sx4, sy0, sy4 = sent
    flow_n = lax.axis_size("flow")
    grp_n = lax.axis_size("grp")
    up_f = [(i, i + 1) for i in range(flow_n - 1)]
    down_f = [(i + 1, i) for i in range(flow_n - 1)]
    up_g = [(i, i + 1) for i in range(grp_n - 1)]
    down_g = [(i + 1, i) for i in range(grp_n - 1)]
    return (
        lax.ppermute(sx4, "flow", up_f),
        lax.ppermute(sx0, "flow", down_f),
        lax.ppermute(sy4, "grp", up_g),
        lax.ppermute(sy0, "grp", down_g),
    )


def body(velocity, eddy_visc, projection, acoustic_state, route_send, route_place):
    vel = velocity
    lamb = None
    nhalo = None
    for turn in range(LES_SECTIONS):
        last = turn == LES_SECTIONS - 1
        if nhalo is None:
            nhalo = halos(jnp.concatenate([vel, eddy_visc[None]], axis=0), 1)
            vhalo = nhalo
        else:
            vhalo = halos(vel, 1)
        res = les_section(vel, eddy_visc, vhalo, nhalo, last)
        vel = res[0]
        if last:
            lamb = res[1]
    source = project(lamb, projection)
    flow_size = lax.axis_size("flow")
    grp_size = lax.axis_size("grp")
    slot_cap = route_send.shape[2]
    elem_count = acoustic_state.shape[2]
    total_slots = flow_size * grp_size * slot_cap
    placing = route_place.reshape(-1)
    padded_state = jnp.pad(acoustic_state, ((0, 0), (0, 3), (0, 0))).reshape(512, elem_count)
    outgoing = jnp.zeros((512, total_slots), jnp.float32).at[:, placing].set(padded_state)
    arrived = lax.all_to_all(outgoing, ("flow", "grp"), split_axis=1, concat_axis=1, tiled=True)
    sending = route_send.reshape(-1)
    filled = sending >= 0
    target = jnp.where(filled, sending, elem_count)
    state = jnp.zeros((512, elem_count), jnp.float32).at[:, target].set(arrived, mode="drop")

    row_len = velocity.shape[3] // 8
    own_np, other_np = dg_matrices()
    own_mat = jnp.asarray(own_np)
    other_mat = jnp.asarray(other_np)
    sent = dg_faces(state, row_len)
    for turn in range(AC_SECTIONS):
        recv = exchange_faces(sent)
        last = turn == AC_SECTIONS - 1
        res = dg_step(state, source, recv, own_mat, other_mat, not last)
        state = res[0]
        if not last:
            sent = res[1:]
    flat_state = state
    leaving = jnp.where(filled[None, :], flat_state[:, jnp.where(filled, sending, 0)], 0.0)
    returned = lax.all_to_all(leaving, ("flow", "grp"), split_axis=1, concat_axis=1, tiled=True)
    acoustic_out = returned[:, placing].reshape(4, 128, elem_count)[:, :125]
    return (vel, acoustic_out)


def solution(mesh):
    placed = (
        P(None, "flow", "grp", None),
        P("flow", "grp", None),
        P(),
        P(None, None, ("flow", "grp")),
        P(("flow", "grp"), None, None),
        P(("flow", "grp"), None),
    )
    return jax.shard_map(
        body,
        mesh=mesh,
        in_specs=placed,
        out_specs=(P(None, "flow", "grp", None), P(None, None, ("flow", "grp"))),
        check_vma=False,
    )
```

```python
import math

import jax
import jax.numpy as jnp
import numpy as np
from jax import lax
from jax.experimental import pallas as pl
from jax.experimental.pallas import tpu as pltpu
from jax.sharding import PartitionSpec as P

LES_SECTIONS = 2
AC_SECTIONS = 2


TIME_STEP_LES = 0.15
TIME_STEP_ACOUSTIC = 0.02
GEOMETRY = 2.0
LIFT_FACTOR = 20.0
HIGH = lax.Precision.HIGHEST


def gll_derivative():
    gll_nodes = np.array([-1.0, -math.sqrt(3.0 / 7.0), 0.0, math.sqrt(3.0 / 7.0), 1.0])
    bary_weights = np.array(
        [
            1.0
            / np.prod([gll_nodes[first] - gll_nodes[other] for other in range(5) if other != first])
            for first in range(5)
        ]
    )
    matrix = np.zeros((5, 5))
    for row_id in range(5):
        for col_id in range(5):
            if row_id != col_id:
                matrix[row_id, col_id] = (
                    bary_weights[col_id]
                    / bary_weights[row_id]
                    / (gll_nodes[row_id] - gll_nodes[col_id])
                )
    for row_id in range(5):
        matrix[row_id, row_id] = -matrix[row_id].sum()
    return matrix


def node_id(coords):
    return coords[0] * 25 + coords[1] * 5 + coords[2]


def face_nodes(dim, at):
    ids = []
    for first in range(5):
        for second in range(5):
            coords = [first, second]
            coords.insert(dim, at)
            ids.append(node_id(coords))
    return ids


def dg_matrices():
    dmat = gll_derivative()
    own = np.zeros((500, 500))
    for a in range(5):
        for b in range(5):
            for c in range(5):
                row = node_id((a, b, c))
                pos = (a, b, c)
                for dim in range(3):
                    for k in range(5):
                        col_pos = list(pos)
                        col_pos[dim] = k
                        col = node_id(col_pos)
                        weight = -GEOMETRY * dmat[pos[dim], k]
                        own[row, (1 + dim) * 125 + col] += weight
                        own[(1 + dim) * 125 + row, col] += weight
    half = LIFT_FACTOR * 0.5
    other = np.zeros((500, 600))
    face_order = []
    for dim in range(3):
        for sign, at in ((-1.0, 0), (1.0, 4)):
            face_order.append((dim, sign, at))
    for slot, (dim, sign, at) in enumerate(face_order):
        for t, node in enumerate(face_nodes(dim, at)):
            col = lambda comp: slot * 100 + comp * 25 + t
            own[node, (1 + dim) * 125 + node] += half * sign
            own[node, node] += -half
            other[node, col(1 + dim)] += -half * sign
            other[node, col(0)] += half
            for k in range(3):
                own[(1 + k) * 125 + node, (1 + k) * 125 + node] += -half
                other[(1 + k) * 125 + node, col(1 + k)] += half
            own[(1 + dim) * 125 + node, node] += half * sign
            other[(1 + dim) * 125 + node, col(0)] += -half * sign
    own_pad = np.zeros((512, 512), np.float32)
    other_pad = np.zeros((512, 768), np.float32)
    for ci in range(4):
        for cj in range(4):
            own_pad[ci * 128:ci * 128 + 125, cj * 128:cj * 128 + 125] = own[ci * 125:(ci + 1) * 125, cj * 125:(cj + 1) * 125]
        for slot in range(6):
            other_pad[ci * 128:ci * 128 + 125, slot * 128:slot * 128 + 100] = other[ci * 125:(ci + 1) * 125, slot * 100:(slot + 1) * 100]
    return own_pad, other_pad


def face_rows(state, dim, at):
    elems = state.shape[-1]
    cube = state.reshape(4, 5, 5, 5, elems)
    face = lax.index_in_dim(cube, at, axis=1 + dim, keepdims=False)
    return face.reshape(100, elems)


def les_kernel(mode, vel_ref, nu_ref, vxlo_ref, vxhi_ref, vylo_ref, vyhi_ref,
               nxlo_ref, nxhi_ref, nylo_ref, nyhi_ref, *rest):
    size_x, size_y, size_z = vel_ref.shape[1], vel_ref.shape[2], vel_ref.shape[3]
    half = size_z // 2
    row = lax.broadcasted_iota(jnp.int32, (size_y, size_z), 0)
    lane = lax.broadcasted_iota(jnp.int32, (size_y, size_z), 1)
    if mode == 0:
        sx0_ref, sx4_ref, sy0_ref, sy4_ref, out_ref, mxup_ref, mxdn_ref, myup_ref, mydn_ref = rest

        def xlo(c):
            return vxlo_ref[c]

        def xhi(c):
            return vxhi_ref[c]

        def ylo(c, x):
            return vylo_ref[c, x]

        def yhi(c, x):
            return vyhi_ref[c, x]
    else:
        out_ref, lamb_ref = rest

        def plane(ref, c):
            return jnp.concatenate(
                [ref[pl.ds(c * 2 * size_y, size_y), :], ref[pl.ds(c * 2 * size_y + size_y, size_y), :]], axis=1)

        def line(ref, c, x):
            return jnp.concatenate(
                [ref[pl.ds(c * 2 * size_x + x, 1), :], ref[pl.ds(c * 2 * size_x + size_x + x, 1), :]], axis=1)

        def xlo(c):
            return plane(vxlo_ref, c)

        def xhi(c):
            return plane(vxhi_ref, c)

        def ylo(c, x):
            return line(vylo_ref, c, x)

        def yhi(c, x):
            return line(vyhi_ref, c, x)

    def yp(f, halo):
        return jnp.where(row == size_y - 1, halo, pltpu.roll(f, size_y - 1, 0))

    def ym(f, halo):
        return jnp.where(row == 0, halo, pltpu.roll(f, 1, 0))

    def zp(f):
        return jnp.where(lane == size_z - 1, 0.0, pltpu.roll(f, size_z - 1, 1))

    def zm(f):
        return jnp.where(lane == 0, 0.0, pltpu.roll(f, 1, 1))

    def step(x, carry):
        lo = jnp.maximum(x - 1, 0)
        hi = jnp.minimum(x + 1, size_x - 1)
        u = [vel_ref[c, x] for c in range(3)]
        uxm = [jnp.where(x == 0, xlo(c), vel_ref[c, lo]) for c in range(3)]
        uxp = [jnp.where(x == size_x - 1, xhi(c), vel_ref[c, hi]) for c in range(3)]
        uym = [ym(u[c], ylo(c, x)) for c in range(3)]
        uyp = [yp(u[c], yhi(c, x)) for c in range(3)]
        uzm = [zm(u[c]) for c in range(3)]
        uzp = [zp(u[c]) for c in range(3)]
        nu = nu_ref[x]
        nxm = jnp.where(x == 0, nxlo_ref[3], nu_ref[lo])
        nxp = jnp.where(x == size_x - 1, nxhi_ref[3], nu_ref[hi])
        nym = ym(nu, nylo_ref[3, x])
        nyp = yp(nu, nyhi_ref[3, x])
        nzm = zm(nu)
        nzp = zp(nu)
        plus = (uxp, uyp, uzp)
        minus = (uxm, uym, uzm)

        def d(c, axis):
            return 0.5 * (plus[axis][c] - minus[axis][c])

        wx = d(2, 1) - d(1, 2)
        wy = d(0, 2) - d(2, 0)
        wz = d(1, 0) - d(0, 1)
        lamb = (wy * u[2] - wz * u[1], wz * u[0] - wx * u[2], wx * u[1] - wy * u[0])
        ups = (0.5 * (nu + nxp), 0.5 * (nu + nyp), 0.5 * (nu + nzp))
        downs = (0.5 * (nu + nxm), 0.5 * (nu + nym), 0.5 * (nu + nzm))
        for c in range(3):
            total = None
            for axis in range(3):
                term = ups[axis] * (plus[axis][c] - u[c]) - downs[axis] * (u[c] - minus[axis][c])
                total = term if total is None else total + term
            out_ref[c, x] = u[c] + TIME_STEP_LES * (total - lamb[c])
            if mode == 1:
                lamb_ref[c, x] = lamb[c].astype(lamb_ref.dtype)
        return carry

    lax.fori_loop(0, size_x, step, 0)
    if mode == 0:
        for c in range(3):
            for h in range(2):
                mxup_ref[pl.ds(c * 2 * size_y + h * size_y, size_y), :] = out_ref[c, size_x - 1, :, pl.ds(h * half, half)]
                mxdn_ref[pl.ds(c * 2 * size_y + h * size_y, size_y), :] = out_ref[c, 0, :, pl.ds(h * half, half)]
                for x in range(size_x):
                    at = c * 2 * size_x + h * size_x + x
                    myup_ref[pl.ds(at, 1), :] = out_ref[c, x, pl.ds(size_y - 1, 1), pl.ds(h * half, half)]
                    mydn_ref[pl.ds(at, 1), :] = out_ref[c, x, pl.ds(0, 1), pl.ds(h * half, half)]
        xrows = 3 * 2 * size_y
        yrows = 3 * 2 * size_x
        mxup_ref[pl.ds(xrows, FACE_ROWS), :] = sx4_ref[...]
        mxdn_ref[pl.ds(xrows, FACE_ROWS), :] = sx0_ref[...]
        zeros = jnp.zeros((FACE_ROWS, half), jnp.float32)
        myup_ref[pl.ds(yrows, FACE_ROWS), :] = zeros
        mydn_ref[pl.ds(yrows, FACE_ROWS), :] = zeros
        myup_ref[pl.ds(yrows, FACE_ROWS), pl.ds(0, sy4_ref.shape[1])] = sy4_ref[...]
        mydn_ref[pl.ds(yrows, FACE_ROWS), pl.ds(0, sy0_ref.shape[1])] = sy0_ref[...]


def les_section_first(vel, nu, joint, faces):
    size_x, size_y, size_z = vel.shape[1], vel.shape[2], vel.shape[3]
    xbuf = jax.ShapeDtypeStruct((3 * 2 * size_y + FACE_ROWS, size_z // 2), jnp.float32)
    ybuf = jax.ShapeDtypeStruct((3 * 2 * size_x + FACE_ROWS, size_z // 2), jnp.float32)
    return pl.pallas_call(
        lambda *refs: les_kernel(0, *refs),
        out_shape=(jax.ShapeDtypeStruct(vel.shape, jnp.float32), xbuf, xbuf, ybuf, ybuf),
    )(vel, nu, *joint, *joint, *faces)


def les_section_last(vel, nu, merged, joint):
    return pl.pallas_call(
        lambda *refs: les_kernel(1, *refs),
        out_shape=(jax.ShapeDtypeStruct(vel.shape, jnp.float32), jax.ShapeDtypeStruct(vel.shape, jnp.bfloat16)),
    )(vel, nu, *merged, *joint)


def halos(field, lead):
    flow_n = lax.axis_size("flow")
    grp_n = lax.axis_size("grp")
    up_f = [(i, i + 1) for i in range(flow_n - 1)]
    down_f = [(i + 1, i) for i in range(flow_n - 1)]
    up_g = [(i, i + 1) for i in range(grp_n - 1)]
    down_g = [(i + 1, i) for i in range(grp_n - 1)]
    size_x, size_y = field.shape[lead], field.shape[lead + 1]
    xlo = lax.ppermute(lax.index_in_dim(field, size_x - 1, lead, keepdims=False), "flow", up_f)
    xhi = lax.ppermute(lax.index_in_dim(field, 0, lead, keepdims=False), "flow", down_f)
    ylo = lax.ppermute(lax.slice_in_dim(field, size_y - 1, size_y, axis=lead + 1), "grp", up_g)
    yhi = lax.ppermute(lax.slice_in_dim(field, 0, 1, axis=lead + 1), "grp", down_g)
    return xlo, xhi, ylo, yhi


def project(lamb, projection):
    size_x, size_y, size_z = (lamb.shape[1], lamb.shape[2], lamb.shape[3])
    bx, by, bz = size_x // 8, size_y // 8, size_z // 8
    perm = np.zeros((size_z, size_z), np.float32)
    for ez in range(bz):
        for cz in range(8):
            perm[ez * 8 + cz, cz * bz + ez] = 1.0
    rows = lamb.reshape(-1, size_z)
    moved = jnp.dot(rows, jnp.asarray(perm, jnp.bfloat16), preferred_element_type=jnp.float32)
    moved = moved.astype(jnp.bfloat16)
    blocks = moved.reshape(3, bx, 8, by, 8, 8, bz).transpose(2, 4, 5, 0, 1, 3, 6).reshape(512, -1)
    padded_proj = jnp.pad(projection, ((0, 3), (0, 0)))
    source = jnp.dot(padded_proj, blocks, preferred_element_type=jnp.float32)
    source = source.reshape(128, 3, -1).transpose(1, 0, 2)
    return source.reshape(384, -1)


FACE_ROWS = 104


def extract_faces(state_ref, face_ref):
    for dim in range(3):
        for side, at in ((0, 0), (1, 4)):
            f = 2 * dim + side
            for comp in range(4):
                base = comp * 128
                if dim == 0:
                    face_ref[f, pl.ds(comp * 25, 25), :] = state_ref[pl.ds(base + at * 25, 25), :]
                elif dim == 1:
                    for a in range(5):
                        face_ref[f, pl.ds(comp * 25 + a * 5, 5), :] = state_ref[pl.ds(base + a * 25 + at * 5, 5), :]
                else:
                    face_ref[f, pl.ds(comp * 25, 25), :] = state_ref[pl.ds(base + at, 25, stride=5), :]


def send_faces(face_ref, sx0_ref, sx4_ref, sy0_ref, sy4_ref, row_len):
    sx0_ref[...] = face_ref[0]
    sx4_ref[...] = face_ref[1]
    sy0_ref[...] = face_ref[2][:, :row_len]
    last = pltpu.roll(face_ref[3], row_len, 1)
    sy4_ref[...] = last[:, :row_len]


def dg_faces_kernel(state_ref, sx0_ref, sx4_ref, sy0_ref, sy4_ref, face_ref):
    face_ref[...] = jnp.zeros(face_ref.shape, jnp.float32)
    extract_faces(state_ref, face_ref)
    send_faces(face_ref, sx0_ref, sx4_ref, sy0_ref, sy4_ref, sy0_ref.shape[1])


def dg_step_kernel(want_faces, xoff, yoff, row_len, state_ref, src_ref, xlo_ref, xhi_ref, ylo_ref, yhi_ref, own_ref, other_ref,
                   out_ref, *rest):
    if want_faces:
        sx0_ref, sx4_ref, sy0_ref, sy4_ref, face_ref, oth_ref, pad_ref = rest
    else:
        face_ref, oth_ref, pad_ref = rest
    elems = state_ref.shape[1]
    lane = lax.broadcasted_iota(jnp.int32, (FACE_ROWS, elems), 1)
    ez = lane % row_len
    face_ref[...] = jnp.zeros(face_ref.shape, jnp.float32)
    oth_ref[...] = jnp.zeros(oth_ref.shape, jnp.float32)
    extract_faces(state_ref, face_ref)
    oth_ref[pl.ds(0, FACE_ROWS), :] = xlo_ref[pl.ds(xoff, FACE_ROWS), :]
    oth_ref[pl.ds(128, FACE_ROWS), :] = xhi_ref[pl.ds(xoff, FACE_ROWS), :]
    pad_ref[:, pl.ds(0, row_len)] = ylo_ref[pl.ds(yoff, FACE_ROWS), pl.ds(0, row_len)]
    oth_ref[pl.ds(256, FACE_ROWS), :] = jnp.where(
        lane < row_len, pad_ref[...], pltpu.roll(face_ref[3], row_len, 1))
    pad_ref[:, pl.ds(0, row_len)] = yhi_ref[pl.ds(yoff, FACE_ROWS), pl.ds(0, row_len)]
    oth_ref[pl.ds(384, FACE_ROWS), :] = jnp.where(
        lane >= elems - row_len, pltpu.roll(pad_ref[...], elems - row_len, 1),
        pltpu.roll(face_ref[2], elems - row_len, 1))
    oth_ref[pl.ds(512, FACE_ROWS), :] = jnp.where(ez == 0, 0.0, pltpu.roll(face_ref[5], 1, 1))
    oth_ref[pl.ds(640, FACE_ROWS), :] = jnp.where(
        ez == row_len - 1, 0.0, pltpu.roll(face_ref[4], elems - 1, 1))
    state = state_ref[...]
    rate = jnp.dot(own_ref[...], state, precision=HIGH, preferred_element_type=jnp.float32)
    rate = rate + jnp.dot(other_ref[...], oth_ref[...], precision=HIGH, preferred_element_type=jnp.float32)
    out_ref[pl.ds(0, 128), :] = state[:128] + TIME_STEP_ACOUSTIC * rate[:128]
    out_ref[pl.ds(128, 384), :] = state[128:] + TIME_STEP_ACOUSTIC * (rate[128:] - src_ref[...])
    if want_faces:
        extract_faces(out_ref, face_ref)
        send_faces(face_ref, sx0_ref, sx4_ref, sy0_ref, sy4_ref, row_len)


def face_shapes(elems, row_len):
    big = jax.ShapeDtypeStruct((FACE_ROWS, elems), jnp.float32)
    small = jax.ShapeDtypeStruct((FACE_ROWS, row_len), jnp.float32)
    return [big, big, small, small]


def dg_faces(state, row_len):
    elems = state.shape[1]
    return pl.pallas_call(
        dg_faces_kernel,
        out_shape=tuple(face_shapes(elems, row_len)),
        scratch_shapes=[pltpu.VMEM((6, FACE_ROWS, elems), jnp.float32)],
    )(state)


def dg_step(state, src, recv, own_mat, other_mat, want_faces, row_len, xoff=0, yoff=0):
    elems = state.shape[1]
    out_shape = [jax.ShapeDtypeStruct(state.shape, jnp.float32)]
    if want_faces:
        out_shape += face_shapes(elems, row_len)
    res = pl.pallas_call(
        lambda *refs: dg_step_kernel(want_faces, xoff, yoff, row_len, *refs),
        out_shape=tuple(out_shape),
        scratch_shapes=[
            pltpu.VMEM((6, FACE_ROWS, elems), jnp.float32),
            pltpu.VMEM((768, elems), jnp.float32),
            pltpu.VMEM((FACE_ROWS, elems), jnp.float32),
        ],
    )(state, src, *recv, own_mat, other_mat)
    return res


def exchange_faces(sent):
    sx0, sx4, sy0, sy4 = sent
    flow_n = lax.axis_size("flow")
    grp_n = lax.axis_size("grp")
    up_f = [(i, i + 1) for i in range(flow_n - 1)]
    down_f = [(i + 1, i) for i in range(flow_n - 1)]
    up_g = [(i, i + 1) for i in range(grp_n - 1)]
    down_g = [(i + 1, i) for i in range(grp_n - 1)]
    return (
        lax.ppermute(sx4, "flow", up_f),
        lax.ppermute(sx0, "flow", down_f),
        lax.ppermute(sy4, "grp", up_g),
        lax.ppermute(sy0, "grp", down_g),
    )


def body(velocity, eddy_visc, projection, acoustic_state, route_send, route_place):
    joint = halos(jnp.concatenate([velocity, eddy_visc[None]], axis=0), 1)
    flow_size = lax.axis_size("flow")
    grp_size = lax.axis_size("grp")
    slot_cap = route_send.shape[2]
    elem_count = acoustic_state.shape[2]
    total_slots = flow_size * grp_size * slot_cap
    placing = route_place.reshape(-1)
    padded_state = jnp.pad(acoustic_state, ((0, 0), (0, 3), (0, 0))).reshape(512, elem_count)
    outgoing = jnp.zeros((512, total_slots), jnp.float32).at[:, placing].set(padded_state)
    arrived = lax.all_to_all(outgoing, ("flow", "grp"), split_axis=1, concat_axis=1, tiled=True)
    sending = route_send.reshape(-1)
    filled = sending >= 0
    target = jnp.where(filled, sending, elem_count)
    state = jnp.zeros((512, elem_count), jnp.float32).at[:, target].set(arrived, mode="drop")

    row_len = velocity.shape[3] // 8
    own_np, other_np = dg_matrices()
    own_mat = jnp.asarray(own_np)
    other_mat = jnp.asarray(other_np)
    sent = dg_faces(state, row_len)
    vel, mxup, mxdn, myup, mydn = les_section_first(velocity, eddy_visc, joint, sent)
    merged = exchange_faces((mxdn, mxup, mydn, myup))
    vel, lamb = les_section_last(vel, eddy_visc, merged, joint)
    source = project(lamb, projection)
    xoff = 3 * 2 * velocity.shape[2]
    yoff = 3 * 2 * velocity.shape[1]
    res = dg_step(state, source, merged, own_mat, other_mat, True, row_len, xoff, yoff)
    state = res[0]
    recv = exchange_faces(res[1:])
    state = dg_step(state, source, recv, own_mat, other_mat, False, row_len)[0]
    flat_state = state
    leaving = jnp.where(filled[None, :], flat_state[:, jnp.where(filled, sending, 0)], 0.0)
    returned = lax.all_to_all(leaving, ("flow", "grp"), split_axis=1, concat_axis=1, tiled=True)
    acoustic_out = returned[:, placing].reshape(4, 128, elem_count)[:, :125]
    return (vel, acoustic_out)


def solution(mesh):
    placed = (
        P(None, "flow", "grp", None),
        P("flow", "grp", None),
        P(),
        P(None, None, ("flow", "grp")),
        P(("flow", "grp"), None, None),
        P(("flow", "grp"), None),
    )
    return jax.shard_map(
        body,
        mesh=mesh,
        in_specs=placed,
        out_specs=(P(None, "flow", "grp", None), P(None, None, ("flow", "grp"))),
        check_vma=False,
    )
```

```python
import math

import jax
import jax.numpy as jnp
import numpy as np
from jax import lax
from jax.experimental import pallas as pl
from jax.experimental.pallas import tpu as pltpu
from jax.sharding import PartitionSpec as P

LES_SECTIONS = 2
AC_SECTIONS = 2


TIME_STEP_LES = 0.15
TIME_STEP_ACOUSTIC = 0.02
GEOMETRY = 2.0
LIFT_FACTOR = 20.0
HIGH = lax.Precision.HIGHEST


def gll_derivative():
    gll_nodes = np.array([-1.0, -math.sqrt(3.0 / 7.0), 0.0, math.sqrt(3.0 / 7.0), 1.0])
    bary_weights = np.array(
        [
            1.0
            / np.prod([gll_nodes[first] - gll_nodes[other] for other in range(5) if other != first])
            for first in range(5)
        ]
    )
    matrix = np.zeros((5, 5))
    for row_id in range(5):
        for col_id in range(5):
            if row_id != col_id:
                matrix[row_id, col_id] = (
                    bary_weights[col_id]
                    / bary_weights[row_id]
                    / (gll_nodes[row_id] - gll_nodes[col_id])
                )
    for row_id in range(5):
        matrix[row_id, row_id] = -matrix[row_id].sum()
    return matrix


def node_id(coords):
    return coords[0] * 25 + coords[1] * 5 + coords[2]


def face_nodes(dim, at):
    ids = []
    for first in range(5):
        for second in range(5):
            coords = [first, second]
            coords.insert(dim, at)
            ids.append(node_id(coords))
    return ids


def dg_matrices():
    dmat = gll_derivative()
    own = np.zeros((500, 500))
    for a in range(5):
        for b in range(5):
            for c in range(5):
                row = node_id((a, b, c))
                pos = (a, b, c)
                for dim in range(3):
                    for k in range(5):
                        col_pos = list(pos)
                        col_pos[dim] = k
                        col = node_id(col_pos)
                        weight = -GEOMETRY * dmat[pos[dim], k]
                        own[row, (1 + dim) * 125 + col] += weight
                        own[(1 + dim) * 125 + row, col] += weight
    half = LIFT_FACTOR * 0.5
    other = np.zeros((500, 600))
    face_order = []
    for dim in range(3):
        for sign, at in ((-1.0, 0), (1.0, 4)):
            face_order.append((dim, sign, at))
    for slot, (dim, sign, at) in enumerate(face_order):
        for t, node in enumerate(face_nodes(dim, at)):
            col = lambda comp: slot * 100 + comp * 25 + t
            own[node, (1 + dim) * 125 + node] += half * sign
            own[node, node] += -half
            other[node, col(1 + dim)] += -half * sign
            other[node, col(0)] += half
            for k in range(3):
                own[(1 + k) * 125 + node, (1 + k) * 125 + node] += -half
                other[(1 + k) * 125 + node, col(1 + k)] += half
            own[(1 + dim) * 125 + node, node] += half * sign
            other[(1 + dim) * 125 + node, col(0)] += -half * sign
    own_pad = np.zeros((512, 512), np.float32)
    other_pad = np.zeros((512, 768), np.float32)
    for ci in range(4):
        for cj in range(4):
            own_pad[ci * 128:ci * 128 + 125, cj * 128:cj * 128 + 125] = own[ci * 125:(ci + 1) * 125, cj * 125:(cj + 1) * 125]
        for slot in range(6):
            other_pad[ci * 128:ci * 128 + 125, slot * 128:slot * 128 + 100] = other[ci * 125:(ci + 1) * 125, slot * 100:(slot + 1) * 100]
    return own_pad, other_pad


def face_rows(state, dim, at):
    elems = state.shape[-1]
    cube = state.reshape(4, 5, 5, 5, elems)
    face = lax.index_in_dim(cube, at, axis=1 + dim, keepdims=False)
    return face.reshape(100, elems)


def les_kernel(mode, vel_ref, nu_ref, vxlo_ref, vxhi_ref, vylo_ref, vyhi_ref,
               nxlo_ref, nxhi_ref, nylo_ref, nyhi_ref, *rest):
    size_x, size_y, size_z = vel_ref.shape[1], vel_ref.shape[2], vel_ref.shape[3]
    half = size_z // 2
    row = lax.broadcasted_iota(jnp.int32, (size_y, size_z), 0)
    lane = lax.broadcasted_iota(jnp.int32, (size_y, size_z), 1)
    if mode == 0:
        (out_ref,) = rest

        def xlo(c):
            return vxlo_ref[c]

        def xhi(c):
            return vxhi_ref[c]

        def ylo(c, x):
            return vylo_ref[c, x]

        def yhi(c, x):
            return vyhi_ref[c, x]
    else:
        out_ref, lamb_ref = rest

        def plane(ref, c):
            return jnp.concatenate(
                [ref[pl.ds(c * 2 * size_y, size_y), :], ref[pl.ds(c * 2 * size_y + size_y, size_y), :]], axis=1)

        def line(ref, c, x):
            return jnp.concatenate(
                [ref[pl.ds(c * 2 * size_x + x, 1), :], ref[pl.ds(c * 2 * size_x + size_x + x, 1), :]], axis=1)

        def xlo(c):
            return plane(vxlo_ref, c)

        def xhi(c):
            return plane(vxhi_ref, c)

        def ylo(c, x):
            return line(vylo_ref, c, x)

        def yhi(c, x):
            return line(vyhi_ref, c, x)

    def yp(f, halo):
        return jnp.where(row == size_y - 1, halo, pltpu.roll(f, size_y - 1, 0))

    def ym(f, halo):
        return jnp.where(row == 0, halo, pltpu.roll(f, 1, 0))

    def zp(f):
        return jnp.where(lane == size_z - 1, 0.0, pltpu.roll(f, size_z - 1, 1))

    def zm(f):
        return jnp.where(lane == 0, 0.0, pltpu.roll(f, 1, 1))

    def step(x, carry):
        lo = jnp.maximum(x - 1, 0)
        hi = jnp.minimum(x + 1, size_x - 1)
        u = [vel_ref[c, x] for c in range(3)]
        uxm = [jnp.where(x == 0, xlo(c), vel_ref[c, lo]) for c in range(3)]
        uxp = [jnp.where(x == size_x - 1, xhi(c), vel_ref[c, hi]) for c in range(3)]
        uym = [ym(u[c], ylo(c, x)) for c in range(3)]
        uyp = [yp(u[c], yhi(c, x)) for c in range(3)]
        uzm = [zm(u[c]) for c in range(3)]
        uzp = [zp(u[c]) for c in range(3)]
        nu = nu_ref[x]
        nxm = jnp.where(x == 0, nxlo_ref[3], nu_ref[lo])
        nxp = jnp.where(x == size_x - 1, nxhi_ref[3], nu_ref[hi])
        nym = ym(nu, nylo_ref[3, x])
        nyp = yp(nu, nyhi_ref[3, x])
        nzm = zm(nu)
        nzp = zp(nu)
        plus = (uxp, uyp, uzp)
        minus = (uxm, uym, uzm)

        def d(c, axis):
            return 0.5 * (plus[axis][c] - minus[axis][c])

        wx = d(2, 1) - d(1, 2)
        wy = d(0, 2) - d(2, 0)
        wz = d(1, 0) - d(0, 1)
        lamb = (wy * u[2] - wz * u[1], wz * u[0] - wx * u[2], wx * u[1] - wy * u[0])
        ups = (0.5 * (nu + nxp), 0.5 * (nu + nyp), 0.5 * (nu + nzp))
        downs = (0.5 * (nu + nxm), 0.5 * (nu + nym), 0.5 * (nu + nzm))
        for c in range(3):
            total = None
            for axis in range(3):
                term = ups[axis] * (plus[axis][c] - u[c]) - downs[axis] * (u[c] - minus[axis][c])
                total = term if total is None else total + term
            out_ref[c, x] = u[c] + TIME_STEP_LES * (total - lamb[c])
            if mode == 1:
                lamb_ref[c, x] = lamb[c].astype(lamb_ref.dtype)
        return carry

    lax.fori_loop(0, size_x, step, 0)


def les_section_first(vel, nu, joint):
    return pl.pallas_call(
        lambda *refs: les_kernel(0, *refs),
        out_shape=(jax.ShapeDtypeStruct(vel.shape, jnp.float32),),
    )(vel, nu, *joint, *joint)[0]


def les_section_last(vel, nu, merged, joint):
    return pl.pallas_call(
        lambda *refs: les_kernel(1, *refs),
        out_shape=(jax.ShapeDtypeStruct(vel.shape, jnp.float32), jax.ShapeDtypeStruct(vel.shape, jnp.bfloat16)),
    )(vel, nu, *merged, *joint)


def halos(field, lead):
    flow_n = lax.axis_size("flow")
    grp_n = lax.axis_size("grp")
    up_f = [(i, i + 1) for i in range(flow_n - 1)]
    down_f = [(i + 1, i) for i in range(flow_n - 1)]
    up_g = [(i, i + 1) for i in range(grp_n - 1)]
    down_g = [(i + 1, i) for i in range(grp_n - 1)]
    size_x, size_y = field.shape[lead], field.shape[lead + 1]
    xlo = lax.ppermute(lax.index_in_dim(field, size_x - 1, lead, keepdims=False), "flow", up_f)
    xhi = lax.ppermute(lax.index_in_dim(field, 0, lead, keepdims=False), "flow", down_f)
    ylo = lax.ppermute(lax.slice_in_dim(field, size_y - 1, size_y, axis=lead + 1), "grp", up_g)
    yhi = lax.ppermute(lax.slice_in_dim(field, 0, 1, axis=lead + 1), "grp", down_g)
    return xlo, xhi, ylo, yhi


def project(lamb, projection):
    size_x, size_y, size_z = (lamb.shape[1], lamb.shape[2], lamb.shape[3])
    bx, by, bz = size_x // 8, size_y // 8, size_z // 8
    perm = np.zeros((size_z, size_z), np.float32)
    for ez in range(bz):
        for cz in range(8):
            perm[ez * 8 + cz, cz * bz + ez] = 1.0
    rows = lamb.reshape(-1, size_z)
    moved = jnp.dot(rows, jnp.asarray(perm, jnp.bfloat16), preferred_element_type=jnp.float32)
    moved = moved.astype(jnp.bfloat16)
    blocks = moved.reshape(3, bx, 8, by, 8, 8, bz).transpose(2, 4, 5, 0, 1, 3, 6).reshape(512, -1)
    padded_proj = jnp.pad(projection, ((0, 3), (0, 0)))
    source = jnp.dot(padded_proj, blocks, preferred_element_type=jnp.float32)
    source = source.reshape(128, 3, -1).transpose(1, 0, 2)
    return source.reshape(384, -1)


FACE_ROWS = 104


def extract_faces(state_ref, face_ref):
    for dim in range(3):
        for side, at in ((0, 0), (1, 4)):
            f = 2 * dim + side
            for comp in range(4):
                base = comp * 128
                if dim == 0:
                    face_ref[f, pl.ds(comp * 25, 25), :] = state_ref[pl.ds(base + at * 25, 25), :]
                elif dim == 1:
                    for a in range(5):
                        face_ref[f, pl.ds(comp * 25 + a * 5, 5), :] = state_ref[pl.ds(base + a * 25 + at * 5, 5), :]
                else:
                    face_ref[f, pl.ds(comp * 25, 25), :] = state_ref[pl.ds(base + at, 25, stride=5), :]


def send_faces(face_ref, sx0_ref, sx4_ref, sy0_ref, sy4_ref, row_len):
    sx0_ref[...] = face_ref[0]
    sx4_ref[...] = face_ref[1]
    sy0_ref[...] = face_ref[2][:, :row_len]
    last = pltpu.roll(face_ref[3], row_len, 1)
    sy4_ref[...] = last[:, :row_len]


def one_hot(shape, ids, axis):
    return jnp.where(lax.broadcasted_iota(jnp.int32, shape, axis) == ids, 1.0, 0.0).astype(jnp.float32)


def route_out_kernel(acoustic_ref, place_ref, out_ref, pad_ref):
    comps, nodes, elems = acoustic_ref.shape
    pad_ref[...] = jnp.zeros(pad_ref.shape, jnp.float32)
    for comp in range(comps):
        pad_ref[pl.ds(comp * 128, nodes), :] = acoustic_ref[comp]
    slots = out_ref.shape[0]
    place_hot = one_hot((slots, elems), place_ref[...], 0)
    out_ref[...] = lax.dot_general(place_hot, pad_ref[...], (((1,), (1,)), ((), ())),
                                   precision=HIGH, preferred_element_type=jnp.float32)


def route_in_kernel(arrived_ref, place_ref, out_ref):
    slots, rows = arrived_ref.shape
    comps, nodes, elems = out_ref.shape
    place_hot = one_hot((slots, elems), place_ref[...], 0)
    back = jnp.dot(arrived_ref[...].T, place_hot, precision=HIGH, preferred_element_type=jnp.float32)
    for comp in range(comps):
        out_ref[comp] = back[comp * 128:comp * 128 + nodes]


def dg_faces_kernel(arrived_ref, send_ref, vel_ref, state_ref, mxup_ref, mxdn_ref, myup_ref, mydn_ref, face_ref):
    slots, rows = arrived_ref.shape
    elems = state_ref.shape[1]
    home_hot = one_hot((slots, elems), send_ref[...], 1)
    state_ref[...] = jnp.dot(arrived_ref[...].T, home_hot, precision=HIGH, preferred_element_type=jnp.float32)
    face_ref[...] = jnp.zeros(face_ref.shape, jnp.float32)
    extract_faces(state_ref, face_ref)
    size_x, size_y, size_z = vel_ref.shape[1], vel_ref.shape[2], vel_ref.shape[3]
    half = size_z // 2
    row_len = size_z // 8
    for c in range(3):
        for h in range(2):
            mxup_ref[pl.ds(c * 2 * size_y + h * size_y, size_y), :] = vel_ref[c, size_x - 1, :, pl.ds(h * half, half)]
            mxdn_ref[pl.ds(c * 2 * size_y + h * size_y, size_y), :] = vel_ref[c, 0, :, pl.ds(h * half, half)]
            for x in range(size_x):
                at = c * 2 * size_x + h * size_x + x
                myup_ref[pl.ds(at, 1), :] = vel_ref[c, x, pl.ds(size_y - 1, 1), pl.ds(h * half, half)]
                mydn_ref[pl.ds(at, 1), :] = vel_ref[c, x, pl.ds(0, 1), pl.ds(h * half, half)]
    xrows = 3 * 2 * size_y
    yrows = 3 * 2 * size_x
    mxup_ref[pl.ds(xrows, FACE_ROWS), :] = face_ref[1]
    mxdn_ref[pl.ds(xrows, FACE_ROWS), :] = face_ref[0]
    lane = lax.broadcasted_iota(jnp.int32, (FACE_ROWS, elems), 1)
    myup_ref[pl.ds(yrows, FACE_ROWS), :] = jnp.where(lane < row_len, pltpu.roll(face_ref[3], row_len, 1), 0.0)
    mydn_ref[pl.ds(yrows, FACE_ROWS), :] = jnp.where(lane < row_len, face_ref[2], 0.0)


def dg_step_kernel(want_faces, xoff, yoff, row_len, state_ref, src_ref, xlo_ref, xhi_ref, ylo_ref, yhi_ref, own_ref, other_ref,
                   send_ref, out_ref, *rest):
    if want_faces:
        sx0_ref, sx4_ref, sy0_ref, sy4_ref, face_ref, oth_ref, pad_ref = rest
    else:
        leave_ref, face_ref, oth_ref, pad_ref = rest
    elems = state_ref.shape[1]
    lane = lax.broadcasted_iota(jnp.int32, (FACE_ROWS, elems), 1)
    ez = lane % row_len
    face_ref[...] = jnp.zeros(face_ref.shape, jnp.float32)
    oth_ref[...] = jnp.zeros(oth_ref.shape, jnp.float32)
    extract_faces(state_ref, face_ref)
    oth_ref[pl.ds(0, FACE_ROWS), :] = xlo_ref[pl.ds(xoff, FACE_ROWS), :]
    oth_ref[pl.ds(128, FACE_ROWS), :] = xhi_ref[pl.ds(xoff, FACE_ROWS), :]
    pad_ref[:, pl.ds(0, row_len)] = ylo_ref[pl.ds(yoff, FACE_ROWS), pl.ds(0, row_len)]
    oth_ref[pl.ds(256, FACE_ROWS), :] = jnp.where(
        lane < row_len, pad_ref[...], pltpu.roll(face_ref[3], row_len, 1))
    pad_ref[:, pl.ds(0, row_len)] = yhi_ref[pl.ds(yoff, FACE_ROWS), pl.ds(0, row_len)]
    oth_ref[pl.ds(384, FACE_ROWS), :] = jnp.where(
        lane >= elems - row_len, pltpu.roll(pad_ref[...], elems - row_len, 1),
        pltpu.roll(face_ref[2], elems - row_len, 1))
    oth_ref[pl.ds(512, FACE_ROWS), :] = jnp.where(ez == 0, 0.0, pltpu.roll(face_ref[5], 1, 1))
    oth_ref[pl.ds(640, FACE_ROWS), :] = jnp.where(
        ez == row_len - 1, 0.0, pltpu.roll(face_ref[4], elems - 1, 1))
    state = state_ref[...]
    rate = jnp.dot(own_ref[...], state, precision=HIGH, preferred_element_type=jnp.float32)
    rate = rate + jnp.dot(other_ref[...], oth_ref[...], precision=HIGH, preferred_element_type=jnp.float32)
    out_ref[pl.ds(0, 128), :] = state[:128] + TIME_STEP_ACOUSTIC * rate[:128]
    out_ref[pl.ds(128, 384), :] = state[128:] + TIME_STEP_ACOUSTIC * (rate[128:] - src_ref[...])
    if want_faces:
        extract_faces(out_ref, face_ref)
        send_faces(face_ref, sx0_ref, sx4_ref, sy0_ref, sy4_ref, row_len)
    else:
        slots = leave_ref.shape[0]
        home_hot = one_hot((slots, elems), send_ref[...], 1)
        leave_ref[...] = lax.dot_general(home_hot, out_ref[...], (((1,), (1,)), ((), ())),
                                         precision=HIGH, preferred_element_type=jnp.float32)


def face_shapes(elems, row_len):
    big = jax.ShapeDtypeStruct((FACE_ROWS, elems), jnp.float32)
    small = jax.ShapeDtypeStruct((FACE_ROWS, row_len), jnp.float32)
    return [big, big, small, small]


def dg_faces(arrived, sending, vel):
    elems = vel.shape[2] // 8 * (vel.shape[3] // 8) * (vel.shape[1] // 8)
    size_x, size_y, size_z = vel.shape[1], vel.shape[2], vel.shape[3]
    xbuf = jax.ShapeDtypeStruct((3 * 2 * size_y + FACE_ROWS, size_z // 2), jnp.float32)
    ybuf = jax.ShapeDtypeStruct((3 * 2 * size_x + FACE_ROWS, size_z // 2), jnp.float32)
    return pl.pallas_call(
        dg_faces_kernel,
        out_shape=(jax.ShapeDtypeStruct((arrived.shape[1], elems), jnp.float32), xbuf, xbuf, ybuf, ybuf),
        scratch_shapes=[pltpu.VMEM((6, FACE_ROWS, elems), jnp.float32)],
    )(arrived, sending, vel)


def route_out(acoustic, placing, slots):
    return pl.pallas_call(
        route_out_kernel,
        out_shape=jax.ShapeDtypeStruct((slots, 512), jnp.float32),
        scratch_shapes=[pltpu.VMEM((512, acoustic.shape[2]), jnp.float32)],
    )(acoustic, placing)


def route_in(returned, placing, nodes):
    elems = placing.shape[1]
    return pl.pallas_call(
        route_in_kernel,
        out_shape=jax.ShapeDtypeStruct((4, nodes, elems), jnp.float32),
    )(returned, placing)


def dg_step(state, src, recv, own_mat, other_mat, want_faces, row_len, xoff=0, yoff=0, sending=None):
    elems = state.shape[1]
    out_shape = [jax.ShapeDtypeStruct(state.shape, jnp.float32)]
    extra = [sending]
    if want_faces:
        out_shape += face_shapes(elems, row_len)
    else:
        out_shape.append(jax.ShapeDtypeStruct((sending.shape[0], state.shape[0]), jnp.float32))
    res = pl.pallas_call(
        lambda *refs: dg_step_kernel(want_faces, xoff, yoff, row_len, *refs),
        out_shape=tuple(out_shape),
        scratch_shapes=[
            pltpu.VMEM((6, FACE_ROWS, elems), jnp.float32),
            pltpu.VMEM((768, elems), jnp.float32),
            pltpu.VMEM((FACE_ROWS, elems), jnp.float32),
        ],
    )(state, src, *recv, own_mat, other_mat, *extra)
    return res


def exchange_faces(sent):
    sx0, sx4, sy0, sy4 = sent
    flow_n = lax.axis_size("flow")
    grp_n = lax.axis_size("grp")
    up_f = [(i, i + 1) for i in range(flow_n - 1)]
    down_f = [(i + 1, i) for i in range(flow_n - 1)]
    up_g = [(i, i + 1) for i in range(grp_n - 1)]
    down_g = [(i + 1, i) for i in range(grp_n - 1)]
    return (
        lax.ppermute(sx4, "flow", up_f),
        lax.ppermute(sx0, "flow", down_f),
        lax.ppermute(sy4, "grp", up_g),
        lax.ppermute(sy0, "grp", down_g),
    )


def body(velocity, eddy_visc, projection, acoustic_state, route_send, route_place):
    joint = halos(jnp.concatenate([velocity, eddy_visc[None]], axis=0), 1)
    flow_size = lax.axis_size("flow")
    grp_size = lax.axis_size("grp")
    slot_cap = route_send.shape[2]
    total_slots = flow_size * grp_size * slot_cap
    sending = route_send.reshape(total_slots, 1)
    outgoing = route_out(acoustic_state, route_place, total_slots)
    arrived = lax.all_to_all(outgoing, ("flow", "grp"), split_axis=0, concat_axis=0, tiled=True)
    vel = les_section_first(velocity, eddy_visc, joint)

    row_len = velocity.shape[3] // 8
    own_np, other_np = dg_matrices()
    own_mat = jnp.asarray(own_np)
    other_mat = jnp.asarray(other_np)
    state, mxup, mxdn, myup, mydn = dg_faces(arrived, sending, vel)
    merged = exchange_faces((mxdn, mxup, mydn, myup))
    vel, lamb = les_section_last(vel, eddy_visc, merged, joint)
    source = project(lamb, projection)
    xoff = 3 * 2 * velocity.shape[2]
    yoff = 3 * 2 * velocity.shape[1]
    res = dg_step(state, source, merged, own_mat, other_mat, True, row_len, xoff, yoff, sending=sending)
    state = res[0]
    recv = exchange_faces(res[1:])
    leaving = dg_step(state, source, recv, own_mat, other_mat, False, row_len, sending=sending)[1]
    returned = lax.all_to_all(leaving, ("flow", "grp"), split_axis=0, concat_axis=0, tiled=True)
    acoustic_out = route_in(returned, route_place, acoustic_state.shape[1])
    return (vel, acoustic_out)


def solution(mesh):
    placed = (
        P(None, "flow", "grp", None),
        P("flow", "grp", None),
        P(),
        P(None, None, ("flow", "grp")),
        P(("flow", "grp"), None, None),
        P(("flow", "grp"), None),
    )
    return jax.shard_map(
        body,
        mesh=mesh,
        in_specs=placed,
        out_specs=(P(None, "flow", "grp", None), P(None, None, ("flow", "grp"))),
        check_vma=False,
    )
```

```python
import math

import jax
import jax.numpy as jnp
import numpy as np
from jax import lax
from jax.experimental import pallas as pl
from jax.experimental.pallas import tpu as pltpu
from jax.sharding import PartitionSpec as P

LES_SECTIONS = 2
AC_SECTIONS = 2


TIME_STEP_LES = 0.15
TIME_STEP_ACOUSTIC = 0.02
GEOMETRY = 2.0
LIFT_FACTOR = 20.0
HIGH = lax.Precision.HIGHEST


def gll_derivative():
    gll_nodes = np.array([-1.0, -math.sqrt(3.0 / 7.0), 0.0, math.sqrt(3.0 / 7.0), 1.0])
    bary_weights = np.array(
        [
            1.0
            / np.prod([gll_nodes[first] - gll_nodes[other] for other in range(5) if other != first])
            for first in range(5)
        ]
    )
    matrix = np.zeros((5, 5))
    for row_id in range(5):
        for col_id in range(5):
            if row_id != col_id:
                matrix[row_id, col_id] = (
                    bary_weights[col_id]
                    / bary_weights[row_id]
                    / (gll_nodes[row_id] - gll_nodes[col_id])
                )
    for row_id in range(5):
        matrix[row_id, row_id] = -matrix[row_id].sum()
    return matrix


def node_id(coords):
    return coords[0] * 25 + coords[1] * 5 + coords[2]


def face_nodes(dim, at):
    ids = []
    for first in range(5):
        for second in range(5):
            coords = [first, second]
            coords.insert(dim, at)
            ids.append(node_id(coords))
    return ids


def dg_matrices():
    dmat = gll_derivative()
    own = np.zeros((500, 500))
    for a in range(5):
        for b in range(5):
            for c in range(5):
                row = node_id((a, b, c))
                pos = (a, b, c)
                for dim in range(3):
                    for k in range(5):
                        col_pos = list(pos)
                        col_pos[dim] = k
                        col = node_id(col_pos)
                        weight = -GEOMETRY * dmat[pos[dim], k]
                        own[row, (1 + dim) * 125 + col] += weight
                        own[(1 + dim) * 125 + row, col] += weight
    half = LIFT_FACTOR * 0.5
    other = np.zeros((500, 600))
    face_order = []
    for dim in range(3):
        for sign, at in ((-1.0, 0), (1.0, 4)):
            face_order.append((dim, sign, at))
    for slot, (dim, sign, at) in enumerate(face_order):
        for t, node in enumerate(face_nodes(dim, at)):
            col = lambda comp: slot * 100 + comp * 25 + t
            own[node, (1 + dim) * 125 + node] += half * sign
            own[node, node] += -half
            other[node, col(1 + dim)] += -half * sign
            other[node, col(0)] += half
            for k in range(3):
                own[(1 + k) * 125 + node, (1 + k) * 125 + node] += -half
                other[(1 + k) * 125 + node, col(1 + k)] += half
            own[(1 + dim) * 125 + node, node] += half * sign
            other[(1 + dim) * 125 + node, col(0)] += -half * sign
    own_pad = np.zeros((512, 512), np.float32)
    other_pad = np.zeros((512, 768), np.float32)
    for ci in range(4):
        for cj in range(4):
            own_pad[ci * 128:ci * 128 + 125, cj * 128:cj * 128 + 125] = own[ci * 125:(ci + 1) * 125, cj * 125:(cj + 1) * 125]
        for slot in range(6):
            other_pad[ci * 128:ci * 128 + 125, slot * 128:slot * 128 + 100] = other[ci * 125:(ci + 1) * 125, slot * 100:(slot + 1) * 100]
    return own_pad, other_pad


def face_rows(state, dim, at):
    elems = state.shape[-1]
    cube = state.reshape(4, 5, 5, 5, elems)
    face = lax.index_in_dim(cube, at, axis=1 + dim, keepdims=False)
    return face.reshape(100, elems)


def les_kernel(mode, vel_ref, nu_ref, vxlo_ref, vxhi_ref, vylo_ref, vyhi_ref,
               nxlo_ref, nxhi_ref, nylo_ref, nyhi_ref, *rest):
    size_x, size_y, size_z = vel_ref.shape[1], vel_ref.shape[2], vel_ref.shape[3]
    half = size_z // 2
    row = lax.broadcasted_iota(jnp.int32, (size_y, size_z), 0)
    lane = lax.broadcasted_iota(jnp.int32, (size_y, size_z), 1)
    if mode == 0:
        (out_ref,) = rest

        def xlo(c):
            return vxlo_ref[c]

        def xhi(c):
            return vxhi_ref[c]

        def ylo(c, x):
            return vylo_ref[c, x]

        def yhi(c, x):
            return vyhi_ref[c, x]
    else:
        out_ref, lamb_ref = rest

        def plane(ref, c):
            return jnp.concatenate(
                [ref[pl.ds(c * 2 * size_y, size_y), :], ref[pl.ds(c * 2 * size_y + size_y, size_y), :]], axis=1)

        def line(ref, c, x):
            return jnp.concatenate(
                [ref[pl.ds(c * 2 * size_x + x, 1), :], ref[pl.ds(c * 2 * size_x + size_x + x, 1), :]], axis=1)

        def xlo(c):
            return plane(vxlo_ref, c)

        def xhi(c):
            return plane(vxhi_ref, c)

        def ylo(c, x):
            return line(vylo_ref, c, x)

        def yhi(c, x):
            return line(vyhi_ref, c, x)

    def yp(f, halo):
        return jnp.where(row == size_y - 1, halo, pltpu.roll(f, size_y - 1, 0))

    def ym(f, halo):
        return jnp.where(row == 0, halo, pltpu.roll(f, 1, 0))

    def zp(f):
        return jnp.where(lane == size_z - 1, 0.0, pltpu.roll(f, size_z - 1, 1))

    def zm(f):
        return jnp.where(lane == 0, 0.0, pltpu.roll(f, 1, 1))

    def step(x, carry):
        lo = jnp.maximum(x - 1, 0)
        hi = jnp.minimum(x + 1, size_x - 1)
        u = [vel_ref[c, x] for c in range(3)]
        uxm = [jnp.where(x == 0, xlo(c), vel_ref[c, lo]) for c in range(3)]
        uxp = [jnp.where(x == size_x - 1, xhi(c), vel_ref[c, hi]) for c in range(3)]
        uym = [ym(u[c], ylo(c, x)) for c in range(3)]
        uyp = [yp(u[c], yhi(c, x)) for c in range(3)]
        uzm = [zm(u[c]) for c in range(3)]
        uzp = [zp(u[c]) for c in range(3)]
        nu = nu_ref[x]
        nxm = jnp.where(x == 0, nxlo_ref[3], nu_ref[lo])
        nxp = jnp.where(x == size_x - 1, nxhi_ref[3], nu_ref[hi])
        nym = ym(nu, nylo_ref[3, x])
        nyp = yp(nu, nyhi_ref[3, x])
        nzm = zm(nu)
        nzp = zp(nu)
        plus = (uxp, uyp, uzp)
        minus = (uxm, uym, uzm)

        def d(c, axis):
            return 0.5 * (plus[axis][c] - minus[axis][c])

        wx = d(2, 1) - d(1, 2)
        wy = d(0, 2) - d(2, 0)
        wz = d(1, 0) - d(0, 1)
        lamb = (wy * u[2] - wz * u[1], wz * u[0] - wx * u[2], wx * u[1] - wy * u[0])
        ups = (0.5 * (nu + nxp), 0.5 * (nu + nyp), 0.5 * (nu + nzp))
        downs = (0.5 * (nu + nxm), 0.5 * (nu + nym), 0.5 * (nu + nzm))
        for c in range(3):
            total = None
            for axis in range(3):
                term = ups[axis] * (plus[axis][c] - u[c]) - downs[axis] * (u[c] - minus[axis][c])
                total = term if total is None else total + term
            out_ref[c, x] = u[c] + TIME_STEP_LES * (total - lamb[c])
            if mode == 1:
                lamb_ref[c, x] = lamb[c].astype(lamb_ref.dtype)
        return carry

    lax.fori_loop(0, size_x, step, 0)


def les_section_first(vel, nu, joint):
    return pl.pallas_call(
        lambda *refs: les_kernel(0, *refs),
        out_shape=(jax.ShapeDtypeStruct(vel.shape, jnp.float32),),
    )(vel, nu, *joint, *joint)[0]


def les_section_last(vel, nu, merged, joint):
    return pl.pallas_call(
        lambda *refs: les_kernel(1, *refs),
        out_shape=(jax.ShapeDtypeStruct(vel.shape, jnp.float32), jax.ShapeDtypeStruct(vel.shape, jnp.bfloat16)),
    )(vel, nu, *merged, *joint)


def halos(field, lead):
    flow_n = lax.axis_size("flow")
    grp_n = lax.axis_size("grp")
    up_f = [(i, i + 1) for i in range(flow_n - 1)]
    down_f = [(i + 1, i) for i in range(flow_n - 1)]
    up_g = [(i, i + 1) for i in range(grp_n - 1)]
    down_g = [(i + 1, i) for i in range(grp_n - 1)]
    size_x, size_y = field.shape[lead], field.shape[lead + 1]
    xlo = lax.ppermute(lax.index_in_dim(field, size_x - 1, lead, keepdims=False), "flow", up_f)
    xhi = lax.ppermute(lax.index_in_dim(field, 0, lead, keepdims=False), "flow", down_f)
    ylo = lax.ppermute(lax.slice_in_dim(field, size_y - 1, size_y, axis=lead + 1), "grp", up_g)
    yhi = lax.ppermute(lax.slice_in_dim(field, 0, 1, axis=lead + 1), "grp", down_g)
    return xlo, xhi, ylo, yhi


def project(lamb, projection):
    size_x, size_y, size_z = (lamb.shape[1], lamb.shape[2], lamb.shape[3])
    bx, by, bz = size_x // 8, size_y // 8, size_z // 8
    perm = np.zeros((size_z, size_z), np.float32)
    for ez in range(bz):
        for cz in range(8):
            perm[ez * 8 + cz, cz * bz + ez] = 1.0
    rows = lamb.reshape(-1, size_z)
    moved = jnp.dot(rows, jnp.asarray(perm, jnp.bfloat16), preferred_element_type=jnp.float32)
    moved = moved.astype(jnp.bfloat16)
    blocks = moved.reshape(3, bx, 8, by, 8, 8, bz).transpose(2, 4, 5, 0, 1, 3, 6).reshape(512, -1)
    padded_proj = jnp.pad(projection, ((0, 3), (0, 0)))
    source = jnp.dot(padded_proj, blocks, preferred_element_type=jnp.float32)
    source = source.reshape(128, 3, -1).transpose(1, 0, 2)
    return source.reshape(384, -1)


FACE_ROWS = 104


def extract_faces(state_ref, face_ref):
    for dim in range(3):
        for side, at in ((0, 0), (1, 4)):
            f = 2 * dim + side
            for comp in range(4):
                base = comp * 128
                if dim == 0:
                    face_ref[f, pl.ds(comp * 25, 25), :] = state_ref[pl.ds(base + at * 25, 25), :]
                elif dim == 1:
                    for a in range(5):
                        face_ref[f, pl.ds(comp * 25 + a * 5, 5), :] = state_ref[pl.ds(base + a * 25 + at * 5, 5), :]
                else:
                    face_ref[f, pl.ds(comp * 25, 25), :] = state_ref[pl.ds(base + at, 25, stride=5), :]


def send_faces(face_ref, sx0_ref, sx4_ref, sy0_ref, sy4_ref, row_len):
    sx0_ref[...] = face_ref[0]
    sx4_ref[...] = face_ref[1]
    sy0_ref[...] = face_ref[2][:, :row_len]
    last = pltpu.roll(face_ref[3], row_len, 1)
    sy4_ref[...] = last[:, :row_len]


def one_hot(shape, ids, axis):
    return jnp.where(lax.broadcasted_iota(jnp.int32, shape, axis) == ids, 1.0, 0.0).astype(jnp.float32)


def dg_faces_kernel(state_ref, vel_ref, mxup_ref, mxdn_ref, myup_ref, mydn_ref, face_ref):
    elems = state_ref.shape[1]
    face_ref[...] = jnp.zeros(face_ref.shape, jnp.float32)
    extract_faces(state_ref, face_ref)
    size_x, size_y, size_z = vel_ref.shape[1], vel_ref.shape[2], vel_ref.shape[3]
    half = size_z // 2
    row_len = size_z // 8
    for c in range(3):
        for h in range(2):
            mxup_ref[pl.ds(c * 2 * size_y + h * size_y, size_y), :] = vel_ref[c, size_x - 1, :, pl.ds(h * half, half)]
            mxdn_ref[pl.ds(c * 2 * size_y + h * size_y, size_y), :] = vel_ref[c, 0, :, pl.ds(h * half, half)]
            for x in range(size_x):
                at = c * 2 * size_x + h * size_x + x
                myup_ref[pl.ds(at, 1), :] = vel_ref[c, x, pl.ds(size_y - 1, 1), pl.ds(h * half, half)]
                mydn_ref[pl.ds(at, 1), :] = vel_ref[c, x, pl.ds(0, 1), pl.ds(h * half, half)]
    xrows = 3 * 2 * size_y
    yrows = 3 * 2 * size_x
    mxup_ref[pl.ds(xrows, FACE_ROWS), :] = face_ref[1]
    mxdn_ref[pl.ds(xrows, FACE_ROWS), :] = face_ref[0]
    lane = lax.broadcasted_iota(jnp.int32, (FACE_ROWS, elems), 1)
    myup_ref[pl.ds(yrows, FACE_ROWS), :] = jnp.where(lane < row_len, pltpu.roll(face_ref[3], row_len, 1), 0.0)
    mydn_ref[pl.ds(yrows, FACE_ROWS), :] = jnp.where(lane < row_len, face_ref[2], 0.0)


def dg_step_kernel(want_faces, xoff, yoff, row_len, state_ref, src_ref, xlo_ref, xhi_ref, ylo_ref, yhi_ref, own_ref, other_ref,
                   send_ref, out_ref, *rest):
    if want_faces:
        sx0_ref, sx4_ref, sy0_ref, sy4_ref, face_ref, oth_ref, pad_ref = rest
    else:
        face_ref, oth_ref, pad_ref = rest
    elems = state_ref.shape[1]
    lane = lax.broadcasted_iota(jnp.int32, (FACE_ROWS, elems), 1)
    ez = lane % row_len
    face_ref[...] = jnp.zeros(face_ref.shape, jnp.float32)
    oth_ref[...] = jnp.zeros(oth_ref.shape, jnp.float32)
    extract_faces(state_ref, face_ref)
    oth_ref[pl.ds(0, FACE_ROWS), :] = xlo_ref[pl.ds(xoff, FACE_ROWS), :]
    oth_ref[pl.ds(128, FACE_ROWS), :] = xhi_ref[pl.ds(xoff, FACE_ROWS), :]
    pad_ref[:, pl.ds(0, row_len)] = ylo_ref[pl.ds(yoff, FACE_ROWS), pl.ds(0, row_len)]
    oth_ref[pl.ds(256, FACE_ROWS), :] = jnp.where(
        lane < row_len, pad_ref[...], pltpu.roll(face_ref[3], row_len, 1))
    pad_ref[:, pl.ds(0, row_len)] = yhi_ref[pl.ds(yoff, FACE_ROWS), pl.ds(0, row_len)]
    oth_ref[pl.ds(384, FACE_ROWS), :] = jnp.where(
        lane >= elems - row_len, pltpu.roll(pad_ref[...], elems - row_len, 1),
        pltpu.roll(face_ref[2], elems - row_len, 1))
    oth_ref[pl.ds(512, FACE_ROWS), :] = jnp.where(ez == 0, 0.0, pltpu.roll(face_ref[5], 1, 1))
    oth_ref[pl.ds(640, FACE_ROWS), :] = jnp.where(
        ez == row_len - 1, 0.0, pltpu.roll(face_ref[4], elems - 1, 1))
    state = state_ref[...]
    rate = jnp.dot(own_ref[...], state, precision=HIGH, preferred_element_type=jnp.float32)
    rate = rate + jnp.dot(other_ref[...], oth_ref[...], precision=HIGH, preferred_element_type=jnp.float32)
    out_ref[pl.ds(0, 128), :] = state[:128] + TIME_STEP_ACOUSTIC * rate[:128]
    out_ref[pl.ds(128, 384), :] = state[128:] + TIME_STEP_ACOUSTIC * (rate[128:] - src_ref[...])
    if want_faces:
        extract_faces(out_ref, face_ref)
        send_faces(face_ref, sx0_ref, sx4_ref, sy0_ref, sy4_ref, row_len)


def face_shapes(elems, row_len):
    big = jax.ShapeDtypeStruct((FACE_ROWS, elems), jnp.float32)
    small = jax.ShapeDtypeStruct((FACE_ROWS, row_len), jnp.float32)
    return [big, big, small, small]


def dg_faces(state, vel):
    elems = state.shape[1]
    size_x, size_y, size_z = vel.shape[1], vel.shape[2], vel.shape[3]
    xbuf = jax.ShapeDtypeStruct((3 * 2 * size_y + FACE_ROWS, size_z // 2), jnp.float32)
    ybuf = jax.ShapeDtypeStruct((3 * 2 * size_x + FACE_ROWS, size_z // 2), jnp.float32)
    return pl.pallas_call(
        dg_faces_kernel,
        out_shape=(xbuf, xbuf, ybuf, ybuf),
        scratch_shapes=[pltpu.VMEM((6, FACE_ROWS, elems), jnp.float32)],
    )(state, vel)


def dg_step(state, src, recv, own_mat, other_mat, want_faces, row_len, xoff=0, yoff=0, sending=None):
    elems = state.shape[1]
    out_shape = [jax.ShapeDtypeStruct(state.shape, jnp.float32)]
    extra = [sending]
    if want_faces:
        out_shape += face_shapes(elems, row_len)
    res = pl.pallas_call(
        lambda *refs: dg_step_kernel(want_faces, xoff, yoff, row_len, *refs),
        out_shape=tuple(out_shape),
        scratch_shapes=[
            pltpu.VMEM((6, FACE_ROWS, elems), jnp.float32),
            pltpu.VMEM((768, elems), jnp.float32),
            pltpu.VMEM((FACE_ROWS, elems), jnp.float32),
        ],
    )(state, src, *recv, own_mat, other_mat, *extra)
    return res


def exchange_faces(sent):
    sx0, sx4, sy0, sy4 = sent
    flow_n = lax.axis_size("flow")
    grp_n = lax.axis_size("grp")
    up_f = [(i, i + 1) for i in range(flow_n - 1)]
    down_f = [(i + 1, i) for i in range(flow_n - 1)]
    up_g = [(i, i + 1) for i in range(grp_n - 1)]
    down_g = [(i + 1, i) for i in range(grp_n - 1)]
    return (
        lax.ppermute(sx4, "flow", up_f),
        lax.ppermute(sx0, "flow", down_f),
        lax.ppermute(sy4, "grp", up_g),
        lax.ppermute(sy0, "grp", down_g),
    )


def body(velocity, eddy_visc, projection, acoustic_state, route_send, route_place):
    joint = halos(jnp.concatenate([velocity, eddy_visc[None]], axis=0), 1)
    flow_size = lax.axis_size("flow")
    grp_size = lax.axis_size("grp")
    slot_cap = route_send.shape[2]
    elem_count = acoustic_state.shape[2]
    total_slots = flow_size * grp_size * slot_cap
    placing = route_place.reshape(-1)
    padded_state = jnp.pad(acoustic_state, ((0, 0), (0, 3), (0, 0))).reshape(512, elem_count)
    outgoing = jnp.zeros((512, total_slots), jnp.float32).at[:, placing].set(padded_state)
    arrived = lax.all_to_all(outgoing, ("flow", "grp"), split_axis=1, concat_axis=1, tiled=True)
    sending = route_send.reshape(-1)
    filled = sending >= 0
    target = jnp.where(filled, sending, elem_count)
    vel = les_section_first(velocity, eddy_visc, joint)
    state = jnp.zeros((512, elem_count), jnp.float32).at[:, target].set(arrived, mode="drop")

    row_len = velocity.shape[3] // 8
    own_np, other_np = dg_matrices()
    own_mat = jnp.asarray(own_np)
    other_mat = jnp.asarray(other_np)
    mxup, mxdn, myup, mydn = dg_faces(state, vel)
    merged = exchange_faces((mxdn, mxup, mydn, myup))
    vel, lamb = les_section_last(vel, eddy_visc, merged, joint)
    source = project(lamb, projection)
    xoff = 3 * 2 * velocity.shape[2]
    yoff = 3 * 2 * velocity.shape[1]
    slot_col = sending.reshape(-1, 1)
    res = dg_step(state, source, merged, own_mat, other_mat, True, row_len, xoff, yoff, sending=slot_col)
    state = res[0]
    recv = exchange_faces(res[1:])
    state = dg_step(state, source, recv, own_mat, other_mat, False, row_len, sending=slot_col)[0]
    leaving = jnp.where(filled[None, :], state[:, jnp.where(filled, sending, 0)], 0.0)
    returned = lax.all_to_all(leaving, ("flow", "grp"), split_axis=1, concat_axis=1, tiled=True)
    acoustic_out = returned[:, placing].reshape(4, 128, elem_count)[:, :125]
    return (vel, acoustic_out)


def solution(mesh):
    placed = (
        P(None, "flow", "grp", None),
        P("flow", "grp", None),
        P(),
        P(None, None, ("flow", "grp")),
        P(("flow", "grp"), None, None),
        P(("flow", "grp"), None),
    )
    return jax.shard_map(
        body,
        mesh=mesh,
        in_specs=placed,
        out_specs=(P(None, "flow", "grp", None), P(None, None, ("flow", "grp"))),
        check_vma=False,
    )
```

```python
import math

import jax
import jax.numpy as jnp
import numpy as np
from jax import lax
from jax.experimental import pallas as pl
from jax.experimental.pallas import tpu as pltpu
from jax.sharding import PartitionSpec as P

LES_SECTIONS = 2
AC_SECTIONS = 2


TIME_STEP_LES = 0.15
TIME_STEP_ACOUSTIC = 0.02
GEOMETRY = 2.0
LIFT_FACTOR = 20.0
HIGH = lax.Precision.HIGHEST
THREE_PASS = lax.Precision.HIGH


def gll_derivative():
    gll_nodes = np.array([-1.0, -math.sqrt(3.0 / 7.0), 0.0, math.sqrt(3.0 / 7.0), 1.0])
    bary_weights = np.array(
        [
            1.0
            / np.prod([gll_nodes[first] - gll_nodes[other] for other in range(5) if other != first])
            for first in range(5)
        ]
    )
    matrix = np.zeros((5, 5))
    for row_id in range(5):
        for col_id in range(5):
            if row_id != col_id:
                matrix[row_id, col_id] = (
                    bary_weights[col_id]
                    / bary_weights[row_id]
                    / (gll_nodes[row_id] - gll_nodes[col_id])
                )
    for row_id in range(5):
        matrix[row_id, row_id] = -matrix[row_id].sum()
    return matrix


def node_id(coords):
    return coords[0] * 25 + coords[1] * 5 + coords[2]


def face_nodes(dim, at):
    ids = []
    for first in range(5):
        for second in range(5):
            coords = [first, second]
            coords.insert(dim, at)
            ids.append(node_id(coords))
    return ids


def dg_matrices():
    dmat = gll_derivative()
    own = np.zeros((500, 500))
    for a in range(5):
        for b in range(5):
            for c in range(5):
                row = node_id((a, b, c))
                pos = (a, b, c)
                for dim in range(3):
                    for k in range(5):
                        col_pos = list(pos)
                        col_pos[dim] = k
                        col = node_id(col_pos)
                        weight = -GEOMETRY * dmat[pos[dim], k]
                        own[row, (1 + dim) * 125 + col] += weight
                        own[(1 + dim) * 125 + row, col] += weight
    half = LIFT_FACTOR * 0.5
    other = np.zeros((500, 600))
    face_order = []
    for dim in range(3):
        for sign, at in ((-1.0, 0), (1.0, 4)):
            face_order.append((dim, sign, at))
    for slot, (dim, sign, at) in enumerate(face_order):
        for t, node in enumerate(face_nodes(dim, at)):
            col = lambda comp: slot * 100 + comp * 25 + t
            own[node, (1 + dim) * 125 + node] += half * sign
            own[node, node] += -half
            other[node, col(1 + dim)] += -half * sign
            other[node, col(0)] += half
            for k in range(3):
                own[(1 + k) * 125 + node, (1 + k) * 125 + node] += -half
                other[(1 + k) * 125 + node, col(1 + k)] += half
            own[(1 + dim) * 125 + node, node] += half * sign
            other[(1 + dim) * 125 + node, col(0)] += -half * sign
    own_pad = np.zeros((512, 512), np.float32)
    other_pad = np.zeros((512, 768), np.float32)
    for ci in range(4):
        for cj in range(4):
            own_pad[ci * 128:ci * 128 + 125, cj * 128:cj * 128 + 125] = own[ci * 125:(ci + 1) * 125, cj * 125:(cj + 1) * 125]
        for slot in range(6):
            other_pad[ci * 128:ci * 128 + 125, slot * 128:slot * 128 + 100] = other[ci * 125:(ci + 1) * 125, slot * 100:(slot + 1) * 100]
    return own_pad, other_pad


def face_rows(state, dim, at):
    elems = state.shape[-1]
    cube = state.reshape(4, 5, 5, 5, elems)
    face = lax.index_in_dim(cube, at, axis=1 + dim, keepdims=False)
    return face.reshape(100, elems)


def les_kernel(mode, vel_ref, nu_ref, vxlo_ref, vxhi_ref, vylo_ref, vyhi_ref,
               nxlo_ref, nxhi_ref, nylo_ref, nyhi_ref, *rest):
    size_x, size_y, size_z = vel_ref.shape[1], vel_ref.shape[2], vel_ref.shape[3]
    half = size_z // 2
    row = lax.broadcasted_iota(jnp.int32, (size_y, size_z), 0)
    lane = lax.broadcasted_iota(jnp.int32, (size_y, size_z), 1)
    if mode == 0:
        sx0_ref, sx4_ref, sy0_ref, sy4_ref, out_ref, mxup_ref, mxdn_ref, myup_ref, mydn_ref = rest

        def xlo(c):
            return vxlo_ref[c]

        def xhi(c):
            return vxhi_ref[c]

        def ylo(c, x):
            return vylo_ref[c, x]

        def yhi(c, x):
            return vyhi_ref[c, x]
    else:
        out_ref, lamb_ref = rest

        def plane(ref, c):
            return jnp.concatenate(
                [ref[pl.ds(c * 2 * size_y, size_y), :], ref[pl.ds(c * 2 * size_y + size_y, size_y), :]], axis=1)

        def line(ref, c, x):
            return jnp.concatenate(
                [ref[pl.ds(c * 2 * size_x + x, 1), :], ref[pl.ds(c * 2 * size_x + size_x + x, 1), :]], axis=1)

        def xlo(c):
            return plane(vxlo_ref, c)

        def xhi(c):
            return plane(vxhi_ref, c)

        def ylo(c, x):
            return line(vylo_ref, c, x)

        def yhi(c, x):
            return line(vyhi_ref, c, x)

    def yp(f, halo):
        return jnp.where(row == size_y - 1, halo, pltpu.roll(f, size_y - 1, 0))

    def ym(f, halo):
        return jnp.where(row == 0, halo, pltpu.roll(f, 1, 0))

    def zp(f):
        return jnp.where(lane == size_z - 1, 0.0, pltpu.roll(f, size_z - 1, 1))

    def zm(f):
        return jnp.where(lane == 0, 0.0, pltpu.roll(f, 1, 1))

    def step(x, carry):
        lo = jnp.maximum(x - 1, 0)
        hi = jnp.minimum(x + 1, size_x - 1)
        u = [vel_ref[c, x] for c in range(3)]
        uxm = [jnp.where(x == 0, xlo(c), vel_ref[c, lo]) for c in range(3)]
        uxp = [jnp.where(x == size_x - 1, xhi(c), vel_ref[c, hi]) for c in range(3)]
        uym = [ym(u[c], ylo(c, x)) for c in range(3)]
        uyp = [yp(u[c], yhi(c, x)) for c in range(3)]
        uzm = [zm(u[c]) for c in range(3)]
        uzp = [zp(u[c]) for c in range(3)]
        nu = nu_ref[x]
        nxm = jnp.where(x == 0, nxlo_ref[3], nu_ref[lo])
        nxp = jnp.where(x == size_x - 1, nxhi_ref[3], nu_ref[hi])
        nym = ym(nu, nylo_ref[3, x])
        nyp = yp(nu, nyhi_ref[3, x])
        nzm = zm(nu)
        nzp = zp(nu)
        plus = (uxp, uyp, uzp)
        minus = (uxm, uym, uzm)

        def d(c, axis):
            return 0.5 * (plus[axis][c] - minus[axis][c])

        wx = d(2, 1) - d(1, 2)
        wy = d(0, 2) - d(2, 0)
        wz = d(1, 0) - d(0, 1)
        lamb = (wy * u[2] - wz * u[1], wz * u[0] - wx * u[2], wx * u[1] - wy * u[0])
        ups = (0.5 * (nu + nxp), 0.5 * (nu + nyp), 0.5 * (nu + nzp))
        downs = (0.5 * (nu + nxm), 0.5 * (nu + nym), 0.5 * (nu + nzm))
        for c in range(3):
            total = None
            for axis in range(3):
                term = ups[axis] * (plus[axis][c] - u[c]) - downs[axis] * (u[c] - minus[axis][c])
                total = term if total is None else total + term
            out_ref[c, x] = u[c] + TIME_STEP_LES * (total - lamb[c])
            if mode == 1:
                lamb_ref[c, x] = lamb[c].astype(lamb_ref.dtype)
        return carry

    lax.fori_loop(0, size_x, step, 0)
    if mode == 0:
        for c in range(3):
            for h in range(2):
                mxup_ref[pl.ds(c * 2 * size_y + h * size_y, size_y), :] = out_ref[c, size_x - 1, :, pl.ds(h * half, half)]
                mxdn_ref[pl.ds(c * 2 * size_y + h * size_y, size_y), :] = out_ref[c, 0, :, pl.ds(h * half, half)]
                for x in range(size_x):
                    at = c * 2 * size_x + h * size_x + x
                    myup_ref[pl.ds(at, 1), :] = out_ref[c, x, pl.ds(size_y - 1, 1), pl.ds(h * half, half)]
                    mydn_ref[pl.ds(at, 1), :] = out_ref[c, x, pl.ds(0, 1), pl.ds(h * half, half)]
        xrows = 3 * 2 * size_y
        yrows = 3 * 2 * size_x
        mxup_ref[pl.ds(xrows, FACE_ROWS), :] = sx4_ref[...]
        mxdn_ref[pl.ds(xrows, FACE_ROWS), :] = sx0_ref[...]
        zeros = jnp.zeros((FACE_ROWS, half), jnp.float32)
        myup_ref[pl.ds(yrows, FACE_ROWS), :] = zeros
        mydn_ref[pl.ds(yrows, FACE_ROWS), :] = zeros
        myup_ref[pl.ds(yrows, FACE_ROWS), pl.ds(0, sy4_ref.shape[1])] = sy4_ref[...]
        mydn_ref[pl.ds(yrows, FACE_ROWS), pl.ds(0, sy0_ref.shape[1])] = sy0_ref[...]


def les_section_first(vel, nu, joint, faces):
    size_x, size_y, size_z = vel.shape[1], vel.shape[2], vel.shape[3]
    xbuf = jax.ShapeDtypeStruct((3 * 2 * size_y + FACE_ROWS, size_z // 2), jnp.float32)
    ybuf = jax.ShapeDtypeStruct((3 * 2 * size_x + FACE_ROWS, size_z // 2), jnp.float32)
    return pl.pallas_call(
        lambda *refs: les_kernel(0, *refs),
        out_shape=(jax.ShapeDtypeStruct(vel.shape, jnp.float32), xbuf, xbuf, ybuf, ybuf),
    )(vel, nu, *joint, *joint, *faces)


def les_section_last(vel, nu, merged, joint):
    return pl.pallas_call(
        lambda *refs: les_kernel(1, *refs),
        out_shape=(jax.ShapeDtypeStruct(vel.shape, jnp.float32), jax.ShapeDtypeStruct(vel.shape, jnp.bfloat16)),
    )(vel, nu, *merged, *joint)


def halos(field, lead):
    flow_n = lax.axis_size("flow")
    grp_n = lax.axis_size("grp")
    up_f = [(i, i + 1) for i in range(flow_n - 1)]
    down_f = [(i + 1, i) for i in range(flow_n - 1)]
    up_g = [(i, i + 1) for i in range(grp_n - 1)]
    down_g = [(i + 1, i) for i in range(grp_n - 1)]
    size_x, size_y = field.shape[lead], field.shape[lead + 1]
    xlo = lax.ppermute(lax.index_in_dim(field, size_x - 1, lead, keepdims=False), "flow", up_f)
    xhi = lax.ppermute(lax.index_in_dim(field, 0, lead, keepdims=False), "flow", down_f)
    ylo = lax.ppermute(lax.slice_in_dim(field, size_y - 1, size_y, axis=lead + 1), "grp", up_g)
    yhi = lax.ppermute(lax.slice_in_dim(field, 0, 1, axis=lead + 1), "grp", down_g)
    return xlo, xhi, ylo, yhi


def project(lamb, projection):
    size_x, size_y, size_z = (lamb.shape[1], lamb.shape[2], lamb.shape[3])
    bx, by, bz = size_x // 8, size_y // 8, size_z // 8
    perm = np.zeros((size_z, size_z), np.float32)
    for ez in range(bz):
        for cz in range(8):
            perm[ez * 8 + cz, cz * bz + ez] = 1.0
    rows = lamb.reshape(-1, size_z)
    moved = jnp.dot(rows, jnp.asarray(perm, jnp.bfloat16), preferred_element_type=jnp.float32)
    moved = moved.astype(jnp.bfloat16)
    blocks = moved.reshape(3, bx, 8, by, 8, 8, bz).transpose(2, 4, 5, 0, 1, 3, 6).reshape(512, -1)
    padded_proj = jnp.pad(projection, ((0, 3), (0, 0)))
    source = jnp.dot(padded_proj, blocks, preferred_element_type=jnp.float32)
    source = source.reshape(128, 3, -1).transpose(1, 0, 2)
    return source.reshape(384, -1)


FACE_ROWS = 104


def extract_faces(state_ref, face_ref):
    for dim in range(3):
        for side, at in ((0, 0), (1, 4)):
            f = 2 * dim + side
            for comp in range(4):
                base = comp * 128
                if dim == 0:
                    face_ref[f, pl.ds(comp * 25, 25), :] = state_ref[pl.ds(base + at * 25, 25), :]
                elif dim == 1:
                    for a in range(5):
                        face_ref[f, pl.ds(comp * 25 + a * 5, 5), :] = state_ref[pl.ds(base + a * 25 + at * 5, 5), :]
                else:
                    face_ref[f, pl.ds(comp * 25, 25), :] = state_ref[pl.ds(base + at, 25, stride=5), :]


def send_faces(face_ref, sx0_ref, sx4_ref, sy0_ref, sy4_ref, row_len):
    sx0_ref[...] = face_ref[0]
    sx4_ref[...] = face_ref[1]
    sy0_ref[...] = face_ref[2][:, :row_len]
    last = pltpu.roll(face_ref[3], row_len, 1)
    sy4_ref[...] = last[:, :row_len]


def dg_faces_kernel(state_ref, sx0_ref, sx4_ref, sy0_ref, sy4_ref, face_ref):
    face_ref[...] = jnp.zeros(face_ref.shape, jnp.float32)
    extract_faces(state_ref, face_ref)
    send_faces(face_ref, sx0_ref, sx4_ref, sy0_ref, sy4_ref, sy0_ref.shape[1])


def dg_step_kernel(want_faces, xoff, yoff, row_len, state_ref, src_ref, xlo_ref, xhi_ref, ylo_ref, yhi_ref, own_ref, other_ref,
                   out_ref, *rest):
    if want_faces:
        sx0_ref, sx4_ref, sy0_ref, sy4_ref, face_ref, oth_ref, pad_ref = rest
    else:
        face_ref, oth_ref, pad_ref = rest
    elems = state_ref.shape[1]
    lane = lax.broadcasted_iota(jnp.int32, (FACE_ROWS, elems), 1)
    ez = lane % row_len
    face_ref[...] = jnp.zeros(face_ref.shape, jnp.float32)
    oth_ref[...] = jnp.zeros(oth_ref.shape, jnp.float32)
    extract_faces(state_ref, face_ref)
    oth_ref[pl.ds(0, FACE_ROWS), :] = xlo_ref[pl.ds(xoff, FACE_ROWS), :]
    oth_ref[pl.ds(128, FACE_ROWS), :] = xhi_ref[pl.ds(xoff, FACE_ROWS), :]
    pad_ref[:, pl.ds(0, row_len)] = ylo_ref[pl.ds(yoff, FACE_ROWS), pl.ds(0, row_len)]
    oth_ref[pl.ds(256, FACE_ROWS), :] = jnp.where(
        lane < row_len, pad_ref[...], pltpu.roll(face_ref[3], row_len, 1))
    pad_ref[:, pl.ds(0, row_len)] = yhi_ref[pl.ds(yoff, FACE_ROWS), pl.ds(0, row_len)]
    oth_ref[pl.ds(384, FACE_ROWS), :] = jnp.where(
        lane >= elems - row_len, pltpu.roll(pad_ref[...], elems - row_len, 1),
        pltpu.roll(face_ref[2], elems - row_len, 1))
    oth_ref[pl.ds(512, FACE_ROWS), :] = jnp.where(ez == 0, 0.0, pltpu.roll(face_ref[5], 1, 1))
    oth_ref[pl.ds(640, FACE_ROWS), :] = jnp.where(
        ez == row_len - 1, 0.0, pltpu.roll(face_ref[4], elems - 1, 1))
    state = state_ref[...]
    rate = jnp.dot(own_ref[...], state, precision=THREE_PASS, preferred_element_type=jnp.float32)
    rate = rate + jnp.dot(other_ref[...], oth_ref[...], precision=THREE_PASS, preferred_element_type=jnp.float32)
    out_ref[pl.ds(0, 128), :] = state[:128] + TIME_STEP_ACOUSTIC * rate[:128]
    out_ref[pl.ds(128, 384), :] = state[128:] + TIME_STEP_ACOUSTIC * (rate[128:] - src_ref[...])
    if want_faces:
        extract_faces(out_ref, face_ref)
        send_faces(face_ref, sx0_ref, sx4_ref, sy0_ref, sy4_ref, row_len)


def face_shapes(elems, row_len):
    big = jax.ShapeDtypeStruct((FACE_ROWS, elems), jnp.float32)
    small = jax.ShapeDtypeStruct((FACE_ROWS, row_len), jnp.float32)
    return [big, big, small, small]


def dg_faces(state, row_len):
    elems = state.shape[1]
    return pl.pallas_call(
        dg_faces_kernel,
        out_shape=tuple(face_shapes(elems, row_len)),
        scratch_shapes=[pltpu.VMEM((6, FACE_ROWS, elems), jnp.float32)],
    )(state)


def dg_step(state, src, recv, own_mat, other_mat, want_faces, row_len, xoff=0, yoff=0):
    elems = state.shape[1]
    out_shape = [jax.ShapeDtypeStruct(state.shape, jnp.float32)]
    if want_faces:
        out_shape += face_shapes(elems, row_len)
    res = pl.pallas_call(
        lambda *refs: dg_step_kernel(want_faces, xoff, yoff, row_len, *refs),
        out_shape=tuple(out_shape),
        scratch_shapes=[
            pltpu.VMEM((6, FACE_ROWS, elems), jnp.float32),
            pltpu.VMEM((768, elems), jnp.float32),
            pltpu.VMEM((FACE_ROWS, elems), jnp.float32),
        ],
    )(state, src, *recv, own_mat, other_mat)
    return res


def exchange_faces(sent):
    sx0, sx4, sy0, sy4 = sent
    flow_n = lax.axis_size("flow")
    grp_n = lax.axis_size("grp")
    up_f = [(i, i + 1) for i in range(flow_n - 1)]
    down_f = [(i + 1, i) for i in range(flow_n - 1)]
    up_g = [(i, i + 1) for i in range(grp_n - 1)]
    down_g = [(i + 1, i) for i in range(grp_n - 1)]
    return (
        lax.ppermute(sx4, "flow", up_f),
        lax.ppermute(sx0, "flow", down_f),
        lax.ppermute(sy4, "grp", up_g),
        lax.ppermute(sy0, "grp", down_g),
    )


def body(velocity, eddy_visc, projection, acoustic_state, route_send, route_place):
    joint = halos(jnp.concatenate([velocity, eddy_visc[None]], axis=0), 1)
    flow_size = lax.axis_size("flow")
    grp_size = lax.axis_size("grp")
    slot_cap = route_send.shape[2]
    elem_count = acoustic_state.shape[2]
    total_slots = flow_size * grp_size * slot_cap
    placing = route_place.reshape(-1)
    padded_state = jnp.pad(acoustic_state, ((0, 0), (0, 3), (0, 0))).reshape(512, elem_count)
    outgoing = jnp.zeros((512, total_slots), jnp.float32).at[:, placing].set(padded_state)
    arrived = lax.all_to_all(outgoing, ("flow", "grp"), split_axis=1, concat_axis=1, tiled=True)
    sending = route_send.reshape(-1)
    filled = sending >= 0
    target = jnp.where(filled, sending, elem_count)
    state = jnp.zeros((512, elem_count), jnp.float32).at[:, target].set(arrived, mode="drop")

    row_len = velocity.shape[3] // 8
    own_np, other_np = dg_matrices()
    own_mat = jnp.asarray(own_np)
    other_mat = jnp.asarray(other_np)
    sent = dg_faces(state, row_len)
    vel, mxup, mxdn, myup, mydn = les_section_first(velocity, eddy_visc, joint, sent)
    merged = exchange_faces((mxdn, mxup, mydn, myup))
    vel, lamb = les_section_last(vel, eddy_visc, merged, joint)
    source = project(lamb, projection)
    xoff = 3 * 2 * velocity.shape[2]
    yoff = 3 * 2 * velocity.shape[1]
    res = dg_step(state, source, merged, own_mat, other_mat, True, row_len, xoff, yoff)
    state = res[0]
    recv = exchange_faces(res[1:])
    state = dg_step(state, source, recv, own_mat, other_mat, False, row_len)[0]
    flat_state = state
    leaving = jnp.where(filled[None, :], flat_state[:, jnp.where(filled, sending, 0)], 0.0)
    returned = lax.all_to_all(leaving, ("flow", "grp"), split_axis=1, concat_axis=1, tiled=True)
    acoustic_out = returned[:, placing].reshape(4, 128, elem_count)[:, :125]
    return (vel, acoustic_out)


def solution(mesh):
    placed = (
        P(None, "flow", "grp", None),
        P("flow", "grp", None),
        P(),
        P(None, None, ("flow", "grp")),
        P(("flow", "grp"), None, None),
        P(("flow", "grp"), None),
    )
    return jax.shard_map(
        body,
        mesh=mesh,
        in_specs=placed,
        out_specs=(P(None, "flow", "grp", None), P(None, None, ("flow", "grp"))),
        check_vma=False,
    )
```

```python
import math

import jax
import jax.numpy as jnp
import numpy as np
from jax import lax
from jax.experimental import pallas as pl
from jax.experimental.pallas import tpu as pltpu
from jax.sharding import PartitionSpec as P

LES_SECTIONS = 2
AC_SECTIONS = 2


TIME_STEP_LES = 0.15
TIME_STEP_ACOUSTIC = 0.02
GEOMETRY = 2.0
LIFT_FACTOR = 20.0
HIGH = lax.Precision.HIGHEST
THREE_PASS = lax.Precision.HIGH


def gll_derivative():
    gll_nodes = np.array([-1.0, -math.sqrt(3.0 / 7.0), 0.0, math.sqrt(3.0 / 7.0), 1.0])
    bary_weights = np.array(
        [
            1.0
            / np.prod([gll_nodes[first] - gll_nodes[other] for other in range(5) if other != first])
            for first in range(5)
        ]
    )
    matrix = np.zeros((5, 5))
    for row_id in range(5):
        for col_id in range(5):
            if row_id != col_id:
                matrix[row_id, col_id] = (
                    bary_weights[col_id]
                    / bary_weights[row_id]
                    / (gll_nodes[row_id] - gll_nodes[col_id])
                )
    for row_id in range(5):
        matrix[row_id, row_id] = -matrix[row_id].sum()
    return matrix


def node_id(coords):
    return coords[0] * 25 + coords[1] * 5 + coords[2]


def face_nodes(dim, at):
    ids = []
    for first in range(5):
        for second in range(5):
            coords = [first, second]
            coords.insert(dim, at)
            ids.append(node_id(coords))
    return ids


def dg_matrices():
    dmat = gll_derivative()
    half = LIFT_FACTOR * 0.5
    apu = np.zeros((128, 384))
    aup = np.zeros((384, 128))
    diag = np.zeros((512, 1))
    lift = np.zeros((128, 152))
    for a in range(5):
        for b in range(5):
            for c in range(5):
                pos = (a, b, c)
                row = node_id(pos)
                for dim in range(3):
                    for k in range(5):
                        col_pos = list(pos)
                        col_pos[dim] = k
                        col = node_id(col_pos)
                        weight = -GEOMETRY * dmat[pos[dim], k]
                        apu[row, dim * 128 + col] += weight
                        aup[dim * 128 + row, col] += weight
    for dim in range(3):
        for side, (sign, at) in enumerate(((-1.0, 0), (1.0, 4))):
            f = 2 * dim + side
            for t, node in enumerate(face_nodes(dim, at)):
                apu[node, dim * 128 + node] += half * sign
                aup[dim * 128 + node, node] += half * sign
                for comp in range(4):
                    diag[comp * 128 + node, 0] += -half
                lift[node, f * 25 + t] = 1.0
    return (apu.astype(np.float32), aup.astype(np.float32), diag.astype(np.float32), lift.astype(np.float32))


def face_rows(state, dim, at):
    elems = state.shape[-1]
    cube = state.reshape(4, 5, 5, 5, elems)
    face = lax.index_in_dim(cube, at, axis=1 + dim, keepdims=False)
    return face.reshape(100, elems)


def les_kernel(mode, vel_ref, nu_ref, vxlo_ref, vxhi_ref, vylo_ref, vyhi_ref,
               nxlo_ref, nxhi_ref, nylo_ref, nyhi_ref, *rest):
    size_x, size_y, size_z = vel_ref.shape[1], vel_ref.shape[2], vel_ref.shape[3]
    half = size_z // 2
    row = lax.broadcasted_iota(jnp.int32, (size_y, size_z), 0)
    lane = lax.broadcasted_iota(jnp.int32, (size_y, size_z), 1)
    if mode == 0:
        sx0_ref, sx4_ref, sy0_ref, sy4_ref, out_ref, mxup_ref, mxdn_ref, myup_ref, mydn_ref = rest

        def xlo(c):
            return vxlo_ref[c]

        def xhi(c):
            return vxhi_ref[c]

        def ylo(c, x):
            return vylo_ref[c, x]

        def yhi(c, x):
            return vyhi_ref[c, x]
    else:
        out_ref, lamb_ref = rest

        def plane(ref, c):
            return jnp.concatenate(
                [ref[pl.ds(c * 2 * size_y, size_y), :], ref[pl.ds(c * 2 * size_y + size_y, size_y), :]], axis=1)

        def line(ref, c, x):
            return jnp.concatenate(
                [ref[pl.ds(c * 2 * size_x + x, 1), :], ref[pl.ds(c * 2 * size_x + size_x + x, 1), :]], axis=1)

        def xlo(c):
            return plane(vxlo_ref, c)

        def xhi(c):
            return plane(vxhi_ref, c)

        def ylo(c, x):
            return line(vylo_ref, c, x)

        def yhi(c, x):
            return line(vyhi_ref, c, x)

    def yp(f, halo):
        return jnp.where(row == size_y - 1, halo, pltpu.roll(f, size_y - 1, 0))

    def ym(f, halo):
        return jnp.where(row == 0, halo, pltpu.roll(f, 1, 0))

    def zp(f):
        return jnp.where(lane == size_z - 1, 0.0, pltpu.roll(f, size_z - 1, 1))

    def zm(f):
        return jnp.where(lane == 0, 0.0, pltpu.roll(f, 1, 1))

    def step(x, carry):
        lo = jnp.maximum(x - 1, 0)
        hi = jnp.minimum(x + 1, size_x - 1)
        u = [vel_ref[c, x] for c in range(3)]
        uxm = [jnp.where(x == 0, xlo(c), vel_ref[c, lo]) for c in range(3)]
        uxp = [jnp.where(x == size_x - 1, xhi(c), vel_ref[c, hi]) for c in range(3)]
        uym = [ym(u[c], ylo(c, x)) for c in range(3)]
        uyp = [yp(u[c], yhi(c, x)) for c in range(3)]
        uzm = [zm(u[c]) for c in range(3)]
        uzp = [zp(u[c]) for c in range(3)]
        nu = nu_ref[x]
        nxm = jnp.where(x == 0, nxlo_ref[3], nu_ref[lo])
        nxp = jnp.where(x == size_x - 1, nxhi_ref[3], nu_ref[hi])
        nym = ym(nu, nylo_ref[3, x])
        nyp = yp(nu, nyhi_ref[3, x])
        nzm = zm(nu)
        nzp = zp(nu)
        plus = (uxp, uyp, uzp)
        minus = (uxm, uym, uzm)

        def d(c, axis):
            return 0.5 * (plus[axis][c] - minus[axis][c])

        wx = d(2, 1) - d(1, 2)
        wy = d(0, 2) - d(2, 0)
        wz = d(1, 0) - d(0, 1)
        lamb = (wy * u[2] - wz * u[1], wz * u[0] - wx * u[2], wx * u[1] - wy * u[0])
        ups = (0.5 * (nu + nxp), 0.5 * (nu + nyp), 0.5 * (nu + nzp))
        downs = (0.5 * (nu + nxm), 0.5 * (nu + nym), 0.5 * (nu + nzm))
        for c in range(3):
            total = None
            for axis in range(3):
                term = ups[axis] * (plus[axis][c] - u[c]) - downs[axis] * (u[c] - minus[axis][c])
                total = term if total is None else total + term
            out_ref[c, x] = u[c] + TIME_STEP_LES * (total - lamb[c])
            if mode == 1:
                lamb_ref[c, x] = lamb[c].astype(lamb_ref.dtype)
        return carry

    lax.fori_loop(0, size_x, step, 0)
    if mode == 0:
        for c in range(3):
            for h in range(2):
                mxup_ref[pl.ds(c * 2 * size_y + h * size_y, size_y), :] = out_ref[c, size_x - 1, :, pl.ds(h * half, half)]
                mxdn_ref[pl.ds(c * 2 * size_y + h * size_y, size_y), :] = out_ref[c, 0, :, pl.ds(h * half, half)]
                for x in range(size_x):
                    at = c * 2 * size_x + h * size_x + x
                    myup_ref[pl.ds(at, 1), :] = out_ref[c, x, pl.ds(size_y - 1, 1), pl.ds(h * half, half)]
                    mydn_ref[pl.ds(at, 1), :] = out_ref[c, x, pl.ds(0, 1), pl.ds(h * half, half)]
        xrows = 3 * 2 * size_y
        yrows = 3 * 2 * size_x
        mxup_ref[pl.ds(xrows, FACE_ROWS), :] = sx4_ref[...]
        mxdn_ref[pl.ds(xrows, FACE_ROWS), :] = sx0_ref[...]
        zeros = jnp.zeros((FACE_ROWS, half), jnp.float32)
        myup_ref[pl.ds(yrows, FACE_ROWS), :] = zeros
        mydn_ref[pl.ds(yrows, FACE_ROWS), :] = zeros
        myup_ref[pl.ds(yrows, FACE_ROWS), pl.ds(0, sy4_ref.shape[1])] = sy4_ref[...]
        mydn_ref[pl.ds(yrows, FACE_ROWS), pl.ds(0, sy0_ref.shape[1])] = sy0_ref[...]


def les_section_first(vel, nu, joint, faces):
    size_x, size_y, size_z = vel.shape[1], vel.shape[2], vel.shape[3]
    xbuf = jax.ShapeDtypeStruct((3 * 2 * size_y + FACE_ROWS, size_z // 2), jnp.float32)
    ybuf = jax.ShapeDtypeStruct((3 * 2 * size_x + FACE_ROWS, size_z // 2), jnp.float32)
    return pl.pallas_call(
        lambda *refs: les_kernel(0, *refs),
        out_shape=(jax.ShapeDtypeStruct(vel.shape, jnp.float32), xbuf, xbuf, ybuf, ybuf),
    )(vel, nu, *joint, *joint, *faces)


def les_section_last(vel, nu, merged, joint):
    return pl.pallas_call(
        lambda *refs: les_kernel(1, *refs),
        out_shape=(jax.ShapeDtypeStruct(vel.shape, jnp.float32), jax.ShapeDtypeStruct(vel.shape, jnp.bfloat16)),
    )(vel, nu, *merged, *joint)


def halos(field, lead):
    flow_n = lax.axis_size("flow")
    grp_n = lax.axis_size("grp")
    up_f = [(i, i + 1) for i in range(flow_n - 1)]
    down_f = [(i + 1, i) for i in range(flow_n - 1)]
    up_g = [(i, i + 1) for i in range(grp_n - 1)]
    down_g = [(i + 1, i) for i in range(grp_n - 1)]
    size_x, size_y = field.shape[lead], field.shape[lead + 1]
    xlo = lax.ppermute(lax.index_in_dim(field, size_x - 1, lead, keepdims=False), "flow", up_f)
    xhi = lax.ppermute(lax.index_in_dim(field, 0, lead, keepdims=False), "flow", down_f)
    ylo = lax.ppermute(lax.slice_in_dim(field, size_y - 1, size_y, axis=lead + 1), "grp", up_g)
    yhi = lax.ppermute(lax.slice_in_dim(field, 0, 1, axis=lead + 1), "grp", down_g)
    return xlo, xhi, ylo, yhi


def project(lamb, projection):
    size_x, size_y, size_z = (lamb.shape[1], lamb.shape[2], lamb.shape[3])
    bx, by, bz = size_x // 8, size_y // 8, size_z // 8
    perm = np.zeros((size_z, size_z), np.float32)
    for ez in range(bz):
        for cz in range(8):
            perm[ez * 8 + cz, cz * bz + ez] = 1.0
    rows = lamb.reshape(-1, size_z)
    moved = jnp.dot(rows, jnp.asarray(perm, jnp.bfloat16), preferred_element_type=jnp.float32)
    moved = moved.astype(jnp.bfloat16)
    blocks = moved.reshape(3, bx, 8, by, 8, 8, bz).transpose(2, 4, 5, 0, 1, 3, 6).reshape(512, -1)
    padded_proj = jnp.pad(projection, ((0, 3), (0, 0)))
    source = jnp.dot(padded_proj, blocks, preferred_element_type=jnp.float32)
    source = source.reshape(128, 3, -1).transpose(1, 0, 2)
    return source.reshape(384, -1)


FACE_ROWS = 104


def extract_faces(state_ref, face_ref):
    for dim in range(3):
        for side, at in ((0, 0), (1, 4)):
            f = 2 * dim + side
            for comp in range(4):
                base = comp * 128
                if dim == 0:
                    face_ref[f, pl.ds(comp * 25, 25), :] = state_ref[pl.ds(base + at * 25, 25), :]
                elif dim == 1:
                    for a in range(5):
                        face_ref[f, pl.ds(comp * 25 + a * 5, 5), :] = state_ref[pl.ds(base + a * 25 + at * 5, 5), :]
                else:
                    face_ref[f, pl.ds(comp * 25, 25), :] = state_ref[pl.ds(base + at, 25, stride=5), :]


def send_faces(face_ref, sx0_ref, sx4_ref, sy0_ref, sy4_ref, row_len):
    sx0_ref[...] = face_ref[0]
    sx4_ref[...] = face_ref[1]
    sy0_ref[...] = face_ref[2][:, :row_len]
    last = pltpu.roll(face_ref[3], row_len, 1)
    sy4_ref[...] = last[:, :row_len]


def dg_faces_kernel(state_ref, sx0_ref, sx4_ref, sy0_ref, sy4_ref, face_ref):
    face_ref[...] = jnp.zeros(face_ref.shape, jnp.float32)
    extract_faces(state_ref, face_ref)
    send_faces(face_ref, sx0_ref, sx4_ref, sy0_ref, sy4_ref, sy0_ref.shape[1])


def dg_step_kernel(want_faces, xoff, yoff, row_len, state_ref, src_ref, xlo_ref, xhi_ref, ylo_ref, yhi_ref,
                   apu_ref, aup_ref, diag_ref, lift_ref, out_ref, *rest):
    if want_faces:
        sx0_ref, sx4_ref, sy0_ref, sy4_ref, face_ref, oth_ref, pad_ref, g_ref = rest
    else:
        face_ref, oth_ref, pad_ref, g_ref = rest
    elems = state_ref.shape[1]
    lane = lax.broadcasted_iota(jnp.int32, (FACE_ROWS, elems), 1)
    ez = lane % row_len
    face_ref[...] = jnp.zeros(face_ref.shape, jnp.float32)
    oth_ref[...] = jnp.zeros(oth_ref.shape, jnp.float32)
    extract_faces(state_ref, face_ref)
    oth_ref[pl.ds(0, FACE_ROWS), :] = xlo_ref[pl.ds(xoff, FACE_ROWS), :]
    oth_ref[pl.ds(128, FACE_ROWS), :] = xhi_ref[pl.ds(xoff, FACE_ROWS), :]
    pad_ref[:, pl.ds(0, row_len)] = ylo_ref[pl.ds(yoff, FACE_ROWS), pl.ds(0, row_len)]
    oth_ref[pl.ds(256, FACE_ROWS), :] = jnp.where(
        lane < row_len, pad_ref[...], pltpu.roll(face_ref[3], row_len, 1))
    pad_ref[:, pl.ds(0, row_len)] = yhi_ref[pl.ds(yoff, FACE_ROWS), pl.ds(0, row_len)]
    oth_ref[pl.ds(384, FACE_ROWS), :] = jnp.where(
        lane >= elems - row_len, pltpu.roll(pad_ref[...], elems - row_len, 1),
        pltpu.roll(face_ref[2], elems - row_len, 1))
    oth_ref[pl.ds(512, FACE_ROWS), :] = jnp.where(ez == 0, 0.0, pltpu.roll(face_ref[5], 1, 1))
    oth_ref[pl.ds(640, FACE_ROWS), :] = jnp.where(
        ez == row_len - 1, 0.0, pltpu.roll(face_ref[4], elems - 1, 1))
    g_ref[pl.ds(144, 8), :] = jnp.zeros((8, 4 * elems), jnp.float32)
    half = LIFT_FACTOR * 0.5
    for dim in range(3):
        for side, sign in ((0, -1.0), (1, 1.0)):
            f = 2 * dim + side
            o_p = oth_ref[pl.ds(f * 128, 25), :]
            o_u = [oth_ref[pl.ds(f * 128 + (1 + k) * 25, 25), :] for k in range(3)]
            g_ref[pl.ds(f * 25, 25), pl.ds(0, elems)] = half * (o_p - sign * o_u[dim])
            for k in range(3):
                value = half * o_u[k]
                if k == dim:
                    value = value - half * sign * o_p
                g_ref[pl.ds(f * 25, 25), pl.ds((1 + k) * elems, elems)] = value
    faces = jnp.dot(lift_ref[...], g_ref[...], precision=THREE_PASS, preferred_element_type=jnp.float32)
    state = state_ref[...]
    pres = state[:128]
    vel = state[128:]
    rate_p = jnp.dot(apu_ref[...], vel, precision=THREE_PASS, preferred_element_type=jnp.float32)
    rate_p = rate_p + diag_ref[pl.ds(0, 128), :] * pres + faces[:, :elems]
    out_ref[pl.ds(0, 128), :] = pres + TIME_STEP_ACOUSTIC * rate_p
    rate_u = jnp.dot(aup_ref[...], pres, precision=THREE_PASS, preferred_element_type=jnp.float32)
    for k in range(3):
        rows = pl.ds(128 + k * 128, 128)
        rate_k = rate_u[k * 128:(k + 1) * 128] + diag_ref[rows, :] * state_ref[rows, :]
        rate_k = rate_k + faces[:, (1 + k) * elems:(2 + k) * elems]
        out_ref[rows, :] = state_ref[rows, :] + TIME_STEP_ACOUSTIC * (rate_k - src_ref[pl.ds(k * 128, 128), :])
    if want_faces:
        extract_faces(out_ref, face_ref)
        send_faces(face_ref, sx0_ref, sx4_ref, sy0_ref, sy4_ref, row_len)


def face_shapes(elems, row_len):
    big = jax.ShapeDtypeStruct((FACE_ROWS, elems), jnp.float32)
    small = jax.ShapeDtypeStruct((FACE_ROWS, row_len), jnp.float32)
    return [big, big, small, small]


def dg_faces(state, row_len):
    elems = state.shape[1]
    return pl.pallas_call(
        dg_faces_kernel,
        out_shape=tuple(face_shapes(elems, row_len)),
        scratch_shapes=[pltpu.VMEM((6, FACE_ROWS, elems), jnp.float32)],
    )(state)


def dg_step(state, src, recv, mats, want_faces, row_len, xoff=0, yoff=0):
    elems = state.shape[1]
    out_shape = [jax.ShapeDtypeStruct(state.shape, jnp.float32)]
    if want_faces:
        out_shape += face_shapes(elems, row_len)
    res = pl.pallas_call(
        lambda *refs: dg_step_kernel(want_faces, xoff, yoff, row_len, *refs),
        out_shape=tuple(out_shape),
        scratch_shapes=[
            pltpu.VMEM((6, FACE_ROWS, elems), jnp.float32),
            pltpu.VMEM((768, elems), jnp.float32),
            pltpu.VMEM((FACE_ROWS, elems), jnp.float32),
            pltpu.VMEM((152, 4 * elems), jnp.float32),
        ],
    )(state, src, *recv, *mats)
    return res


def exchange_faces(sent):
    sx0, sx4, sy0, sy4 = sent
    flow_n = lax.axis_size("flow")
    grp_n = lax.axis_size("grp")
    up_f = [(i, i + 1) for i in range(flow_n - 1)]
    down_f = [(i + 1, i) for i in range(flow_n - 1)]
    up_g = [(i, i + 1) for i in range(grp_n - 1)]
    down_g = [(i + 1, i) for i in range(grp_n - 1)]
    return (
        lax.ppermute(sx4, "flow", up_f),
        lax.ppermute(sx0, "flow", down_f),
        lax.ppermute(sy4, "grp", up_g),
        lax.ppermute(sy0, "grp", down_g),
    )


def body(velocity, eddy_visc, projection, acoustic_state, route_send, route_place):
    joint = halos(jnp.concatenate([velocity, eddy_visc[None]], axis=0), 1)
    flow_size = lax.axis_size("flow")
    grp_size = lax.axis_size("grp")
    slot_cap = route_send.shape[2]
    elem_count = acoustic_state.shape[2]
    total_slots = flow_size * grp_size * slot_cap
    placing = route_place.reshape(-1)
    padded_state = jnp.pad(acoustic_state, ((0, 0), (0, 3), (0, 0))).reshape(512, elem_count)
    outgoing = jnp.zeros((512, total_slots), jnp.float32).at[:, placing].set(padded_state)
    arrived = lax.all_to_all(outgoing, ("flow", "grp"), split_axis=1, concat_axis=1, tiled=True)
    sending = route_send.reshape(-1)
    filled = sending >= 0
    target = jnp.where(filled, sending, elem_count)
    state = jnp.zeros((512, elem_count), jnp.float32).at[:, target].set(arrived, mode="drop")

    row_len = velocity.shape[3] // 8
    mats = [jnp.asarray(m) for m in dg_matrices()]
    sent = dg_faces(state, row_len)
    vel, mxup, mxdn, myup, mydn = les_section_first(velocity, eddy_visc, joint, sent)
    merged = exchange_faces((mxdn, mxup, mydn, myup))
    vel, lamb = les_section_last(vel, eddy_visc, merged, joint)
    source = project(lamb, projection)
    xoff = 3 * 2 * velocity.shape[2]
    yoff = 3 * 2 * velocity.shape[1]
    res = dg_step(state, source, merged, mats, True, row_len, xoff, yoff)
    state = res[0]
    recv = exchange_faces(res[1:])
    state = dg_step(state, source, recv, mats, False, row_len)[0]
    flat_state = state
    leaving = jnp.where(filled[None, :], flat_state[:, jnp.where(filled, sending, 0)], 0.0)
    returned = lax.all_to_all(leaving, ("flow", "grp"), split_axis=1, concat_axis=1, tiled=True)
    acoustic_out = returned[:, placing].reshape(4, 128, elem_count)[:, :125]
    return (vel, acoustic_out)


def solution(mesh):
    placed = (
        P(None, "flow", "grp", None),
        P("flow", "grp", None),
        P(),
        P(None, None, ("flow", "grp")),
        P(("flow", "grp"), None, None),
        P(("flow", "grp"), None),
    )
    return jax.shard_map(
        body,
        mesh=mesh,
        in_specs=placed,
        out_specs=(P(None, "flow", "grp", None), P(None, None, ("flow", "grp"))),
        check_vma=False,
    )
```

```python
import math

import jax
import jax.numpy as jnp
import numpy as np
from jax import lax
from jax.experimental import pallas as pl
from jax.experimental.pallas import tpu as pltpu
from jax.sharding import PartitionSpec as P

LES_SECTIONS = 2
AC_SECTIONS = 2


TIME_STEP_LES = 0.15
TIME_STEP_ACOUSTIC = 0.02
GEOMETRY = 2.0
LIFT_FACTOR = 20.0
HIGH = lax.Precision.HIGHEST
THREE_PASS = lax.Precision.HIGH


def gll_derivative():
    gll_nodes = np.array([-1.0, -math.sqrt(3.0 / 7.0), 0.0, math.sqrt(3.0 / 7.0), 1.0])
    bary_weights = np.array(
        [
            1.0
            / np.prod([gll_nodes[first] - gll_nodes[other] for other in range(5) if other != first])
            for first in range(5)
        ]
    )
    matrix = np.zeros((5, 5))
    for row_id in range(5):
        for col_id in range(5):
            if row_id != col_id:
                matrix[row_id, col_id] = (
                    bary_weights[col_id]
                    / bary_weights[row_id]
                    / (gll_nodes[row_id] - gll_nodes[col_id])
                )
    for row_id in range(5):
        matrix[row_id, row_id] = -matrix[row_id].sum()
    return matrix


def node_id(coords):
    return coords[0] * 25 + coords[1] * 5 + coords[2]


def face_nodes(dim, at):
    ids = []
    for first in range(5):
        for second in range(5):
            coords = [first, second]
            coords.insert(dim, at)
            ids.append(node_id(coords))
    return ids


def dg_matrices():
    dmat = gll_derivative()
    half = LIFT_FACTOR * 0.5
    apu = np.zeros((128, 384))
    aup = np.zeros((384, 128))
    diag = np.zeros((512, 1))
    lift = np.zeros((128, 152))
    for a in range(5):
        for b in range(5):
            for c in range(5):
                pos = (a, b, c)
                row = node_id(pos)
                for dim in range(3):
                    for k in range(5):
                        col_pos = list(pos)
                        col_pos[dim] = k
                        col = node_id(col_pos)
                        weight = -GEOMETRY * dmat[pos[dim], k]
                        apu[row, dim * 128 + col] += weight
                        aup[dim * 128 + row, col] += weight
    for dim in range(3):
        for side, (sign, at) in enumerate(((-1.0, 0), (1.0, 4))):
            f = 2 * dim + side
            for t, node in enumerate(face_nodes(dim, at)):
                apu[node, dim * 128 + node] += half * sign
                aup[dim * 128 + node, node] += half * sign
                for comp in range(4):
                    diag[comp * 128 + node, 0] += -half
                lift[node, f * 25 + t] = 1.0
    return (apu.astype(np.float32), aup.astype(np.float32), diag.astype(np.float32), lift.astype(np.float32))


def face_rows(state, dim, at):
    elems = state.shape[-1]
    cube = state.reshape(4, 5, 5, 5, elems)
    face = lax.index_in_dim(cube, at, axis=1 + dim, keepdims=False)
    return face.reshape(100, elems)


def les_kernel(mode, vel_ref, nu_ref, vxlo_ref, vxhi_ref, vylo_ref, vyhi_ref,
               nxlo_ref, nxhi_ref, nylo_ref, nyhi_ref, *rest):
    size_x, size_y, size_z = vel_ref.shape[1], vel_ref.shape[2], vel_ref.shape[3]
    half = size_z // 2
    row = lax.broadcasted_iota(jnp.int32, (size_y, size_z), 0)
    lane = lax.broadcasted_iota(jnp.int32, (size_y, size_z), 1)
    if mode == 0:
        sx0_ref, sx4_ref, sy0_ref, sy4_ref, out_ref, mxup_ref, mxdn_ref, myup_ref, mydn_ref = rest

        def xlo(c):
            return vxlo_ref[c]

        def xhi(c):
            return vxhi_ref[c]

        def ylo(c, x):
            return vylo_ref[c, x]

        def yhi(c, x):
            return vyhi_ref[c, x]
    else:
        out_ref, lamb_ref = rest

        def plane(ref, c):
            return jnp.concatenate(
                [ref[pl.ds(c * 2 * size_y, size_y), :], ref[pl.ds(c * 2 * size_y + size_y, size_y), :]], axis=1)

        def line(ref, c, x):
            return jnp.concatenate(
                [ref[pl.ds(c * 2 * size_x + x, 1), :], ref[pl.ds(c * 2 * size_x + size_x + x, 1), :]], axis=1)

        def xlo(c):
            return plane(vxlo_ref, c)

        def xhi(c):
            return plane(vxhi_ref, c)

        def ylo(c, x):
            return line(vylo_ref, c, x)

        def yhi(c, x):
            return line(vyhi_ref, c, x)

    def yp(f, halo):
        return jnp.where(row == size_y - 1, halo, pltpu.roll(f, size_y - 1, 0))

    def ym(f, halo):
        return jnp.where(row == 0, halo, pltpu.roll(f, 1, 0))

    def zp(f):
        return jnp.where(lane == size_z - 1, 0.0, pltpu.roll(f, size_z - 1, 1))

    def zm(f):
        return jnp.where(lane == 0, 0.0, pltpu.roll(f, 1, 1))

    def step(x, carry):
        lo = jnp.maximum(x - 1, 0)
        hi = jnp.minimum(x + 1, size_x - 1)
        u = [vel_ref[c, x] for c in range(3)]
        uxm = [jnp.where(x == 0, xlo(c), vel_ref[c, lo]) for c in range(3)]
        uxp = [jnp.where(x == size_x - 1, xhi(c), vel_ref[c, hi]) for c in range(3)]
        uym = [ym(u[c], ylo(c, x)) for c in range(3)]
        uyp = [yp(u[c], yhi(c, x)) for c in range(3)]
        uzm = [zm(u[c]) for c in range(3)]
        uzp = [zp(u[c]) for c in range(3)]
        nu = nu_ref[x]
        nxm = jnp.where(x == 0, nxlo_ref[3], nu_ref[lo])
        nxp = jnp.where(x == size_x - 1, nxhi_ref[3], nu_ref[hi])
        nym = ym(nu, nylo_ref[3, x])
        nyp = yp(nu, nyhi_ref[3, x])
        nzm = zm(nu)
        nzp = zp(nu)
        plus = (uxp, uyp, uzp)
        minus = (uxm, uym, uzm)

        def d(c, axis):
            return 0.5 * (plus[axis][c] - minus[axis][c])

        wx = d(2, 1) - d(1, 2)
        wy = d(0, 2) - d(2, 0)
        wz = d(1, 0) - d(0, 1)
        lamb = (wy * u[2] - wz * u[1], wz * u[0] - wx * u[2], wx * u[1] - wy * u[0])
        ups = (0.5 * (nu + nxp), 0.5 * (nu + nyp), 0.5 * (nu + nzp))
        downs = (0.5 * (nu + nxm), 0.5 * (nu + nym), 0.5 * (nu + nzm))
        for c in range(3):
            total = None
            for axis in range(3):
                term = ups[axis] * (plus[axis][c] - u[c]) - downs[axis] * (u[c] - minus[axis][c])
                total = term if total is None else total + term
            out_ref[c, x] = u[c] + TIME_STEP_LES * (total - lamb[c])
            if mode == 1:
                lamb_ref[c, x] = lamb[c].astype(lamb_ref.dtype)
        return carry

    lax.fori_loop(0, size_x, step, 0)
    if mode == 0:
        for c in range(3):
            for h in range(2):
                mxup_ref[pl.ds(c * 2 * size_y + h * size_y, size_y), :] = out_ref[c, size_x - 1, :, pl.ds(h * half, half)]
                mxdn_ref[pl.ds(c * 2 * size_y + h * size_y, size_y), :] = out_ref[c, 0, :, pl.ds(h * half, half)]
                for x in range(size_x):
                    at = c * 2 * size_x + h * size_x + x
                    myup_ref[pl.ds(at, 1), :] = out_ref[c, x, pl.ds(size_y - 1, 1), pl.ds(h * half, half)]
                    mydn_ref[pl.ds(at, 1), :] = out_ref[c, x, pl.ds(0, 1), pl.ds(h * half, half)]
        xrows = 3 * 2 * size_y
        yrows = 3 * 2 * size_x
        mxup_ref[pl.ds(xrows, FACE_ROWS), :] = sx4_ref[...]
        mxdn_ref[pl.ds(xrows, FACE_ROWS), :] = sx0_ref[...]
        zeros = jnp.zeros((FACE_ROWS, half), jnp.float32)
        myup_ref[pl.ds(yrows, FACE_ROWS), :] = zeros
        mydn_ref[pl.ds(yrows, FACE_ROWS), :] = zeros
        myup_ref[pl.ds(yrows, FACE_ROWS), pl.ds(0, sy4_ref.shape[1])] = sy4_ref[...]
        mydn_ref[pl.ds(yrows, FACE_ROWS), pl.ds(0, sy0_ref.shape[1])] = sy0_ref[...]


def les_section_first(vel, nu, joint, faces):
    size_x, size_y, size_z = vel.shape[1], vel.shape[2], vel.shape[3]
    xbuf = jax.ShapeDtypeStruct((3 * 2 * size_y + FACE_ROWS, size_z // 2), jnp.float32)
    ybuf = jax.ShapeDtypeStruct((3 * 2 * size_x + FACE_ROWS, size_z // 2), jnp.float32)
    return pl.pallas_call(
        lambda *refs: les_kernel(0, *refs),
        out_shape=(jax.ShapeDtypeStruct(vel.shape, jnp.float32), xbuf, xbuf, ybuf, ybuf),
    )(vel, nu, *joint, *joint, *faces)


def les_section_last(vel, nu, merged, joint):
    return pl.pallas_call(
        lambda *refs: les_kernel(1, *refs),
        out_shape=(jax.ShapeDtypeStruct(vel.shape, jnp.float32), jax.ShapeDtypeStruct(vel.shape, jnp.bfloat16)),
    )(vel, nu, *merged, *joint)


def halos(field, lead):
    flow_n = lax.axis_size("flow")
    grp_n = lax.axis_size("grp")
    up_f = [(i, i + 1) for i in range(flow_n - 1)]
    down_f = [(i + 1, i) for i in range(flow_n - 1)]
    up_g = [(i, i + 1) for i in range(grp_n - 1)]
    down_g = [(i + 1, i) for i in range(grp_n - 1)]
    size_x, size_y = field.shape[lead], field.shape[lead + 1]
    xlo = lax.ppermute(lax.index_in_dim(field, size_x - 1, lead, keepdims=False), "flow", up_f)
    xhi = lax.ppermute(lax.index_in_dim(field, 0, lead, keepdims=False), "flow", down_f)
    ylo = lax.ppermute(lax.slice_in_dim(field, size_y - 1, size_y, axis=lead + 1), "grp", up_g)
    yhi = lax.ppermute(lax.slice_in_dim(field, 0, 1, axis=lead + 1), "grp", down_g)
    return xlo, xhi, ylo, yhi


def project(lamb, projection):
    size_x, size_y, size_z = (lamb.shape[1], lamb.shape[2], lamb.shape[3])
    bx, by, bz = size_x // 8, size_y // 8, size_z // 8
    perm = np.zeros((size_z, size_z), np.float32)
    for ez in range(bz):
        for cz in range(8):
            perm[ez * 8 + cz, cz * bz + ez] = 1.0
    rows = lamb.reshape(-1, size_z)
    moved = jnp.dot(rows, jnp.asarray(perm, jnp.bfloat16), preferred_element_type=jnp.float32)
    moved = moved.astype(jnp.bfloat16)
    blocks = moved.reshape(3, bx, 8, by, 8, 8, bz).transpose(2, 4, 5, 0, 1, 3, 6).reshape(512, -1)
    padded_proj = jnp.pad(projection, ((0, 3), (0, 0)))
    source = jnp.dot(padded_proj, blocks, preferred_element_type=jnp.float32)
    source = source.reshape(128, 3, -1).transpose(1, 0, 2)
    return source.reshape(384, -1)


FACE_ROWS = 104


def extract_faces(state_ref, face_ref):
    for dim in range(3):
        for side, at in ((0, 0), (1, 4)):
            f = 2 * dim + side
            for comp in range(4):
                base = comp * 128
                if dim == 0:
                    face_ref[f, pl.ds(comp * 25, 25), :] = state_ref[pl.ds(base + at * 25, 25), :]
                elif dim == 1:
                    for a in range(5):
                        face_ref[f, pl.ds(comp * 25 + a * 5, 5), :] = state_ref[pl.ds(base + a * 25 + at * 5, 5), :]
                else:
                    face_ref[f, pl.ds(comp * 25, 25), :] = state_ref[pl.ds(base + at, 25, stride=5), :]


def send_faces(face_ref, sx0_ref, sx4_ref, sy0_ref, sy4_ref, row_len):
    sx0_ref[...] = face_ref[0]
    sx4_ref[...] = face_ref[1]
    sy0_ref[...] = face_ref[2][:, :row_len]
    last = pltpu.roll(face_ref[3], row_len, 1)
    sy4_ref[...] = last[:, :row_len]


def dg_faces_kernel(state_ref, sx0_ref, sx4_ref, sy0_ref, sy4_ref, face_ref):
    face_ref[...] = jnp.zeros(face_ref.shape, jnp.float32)
    extract_faces(state_ref, face_ref)
    send_faces(face_ref, sx0_ref, sx4_ref, sy0_ref, sy4_ref, sy0_ref.shape[1])


def dg_step_kernel(want_faces, xoff, yoff, row_len, state_ref, src_ref, xlo_ref, xhi_ref, ylo_ref, yhi_ref,
                   apu_ref, aup_ref, diag_ref, lift_ref, out_ref, *rest):
    if want_faces:
        sx0_ref, sx4_ref, sy0_ref, sy4_ref, face_ref, oth_ref, pad_ref, g_ref = rest
    else:
        face_ref, oth_ref, pad_ref, g_ref = rest
    elems = state_ref.shape[1]
    lane = lax.broadcasted_iota(jnp.int32, (FACE_ROWS, elems), 1)
    ez = lane % row_len
    face_ref[...] = jnp.zeros(face_ref.shape, jnp.float32)
    oth_ref[...] = jnp.zeros(oth_ref.shape, jnp.float32)
    extract_faces(state_ref, face_ref)
    oth_ref[pl.ds(0, FACE_ROWS), :] = xlo_ref[pl.ds(xoff, FACE_ROWS), :]
    oth_ref[pl.ds(128, FACE_ROWS), :] = xhi_ref[pl.ds(xoff, FACE_ROWS), :]
    pad_ref[:, pl.ds(0, row_len)] = ylo_ref[pl.ds(yoff, FACE_ROWS), pl.ds(0, row_len)]
    oth_ref[pl.ds(256, FACE_ROWS), :] = jnp.where(
        lane < row_len, pad_ref[...], pltpu.roll(face_ref[3], row_len, 1))
    pad_ref[:, pl.ds(0, row_len)] = yhi_ref[pl.ds(yoff, FACE_ROWS), pl.ds(0, row_len)]
    oth_ref[pl.ds(384, FACE_ROWS), :] = jnp.where(
        lane >= elems - row_len, pltpu.roll(pad_ref[...], elems - row_len, 1),
        pltpu.roll(face_ref[2], elems - row_len, 1))
    oth_ref[pl.ds(512, FACE_ROWS), :] = jnp.where(ez == 0, 0.0, pltpu.roll(face_ref[5], 1, 1))
    oth_ref[pl.ds(640, FACE_ROWS), :] = jnp.where(
        ez == row_len - 1, 0.0, pltpu.roll(face_ref[4], elems - 1, 1))
    g_ref[pl.ds(144, 8), :] = jnp.zeros((8, 4 * elems), jnp.float32)
    half = LIFT_FACTOR * 0.5
    for dim in range(3):
        for side, sign in ((0, -1.0), (1, 1.0)):
            f = 2 * dim + side
            o_p = oth_ref[pl.ds(f * 128, 25), :]
            o_u = [oth_ref[pl.ds(f * 128 + (1 + k) * 25, 25), :] for k in range(3)]
            g_ref[pl.ds(f * 25, 25), pl.ds(0, elems)] = half * (o_p - sign * o_u[dim])
            for k in range(3):
                value = half * o_u[k]
                if k == dim:
                    value = value - half * sign * o_p
                g_ref[pl.ds(f * 25, 25), pl.ds((1 + k) * elems, elems)] = value
    faces = jnp.dot(lift_ref[...], g_ref[...], precision=THREE_PASS, preferred_element_type=jnp.float32)
    state = state_ref[...]
    pres = state[:128]
    vel = state[128:]
    rate_p = jnp.dot(apu_ref[...], vel, precision=THREE_PASS, preferred_element_type=jnp.float32)
    rate_p = rate_p + diag_ref[pl.ds(0, 128), :] * pres + faces[:, :elems]
    out_ref[pl.ds(0, 128), :] = pres + TIME_STEP_ACOUSTIC * rate_p
    rate_u = jnp.dot(aup_ref[...], pres, precision=THREE_PASS, preferred_element_type=jnp.float32)
    for k in range(3):
        rows = pl.ds(128 + k * 128, 128)
        rate_k = rate_u[k * 128:(k + 1) * 128] + diag_ref[rows, :] * state_ref[rows, :]
        rate_k = rate_k + faces[:, (1 + k) * elems:(2 + k) * elems]
        out_ref[rows, :] = state_ref[rows, :] + TIME_STEP_ACOUSTIC * (rate_k - src_ref[pl.ds(k * 128, 128), :])
    if want_faces:
        extract_faces(out_ref, face_ref)
        send_faces(face_ref, sx0_ref, sx4_ref, sy0_ref, sy4_ref, row_len)


def face_shapes(elems, row_len):
    big = jax.ShapeDtypeStruct((FACE_ROWS, elems), jnp.float32)
    small = jax.ShapeDtypeStruct((FACE_ROWS, row_len), jnp.float32)
    return [big, big, small, small]


def dg_faces(state, row_len):
    elems = state.shape[1]
    return pl.pallas_call(
        dg_faces_kernel,
        out_shape=tuple(face_shapes(elems, row_len)),
        scratch_shapes=[pltpu.VMEM((6, FACE_ROWS, elems), jnp.float32)],
    )(state)


def dg_step(state, src, recv, mats, want_faces, row_len, xoff=0, yoff=0):
    elems = state.shape[1]
    out_shape = [jax.ShapeDtypeStruct(state.shape, jnp.float32)]
    if want_faces:
        out_shape += face_shapes(elems, row_len)
    res = pl.pallas_call(
        lambda *refs: dg_step_kernel(want_faces, xoff, yoff, row_len, *refs),
        out_shape=tuple(out_shape),
        scratch_shapes=[
            pltpu.VMEM((6, FACE_ROWS, elems), jnp.float32),
            pltpu.VMEM((768, elems), jnp.float32),
            pltpu.VMEM((FACE_ROWS, elems), jnp.float32),
            pltpu.VMEM((152, 4 * elems), jnp.float32),
        ],
    )(state, src, *recv, *mats)
    return res


def exchange_faces(sent):
    sx0, sx4, sy0, sy4 = sent
    flow_n = lax.axis_size("flow")
    grp_n = lax.axis_size("grp")
    up_f = [(i, i + 1) for i in range(flow_n - 1)]
    down_f = [(i + 1, i) for i in range(flow_n - 1)]
    up_g = [(i, i + 1) for i in range(grp_n - 1)]
    down_g = [(i + 1, i) for i in range(grp_n - 1)]
    return (
        lax.ppermute(sx4, "flow", up_f),
        lax.ppermute(sx0, "flow", down_f),
        lax.ppermute(sy4, "grp", up_g),
        lax.ppermute(sy0, "grp", down_g),
    )


def body(velocity, eddy_visc, projection, acoustic_state, route_send, route_place):
    joint = halos(jnp.concatenate([velocity, eddy_visc[None]], axis=0), 1)
    flow_size = lax.axis_size("flow")
    grp_size = lax.axis_size("grp")
    slot_cap = route_send.shape[2]
    elem_count = acoustic_state.shape[2]
    total_slots = flow_size * grp_size * slot_cap
    placing = route_place.reshape(-1)
    sending = route_send.reshape(-1)
    place_hot = (placing[:, None] == jnp.arange(total_slots, dtype=jnp.int32)[None, :]).astype(jnp.float32)
    home_hot = (sending[:, None] == jnp.arange(elem_count, dtype=jnp.int32)[None, :]).astype(jnp.float32)
    padded_state = jnp.pad(acoustic_state, ((0, 0), (0, 3), (0, 0))).reshape(512, elem_count)
    outgoing = jnp.dot(padded_state, place_hot, precision=HIGH)
    arrived = lax.all_to_all(outgoing, ("flow", "grp"), split_axis=1, concat_axis=1, tiled=True)
    state = jnp.dot(arrived, home_hot, precision=HIGH)

    row_len = velocity.shape[3] // 8
    mats = [jnp.asarray(m) for m in dg_matrices()]
    sent = dg_faces(state, row_len)
    vel, mxup, mxdn, myup, mydn = les_section_first(velocity, eddy_visc, joint, sent)
    merged = exchange_faces((mxdn, mxup, mydn, myup))
    vel, lamb = les_section_last(vel, eddy_visc, merged, joint)
    source = project(lamb, projection)
    xoff = 3 * 2 * velocity.shape[2]
    yoff = 3 * 2 * velocity.shape[1]
    res = dg_step(state, source, merged, mats, True, row_len, xoff, yoff)
    state = res[0]
    recv = exchange_faces(res[1:])
    state = dg_step(state, source, recv, mats, False, row_len)[0]
    leaving = lax.dot_general(state, home_hot, (((1,), (1,)), ((), ())), precision=HIGH)
    returned = lax.all_to_all(leaving, ("flow", "grp"), split_axis=1, concat_axis=1, tiled=True)
    acoustic_out = lax.dot_general(returned, place_hot, (((1,), (1,)), ((), ())), precision=HIGH)
    acoustic_out = acoustic_out.reshape(4, 128, elem_count)[:, :125]
    return (vel, acoustic_out)


def solution(mesh):
    placed = (
        P(None, "flow", "grp", None),
        P("flow", "grp", None),
        P(),
        P(None, None, ("flow", "grp")),
        P(("flow", "grp"), None, None),
        P(("flow", "grp"), None),
    )
    return jax.shard_map(
        body,
        mesh=mesh,
        in_specs=placed,
        out_specs=(P(None, "flow", "grp", None), P(None, None, ("flow", "grp"))),
        check_vma=False,
    )
```

```python
import math

import jax
import jax.numpy as jnp
import numpy as np
from jax import lax
from jax.experimental import pallas as pl
from jax.experimental.pallas import tpu as pltpu
from jax.sharding import PartitionSpec as P

LES_SECTIONS = 2
AC_SECTIONS = 2


TIME_STEP_LES = 0.15
TIME_STEP_ACOUSTIC = 0.02
GEOMETRY = 2.0
LIFT_FACTOR = 20.0
HIGH = lax.Precision.HIGHEST
THREE_PASS = lax.Precision.HIGH


def gll_derivative():
    gll_nodes = np.array([-1.0, -math.sqrt(3.0 / 7.0), 0.0, math.sqrt(3.0 / 7.0), 1.0])
    bary_weights = np.array(
        [
            1.0
            / np.prod([gll_nodes[first] - gll_nodes[other] for other in range(5) if other != first])
            for first in range(5)
        ]
    )
    matrix = np.zeros((5, 5))
    for row_id in range(5):
        for col_id in range(5):
            if row_id != col_id:
                matrix[row_id, col_id] = (
                    bary_weights[col_id]
                    / bary_weights[row_id]
                    / (gll_nodes[row_id] - gll_nodes[col_id])
                )
    for row_id in range(5):
        matrix[row_id, row_id] = -matrix[row_id].sum()
    return matrix


def node_id(coords):
    return coords[0] * 25 + coords[1] * 5 + coords[2]


def face_nodes(dim, at):
    ids = []
    for first in range(5):
        for second in range(5):
            coords = [first, second]
            coords.insert(dim, at)
            ids.append(node_id(coords))
    return ids


def dg_matrices():
    dmat = gll_derivative()
    half = LIFT_FACTOR * 0.5
    apu = np.zeros((128, 384))
    aup = np.zeros((384, 128))
    diag = np.zeros((512, 1))
    lift = np.zeros((128, 152))
    for a in range(5):
        for b in range(5):
            for c in range(5):
                pos = (a, b, c)
                row = node_id(pos)
                for dim in range(3):
                    for k in range(5):
                        col_pos = list(pos)
                        col_pos[dim] = k
                        col = node_id(col_pos)
                        weight = -GEOMETRY * dmat[pos[dim], k]
                        apu[row, dim * 128 + col] += weight
                        aup[dim * 128 + row, col] += weight
    for dim in range(3):
        for side, (sign, at) in enumerate(((-1.0, 0), (1.0, 4))):
            f = 2 * dim + side
            for t, node in enumerate(face_nodes(dim, at)):
                apu[node, dim * 128 + node] += half * sign
                aup[dim * 128 + node, node] += half * sign
                for comp in range(4):
                    diag[comp * 128 + node, 0] += -half
                lift[node, f * 25 + t] = 1.0
    return (apu.astype(np.float32), aup.astype(np.float32), diag.astype(np.float32), lift.astype(np.float32))


def face_rows(state, dim, at):
    elems = state.shape[-1]
    cube = state.reshape(4, 5, 5, 5, elems)
    face = lax.index_in_dim(cube, at, axis=1 + dim, keepdims=False)
    return face.reshape(100, elems)


def les_kernel(mode, vel_ref, nu_ref, vxlo_ref, vxhi_ref, vylo_ref, vyhi_ref,
               nxlo_ref, nxhi_ref, nylo_ref, nyhi_ref, *rest):
    size_x, size_y, size_z = vel_ref.shape[1], vel_ref.shape[2], vel_ref.shape[3]
    half = size_z // 2
    row = lax.broadcasted_iota(jnp.int32, (size_y, size_z), 0)
    lane = lax.broadcasted_iota(jnp.int32, (size_y, size_z), 1)
    if mode == 0:
        sx0_ref, sx4_ref, sy0_ref, sy4_ref, out_ref, mxup_ref, mxdn_ref, myup_ref, mydn_ref = rest

        def xlo(c):
            return vxlo_ref[c]

        def xhi(c):
            return vxhi_ref[c]

        def ylo(c, x):
            return vylo_ref[c, x]

        def yhi(c, x):
            return vyhi_ref[c, x]
    else:
        perm_ref, out_ref, lamb_ref = rest

        def plane(ref, c):
            return jnp.concatenate(
                [ref[pl.ds(c * 2 * size_y, size_y), :], ref[pl.ds(c * 2 * size_y + size_y, size_y), :]], axis=1)

        def line(ref, c, x):
            return jnp.concatenate(
                [ref[pl.ds(c * 2 * size_x + x, 1), :], ref[pl.ds(c * 2 * size_x + size_x + x, 1), :]], axis=1)

        def xlo(c):
            return plane(vxlo_ref, c)

        def xhi(c):
            return plane(vxhi_ref, c)

        def ylo(c, x):
            return line(vylo_ref, c, x)

        def yhi(c, x):
            return line(vyhi_ref, c, x)

    def yp(f, halo):
        return jnp.where(row == size_y - 1, halo, pltpu.roll(f, size_y - 1, 0))

    def ym(f, halo):
        return jnp.where(row == 0, halo, pltpu.roll(f, 1, 0))

    def zp(f):
        return jnp.where(lane == size_z - 1, 0.0, pltpu.roll(f, size_z - 1, 1))

    def zm(f):
        return jnp.where(lane == 0, 0.0, pltpu.roll(f, 1, 1))

    def step(x, carry):
        lo = jnp.maximum(x - 1, 0)
        hi = jnp.minimum(x + 1, size_x - 1)
        u = [vel_ref[c, x] for c in range(3)]
        uxm = [jnp.where(x == 0, xlo(c), vel_ref[c, lo]) for c in range(3)]
        uxp = [jnp.where(x == size_x - 1, xhi(c), vel_ref[c, hi]) for c in range(3)]
        uym = [ym(u[c], ylo(c, x)) for c in range(3)]
        uyp = [yp(u[c], yhi(c, x)) for c in range(3)]
        uzm = [zm(u[c]) for c in range(3)]
        uzp = [zp(u[c]) for c in range(3)]
        nu = nu_ref[x]
        nxm = jnp.where(x == 0, nxlo_ref[3], nu_ref[lo])
        nxp = jnp.where(x == size_x - 1, nxhi_ref[3], nu_ref[hi])
        nym = ym(nu, nylo_ref[3, x])
        nyp = yp(nu, nyhi_ref[3, x])
        nzm = zm(nu)
        nzp = zp(nu)
        plus = (uxp, uyp, uzp)
        minus = (uxm, uym, uzm)

        def d(c, axis):
            return 0.5 * (plus[axis][c] - minus[axis][c])

        wx = d(2, 1) - d(1, 2)
        wy = d(0, 2) - d(2, 0)
        wz = d(1, 0) - d(0, 1)
        lamb = (wy * u[2] - wz * u[1], wz * u[0] - wx * u[2], wx * u[1] - wy * u[0])
        ups = (0.5 * (nu + nxp), 0.5 * (nu + nyp), 0.5 * (nu + nzp))
        downs = (0.5 * (nu + nxm), 0.5 * (nu + nym), 0.5 * (nu + nzm))
        for c in range(3):
            total = None
            for axis in range(3):
                term = ups[axis] * (plus[axis][c] - u[c]) - downs[axis] * (u[c] - minus[axis][c])
                total = term if total is None else total + term
            out_ref[c, x] = u[c] + TIME_STEP_LES * (total - lamb[c])
            if mode == 1:
                rounded = lamb[c].astype(jnp.bfloat16)
                moved = jnp.dot(rounded, perm_ref[...], preferred_element_type=jnp.float32)
                lamb_ref[c, x] = moved.astype(lamb_ref.dtype)
        return carry

    lax.fori_loop(0, size_x, step, 0)
    if mode == 0:
        for c in range(3):
            for h in range(2):
                mxup_ref[pl.ds(c * 2 * size_y + h * size_y, size_y), :] = out_ref[c, size_x - 1, :, pl.ds(h * half, half)]
                mxdn_ref[pl.ds(c * 2 * size_y + h * size_y, size_y), :] = out_ref[c, 0, :, pl.ds(h * half, half)]
                for x in range(size_x):
                    at = c * 2 * size_x + h * size_x + x
                    myup_ref[pl.ds(at, 1), :] = out_ref[c, x, pl.ds(size_y - 1, 1), pl.ds(h * half, half)]
                    mydn_ref[pl.ds(at, 1), :] = out_ref[c, x, pl.ds(0, 1), pl.ds(h * half, half)]
        xrows = 3 * 2 * size_y
        yrows = 3 * 2 * size_x
        mxup_ref[pl.ds(xrows, FACE_ROWS), :] = sx4_ref[...]
        mxdn_ref[pl.ds(xrows, FACE_ROWS), :] = sx0_ref[...]
        zeros = jnp.zeros((FACE_ROWS, half), jnp.float32)
        myup_ref[pl.ds(yrows, FACE_ROWS), :] = zeros
        mydn_ref[pl.ds(yrows, FACE_ROWS), :] = zeros
        myup_ref[pl.ds(yrows, FACE_ROWS), pl.ds(0, sy4_ref.shape[1])] = sy4_ref[...]
        mydn_ref[pl.ds(yrows, FACE_ROWS), pl.ds(0, sy0_ref.shape[1])] = sy0_ref[...]


def les_section_first(vel, nu, joint, faces):
    size_x, size_y, size_z = vel.shape[1], vel.shape[2], vel.shape[3]
    xbuf = jax.ShapeDtypeStruct((3 * 2 * size_y + FACE_ROWS, size_z // 2), jnp.float32)
    ybuf = jax.ShapeDtypeStruct((3 * 2 * size_x + FACE_ROWS, size_z // 2), jnp.float32)
    return pl.pallas_call(
        lambda *refs: les_kernel(0, *refs),
        out_shape=(jax.ShapeDtypeStruct(vel.shape, jnp.float32), xbuf, xbuf, ybuf, ybuf),
    )(vel, nu, *joint, *joint, *faces)


def lane_perm(size_z):
    bz = size_z // 8
    perm = np.zeros((size_z, size_z), np.float32)
    for ez in range(bz):
        for cz in range(8):
            perm[ez * 8 + cz, cz * bz + ez] = 1.0
    return jnp.asarray(perm, jnp.bfloat16)


def les_section_last(vel, nu, merged, joint):
    return pl.pallas_call(
        lambda *refs: les_kernel(1, *refs),
        out_shape=(jax.ShapeDtypeStruct(vel.shape, jnp.float32), jax.ShapeDtypeStruct(vel.shape, jnp.bfloat16)),
    )(vel, nu, *merged, *joint, lane_perm(vel.shape[3]))


def halos(field, lead):
    flow_n = lax.axis_size("flow")
    grp_n = lax.axis_size("grp")
    up_f = [(i, i + 1) for i in range(flow_n - 1)]
    down_f = [(i + 1, i) for i in range(flow_n - 1)]
    up_g = [(i, i + 1) for i in range(grp_n - 1)]
    down_g = [(i + 1, i) for i in range(grp_n - 1)]
    size_x, size_y = field.shape[lead], field.shape[lead + 1]
    xlo = lax.ppermute(lax.index_in_dim(field, size_x - 1, lead, keepdims=False), "flow", up_f)
    xhi = lax.ppermute(lax.index_in_dim(field, 0, lead, keepdims=False), "flow", down_f)
    ylo = lax.ppermute(lax.slice_in_dim(field, size_y - 1, size_y, axis=lead + 1), "grp", up_g)
    yhi = lax.ppermute(lax.slice_in_dim(field, 0, 1, axis=lead + 1), "grp", down_g)
    return xlo, xhi, ylo, yhi


def project(moved, projection):
    size_x, size_y, size_z = (moved.shape[1], moved.shape[2], moved.shape[3])
    bx, by, bz = size_x // 8, size_y // 8, size_z // 8
    blocks = moved.reshape(3, bx, 8, by, 8, 8, bz).transpose(2, 4, 5, 0, 1, 3, 6).reshape(512, -1)
    padded_proj = jnp.pad(projection, ((0, 3), (0, 0)))
    source = jnp.dot(padded_proj, blocks, preferred_element_type=jnp.float32)
    source = source.reshape(128, 3, -1).transpose(1, 0, 2)
    return source.reshape(384, -1)


FACE_ROWS = 104


def extract_faces(state_ref, face_ref):
    for dim in range(3):
        for side, at in ((0, 0), (1, 4)):
            f = 2 * dim + side
            for comp in range(4):
                base = comp * 128
                if dim == 0:
                    face_ref[f, pl.ds(comp * 25, 25), :] = state_ref[pl.ds(base + at * 25, 25), :]
                elif dim == 1:
                    for a in range(5):
                        face_ref[f, pl.ds(comp * 25 + a * 5, 5), :] = state_ref[pl.ds(base + a * 25 + at * 5, 5), :]
                else:
                    face_ref[f, pl.ds(comp * 25, 25), :] = state_ref[pl.ds(base + at, 25, stride=5), :]


def send_faces(face_ref, sx0_ref, sx4_ref, sy0_ref, sy4_ref, row_len):
    sx0_ref[...] = face_ref[0]
    sx4_ref[...] = face_ref[1]
    sy0_ref[...] = face_ref[2][:, :row_len]
    last = pltpu.roll(face_ref[3], row_len, 1)
    sy4_ref[...] = last[:, :row_len]


def dg_faces_kernel(state_ref, sx0_ref, sx4_ref, sy0_ref, sy4_ref, face_ref):
    face_ref[...] = jnp.zeros(face_ref.shape, jnp.float32)
    extract_faces(state_ref, face_ref)
    send_faces(face_ref, sx0_ref, sx4_ref, sy0_ref, sy4_ref, sy0_ref.shape[1])


def dg_volume_kernel(state_ref, apu_ref, aup_ref, diag_ref, out_ref):
    state = state_ref[...]
    pres = state[:128]
    vel = state[128:]
    rate_p = jnp.dot(apu_ref[...], vel, precision=THREE_PASS, preferred_element_type=jnp.float32)
    rate_p = rate_p + diag_ref[pl.ds(0, 128), :] * pres
    out_ref[pl.ds(0, 128), :] = pres + TIME_STEP_ACOUSTIC * rate_p
    rate_u = jnp.dot(aup_ref[...], pres, precision=THREE_PASS, preferred_element_type=jnp.float32)
    for k in range(3):
        rows = pl.ds(128 + k * 128, 128)
        rate_k = rate_u[k * 128:(k + 1) * 128] + diag_ref[rows, :] * state_ref[rows, :]
        out_ref[rows, :] = state_ref[rows, :] + TIME_STEP_ACOUSTIC * rate_k


def dg_volume(state, mats):
    return pl.pallas_call(
        dg_volume_kernel,
        out_shape=jax.ShapeDtypeStruct(state.shape, jnp.float32),
    )(state, *mats[:3])


def dg_step_kernel(want_faces, xoff, yoff, row_len, state_ref, part_ref, src_ref, xlo_ref, xhi_ref, ylo_ref, yhi_ref,
                   lift_ref, out_ref, *rest):
    if want_faces:
        sx0_ref, sx4_ref, sy0_ref, sy4_ref, face_ref, oth_ref, pad_ref, g_ref = rest
    else:
        face_ref, oth_ref, pad_ref, g_ref = rest
    elems = state_ref.shape[1]
    lane = lax.broadcasted_iota(jnp.int32, (FACE_ROWS, elems), 1)
    ez = lane % row_len
    face_ref[...] = jnp.zeros(face_ref.shape, jnp.float32)
    oth_ref[...] = jnp.zeros(oth_ref.shape, jnp.float32)
    extract_faces(state_ref, face_ref)
    oth_ref[pl.ds(0, FACE_ROWS), :] = xlo_ref[pl.ds(xoff, FACE_ROWS), :]
    oth_ref[pl.ds(128, FACE_ROWS), :] = xhi_ref[pl.ds(xoff, FACE_ROWS), :]
    pad_ref[:, pl.ds(0, row_len)] = ylo_ref[pl.ds(yoff, FACE_ROWS), pl.ds(0, row_len)]
    oth_ref[pl.ds(256, FACE_ROWS), :] = jnp.where(
        lane < row_len, pad_ref[...], pltpu.roll(face_ref[3], row_len, 1))
    pad_ref[:, pl.ds(0, row_len)] = yhi_ref[pl.ds(yoff, FACE_ROWS), pl.ds(0, row_len)]
    oth_ref[pl.ds(384, FACE_ROWS), :] = jnp.where(
        lane >= elems - row_len, pltpu.roll(pad_ref[...], elems - row_len, 1),
        pltpu.roll(face_ref[2], elems - row_len, 1))
    oth_ref[pl.ds(512, FACE_ROWS), :] = jnp.where(ez == 0, 0.0, pltpu.roll(face_ref[5], 1, 1))
    oth_ref[pl.ds(640, FACE_ROWS), :] = jnp.where(
        ez == row_len - 1, 0.0, pltpu.roll(face_ref[4], elems - 1, 1))
    g_ref[pl.ds(144, 8), :] = jnp.zeros((8, 4 * elems), jnp.float32)
    half = LIFT_FACTOR * 0.5
    for dim in range(3):
        for side, sign in ((0, -1.0), (1, 1.0)):
            f = 2 * dim + side
            o_p = oth_ref[pl.ds(f * 128, 25), :]
            o_u = [oth_ref[pl.ds(f * 128 + (1 + k) * 25, 25), :] for k in range(3)]
            g_ref[pl.ds(f * 25, 25), pl.ds(0, elems)] = half * (o_p - sign * o_u[dim])
            for k in range(3):
                value = half * o_u[k]
                if k == dim:
                    value = value - half * sign * o_p
                g_ref[pl.ds(f * 25, 25), pl.ds((1 + k) * elems, elems)] = value
    faces = jnp.dot(lift_ref[...], g_ref[...], precision=THREE_PASS, preferred_element_type=jnp.float32)
    out_ref[pl.ds(0, 128), :] = part_ref[pl.ds(0, 128), :] + TIME_STEP_ACOUSTIC * faces[:, :elems]
    for k in range(3):
        rows = pl.ds(128 + k * 128, 128)
        rate_k = faces[:, (1 + k) * elems:(2 + k) * elems] - src_ref[pl.ds(k * 128, 128), :]
        out_ref[rows, :] = part_ref[rows, :] + TIME_STEP_ACOUSTIC * rate_k
    if want_faces:
        extract_faces(out_ref, face_ref)
        send_faces(face_ref, sx0_ref, sx4_ref, sy0_ref, sy4_ref, row_len)


def face_shapes(elems, row_len):
    big = jax.ShapeDtypeStruct((FACE_ROWS, elems), jnp.float32)
    small = jax.ShapeDtypeStruct((FACE_ROWS, row_len), jnp.float32)
    return [big, big, small, small]


def dg_faces(state, row_len):
    elems = state.shape[1]
    return pl.pallas_call(
        dg_faces_kernel,
        out_shape=tuple(face_shapes(elems, row_len)),
        scratch_shapes=[pltpu.VMEM((6, FACE_ROWS, elems), jnp.float32)],
    )(state)


def dg_step(state, src, recv, mats, want_faces, row_len, xoff=0, yoff=0):
    elems = state.shape[1]
    out_shape = [jax.ShapeDtypeStruct(state.shape, jnp.float32)]
    if want_faces:
        out_shape += face_shapes(elems, row_len)
    res = pl.pallas_call(
        lambda *refs: dg_step_kernel(want_faces, xoff, yoff, row_len, *refs),
        out_shape=tuple(out_shape),
        scratch_shapes=[
            pltpu.VMEM((6, FACE_ROWS, elems), jnp.float32),
            pltpu.VMEM((768, elems), jnp.float32),
            pltpu.VMEM((FACE_ROWS, elems), jnp.float32),
            pltpu.VMEM((152, 4 * elems), jnp.float32),
        ],
    )(state, dg_volume(state, mats), src, *recv, mats[3])
    return res


def exchange_faces(sent):
    sx0, sx4, sy0, sy4 = sent
    flow_n = lax.axis_size("flow")
    grp_n = lax.axis_size("grp")
    up_f = [(i, i + 1) for i in range(flow_n - 1)]
    down_f = [(i + 1, i) for i in range(flow_n - 1)]
    up_g = [(i, i + 1) for i in range(grp_n - 1)]
    down_g = [(i + 1, i) for i in range(grp_n - 1)]
    return (
        lax.ppermute(sx4, "flow", up_f),
        lax.ppermute(sx0, "flow", down_f),
        lax.ppermute(sy4, "grp", up_g),
        lax.ppermute(sy0, "grp", down_g),
    )


def body(velocity, eddy_visc, projection, acoustic_state, route_send, route_place):
    joint = halos(jnp.concatenate([velocity, eddy_visc[None]], axis=0), 1)
    flow_size = lax.axis_size("flow")
    grp_size = lax.axis_size("grp")
    slot_cap = route_send.shape[2]
    elem_count = acoustic_state.shape[2]
    total_slots = flow_size * grp_size * slot_cap
    placing = route_place.reshape(-1)
    sending = route_send.reshape(-1)
    place_hot = (placing[:, None] == jnp.arange(total_slots, dtype=jnp.int32)[None, :]).astype(jnp.float32)
    home_hot = (sending[:, None] == jnp.arange(elem_count, dtype=jnp.int32)[None, :]).astype(jnp.float32)
    padded_state = jnp.pad(acoustic_state, ((0, 0), (0, 3), (0, 0))).reshape(512, elem_count)
    outgoing = jnp.dot(padded_state, place_hot, precision=HIGH)
    arrived = lax.all_to_all(outgoing, ("flow", "grp"), split_axis=1, concat_axis=1, tiled=True)
    state = jnp.dot(arrived, home_hot, precision=HIGH)

    row_len = velocity.shape[3] // 8
    mats = [jnp.asarray(m) for m in dg_matrices()]
    sent = dg_faces(state, row_len)
    vel, mxup, mxdn, myup, mydn = les_section_first(velocity, eddy_visc, joint, sent)
    merged = exchange_faces((mxdn, mxup, mydn, myup))
    vel, lamb = les_section_last(vel, eddy_visc, merged, joint)
    source = project(lamb, projection)
    xoff = 3 * 2 * velocity.shape[2]
    yoff = 3 * 2 * velocity.shape[1]
    res = dg_step(state, source, merged, mats, True, row_len, xoff, yoff)
    state = res[0]
    recv = exchange_faces(res[1:])
    state = dg_step(state, source, recv, mats, False, row_len)[0]
    leaving = lax.dot_general(state, home_hot, (((1,), (1,)), ((), ())), precision=HIGH)
    returned = lax.all_to_all(leaving, ("flow", "grp"), split_axis=1, concat_axis=1, tiled=True)
    acoustic_out = lax.dot_general(returned, place_hot, (((1,), (1,)), ((), ())), precision=HIGH)
    acoustic_out = acoustic_out.reshape(4, 128, elem_count)[:, :125]
    return (vel, acoustic_out)


def solution(mesh):
    placed = (
        P(None, "flow", "grp", None),
        P("flow", "grp", None),
        P(),
        P(None, None, ("flow", "grp")),
        P(("flow", "grp"), None, None),
        P(("flow", "grp"), None),
    )
    return jax.shard_map(
        body,
        mesh=mesh,
        in_specs=placed,
        out_specs=(P(None, "flow", "grp", None), P(None, None, ("flow", "grp"))),
        check_vma=False,
    )
```

```python
import math

import jax
import jax.numpy as jnp
import numpy as np
from jax import lax
from jax.experimental import pallas as pl
from jax.experimental.pallas import tpu as pltpu
from jax.sharding import PartitionSpec as P

LES_SECTIONS = 2
AC_SECTIONS = 2


TIME_STEP_LES = 0.15
TIME_STEP_ACOUSTIC = 0.02
GEOMETRY = 2.0
LIFT_FACTOR = 20.0
HIGH = lax.Precision.HIGHEST
THREE_PASS = lax.Precision.HIGH


def gll_derivative():
    gll_nodes = np.array([-1.0, -math.sqrt(3.0 / 7.0), 0.0, math.sqrt(3.0 / 7.0), 1.0])
    bary_weights = np.array(
        [
            1.0
            / np.prod([gll_nodes[first] - gll_nodes[other] for other in range(5) if other != first])
            for first in range(5)
        ]
    )
    matrix = np.zeros((5, 5))
    for row_id in range(5):
        for col_id in range(5):
            if row_id != col_id:
                matrix[row_id, col_id] = (
                    bary_weights[col_id]
                    / bary_weights[row_id]
                    / (gll_nodes[row_id] - gll_nodes[col_id])
                )
    for row_id in range(5):
        matrix[row_id, row_id] = -matrix[row_id].sum()
    return matrix


def node_id(coords):
    return coords[0] * 25 + coords[1] * 5 + coords[2]


def face_nodes(dim, at):
    ids = []
    for first in range(5):
        for second in range(5):
            coords = [first, second]
            coords.insert(dim, at)
            ids.append(node_id(coords))
    return ids


def dg_matrices():
    dmat = gll_derivative()
    half = LIFT_FACTOR * 0.5
    apu = np.zeros((128, 384))
    aup = np.zeros((384, 128))
    diag = np.zeros((512, 1))
    lift = np.zeros((128, 152))
    for a in range(5):
        for b in range(5):
            for c in range(5):
                pos = (a, b, c)
                row = node_id(pos)
                for dim in range(3):
                    for k in range(5):
                        col_pos = list(pos)
                        col_pos[dim] = k
                        col = node_id(col_pos)
                        weight = -GEOMETRY * dmat[pos[dim], k]
                        apu[row, dim * 128 + col] += weight
                        aup[dim * 128 + row, col] += weight
    for dim in range(3):
        for side, (sign, at) in enumerate(((-1.0, 0), (1.0, 4))):
            f = 2 * dim + side
            for t, node in enumerate(face_nodes(dim, at)):
                apu[node, dim * 128 + node] += half * sign
                aup[dim * 128 + node, node] += half * sign
                for comp in range(4):
                    diag[comp * 128 + node, 0] += -half
                lift[node, f * 25 + t] = 1.0
    return (apu.astype(np.float32), aup.astype(np.float32), diag.astype(np.float32), lift.astype(np.float32))


def face_rows(state, dim, at):
    elems = state.shape[-1]
    cube = state.reshape(4, 5, 5, 5, elems)
    face = lax.index_in_dim(cube, at, axis=1 + dim, keepdims=False)
    return face.reshape(100, elems)


def les_kernel(mode, flow_n, grp_n, vel_ref, nu_ref, vxlo_ref, vxhi_ref, vylo_ref, vyhi_ref,
               nxlo_ref, nxhi_ref, nylo_ref, nyhi_ref, *rest):
    size_x, size_y, size_z = vel_ref.shape[1], vel_ref.shape[2], vel_ref.shape[3]
    half = size_z // 2
    flow_i = lax.axis_index("flow")
    grp_i = lax.axis_index("grp")
    at_lo_f = flow_i == 0
    at_hi_f = flow_i == flow_n - 1
    at_lo_g = grp_i == 0
    at_hi_g = grp_i == grp_n - 1
    row = lax.broadcasted_iota(jnp.int32, (size_y, size_z), 0)
    lane = lax.broadcasted_iota(jnp.int32, (size_y, size_z), 1)
    if mode == 0:
        sx0_ref, sx4_ref, sy0_ref, sy4_ref, out_ref, mxup_ref, mxdn_ref, myup_ref, mydn_ref = rest

        def xlo(c):
            return jnp.where(at_lo_f, 0.0, vxlo_ref[c])

        def xhi(c):
            return jnp.where(at_hi_f, 0.0, vxhi_ref[c])

        def ylo(c, x):
            return jnp.where(at_lo_g, 0.0, vylo_ref[c, x])

        def yhi(c, x):
            return jnp.where(at_hi_g, 0.0, vyhi_ref[c, x])
    else:
        out_ref, lamb_ref = rest

        def plane(ref, c):
            return jnp.concatenate(
                [ref[pl.ds(c * 2 * size_y, size_y), :], ref[pl.ds(c * 2 * size_y + size_y, size_y), :]], axis=1)

        def line(ref, c, x):
            return jnp.concatenate(
                [ref[pl.ds(c * 2 * size_x + x, 1), :], ref[pl.ds(c * 2 * size_x + size_x + x, 1), :]], axis=1)

        def xlo(c):
            return jnp.where(at_lo_f, 0.0, plane(vxlo_ref, c))

        def xhi(c):
            return jnp.where(at_hi_f, 0.0, plane(vxhi_ref, c))

        def ylo(c, x):
            return jnp.where(at_lo_g, 0.0, line(vylo_ref, c, x))

        def yhi(c, x):
            return jnp.where(at_hi_g, 0.0, line(vyhi_ref, c, x))

    def yp(f, halo):
        return jnp.where(row == size_y - 1, halo, pltpu.roll(f, size_y - 1, 0))

    def ym(f, halo):
        return jnp.where(row == 0, halo, pltpu.roll(f, 1, 0))

    def zp(f):
        return jnp.where(lane == size_z - 1, 0.0, pltpu.roll(f, size_z - 1, 1))

    def zm(f):
        return jnp.where(lane == 0, 0.0, pltpu.roll(f, 1, 1))

    def step(x, carry):
        lo = jnp.maximum(x - 1, 0)
        hi = jnp.minimum(x + 1, size_x - 1)
        u = [vel_ref[c, x] for c in range(3)]
        uxm = [jnp.where(x == 0, xlo(c), vel_ref[c, lo]) for c in range(3)]
        uxp = [jnp.where(x == size_x - 1, xhi(c), vel_ref[c, hi]) for c in range(3)]
        uym = [ym(u[c], ylo(c, x)) for c in range(3)]
        uyp = [yp(u[c], yhi(c, x)) for c in range(3)]
        uzm = [zm(u[c]) for c in range(3)]
        uzp = [zp(u[c]) for c in range(3)]
        nu = nu_ref[x]
        nxm = jnp.where(x == 0, jnp.where(at_lo_f, 0.0, nxlo_ref[3]), nu_ref[lo])
        nxp = jnp.where(x == size_x - 1, jnp.where(at_hi_f, 0.0, nxhi_ref[3]), nu_ref[hi])
        nym = ym(nu, jnp.where(at_lo_g, 0.0, nylo_ref[3, x]))
        nyp = yp(nu, jnp.where(at_hi_g, 0.0, nyhi_ref[3, x]))
        nzm = zm(nu)
        nzp = zp(nu)
        plus = (uxp, uyp, uzp)
        minus = (uxm, uym, uzm)

        def d(c, axis):
            return 0.5 * (plus[axis][c] - minus[axis][c])

        wx = d(2, 1) - d(1, 2)
        wy = d(0, 2) - d(2, 0)
        wz = d(1, 0) - d(0, 1)
        lamb = (wy * u[2] - wz * u[1], wz * u[0] - wx * u[2], wx * u[1] - wy * u[0])
        ups = (0.5 * (nu + nxp), 0.5 * (nu + nyp), 0.5 * (nu + nzp))
        downs = (0.5 * (nu + nxm), 0.5 * (nu + nym), 0.5 * (nu + nzm))
        for c in range(3):
            total = None
            for axis in range(3):
                term = ups[axis] * (plus[axis][c] - u[c]) - downs[axis] * (u[c] - minus[axis][c])
                total = term if total is None else total + term
            out_ref[c, x] = u[c] + TIME_STEP_LES * (total - lamb[c])
            if mode == 1:
                lamb_ref[c, x] = lamb[c].astype(lamb_ref.dtype)
        return carry

    lax.fori_loop(0, size_x, step, 0)
    if mode == 0:
        for c in range(3):
            for h in range(2):
                mxup_ref[pl.ds(c * 2 * size_y + h * size_y, size_y), :] = out_ref[c, size_x - 1, :, pl.ds(h * half, half)]
                mxdn_ref[pl.ds(c * 2 * size_y + h * size_y, size_y), :] = out_ref[c, 0, :, pl.ds(h * half, half)]
                for x in range(size_x):
                    at = c * 2 * size_x + h * size_x + x
                    myup_ref[pl.ds(at, 1), :] = out_ref[c, x, pl.ds(size_y - 1, 1), pl.ds(h * half, half)]
                    mydn_ref[pl.ds(at, 1), :] = out_ref[c, x, pl.ds(0, 1), pl.ds(h * half, half)]
        xrows = 3 * 2 * size_y
        yrows = 3 * 2 * size_x
        mxup_ref[pl.ds(xrows, FACE_ROWS), :] = sx4_ref[...]
        mxdn_ref[pl.ds(xrows, FACE_ROWS), :] = sx0_ref[...]
        zeros = jnp.zeros((FACE_ROWS, half), jnp.float32)
        myup_ref[pl.ds(yrows, FACE_ROWS), :] = zeros
        mydn_ref[pl.ds(yrows, FACE_ROWS), :] = zeros
        myup_ref[pl.ds(yrows, FACE_ROWS), pl.ds(0, sy4_ref.shape[1])] = sy4_ref[...]
        mydn_ref[pl.ds(yrows, FACE_ROWS), pl.ds(0, sy0_ref.shape[1])] = sy0_ref[...]


def les_section_first(vel, nu, joint, faces):
    size_x, size_y, size_z = vel.shape[1], vel.shape[2], vel.shape[3]
    xbuf = jax.ShapeDtypeStruct((3 * 2 * size_y + FACE_ROWS, size_z // 2), jnp.float32)
    ybuf = jax.ShapeDtypeStruct((3 * 2 * size_x + FACE_ROWS, size_z // 2), jnp.float32)
    return pl.pallas_call(
        lambda *refs: les_kernel(0, lax.axis_size("flow"), lax.axis_size("grp"), *refs),
        out_shape=(jax.ShapeDtypeStruct(vel.shape, jnp.float32), xbuf, xbuf, ybuf, ybuf),
    )(vel, nu, *joint, *joint, *faces)


def les_section_last(vel, nu, merged, joint):
    return pl.pallas_call(
        lambda *refs: les_kernel(1, lax.axis_size("flow"), lax.axis_size("grp"), *refs),
        out_shape=(jax.ShapeDtypeStruct(vel.shape, jnp.float32), jax.ShapeDtypeStruct(vel.shape, jnp.bfloat16)),
    )(vel, nu, *merged, *joint)


def halos(field, lead):
    flow_n = lax.axis_size("flow")
    grp_n = lax.axis_size("grp")
    up_f = [(i, (i + 1) % flow_n) for i in range(flow_n)]
    down_f = [((i + 1) % flow_n, i) for i in range(flow_n)]
    up_g = [(i, (i + 1) % grp_n) for i in range(grp_n)]
    down_g = [((i + 1) % grp_n, i) for i in range(grp_n)]
    size_x, size_y = field.shape[lead], field.shape[lead + 1]
    xlo = lax.ppermute(lax.index_in_dim(field, size_x - 1, lead, keepdims=False), "flow", up_f)
    xhi = lax.ppermute(lax.index_in_dim(field, 0, lead, keepdims=False), "flow", down_f)
    ylo = lax.ppermute(lax.slice_in_dim(field, size_y - 1, size_y, axis=lead + 1), "grp", up_g)
    yhi = lax.ppermute(lax.slice_in_dim(field, 0, 1, axis=lead + 1), "grp", down_g)
    return xlo, xhi, ylo, yhi


def project(lamb, projection):
    size_x, size_y, size_z = (lamb.shape[1], lamb.shape[2], lamb.shape[3])
    bx, by, bz = size_x // 8, size_y // 8, size_z // 8
    perm = np.zeros((size_z, size_z), np.float32)
    for ez in range(bz):
        for cz in range(8):
            perm[ez * 8 + cz, cz * bz + ez] = 1.0
    rows = lamb.reshape(-1, size_z)
    moved = jnp.dot(rows, jnp.asarray(perm, jnp.bfloat16), preferred_element_type=jnp.float32)
    moved = moved.astype(jnp.bfloat16)
    blocks = moved.reshape(3, bx, 8, by, 8, 8, bz).transpose(2, 4, 5, 0, 1, 3, 6).reshape(512, -1)
    padded_proj = jnp.pad(projection, ((0, 3), (0, 0)))
    source = jnp.dot(padded_proj, blocks, preferred_element_type=jnp.float32)
    source = source.reshape(128, 3, -1).transpose(1, 0, 2)
    return source.reshape(384, -1)


FACE_ROWS = 104


def extract_faces(state_ref, face_ref):
    for dim in range(3):
        for side, at in ((0, 0), (1, 4)):
            f = 2 * dim + side
            for comp in range(4):
                base = comp * 128
                if dim == 0:
                    face_ref[f, pl.ds(comp * 25, 25), :] = state_ref[pl.ds(base + at * 25, 25), :]
                elif dim == 1:
                    for a in range(5):
                        face_ref[f, pl.ds(comp * 25 + a * 5, 5), :] = state_ref[pl.ds(base + a * 25 + at * 5, 5), :]
                else:
                    face_ref[f, pl.ds(comp * 25, 25), :] = state_ref[pl.ds(base + at, 25, stride=5), :]


def send_faces(face_ref, sx0_ref, sx4_ref, sy0_ref, sy4_ref, row_len):
    sx0_ref[...] = face_ref[0]
    sx4_ref[...] = face_ref[1]
    sy0_ref[...] = face_ref[2][:, :row_len]
    last = pltpu.roll(face_ref[3], row_len, 1)
    sy4_ref[...] = last[:, :row_len]


def dg_faces_kernel(state_ref, sx0_ref, sx4_ref, sy0_ref, sy4_ref, face_ref):
    face_ref[...] = jnp.zeros(face_ref.shape, jnp.float32)
    extract_faces(state_ref, face_ref)
    send_faces(face_ref, sx0_ref, sx4_ref, sy0_ref, sy4_ref, sy0_ref.shape[1])


def dg_step_kernel(want_faces, xoff, yoff, row_len, flow_n, grp_n, state_ref, src_ref, xlo_ref, xhi_ref, ylo_ref, yhi_ref,
                   apu_ref, aup_ref, diag_ref, lift_ref, out_ref, *rest):
    if want_faces:
        sx0_ref, sx4_ref, sy0_ref, sy4_ref, face_ref, oth_ref, pad_ref, g_ref = rest
    else:
        face_ref, oth_ref, pad_ref, g_ref = rest
    elems = state_ref.shape[1]
    lane = lax.broadcasted_iota(jnp.int32, (FACE_ROWS, elems), 1)
    ez = lane % row_len
    face_ref[...] = jnp.zeros(face_ref.shape, jnp.float32)
    oth_ref[...] = jnp.zeros(oth_ref.shape, jnp.float32)
    extract_faces(state_ref, face_ref)
    flow_i = lax.axis_index("flow")
    grp_i = lax.axis_index("grp")
    oth_ref[pl.ds(0, FACE_ROWS), :] = jnp.where(flow_i == 0, 0.0, xlo_ref[pl.ds(xoff, FACE_ROWS), :])
    oth_ref[pl.ds(128, FACE_ROWS), :] = jnp.where(flow_i == flow_n - 1, 0.0, xhi_ref[pl.ds(xoff, FACE_ROWS), :])
    pad_ref[:, pl.ds(0, row_len)] = jnp.where(
        grp_i == 0, 0.0, ylo_ref[pl.ds(yoff, FACE_ROWS), pl.ds(0, row_len)])
    oth_ref[pl.ds(256, FACE_ROWS), :] = jnp.where(
        lane < row_len, pad_ref[...], pltpu.roll(face_ref[3], row_len, 1))
    pad_ref[:, pl.ds(0, row_len)] = jnp.where(
        grp_i == grp_n - 1, 0.0, yhi_ref[pl.ds(yoff, FACE_ROWS), pl.ds(0, row_len)])
    oth_ref[pl.ds(384, FACE_ROWS), :] = jnp.where(
        lane >= elems - row_len, pltpu.roll(pad_ref[...], elems - row_len, 1),
        pltpu.roll(face_ref[2], elems - row_len, 1))
    oth_ref[pl.ds(512, FACE_ROWS), :] = jnp.where(ez == 0, 0.0, pltpu.roll(face_ref[5], 1, 1))
    oth_ref[pl.ds(640, FACE_ROWS), :] = jnp.where(
        ez == row_len - 1, 0.0, pltpu.roll(face_ref[4], elems - 1, 1))
    g_ref[pl.ds(144, 8), :] = jnp.zeros((8, 4 * elems), jnp.float32)
    half = LIFT_FACTOR * 0.5
    for dim in range(3):
        for side, sign in ((0, -1.0), (1, 1.0)):
            f = 2 * dim + side
            o_p = oth_ref[pl.ds(f * 128, 25), :]
            o_u = [oth_ref[pl.ds(f * 128 + (1 + k) * 25, 25), :] for k in range(3)]
            g_ref[pl.ds(f * 25, 25), pl.ds(0, elems)] = half * (o_p - sign * o_u[dim])
            for k in range(3):
                value = half * o_u[k]
                if k == dim:
                    value = value - half * sign * o_p
                g_ref[pl.ds(f * 25, 25), pl.ds((1 + k) * elems, elems)] = value
    faces = jnp.dot(lift_ref[...], g_ref[...], precision=THREE_PASS, preferred_element_type=jnp.float32)
    state = state_ref[...]
    pres = state[:128]
    vel = state[128:]
    rate_p = jnp.dot(apu_ref[...], vel, precision=THREE_PASS, preferred_element_type=jnp.float32)
    rate_p = rate_p + diag_ref[pl.ds(0, 128), :] * pres + faces[:, :elems]
    out_ref[pl.ds(0, 128), :] = pres + TIME_STEP_ACOUSTIC * rate_p
    rate_u = jnp.dot(aup_ref[...], pres, precision=THREE_PASS, preferred_element_type=jnp.float32)
    for k in range(3):
        rows = pl.ds(128 + k * 128, 128)
        rate_k = rate_u[k * 128:(k + 1) * 128] + diag_ref[rows, :] * state_ref[rows, :]
        rate_k = rate_k + faces[:, (1 + k) * elems:(2 + k) * elems]
        out_ref[rows, :] = state_ref[rows, :] + TIME_STEP_ACOUSTIC * (rate_k - src_ref[pl.ds(k * 128, 128), :])
    if want_faces:
        extract_faces(out_ref, face_ref)
        send_faces(face_ref, sx0_ref, sx4_ref, sy0_ref, sy4_ref, row_len)


def face_shapes(elems, row_len):
    big = jax.ShapeDtypeStruct((FACE_ROWS, elems), jnp.float32)
    small = jax.ShapeDtypeStruct((FACE_ROWS, row_len), jnp.float32)
    return [big, big, small, small]


def dg_faces(state, row_len):
    elems = state.shape[1]
    return pl.pallas_call(
        dg_faces_kernel,
        out_shape=tuple(face_shapes(elems, row_len)),
        scratch_shapes=[pltpu.VMEM((6, FACE_ROWS, elems), jnp.float32)],
    )(state)


def dg_step(state, src, recv, mats, want_faces, row_len, xoff=0, yoff=0):
    elems = state.shape[1]
    out_shape = [jax.ShapeDtypeStruct(state.shape, jnp.float32)]
    if want_faces:
        out_shape += face_shapes(elems, row_len)
    res = pl.pallas_call(
        lambda *refs: dg_step_kernel(want_faces, xoff, yoff, row_len, lax.axis_size("flow"), lax.axis_size("grp"), *refs),
        out_shape=tuple(out_shape),
        scratch_shapes=[
            pltpu.VMEM((6, FACE_ROWS, elems), jnp.float32),
            pltpu.VMEM((768, elems), jnp.float32),
            pltpu.VMEM((FACE_ROWS, elems), jnp.float32),
            pltpu.VMEM((152, 4 * elems), jnp.float32),
        ],
    )(state, src, *recv, *mats)
    return res


def exchange_faces(sent):
    sx0, sx4, sy0, sy4 = sent
    flow_n = lax.axis_size("flow")
    grp_n = lax.axis_size("grp")
    up_f = [(i, (i + 1) % flow_n) for i in range(flow_n)]
    down_f = [((i + 1) % flow_n, i) for i in range(flow_n)]
    up_g = [(i, (i + 1) % grp_n) for i in range(grp_n)]
    down_g = [((i + 1) % grp_n, i) for i in range(grp_n)]
    return (
        lax.ppermute(sx4, "flow", up_f),
        lax.ppermute(sx0, "flow", down_f),
        lax.ppermute(sy4, "grp", up_g),
        lax.ppermute(sy0, "grp", down_g),
    )


def body(velocity, eddy_visc, projection, acoustic_state, route_send, route_place):
    joint = halos(jnp.concatenate([velocity, eddy_visc[None]], axis=0), 1)
    flow_size = lax.axis_size("flow")
    grp_size = lax.axis_size("grp")
    slot_cap = route_send.shape[2]
    elem_count = acoustic_state.shape[2]
    total_slots = flow_size * grp_size * slot_cap
    placing = route_place.reshape(-1)
    sending = route_send.reshape(-1)
    place_hot = (placing[:, None] == jnp.arange(total_slots, dtype=jnp.int32)[None, :]).astype(jnp.float32)
    home_hot = (sending[:, None] == jnp.arange(elem_count, dtype=jnp.int32)[None, :]).astype(jnp.float32)
    padded_state = jnp.pad(acoustic_state, ((0, 0), (0, 3), (0, 0))).reshape(512, elem_count)
    outgoing = jnp.dot(padded_state, place_hot, precision=HIGH)
    arrived = lax.all_to_all(outgoing, ("flow", "grp"), split_axis=1, concat_axis=1, tiled=True)
    state = jnp.dot(arrived, home_hot, precision=HIGH)

    row_len = velocity.shape[3] // 8
    mats = [jnp.asarray(m) for m in dg_matrices()]
    sent = dg_faces(state, row_len)
    vel, mxup, mxdn, myup, mydn = les_section_first(velocity, eddy_visc, joint, sent)
    merged = exchange_faces((mxdn, mxup, mydn, myup))
    vel, lamb = les_section_last(vel, eddy_visc, merged, joint)
    source = project(lamb, projection)
    xoff = 3 * 2 * velocity.shape[2]
    yoff = 3 * 2 * velocity.shape[1]
    res = dg_step(state, source, merged, mats, True, row_len, xoff, yoff)
    state = res[0]
    recv = exchange_faces(res[1:])
    state = dg_step(state, source, recv, mats, False, row_len)[0]
    leaving = lax.dot_general(state, home_hot, (((1,), (1,)), ((), ())), precision=HIGH)
    returned = lax.all_to_all(leaving, ("flow", "grp"), split_axis=1, concat_axis=1, tiled=True)
    acoustic_out = lax.dot_general(returned, place_hot, (((1,), (1,)), ((), ())), precision=HIGH)
    acoustic_out = acoustic_out.reshape(4, 128, elem_count)[:, :125]
    return (vel, acoustic_out)


def solution(mesh):
    placed = (
        P(None, "flow", "grp", None),
        P("flow", "grp", None),
        P(),
        P(None, None, ("flow", "grp")),
        P(("flow", "grp"), None, None),
        P(("flow", "grp"), None),
    )
    return jax.shard_map(
        body,
        mesh=mesh,
        in_specs=placed,
        out_specs=(P(None, "flow", "grp", None), P(None, None, ("flow", "grp"))),
        check_vma=False,
    )
```

```python
import math

import jax
import jax.numpy as jnp
import numpy as np
from jax import lax
from jax.experimental import pallas as pl
from jax.experimental.pallas import tpu as pltpu
from jax.sharding import PartitionSpec as P

LES_SECTIONS = 2
AC_SECTIONS = 2


TIME_STEP_LES = 0.15
TIME_STEP_ACOUSTIC = 0.02
GEOMETRY = 2.0
LIFT_FACTOR = 20.0
HIGH = lax.Precision.HIGHEST
THREE_PASS = lax.Precision.HIGH


def gll_derivative():
    gll_nodes = np.array([-1.0, -math.sqrt(3.0 / 7.0), 0.0, math.sqrt(3.0 / 7.0), 1.0])
    bary_weights = np.array(
        [
            1.0
            / np.prod([gll_nodes[first] - gll_nodes[other] for other in range(5) if other != first])
            for first in range(5)
        ]
    )
    matrix = np.zeros((5, 5))
    for row_id in range(5):
        for col_id in range(5):
            if row_id != col_id:
                matrix[row_id, col_id] = (
                    bary_weights[col_id]
                    / bary_weights[row_id]
                    / (gll_nodes[row_id] - gll_nodes[col_id])
                )
    for row_id in range(5):
        matrix[row_id, row_id] = -matrix[row_id].sum()
    return matrix


def node_id(coords):
    return coords[0] * 25 + coords[1] * 5 + coords[2]


def face_nodes(dim, at):
    ids = []
    for first in range(5):
        for second in range(5):
            coords = [first, second]
            coords.insert(dim, at)
            ids.append(node_id(coords))
    return ids


def dg_matrices():
    dmat = gll_derivative()
    half = LIFT_FACTOR * 0.5
    apu = np.zeros((128, 384))
    aup = np.zeros((384, 128))
    diag = np.zeros((512, 1))
    lift = np.zeros((128, 152))
    for a in range(5):
        for b in range(5):
            for c in range(5):
                pos = (a, b, c)
                row = node_id(pos)
                for dim in range(3):
                    for k in range(5):
                        col_pos = list(pos)
                        col_pos[dim] = k
                        col = node_id(col_pos)
                        weight = -GEOMETRY * dmat[pos[dim], k]
                        apu[row, dim * 128 + col] += weight
                        aup[dim * 128 + row, col] += weight
    for dim in range(3):
        for side, (sign, at) in enumerate(((-1.0, 0), (1.0, 4))):
            f = 2 * dim + side
            for t, node in enumerate(face_nodes(dim, at)):
                apu[node, dim * 128 + node] += half * sign
                aup[dim * 128 + node, node] += half * sign
                for comp in range(4):
                    diag[comp * 128 + node, 0] += -half
                lift[node, f * 25 + t] = 1.0
    return (apu.astype(np.float32), aup.astype(np.float32), diag.astype(np.float32), lift.astype(np.float32))


def face_rows(state, dim, at):
    elems = state.shape[-1]
    cube = state.reshape(4, 5, 5, 5, elems)
    face = lax.index_in_dim(cube, at, axis=1 + dim, keepdims=False)
    return face.reshape(100, elems)


def les_kernel(mode, flow_n, grp_n, vel_ref, nu_ref, vxlo_ref, vxhi_ref, vylo_ref, vyhi_ref,
               nxlo_ref, nxhi_ref, nylo_ref, nyhi_ref, *rest):
    size_x, size_y, size_z = vel_ref.shape[1], vel_ref.shape[2], vel_ref.shape[3]
    half = size_z // 2
    flow_i = lax.axis_index("flow")
    grp_i = lax.axis_index("grp")
    at_lo_f = flow_i == 0
    at_hi_f = flow_i == flow_n - 1
    at_lo_g = grp_i == 0
    at_hi_g = grp_i == grp_n - 1
    row = lax.broadcasted_iota(jnp.int32, (size_y, size_z), 0)
    lane = lax.broadcasted_iota(jnp.int32, (size_y, size_z), 1)
    if mode == 0:
        (out_ref,) = rest

        def xlo(c):
            return jnp.where(at_lo_f, 0.0, vxlo_ref[c])

        def xhi(c):
            return jnp.where(at_hi_f, 0.0, vxhi_ref[c])

        def ylo(c, x):
            return jnp.where(at_lo_g, 0.0, vylo_ref[c, x])

        def yhi(c, x):
            return jnp.where(at_hi_g, 0.0, vyhi_ref[c, x])
    else:
        out_ref, lamb_ref = rest

        def plane(ref, c):
            return jnp.concatenate(
                [ref[pl.ds(c * 2 * size_y, size_y), :], ref[pl.ds(c * 2 * size_y + size_y, size_y), :]], axis=1)

        def line(ref, c, x):
            return jnp.concatenate(
                [ref[pl.ds(c * 2 * size_x + x, 1), :], ref[pl.ds(c * 2 * size_x + size_x + x, 1), :]], axis=1)

        def xlo(c):
            return jnp.where(at_lo_f, 0.0, plane(vxlo_ref, c))

        def xhi(c):
            return jnp.where(at_hi_f, 0.0, plane(vxhi_ref, c))

        def ylo(c, x):
            return jnp.where(at_lo_g, 0.0, line(vylo_ref, c, x))

        def yhi(c, x):
            return jnp.where(at_hi_g, 0.0, line(vyhi_ref, c, x))

    def yp(f, halo):
        return jnp.where(row == size_y - 1, halo, pltpu.roll(f, size_y - 1, 0))

    def ym(f, halo):
        return jnp.where(row == 0, halo, pltpu.roll(f, 1, 0))

    def zp(f):
        return jnp.where(lane == size_z - 1, 0.0, pltpu.roll(f, size_z - 1, 1))

    def zm(f):
        return jnp.where(lane == 0, 0.0, pltpu.roll(f, 1, 1))

    def step(x, carry):
        lo = jnp.maximum(x - 1, 0)
        hi = jnp.minimum(x + 1, size_x - 1)
        u = [vel_ref[c, x] for c in range(3)]
        uxm = [jnp.where(x == 0, xlo(c), vel_ref[c, lo]) for c in range(3)]
        uxp = [jnp.where(x == size_x - 1, xhi(c), vel_ref[c, hi]) for c in range(3)]
        uym = [ym(u[c], ylo(c, x)) for c in range(3)]
        uyp = [yp(u[c], yhi(c, x)) for c in range(3)]
        uzm = [zm(u[c]) for c in range(3)]
        uzp = [zp(u[c]) for c in range(3)]
        nu = nu_ref[x]
        nxm = jnp.where(x == 0, jnp.where(at_lo_f, 0.0, nxlo_ref[3]), nu_ref[lo])
        nxp = jnp.where(x == size_x - 1, jnp.where(at_hi_f, 0.0, nxhi_ref[3]), nu_ref[hi])
        nym = ym(nu, jnp.where(at_lo_g, 0.0, nylo_ref[3, x]))
        nyp = yp(nu, jnp.where(at_hi_g, 0.0, nyhi_ref[3, x]))
        nzm = zm(nu)
        nzp = zp(nu)
        plus = (uxp, uyp, uzp)
        minus = (uxm, uym, uzm)

        def d(c, axis):
            return 0.5 * (plus[axis][c] - minus[axis][c])

        wx = d(2, 1) - d(1, 2)
        wy = d(0, 2) - d(2, 0)
        wz = d(1, 0) - d(0, 1)
        lamb = (wy * u[2] - wz * u[1], wz * u[0] - wx * u[2], wx * u[1] - wy * u[0])
        ups = (0.5 * (nu + nxp), 0.5 * (nu + nyp), 0.5 * (nu + nzp))
        downs = (0.5 * (nu + nxm), 0.5 * (nu + nym), 0.5 * (nu + nzm))
        for c in range(3):
            total = None
            for axis in range(3):
                term = ups[axis] * (plus[axis][c] - u[c]) - downs[axis] * (u[c] - minus[axis][c])
                total = term if total is None else total + term
            out_ref[c, x] = u[c] + TIME_STEP_LES * (total - lamb[c])
            if mode == 1:
                lamb_ref[c, x] = lamb[c].astype(lamb_ref.dtype)
        return carry

    lax.fori_loop(0, size_x, step, 0)


def les_section_first(vel, nu, joint):
    return pl.pallas_call(
        lambda *refs: les_kernel(0, lax.axis_size("flow"), lax.axis_size("grp"), *refs),
        out_shape=(jax.ShapeDtypeStruct(vel.shape, jnp.float32),),
    )(vel, nu, *joint, *joint)[0]


def les_section_last(vel, nu, merged, joint):
    return pl.pallas_call(
        lambda *refs: les_kernel(1, lax.axis_size("flow"), lax.axis_size("grp"), *refs),
        out_shape=(jax.ShapeDtypeStruct(vel.shape, jnp.float32), jax.ShapeDtypeStruct(vel.shape, jnp.bfloat16)),
    )(vel, nu, *merged, *joint)


def halos(field, lead):
    flow_n = lax.axis_size("flow")
    grp_n = lax.axis_size("grp")
    up_f = [(i, (i + 1) % flow_n) for i in range(flow_n)]
    down_f = [((i + 1) % flow_n, i) for i in range(flow_n)]
    up_g = [(i, (i + 1) % grp_n) for i in range(grp_n)]
    down_g = [((i + 1) % grp_n, i) for i in range(grp_n)]
    size_x, size_y = field.shape[lead], field.shape[lead + 1]
    xlo = lax.ppermute(lax.index_in_dim(field, size_x - 1, lead, keepdims=False), "flow", up_f)
    xhi = lax.ppermute(lax.index_in_dim(field, 0, lead, keepdims=False), "flow", down_f)
    ylo = lax.ppermute(lax.slice_in_dim(field, size_y - 1, size_y, axis=lead + 1), "grp", up_g)
    yhi = lax.ppermute(lax.slice_in_dim(field, 0, 1, axis=lead + 1), "grp", down_g)
    return xlo, xhi, ylo, yhi


def project(lamb, projection):
    size_x, size_y, size_z = (lamb.shape[1], lamb.shape[2], lamb.shape[3])
    bx, by, bz = size_x // 8, size_y // 8, size_z // 8
    perm = np.zeros((size_z, size_z), np.float32)
    for ez in range(bz):
        for cz in range(8):
            perm[ez * 8 + cz, cz * bz + ez] = 1.0
    rows = lamb.reshape(-1, size_z)
    moved = jnp.dot(rows, jnp.asarray(perm, jnp.bfloat16), preferred_element_type=jnp.float32)
    moved = moved.astype(jnp.bfloat16)
    blocks = moved.reshape(3, bx, 8, by, 8, 8, bz).transpose(2, 4, 5, 0, 1, 3, 6).reshape(512, -1)
    padded_proj = jnp.pad(projection, ((0, 3), (0, 0)))
    source = jnp.dot(padded_proj, blocks, preferred_element_type=jnp.float32)
    source = source.reshape(128, 3, -1).transpose(1, 0, 2)
    return source.reshape(384, -1)


FACE_ROWS = 104


def extract_faces(state_ref, face_ref):
    for dim in range(3):
        for side, at in ((0, 0), (1, 4)):
            f = 2 * dim + side
            for comp in range(4):
                base = comp * 128
                if dim == 0:
                    face_ref[f, pl.ds(comp * 25, 25), :] = state_ref[pl.ds(base + at * 25, 25), :]
                elif dim == 1:
                    for a in range(5):
                        face_ref[f, pl.ds(comp * 25 + a * 5, 5), :] = state_ref[pl.ds(base + a * 25 + at * 5, 5), :]
                else:
                    face_ref[f, pl.ds(comp * 25, 25), :] = state_ref[pl.ds(base + at, 25, stride=5), :]


def send_faces(face_ref, sx0_ref, sx4_ref, sy0_ref, sy4_ref, row_len):
    sx0_ref[...] = face_ref[0]
    sx4_ref[...] = face_ref[1]
    sy0_ref[...] = face_ref[2][:, :row_len]
    last = pltpu.roll(face_ref[3], row_len, 1)
    sy4_ref[...] = last[:, :row_len]


def dg_faces_kernel(state_ref, vel_ref, mxup_ref, mxdn_ref, myup_ref, mydn_ref, face_ref):
    elems = state_ref.shape[1]
    face_ref[...] = jnp.zeros(face_ref.shape, jnp.float32)
    extract_faces(state_ref, face_ref)
    size_x, size_y, size_z = vel_ref.shape[1], vel_ref.shape[2], vel_ref.shape[3]
    half = size_z // 2
    row_len = size_z // 8
    for c in range(3):
        for h in range(2):
            mxup_ref[pl.ds(c * 2 * size_y + h * size_y, size_y), :] = vel_ref[c, size_x - 1, :, pl.ds(h * half, half)]
            mxdn_ref[pl.ds(c * 2 * size_y + h * size_y, size_y), :] = vel_ref[c, 0, :, pl.ds(h * half, half)]
            for x in range(size_x):
                at = c * 2 * size_x + h * size_x + x
                myup_ref[pl.ds(at, 1), :] = vel_ref[c, x, pl.ds(size_y - 1, 1), pl.ds(h * half, half)]
                mydn_ref[pl.ds(at, 1), :] = vel_ref[c, x, pl.ds(0, 1), pl.ds(h * half, half)]
    xrows = 3 * 2 * size_y
    yrows = 3 * 2 * size_x
    mxup_ref[pl.ds(xrows, FACE_ROWS), :] = face_ref[1]
    mxdn_ref[pl.ds(xrows, FACE_ROWS), :] = face_ref[0]
    lane = lax.broadcasted_iota(jnp.int32, (FACE_ROWS, elems), 1)
    myup_ref[pl.ds(yrows, FACE_ROWS), :] = jnp.where(lane < row_len, pltpu.roll(face_ref[3], row_len, 1), 0.0)
    mydn_ref[pl.ds(yrows, FACE_ROWS), :] = jnp.where(lane < row_len, face_ref[2], 0.0)


def dg_step_kernel(want_faces, xoff, yoff, row_len, flow_n, grp_n, state_ref, src_ref, xlo_ref, xhi_ref, ylo_ref, yhi_ref,
                   apu_ref, aup_ref, diag_ref, lift_ref, out_ref, *rest):
    if want_faces:
        sx0_ref, sx4_ref, sy0_ref, sy4_ref, face_ref, oth_ref, pad_ref, g_ref = rest
    else:
        face_ref, oth_ref, pad_ref, g_ref = rest
    elems = state_ref.shape[1]
    lane = lax.broadcasted_iota(jnp.int32, (FACE_ROWS, elems), 1)
    ez = lane % row_len
    face_ref[...] = jnp.zeros(face_ref.shape, jnp.float32)
    oth_ref[...] = jnp.zeros(oth_ref.shape, jnp.float32)
    extract_faces(state_ref, face_ref)
    flow_i = lax.axis_index("flow")
    grp_i = lax.axis_index("grp")
    oth_ref[pl.ds(0, FACE_ROWS), :] = jnp.where(flow_i == 0, 0.0, xlo_ref[pl.ds(xoff, FACE_ROWS), :])
    oth_ref[pl.ds(128, FACE_ROWS), :] = jnp.where(flow_i == flow_n - 1, 0.0, xhi_ref[pl.ds(xoff, FACE_ROWS), :])
    pad_ref[:, pl.ds(0, row_len)] = jnp.where(
        grp_i == 0, 0.0, ylo_ref[pl.ds(yoff, FACE_ROWS), pl.ds(0, row_len)])
    oth_ref[pl.ds(256, FACE_ROWS), :] = jnp.where(
        lane < row_len, pad_ref[...], pltpu.roll(face_ref[3], row_len, 1))
    pad_ref[:, pl.ds(0, row_len)] = jnp.where(
        grp_i == grp_n - 1, 0.0, yhi_ref[pl.ds(yoff, FACE_ROWS), pl.ds(0, row_len)])
    oth_ref[pl.ds(384, FACE_ROWS), :] = jnp.where(
        lane >= elems - row_len, pltpu.roll(pad_ref[...], elems - row_len, 1),
        pltpu.roll(face_ref[2], elems - row_len, 1))
    oth_ref[pl.ds(512, FACE_ROWS), :] = jnp.where(ez == 0, 0.0, pltpu.roll(face_ref[5], 1, 1))
    oth_ref[pl.ds(640, FACE_ROWS), :] = jnp.where(
        ez == row_len - 1, 0.0, pltpu.roll(face_ref[4], elems - 1, 1))
    g_ref[pl.ds(144, 8), :] = jnp.zeros((8, 4 * elems), jnp.float32)
    half = LIFT_FACTOR * 0.5
    for dim in range(3):
        for side, sign in ((0, -1.0), (1, 1.0)):
            f = 2 * dim + side
            o_p = oth_ref[pl.ds(f * 128, 25), :]
            o_u = [oth_ref[pl.ds(f * 128 + (1 + k) * 25, 25), :] for k in range(3)]
            g_ref[pl.ds(f * 25, 25), pl.ds(0, elems)] = half * (o_p - sign * o_u[dim])
            for k in range(3):
                value = half * o_u[k]
                if k == dim:
                    value = value - half * sign * o_p
                g_ref[pl.ds(f * 25, 25), pl.ds((1 + k) * elems, elems)] = value
    faces = jnp.dot(lift_ref[...], g_ref[...], precision=THREE_PASS, preferred_element_type=jnp.float32)
    state = state_ref[...]
    pres = state[:128]
    vel = state[128:]
    rate_p = jnp.dot(apu_ref[...], vel, precision=THREE_PASS, preferred_element_type=jnp.float32)
    rate_p = rate_p + diag_ref[pl.ds(0, 128), :] * pres + faces[:, :elems]
    out_ref[pl.ds(0, 128), :] = pres + TIME_STEP_ACOUSTIC * rate_p
    rate_u = jnp.dot(aup_ref[...], pres, precision=THREE_PASS, preferred_element_type=jnp.float32)
    for k in range(3):
        rows = pl.ds(128 + k * 128, 128)
        rate_k = rate_u[k * 128:(k + 1) * 128] + diag_ref[rows, :] * state_ref[rows, :]
        rate_k = rate_k + faces[:, (1 + k) * elems:(2 + k) * elems]
        out_ref[rows, :] = state_ref[rows, :] + TIME_STEP_ACOUSTIC * (rate_k - src_ref[pl.ds(k * 128, 128), :])
    if want_faces:
        extract_faces(out_ref, face_ref)
        send_faces(face_ref, sx0_ref, sx4_ref, sy0_ref, sy4_ref, row_len)


def face_shapes(elems, row_len):
    big = jax.ShapeDtypeStruct((FACE_ROWS, elems), jnp.float32)
    small = jax.ShapeDtypeStruct((FACE_ROWS, row_len), jnp.float32)
    return [big, big, small, small]


def dg_faces(state, vel):
    elems = state.shape[1]
    size_x, size_y, size_z = vel.shape[1], vel.shape[2], vel.shape[3]
    xbuf = jax.ShapeDtypeStruct((3 * 2 * size_y + FACE_ROWS, size_z // 2), jnp.float32)
    ybuf = jax.ShapeDtypeStruct((3 * 2 * size_x + FACE_ROWS, size_z // 2), jnp.float32)
    return pl.pallas_call(
        dg_faces_kernel,
        out_shape=(xbuf, xbuf, ybuf, ybuf),
        scratch_shapes=[pltpu.VMEM((6, FACE_ROWS, elems), jnp.float32)],
    )(state, vel)


def dg_step(state, src, recv, mats, want_faces, row_len, xoff=0, yoff=0):
    elems = state.shape[1]
    out_shape = [jax.ShapeDtypeStruct(state.shape, jnp.float32)]
    if want_faces:
        out_shape += face_shapes(elems, row_len)
    res = pl.pallas_call(
        lambda *refs: dg_step_kernel(want_faces, xoff, yoff, row_len, lax.axis_size("flow"), lax.axis_size("grp"), *refs),
        out_shape=tuple(out_shape),
        scratch_shapes=[
            pltpu.VMEM((6, FACE_ROWS, elems), jnp.float32),
            pltpu.VMEM((768, elems), jnp.float32),
            pltpu.VMEM((FACE_ROWS, elems), jnp.float32),
            pltpu.VMEM((152, 4 * elems), jnp.float32),
        ],
    )(state, src, *recv, *mats)
    return res


def exchange_faces(sent):
    sx0, sx4, sy0, sy4 = sent
    flow_n = lax.axis_size("flow")
    grp_n = lax.axis_size("grp")
    up_f = [(i, (i + 1) % flow_n) for i in range(flow_n)]
    down_f = [((i + 1) % flow_n, i) for i in range(flow_n)]
    up_g = [(i, (i + 1) % grp_n) for i in range(grp_n)]
    down_g = [((i + 1) % grp_n, i) for i in range(grp_n)]
    return (
        lax.ppermute(sx4, "flow", up_f),
        lax.ppermute(sx0, "flow", down_f),
        lax.ppermute(sy4, "grp", up_g),
        lax.ppermute(sy0, "grp", down_g),
    )


def body(velocity, eddy_visc, projection, acoustic_state, route_send, route_place):
    joint = halos(jnp.concatenate([velocity, eddy_visc[None]], axis=0), 1)
    flow_size = lax.axis_size("flow")
    grp_size = lax.axis_size("grp")
    slot_cap = route_send.shape[2]
    elem_count = acoustic_state.shape[2]
    total_slots = flow_size * grp_size * slot_cap
    placing = route_place.reshape(-1)
    sending = route_send.reshape(-1)
    place_hot = (placing[:, None] == jnp.arange(total_slots, dtype=jnp.int32)[None, :]).astype(jnp.float32)
    home_hot = (sending[:, None] == jnp.arange(elem_count, dtype=jnp.int32)[None, :]).astype(jnp.float32)
    padded_state = jnp.pad(acoustic_state, ((0, 0), (0, 3), (0, 0))).reshape(512, elem_count)
    outgoing = jnp.dot(padded_state, place_hot, precision=HIGH)
    arrived = lax.all_to_all(outgoing, ("flow", "grp"), split_axis=1, concat_axis=1, tiled=True)
    state = jnp.dot(arrived, home_hot, precision=HIGH)

    row_len = velocity.shape[3] // 8
    mats = [jnp.asarray(m) for m in dg_matrices()]
    vel = les_section_first(velocity, eddy_visc, joint)
    mxup, mxdn, myup, mydn = dg_faces(state, vel)
    merged = exchange_faces((mxdn, mxup, mydn, myup))
    vel, lamb = les_section_last(vel, eddy_visc, merged, joint)
    source = project(lamb, projection)
    xoff = 3 * 2 * velocity.shape[2]
    yoff = 3 * 2 * velocity.shape[1]
    res = dg_step(state, source, merged, mats, True, row_len, xoff, yoff)
    state = res[0]
    recv = exchange_faces(res[1:])
    state = dg_step(state, source, recv, mats, False, row_len)[0]
    leaving = lax.dot_general(state, home_hot, (((1,), (1,)), ((), ())), precision=HIGH)
    returned = lax.all_to_all(leaving, ("flow", "grp"), split_axis=1, concat_axis=1, tiled=True)
    acoustic_out = lax.dot_general(returned, place_hot, (((1,), (1,)), ((), ())), precision=HIGH)
    acoustic_out = acoustic_out.reshape(4, 128, elem_count)[:, :125]
    return (vel, acoustic_out)


def solution(mesh):
    placed = (
        P(None, "flow", "grp", None),
        P("flow", "grp", None),
        P(),
        P(None, None, ("flow", "grp")),
        P(("flow", "grp"), None, None),
        P(("flow", "grp"), None),
    )
    return jax.shard_map(
        body,
        mesh=mesh,
        in_specs=placed,
        out_specs=(P(None, "flow", "grp", None), P(None, None, ("flow", "grp"))),
        check_vma=False,
    )
```

```python
import math

import jax
import jax.numpy as jnp
import numpy as np
from jax import lax
from jax.experimental import pallas as pl
from jax.experimental.pallas import tpu as pltpu
from jax.sharding import PartitionSpec as P

LES_SECTIONS = 2
AC_SECTIONS = 2


TIME_STEP_LES = 0.15
TIME_STEP_ACOUSTIC = 0.02
GEOMETRY = 2.0
LIFT_FACTOR = 20.0
HIGH = lax.Precision.HIGHEST
THREE_PASS = lax.Precision.HIGH


def gll_derivative():
    gll_nodes = np.array([-1.0, -math.sqrt(3.0 / 7.0), 0.0, math.sqrt(3.0 / 7.0), 1.0])
    bary_weights = np.array(
        [
            1.0
            / np.prod([gll_nodes[first] - gll_nodes[other] for other in range(5) if other != first])
            for first in range(5)
        ]
    )
    matrix = np.zeros((5, 5))
    for row_id in range(5):
        for col_id in range(5):
            if row_id != col_id:
                matrix[row_id, col_id] = (
                    bary_weights[col_id]
                    / bary_weights[row_id]
                    / (gll_nodes[row_id] - gll_nodes[col_id])
                )
    for row_id in range(5):
        matrix[row_id, row_id] = -matrix[row_id].sum()
    return matrix


def node_id(coords):
    return coords[0] * 25 + coords[1] * 5 + coords[2]


def face_nodes(dim, at):
    ids = []
    for first in range(5):
        for second in range(5):
            coords = [first, second]
            coords.insert(dim, at)
            ids.append(node_id(coords))
    return ids


def dg_matrices():
    dmat = gll_derivative()
    half = LIFT_FACTOR * 0.5
    apu = np.zeros((128, 384))
    aup = np.zeros((384, 128))
    diag = np.zeros((512, 1))
    lift = np.zeros((128, 152))
    for a in range(5):
        for b in range(5):
            for c in range(5):
                pos = (a, b, c)
                row = node_id(pos)
                for dim in range(3):
                    for k in range(5):
                        col_pos = list(pos)
                        col_pos[dim] = k
                        col = node_id(col_pos)
                        weight = -GEOMETRY * dmat[pos[dim], k]
                        apu[row, dim * 128 + col] += weight
                        aup[dim * 128 + row, col] += weight
    for dim in range(3):
        for side, (sign, at) in enumerate(((-1.0, 0), (1.0, 4))):
            f = 2 * dim + side
            for t, node in enumerate(face_nodes(dim, at)):
                apu[node, dim * 128 + node] += half * sign
                aup[dim * 128 + node, node] += half * sign
                for comp in range(4):
                    diag[comp * 128 + node, 0] += -half
                lift[node, f * 25 + t] = 1.0
    return (apu.astype(np.float32), aup.astype(np.float32), diag.astype(np.float32), lift.astype(np.float32))


def face_rows(state, dim, at):
    elems = state.shape[-1]
    cube = state.reshape(4, 5, 5, 5, elems)
    face = lax.index_in_dim(cube, at, axis=1 + dim, keepdims=False)
    return face.reshape(100, elems)


def les_kernel(mode, flow_n, grp_n, vel_ref, nu_ref, vxlo_ref, vxhi_ref, vylo_ref, vyhi_ref,
               nxlo_ref, nxhi_ref, nylo_ref, nyhi_ref, *rest):
    size_x, size_y, size_z = vel_ref.shape[1], vel_ref.shape[2], vel_ref.shape[3]
    half = size_z // 2
    flow_i = lax.axis_index("flow")
    grp_i = lax.axis_index("grp")
    at_lo_f = flow_i == 0
    at_hi_f = flow_i == flow_n - 1
    at_lo_g = grp_i == 0
    at_hi_g = grp_i == grp_n - 1
    row = lax.broadcasted_iota(jnp.int32, (size_y, size_z), 0)
    lane = lax.broadcasted_iota(jnp.int32, (size_y, size_z), 1)
    if mode == 0:
        state_ref, out_ref, mxup_ref, mxdn_ref, myup_ref, mydn_ref, face_ref = rest

        def xlo(c):
            return jnp.where(at_lo_f, 0.0, vxlo_ref[c])

        def xhi(c):
            return jnp.where(at_hi_f, 0.0, vxhi_ref[c])

        def ylo(c, x):
            return jnp.where(at_lo_g, 0.0, vylo_ref[c, x])

        def yhi(c, x):
            return jnp.where(at_hi_g, 0.0, vyhi_ref[c, x])
    else:
        out_ref, lamb_ref = rest

        def plane(ref, c):
            return jnp.concatenate(
                [ref[pl.ds(c * 2 * size_y, size_y), :], ref[pl.ds(c * 2 * size_y + size_y, size_y), :]], axis=1)

        def line(ref, c, x):
            return jnp.concatenate(
                [ref[pl.ds(c * 2 * size_x + x, 1), :], ref[pl.ds(c * 2 * size_x + size_x + x, 1), :]], axis=1)

        def xlo(c):
            return jnp.where(at_lo_f, 0.0, plane(vxlo_ref, c))

        def xhi(c):
            return jnp.where(at_hi_f, 0.0, plane(vxhi_ref, c))

        def ylo(c, x):
            return jnp.where(at_lo_g, 0.0, line(vylo_ref, c, x))

        def yhi(c, x):
            return jnp.where(at_hi_g, 0.0, line(vyhi_ref, c, x))

    def yp(f, halo):
        return jnp.where(row == size_y - 1, halo, pltpu.roll(f, size_y - 1, 0))

    def ym(f, halo):
        return jnp.where(row == 0, halo, pltpu.roll(f, 1, 0))

    def zp(f):
        return jnp.where(lane == size_z - 1, 0.0, pltpu.roll(f, size_z - 1, 1))

    def zm(f):
        return jnp.where(lane == 0, 0.0, pltpu.roll(f, 1, 1))

    def step(x, carry):
        lo = jnp.maximum(x - 1, 0)
        hi = jnp.minimum(x + 1, size_x - 1)
        u = [vel_ref[c, x] for c in range(3)]
        uxm = [jnp.where(x == 0, xlo(c), vel_ref[c, lo]) for c in range(3)]
        uxp = [jnp.where(x == size_x - 1, xhi(c), vel_ref[c, hi]) for c in range(3)]
        uym = [ym(u[c], ylo(c, x)) for c in range(3)]
        uyp = [yp(u[c], yhi(c, x)) for c in range(3)]
        uzm = [zm(u[c]) for c in range(3)]
        uzp = [zp(u[c]) for c in range(3)]
        nu = nu_ref[x]
        nxm = jnp.where(x == 0, jnp.where(at_lo_f, 0.0, nxlo_ref[3]), nu_ref[lo])
        nxp = jnp.where(x == size_x - 1, jnp.where(at_hi_f, 0.0, nxhi_ref[3]), nu_ref[hi])
        nym = ym(nu, jnp.where(at_lo_g, 0.0, nylo_ref[3, x]))
        nyp = yp(nu, jnp.where(at_hi_g, 0.0, nyhi_ref[3, x]))
        nzm = zm(nu)
        nzp = zp(nu)
        plus = (uxp, uyp, uzp)
        minus = (uxm, uym, uzm)

        def d(c, axis):
            return 0.5 * (plus[axis][c] - minus[axis][c])

        wx = d(2, 1) - d(1, 2)
        wy = d(0, 2) - d(2, 0)
        wz = d(1, 0) - d(0, 1)
        lamb = (wy * u[2] - wz * u[1], wz * u[0] - wx * u[2], wx * u[1] - wy * u[0])
        ups = (0.5 * (nu + nxp), 0.5 * (nu + nyp), 0.5 * (nu + nzp))
        downs = (0.5 * (nu + nxm), 0.5 * (nu + nym), 0.5 * (nu + nzm))
        for c in range(3):
            total = None
            for axis in range(3):
                term = ups[axis] * (plus[axis][c] - u[c]) - downs[axis] * (u[c] - minus[axis][c])
                total = term if total is None else total + term
            out_ref[c, x] = u[c] + TIME_STEP_LES * (total - lamb[c])
            if mode == 1:
                lamb_ref[c, x] = lamb[c].astype(lamb_ref.dtype)
        return carry

    lax.fori_loop(0, size_x, step, 0)
    if mode == 0:
        for c in range(3):
            for h in range(2):
                mxup_ref[pl.ds(c * 2 * size_y + h * size_y, size_y), :] = out_ref[c, size_x - 1, :, pl.ds(h * half, half)]
                mxdn_ref[pl.ds(c * 2 * size_y + h * size_y, size_y), :] = out_ref[c, 0, :, pl.ds(h * half, half)]
                for x in range(size_x):
                    at = c * 2 * size_x + h * size_x + x
                    myup_ref[pl.ds(at, 1), :] = out_ref[c, x, pl.ds(size_y - 1, 1), pl.ds(h * half, half)]
                    mydn_ref[pl.ds(at, 1), :] = out_ref[c, x, pl.ds(0, 1), pl.ds(h * half, half)]
        xrows = 3 * 2 * size_y
        yrows = 3 * 2 * size_x
        elems = state_ref.shape[1]
        row_len = size_z // 8
        face_ref[...] = jnp.zeros(face_ref.shape, jnp.float32)
        extract_faces(state_ref, face_ref)
        mxup_ref[pl.ds(xrows, FACE_ROWS), :] = face_ref[1]
        mxdn_ref[pl.ds(xrows, FACE_ROWS), :] = face_ref[0]
        lane = lax.broadcasted_iota(jnp.int32, (FACE_ROWS, elems), 1)
        myup_ref[pl.ds(yrows, FACE_ROWS), :] = jnp.where(lane < row_len, pltpu.roll(face_ref[3], row_len, 1), 0.0)
        mydn_ref[pl.ds(yrows, FACE_ROWS), :] = jnp.where(lane < row_len, face_ref[2], 0.0)


def les_section_first(vel, nu, joint, state):
    size_x, size_y, size_z = vel.shape[1], vel.shape[2], vel.shape[3]
    xbuf = jax.ShapeDtypeStruct((3 * 2 * size_y + FACE_ROWS, size_z // 2), jnp.float32)
    ybuf = jax.ShapeDtypeStruct((3 * 2 * size_x + FACE_ROWS, size_z // 2), jnp.float32)
    return pl.pallas_call(
        lambda *refs: les_kernel(0, lax.axis_size("flow"), lax.axis_size("grp"), *refs),
        out_shape=(jax.ShapeDtypeStruct(vel.shape, jnp.float32), xbuf, xbuf, ybuf, ybuf),
        scratch_shapes=[pltpu.VMEM((6, FACE_ROWS, state.shape[1]), jnp.float32)],
    )(vel, nu, *joint, *joint, state)


def les_section_last(vel, nu, merged, joint):
    return pl.pallas_call(
        lambda *refs: les_kernel(1, lax.axis_size("flow"), lax.axis_size("grp"), *refs),
        out_shape=(jax.ShapeDtypeStruct(vel.shape, jnp.float32), jax.ShapeDtypeStruct(vel.shape, jnp.bfloat16)),
    )(vel, nu, *merged, *joint)


def halos(field, lead):
    flow_n = lax.axis_size("flow")
    grp_n = lax.axis_size("grp")
    up_f = [(i, (i + 1) % flow_n) for i in range(flow_n)]
    down_f = [((i + 1) % flow_n, i) for i in range(flow_n)]
    up_g = [(i, (i + 1) % grp_n) for i in range(grp_n)]
    down_g = [((i + 1) % grp_n, i) for i in range(grp_n)]
    size_x, size_y = field.shape[lead], field.shape[lead + 1]
    xlo = lax.ppermute(lax.index_in_dim(field, size_x - 1, lead, keepdims=False), "flow", up_f)
    xhi = lax.ppermute(lax.index_in_dim(field, 0, lead, keepdims=False), "flow", down_f)
    ylo = lax.ppermute(lax.slice_in_dim(field, size_y - 1, size_y, axis=lead + 1), "grp", up_g)
    yhi = lax.ppermute(lax.slice_in_dim(field, 0, 1, axis=lead + 1), "grp", down_g)
    return xlo, xhi, ylo, yhi


def halos_joint(vel, nu):
    flow_n = lax.axis_size("flow")
    grp_n = lax.axis_size("grp")
    up_f = [(i, (i + 1) % flow_n) for i in range(flow_n)]
    down_f = [((i + 1) % flow_n, i) for i in range(flow_n)]
    up_g = [(i, (i + 1) % grp_n) for i in range(grp_n)]
    down_g = [((i + 1) % grp_n, i) for i in range(grp_n)]
    size_x, size_y = nu.shape[0], nu.shape[1]

    def joined(vel_part, nu_part):
        return jnp.concatenate([vel_part, nu_part[None]], axis=0)

    xlo = lax.ppermute(joined(vel[:, size_x - 1], nu[size_x - 1]), "flow", up_f)
    xhi = lax.ppermute(joined(vel[:, 0], nu[0]), "flow", down_f)
    ylo = lax.ppermute(joined(vel[:, :, size_y - 1:], nu[:, size_y - 1:]), "grp", up_g)
    yhi = lax.ppermute(joined(vel[:, :, :1], nu[:, :1]), "grp", down_g)
    return xlo, xhi, ylo, yhi


def project(lamb, projection):
    size_x, size_y, size_z = (lamb.shape[1], lamb.shape[2], lamb.shape[3])
    bx, by, bz = size_x // 8, size_y // 8, size_z // 8
    perm = np.zeros((size_z, size_z), np.float32)
    for ez in range(bz):
        for cz in range(8):
            perm[ez * 8 + cz, cz * bz + ez] = 1.0
    rows = lamb.reshape(-1, size_z)
    moved = jnp.dot(rows, jnp.asarray(perm, jnp.bfloat16), preferred_element_type=jnp.float32)
    moved = moved.astype(jnp.bfloat16)
    blocks = moved.reshape(3, bx, 8, by, 8, 8, bz).transpose(2, 4, 5, 0, 1, 3, 6).reshape(512, -1)
    padded_proj = jnp.pad(projection, ((0, 3), (0, 0)))
    source = jnp.dot(padded_proj, blocks, preferred_element_type=jnp.float32)
    source = source.reshape(128, 3, -1).transpose(1, 0, 2)
    return source.reshape(384, -1)


FACE_ROWS = 104


def extract_faces(state_ref, face_ref):
    for dim in range(3):
        for side, at in ((0, 0), (1, 4)):
            f = 2 * dim + side
            for comp in range(4):
                base = comp * 128
                if dim == 0:
                    face_ref[f, pl.ds(comp * 25, 25), :] = state_ref[pl.ds(base + at * 25, 25), :]
                elif dim == 1:
                    for a in range(5):
                        face_ref[f, pl.ds(comp * 25 + a * 5, 5), :] = state_ref[pl.ds(base + a * 25 + at * 5, 5), :]
                else:
                    face_ref[f, pl.ds(comp * 25, 25), :] = state_ref[pl.ds(base + at, 25, stride=5), :]


def send_faces(face_ref, sx0_ref, sx4_ref, sy0_ref, sy4_ref, row_len):
    sx0_ref[...] = face_ref[0]
    sx4_ref[...] = face_ref[1]
    sy0_ref[...] = face_ref[2][:, :row_len]
    last = pltpu.roll(face_ref[3], row_len, 1)
    sy4_ref[...] = last[:, :row_len]


def dg_faces_kernel(state_ref, sx0_ref, sx4_ref, sy0_ref, sy4_ref, face_ref):
    face_ref[...] = jnp.zeros(face_ref.shape, jnp.float32)
    extract_faces(state_ref, face_ref)
    send_faces(face_ref, sx0_ref, sx4_ref, sy0_ref, sy4_ref, sy0_ref.shape[1])


def dg_step_kernel(want_faces, xoff, yoff, row_len, flow_n, grp_n, state_ref, src_ref, xlo_ref, xhi_ref, ylo_ref, yhi_ref,
                   apu_ref, aup_ref, diag_ref, lift_ref, out_ref, *rest):
    if want_faces:
        sx0_ref, sx4_ref, sy0_ref, sy4_ref, face_ref, oth_ref, pad_ref, g_ref = rest
    else:
        face_ref, oth_ref, pad_ref, g_ref = rest
    elems = state_ref.shape[1]
    lane = lax.broadcasted_iota(jnp.int32, (FACE_ROWS, elems), 1)
    ez = lane % row_len
    face_ref[...] = jnp.zeros(face_ref.shape, jnp.float32)
    oth_ref[...] = jnp.zeros(oth_ref.shape, jnp.float32)
    extract_faces(state_ref, face_ref)
    flow_i = lax.axis_index("flow")
    grp_i = lax.axis_index("grp")
    oth_ref[pl.ds(0, FACE_ROWS), :] = jnp.where(flow_i == 0, 0.0, xlo_ref[pl.ds(xoff, FACE_ROWS), :])
    oth_ref[pl.ds(128, FACE_ROWS), :] = jnp.where(flow_i == flow_n - 1, 0.0, xhi_ref[pl.ds(xoff, FACE_ROWS), :])
    pad_ref[:, pl.ds(0, row_len)] = jnp.where(
        grp_i == 0, 0.0, ylo_ref[pl.ds(yoff, FACE_ROWS), pl.ds(0, row_len)])
    oth_ref[pl.ds(256, FACE_ROWS), :] = jnp.where(
        lane < row_len, pad_ref[...], pltpu.roll(face_ref[3], row_len, 1))
    pad_ref[:, pl.ds(0, row_len)] = jnp.where(
        grp_i == grp_n - 1, 0.0, yhi_ref[pl.ds(yoff, FACE_ROWS), pl.ds(0, row_len)])
    oth_ref[pl.ds(384, FACE_ROWS), :] = jnp.where(
        lane >= elems - row_len, pltpu.roll(pad_ref[...], elems - row_len, 1),
        pltpu.roll(face_ref[2], elems - row_len, 1))
    oth_ref[pl.ds(512, FACE_ROWS), :] = jnp.where(ez == 0, 0.0, pltpu.roll(face_ref[5], 1, 1))
    oth_ref[pl.ds(640, FACE_ROWS), :] = jnp.where(
        ez == row_len - 1, 0.0, pltpu.roll(face_ref[4], elems - 1, 1))
    g_ref[pl.ds(144, 8), :] = jnp.zeros((8, 4 * elems), jnp.float32)
    half = LIFT_FACTOR * 0.5
    for dim in range(3):
        for side, sign in ((0, -1.0), (1, 1.0)):
            f = 2 * dim + side
            o_p = oth_ref[pl.ds(f * 128, 25), :]
            o_u = [oth_ref[pl.ds(f * 128 + (1 + k) * 25, 25), :] for k in range(3)]
            g_ref[pl.ds(f * 25, 25), pl.ds(0, elems)] = half * (o_p - sign * o_u[dim])
            for k in range(3):
                value = half * o_u[k]
                if k == dim:
                    value = value - half * sign * o_p
                g_ref[pl.ds(f * 25, 25), pl.ds((1 + k) * elems, elems)] = value
    faces = jnp.dot(lift_ref[...], g_ref[...], precision=THREE_PASS, preferred_element_type=jnp.float32)
    state = state_ref[...]
    pres = state[:128]
    vel = state[128:]
    rate_p = jnp.dot(apu_ref[...], vel, precision=THREE_PASS, preferred_element_type=jnp.float32)
    rate_p = rate_p + diag_ref[pl.ds(0, 128), :] * pres + faces[:, :elems]
    out_ref[pl.ds(0, 128), :] = pres + TIME_STEP_ACOUSTIC * rate_p
    rate_u = jnp.dot(aup_ref[...], pres, precision=THREE_PASS, preferred_element_type=jnp.float32)
    for k in range(3):
        rows = pl.ds(128 + k * 128, 128)
        rate_k = rate_u[k * 128:(k + 1) * 128] + diag_ref[rows, :] * state_ref[rows, :]
        rate_k = rate_k + faces[:, (1 + k) * elems:(2 + k) * elems]
        out_ref[rows, :] = state_ref[rows, :] + TIME_STEP_ACOUSTIC * (rate_k - src_ref[pl.ds(k * 128, 128), :])
    if want_faces:
        extract_faces(out_ref, face_ref)
        send_faces(face_ref, sx0_ref, sx4_ref, sy0_ref, sy4_ref, row_len)


def face_shapes(elems, row_len):
    big = jax.ShapeDtypeStruct((FACE_ROWS, elems), jnp.float32)
    small = jax.ShapeDtypeStruct((FACE_ROWS, row_len), jnp.float32)
    return [big, big, small, small]


def dg_faces(state, row_len):
    elems = state.shape[1]
    return pl.pallas_call(
        dg_faces_kernel,
        out_shape=tuple(face_shapes(elems, row_len)),
        scratch_shapes=[pltpu.VMEM((6, FACE_ROWS, elems), jnp.float32)],
    )(state)


def dg_step(state, src, recv, mats, want_faces, row_len, xoff=0, yoff=0):
    elems = state.shape[1]
    out_shape = [jax.ShapeDtypeStruct(state.shape, jnp.float32)]
    if want_faces:
        out_shape += face_shapes(elems, row_len)
    res = pl.pallas_call(
        lambda *refs: dg_step_kernel(want_faces, xoff, yoff, row_len, lax.axis_size("flow"), lax.axis_size("grp"), *refs),
        out_shape=tuple(out_shape),
        scratch_shapes=[
            pltpu.VMEM((6, FACE_ROWS, elems), jnp.float32),
            pltpu.VMEM((768, elems), jnp.float32),
            pltpu.VMEM((FACE_ROWS, elems), jnp.float32),
            pltpu.VMEM((152, 4 * elems), jnp.float32),
        ],
    )(state, src, *recv, *mats)
    return res


def exchange_faces(sent):
    sx0, sx4, sy0, sy4 = sent
    flow_n = lax.axis_size("flow")
    grp_n = lax.axis_size("grp")
    up_f = [(i, (i + 1) % flow_n) for i in range(flow_n)]
    down_f = [((i + 1) % flow_n, i) for i in range(flow_n)]
    up_g = [(i, (i + 1) % grp_n) for i in range(grp_n)]
    down_g = [((i + 1) % grp_n, i) for i in range(grp_n)]
    return (
        lax.ppermute(sx4, "flow", up_f),
        lax.ppermute(sx0, "flow", down_f),
        lax.ppermute(sy4, "grp", up_g),
        lax.ppermute(sy0, "grp", down_g),
    )


def body(velocity, eddy_visc, projection, acoustic_state, route_send, route_place):
    joint = halos_joint(velocity, eddy_visc)
    flow_size = lax.axis_size("flow")
    grp_size = lax.axis_size("grp")
    slot_cap = route_send.shape[2]
    elem_count = acoustic_state.shape[2]
    total_slots = flow_size * grp_size * slot_cap
    placing = route_place.reshape(-1)
    sending = route_send.reshape(-1)
    place_hot = (placing[:, None] == jnp.arange(total_slots, dtype=jnp.int32)[None, :]).astype(jnp.float32)
    home_hot = (sending[:, None] == jnp.arange(elem_count, dtype=jnp.int32)[None, :]).astype(jnp.float32)
    padded_state = jnp.pad(acoustic_state, ((0, 0), (0, 3), (0, 0))).reshape(512, elem_count)
    outgoing = jnp.dot(padded_state, place_hot, precision=HIGH)
    arrived = lax.all_to_all(outgoing, ("flow", "grp"), split_axis=1, concat_axis=1, tiled=True)
    state = jnp.dot(arrived, home_hot, precision=HIGH)

    row_len = velocity.shape[3] // 8
    mats = [jnp.asarray(m) for m in dg_matrices()]
    vel, mxup, mxdn, myup, mydn = les_section_first(velocity, eddy_visc, joint, state)
    merged = exchange_faces((mxdn, mxup, mydn, myup))
    vel, lamb = les_section_last(vel, eddy_visc, merged, joint)
    source = project(lamb, projection)
    xoff = 3 * 2 * velocity.shape[2]
    yoff = 3 * 2 * velocity.shape[1]
    res = dg_step(state, source, merged, mats, True, row_len, xoff, yoff)
    state = res[0]
    recv = exchange_faces(res[1:])
    state = dg_step(state, source, recv, mats, False, row_len)[0]
    leaving = lax.dot_general(state, home_hot, (((1,), (1,)), ((), ())), precision=HIGH)
    returned = lax.all_to_all(leaving, ("flow", "grp"), split_axis=1, concat_axis=1, tiled=True)
    returned = returned.reshape(4, 128, total_slots)[:, :acoustic_state.shape[1]]
    acoustic_out = lax.dot_general(returned, place_hot, (((2,), (1,)), ((), ())), precision=HIGH)
    return (vel, acoustic_out)


def solution(mesh):
    placed = (
        P(None, "flow", "grp", None),
        P("flow", "grp", None),
        P(),
        P(None, None, ("flow", "grp")),
        P(("flow", "grp"), None, None),
        P(("flow", "grp"), None),
    )
    return jax.shard_map(
        body,
        mesh=mesh,
        in_specs=placed,
        out_specs=(P(None, "flow", "grp", None), P(None, None, ("flow", "grp"))),
        check_vma=False,
    )
```

```python
import math

import jax
import jax.numpy as jnp
import numpy as np
from jax import lax
from jax.experimental import pallas as pl
from jax.experimental.pallas import tpu as pltpu
from jax.sharding import PartitionSpec as P

LES_SECTIONS = 2
AC_SECTIONS = 2


TIME_STEP_LES = 0.15
TIME_STEP_ACOUSTIC = 0.02
GEOMETRY = 2.0
LIFT_FACTOR = 20.0
HIGH = lax.Precision.HIGHEST
THREE_PASS = lax.Precision.HIGH


def gll_derivative():
    gll_nodes = np.array([-1.0, -math.sqrt(3.0 / 7.0), 0.0, math.sqrt(3.0 / 7.0), 1.0])
    bary_weights = np.array(
        [
            1.0
            / np.prod([gll_nodes[first] - gll_nodes[other] for other in range(5) if other != first])
            for first in range(5)
        ]
    )
    matrix = np.zeros((5, 5))
    for row_id in range(5):
        for col_id in range(5):
            if row_id != col_id:
                matrix[row_id, col_id] = (
                    bary_weights[col_id]
                    / bary_weights[row_id]
                    / (gll_nodes[row_id] - gll_nodes[col_id])
                )
    for row_id in range(5):
        matrix[row_id, row_id] = -matrix[row_id].sum()
    return matrix


def node_id(coords):
    return coords[0] * 25 + coords[1] * 5 + coords[2]


def face_nodes(dim, at):
    ids = []
    for first in range(5):
        for second in range(5):
            coords = [first, second]
            coords.insert(dim, at)
            ids.append(node_id(coords))
    return ids


def dg_matrices():
    dmat = gll_derivative()
    half = LIFT_FACTOR * 0.5
    apu = np.zeros((128, 384))
    aup = np.zeros((384, 128))
    diag = np.zeros((512, 1))
    lift = np.zeros((128, 152))
    for a in range(5):
        for b in range(5):
            for c in range(5):
                pos = (a, b, c)
                row = node_id(pos)
                for dim in range(3):
                    for k in range(5):
                        col_pos = list(pos)
                        col_pos[dim] = k
                        col = node_id(col_pos)
                        weight = -GEOMETRY * dmat[pos[dim], k]
                        apu[row, dim * 128 + col] += weight
                        aup[dim * 128 + row, col] += weight
    for dim in range(3):
        for side, (sign, at) in enumerate(((-1.0, 0), (1.0, 4))):
            f = 2 * dim + side
            for t, node in enumerate(face_nodes(dim, at)):
                apu[node, dim * 128 + node] += half * sign
                aup[dim * 128 + node, node] += half * sign
                for comp in range(4):
                    diag[comp * 128 + node, 0] += -half
                lift[node, f * 25 + t] = 1.0
    return (apu.astype(np.float32), aup.astype(np.float32), diag.astype(np.float32), lift.astype(np.float32))


def face_rows(state, dim, at):
    elems = state.shape[-1]
    cube = state.reshape(4, 5, 5, 5, elems)
    face = lax.index_in_dim(cube, at, axis=1 + dim, keepdims=False)
    return face.reshape(100, elems)


def les_kernel(mode, flow_n, grp_n, vel_ref, nu_ref, vxlo_ref, vxhi_ref, vylo_ref, vyhi_ref,
               nxlo_ref, nxhi_ref, nylo_ref, nyhi_ref, *rest):
    size_x, size_y, size_z = vel_ref.shape[1], vel_ref.shape[2], vel_ref.shape[3]
    half = size_z // 2
    flow_i = lax.axis_index("flow")
    grp_i = lax.axis_index("grp")
    at_lo_f = flow_i == 0
    at_hi_f = flow_i == flow_n - 1
    at_lo_g = grp_i == 0
    at_hi_g = grp_i == grp_n - 1
    row = lax.broadcasted_iota(jnp.int32, (size_y, size_z), 0)
    lane = lax.broadcasted_iota(jnp.int32, (size_y, size_z), 1)
    if mode == 0:
        state_ref, out_ref, mxup_ref, mxdn_ref, myup_ref, mydn_ref, face_ref = rest

        def xlo(c):
            return jnp.where(at_lo_f, 0.0, vxlo_ref[c])

        def xhi(c):
            return jnp.where(at_hi_f, 0.0, vxhi_ref[c])

        def ylo(c, x):
            return jnp.where(at_lo_g, 0.0, vylo_ref[c, x])

        def yhi(c, x):
            return jnp.where(at_hi_g, 0.0, vyhi_ref[c, x])
    else:
        out_ref, lamb_ref = rest

        def plane(ref, c):
            return jnp.concatenate(
                [ref[pl.ds(c * 2 * size_y, size_y), :], ref[pl.ds(c * 2 * size_y + size_y, size_y), :]], axis=1)

        def line(ref, c, x):
            return jnp.concatenate(
                [ref[pl.ds(c * 2 * size_x + x, 1), :], ref[pl.ds(c * 2 * size_x + size_x + x, 1), :]], axis=1)

        def xlo(c):
            return jnp.where(at_lo_f, 0.0, plane(vxlo_ref, c))

        def xhi(c):
            return jnp.where(at_hi_f, 0.0, plane(vxhi_ref, c))

        def ylo(c, x):
            return jnp.where(at_lo_g, 0.0, line(vylo_ref, c, x))

        def yhi(c, x):
            return jnp.where(at_hi_g, 0.0, line(vyhi_ref, c, x))

    def yp(f, halo):
        return jnp.where(row == size_y - 1, halo, pltpu.roll(f, size_y - 1, 0))

    def ym(f, halo):
        return jnp.where(row == 0, halo, pltpu.roll(f, 1, 0))

    def zp(f):
        return jnp.where(lane == size_z - 1, 0.0, pltpu.roll(f, size_z - 1, 1))

    def zm(f):
        return jnp.where(lane == 0, 0.0, pltpu.roll(f, 1, 1))

    def step(x, carry):
        lo = jnp.maximum(x - 1, 0)
        hi = jnp.minimum(x + 1, size_x - 1)
        u = [vel_ref[c, x] for c in range(3)]
        uxm = [jnp.where(x == 0, xlo(c), vel_ref[c, lo]) for c in range(3)]
        uxp = [jnp.where(x == size_x - 1, xhi(c), vel_ref[c, hi]) for c in range(3)]
        uym = [ym(u[c], ylo(c, x)) for c in range(3)]
        uyp = [yp(u[c], yhi(c, x)) for c in range(3)]
        uzm = [zm(u[c]) for c in range(3)]
        uzp = [zp(u[c]) for c in range(3)]
        nu = nu_ref[x]
        nxm = jnp.where(x == 0, jnp.where(at_lo_f, 0.0, nxlo_ref[3]), nu_ref[lo])
        nxp = jnp.where(x == size_x - 1, jnp.where(at_hi_f, 0.0, nxhi_ref[3]), nu_ref[hi])
        nym = ym(nu, jnp.where(at_lo_g, 0.0, nylo_ref[3, x]))
        nyp = yp(nu, jnp.where(at_hi_g, 0.0, nyhi_ref[3, x]))
        nzm = zm(nu)
        nzp = zp(nu)
        plus = (uxp, uyp, uzp)
        minus = (uxm, uym, uzm)

        def d(c, axis):
            return 0.5 * (plus[axis][c] - minus[axis][c])

        wx = d(2, 1) - d(1, 2)
        wy = d(0, 2) - d(2, 0)
        wz = d(1, 0) - d(0, 1)
        lamb = (wy * u[2] - wz * u[1], wz * u[0] - wx * u[2], wx * u[1] - wy * u[0])
        ups = (0.5 * (nu + nxp), 0.5 * (nu + nyp), 0.5 * (nu + nzp))
        downs = (0.5 * (nu + nxm), 0.5 * (nu + nym), 0.5 * (nu + nzm))
        for c in range(3):
            total = None
            for axis in range(3):
                term = ups[axis] * (plus[axis][c] - u[c]) - downs[axis] * (u[c] - minus[axis][c])
                total = term if total is None else total + term
            out_ref[c, x] = u[c] + TIME_STEP_LES * (total - lamb[c])
            if mode == 1:
                lamb_ref[c, x] = lamb[c].astype(lamb_ref.dtype)
        return carry

    lax.fori_loop(0, size_x, step, 0)
    if mode == 0:
        for c in range(3):
            for h in range(2):
                mxup_ref[pl.ds(c * 2 * size_y + h * size_y, size_y), :] = out_ref[c, size_x - 1, :, pl.ds(h * half, half)]
                mxdn_ref[pl.ds(c * 2 * size_y + h * size_y, size_y), :] = out_ref[c, 0, :, pl.ds(h * half, half)]
                for x in range(size_x):
                    at = c * 2 * size_x + h * size_x + x
                    myup_ref[pl.ds(at, 1), :] = out_ref[c, x, pl.ds(size_y - 1, 1), pl.ds(h * half, half)]
                    mydn_ref[pl.ds(at, 1), :] = out_ref[c, x, pl.ds(0, 1), pl.ds(h * half, half)]
        xrows = 3 * 2 * size_y
        yrows = 3 * 2 * size_x
        elems = state_ref.shape[1]
        row_len = size_z // 8
        face_ref[...] = jnp.zeros(face_ref.shape, jnp.float32)
        extract_faces(state_ref, face_ref)
        mxup_ref[pl.ds(xrows, FACE_ROWS), :] = face_ref[1]
        mxdn_ref[pl.ds(xrows, FACE_ROWS), :] = face_ref[0]
        lane = lax.broadcasted_iota(jnp.int32, (FACE_ROWS, elems), 1)
        myup_ref[pl.ds(yrows, FACE_ROWS), :] = jnp.where(lane < row_len, pltpu.roll(face_ref[3], row_len, 1), 0.0)
        mydn_ref[pl.ds(yrows, FACE_ROWS), :] = jnp.where(lane < row_len, face_ref[2], 0.0)


def les_section_first(vel, nu, joint, state):
    size_x, size_y, size_z = vel.shape[1], vel.shape[2], vel.shape[3]
    xbuf = jax.ShapeDtypeStruct((3 * 2 * size_y + FACE_ROWS, size_z // 2), jnp.float32)
    ybuf = jax.ShapeDtypeStruct((3 * 2 * size_x + FACE_ROWS, size_z // 2), jnp.float32)
    return pl.pallas_call(
        lambda *refs: les_kernel(0, lax.axis_size("flow"), lax.axis_size("grp"), *refs),
        out_shape=(jax.ShapeDtypeStruct(vel.shape, jnp.float32), xbuf, xbuf, ybuf, ybuf),
        scratch_shapes=[pltpu.VMEM((6, FACE_ROWS, state.shape[1]), jnp.float32)],
    )(vel, nu, *joint, *joint, state)


def les_section_last(vel, nu, merged, joint):
    return pl.pallas_call(
        lambda *refs: les_kernel(1, lax.axis_size("flow"), lax.axis_size("grp"), *refs),
        out_shape=(jax.ShapeDtypeStruct(vel.shape, jnp.float32), jax.ShapeDtypeStruct(vel.shape, jnp.bfloat16)),
    )(vel, nu, *merged, *joint)


def halos(field, lead):
    flow_n = lax.axis_size("flow")
    grp_n = lax.axis_size("grp")
    up_f = [(i, (i + 1) % flow_n) for i in range(flow_n)]
    down_f = [((i + 1) % flow_n, i) for i in range(flow_n)]
    up_g = [(i, (i + 1) % grp_n) for i in range(grp_n)]
    down_g = [((i + 1) % grp_n, i) for i in range(grp_n)]
    size_x, size_y = field.shape[lead], field.shape[lead + 1]
    xlo = lax.ppermute(lax.index_in_dim(field, size_x - 1, lead, keepdims=False), "flow", up_f)
    xhi = lax.ppermute(lax.index_in_dim(field, 0, lead, keepdims=False), "flow", down_f)
    ylo = lax.ppermute(lax.slice_in_dim(field, size_y - 1, size_y, axis=lead + 1), "grp", up_g)
    yhi = lax.ppermute(lax.slice_in_dim(field, 0, 1, axis=lead + 1), "grp", down_g)
    return xlo, xhi, ylo, yhi


def project(lamb, projection):
    size_x, size_y, size_z = (lamb.shape[1], lamb.shape[2], lamb.shape[3])
    bx, by, bz = size_x // 8, size_y // 8, size_z // 8
    perm = np.zeros((size_z, size_z), np.float32)
    for ez in range(bz):
        for cz in range(8):
            perm[ez * 8 + cz, cz * bz + ez] = 1.0
    rows = lamb.reshape(-1, size_z)
    moved = jnp.dot(rows, jnp.asarray(perm, jnp.bfloat16), preferred_element_type=jnp.float32)
    moved = moved.astype(jnp.bfloat16)
    blocks = moved.reshape(3, bx, 8, by, 8, 8, bz).transpose(2, 4, 5, 0, 1, 3, 6).reshape(512, -1)
    padded_proj = jnp.pad(projection, ((0, 3), (0, 0)))
    source = jnp.dot(padded_proj, blocks, preferred_element_type=jnp.float32)
    source = source.reshape(128, 3, -1).transpose(1, 0, 2)
    return source.reshape(384, -1)


FACE_ROWS = 104


def extract_faces(state_ref, face_ref):
    for dim in range(3):
        for side, at in ((0, 0), (1, 4)):
            f = 2 * dim + side
            for comp in range(4):
                base = comp * 128
                if dim == 0:
                    face_ref[f, pl.ds(comp * 25, 25), :] = state_ref[pl.ds(base + at * 25, 25), :]
                elif dim == 1:
                    for a in range(5):
                        face_ref[f, pl.ds(comp * 25 + a * 5, 5), :] = state_ref[pl.ds(base + a * 25 + at * 5, 5), :]
                else:
                    face_ref[f, pl.ds(comp * 25, 25), :] = state_ref[pl.ds(base + at, 25, stride=5), :]


def send_faces(face_ref, sx0_ref, sx4_ref, sy0_ref, sy4_ref, row_len):
    sx0_ref[...] = face_ref[0]
    sx4_ref[...] = face_ref[1]
    sy0_ref[...] = face_ref[2][:, :row_len]
    last = pltpu.roll(face_ref[3], row_len, 1)
    sy4_ref[...] = last[:, :row_len]


def dg_faces_kernel(state_ref, sx0_ref, sx4_ref, sy0_ref, sy4_ref, face_ref):
    face_ref[...] = jnp.zeros(face_ref.shape, jnp.float32)
    extract_faces(state_ref, face_ref)
    send_faces(face_ref, sx0_ref, sx4_ref, sy0_ref, sy4_ref, sy0_ref.shape[1])


def dg_step_kernel(want_faces, xoff, yoff, row_len, flow_n, grp_n, state_ref, src_ref, xlo_ref, xhi_ref, ylo_ref, yhi_ref,
                   apu_ref, aup_ref, diag_ref, lift_ref, out_ref, *rest):
    if want_faces:
        sx0_ref, sx4_ref, sy0_ref, sy4_ref, face_ref, oth_ref, pad_ref, g_ref = rest
    else:
        face_ref, oth_ref, pad_ref, g_ref = rest
    elems = state_ref.shape[1]
    lane = lax.broadcasted_iota(jnp.int32, (FACE_ROWS, elems), 1)
    ez = lane % row_len
    face_ref[...] = jnp.zeros(face_ref.shape, jnp.float32)
    oth_ref[...] = jnp.zeros(oth_ref.shape, jnp.float32)
    extract_faces(state_ref, face_ref)
    flow_i = lax.axis_index("flow")
    grp_i = lax.axis_index("grp")
    oth_ref[pl.ds(0, FACE_ROWS), :] = jnp.where(flow_i == 0, 0.0, xlo_ref[pl.ds(xoff, FACE_ROWS), :])
    oth_ref[pl.ds(128, FACE_ROWS), :] = jnp.where(flow_i == flow_n - 1, 0.0, xhi_ref[pl.ds(xoff, FACE_ROWS), :])
    pad_ref[:, pl.ds(0, row_len)] = jnp.where(
        grp_i == 0, 0.0, ylo_ref[pl.ds(yoff, FACE_ROWS), pl.ds(0, row_len)])
    oth_ref[pl.ds(256, FACE_ROWS), :] = jnp.where(
        lane < row_len, pad_ref[...], pltpu.roll(face_ref[3], row_len, 1))
    pad_ref[:, pl.ds(0, row_len)] = jnp.where(
        grp_i == grp_n - 1, 0.0, yhi_ref[pl.ds(yoff, FACE_ROWS), pl.ds(0, row_len)])
    oth_ref[pl.ds(384, FACE_ROWS), :] = jnp.where(
        lane >= elems - row_len, pltpu.roll(pad_ref[...], elems - row_len, 1),
        pltpu.roll(face_ref[2], elems - row_len, 1))
    oth_ref[pl.ds(512, FACE_ROWS), :] = jnp.where(ez == 0, 0.0, pltpu.roll(face_ref[5], 1, 1))
    oth_ref[pl.ds(640, FACE_ROWS), :] = jnp.where(
        ez == row_len - 1, 0.0, pltpu.roll(face_ref[4], elems - 1, 1))
    g_ref[pl.ds(144, 8), :] = jnp.zeros((8, 4 * elems), jnp.float32)
    half = LIFT_FACTOR * 0.5
    for dim in range(3):
        for side, sign in ((0, -1.0), (1, 1.0)):
            f = 2 * dim + side
            o_p = oth_ref[pl.ds(f * 128, 25), :]
            o_u = [oth_ref[pl.ds(f * 128 + (1 + k) * 25, 25), :] for k in range(3)]
            g_ref[pl.ds(f * 25, 25), pl.ds(0, elems)] = half * (o_p - sign * o_u[dim])
            for k in range(3):
                value = half * o_u[k]
                if k == dim:
                    value = value - half * sign * o_p
                g_ref[pl.ds(f * 25, 25), pl.ds((1 + k) * elems, elems)] = value
    faces = jnp.dot(lift_ref[...], g_ref[...], precision=THREE_PASS, preferred_element_type=jnp.float32)
    state = state_ref[...]
    pres = state[:128]
    vel = state[128:]
    rate_p = jnp.dot(apu_ref[...], vel, precision=THREE_PASS, preferred_element_type=jnp.float32)
    rate_p = rate_p + diag_ref[pl.ds(0, 128), :] * pres + faces[:, :elems]
    out_ref[pl.ds(0, 128), :] = pres + TIME_STEP_ACOUSTIC * rate_p
    rate_u = jnp.dot(aup_ref[...], pres, precision=THREE_PASS, preferred_element_type=jnp.float32)
    for k in range(3):
        rows = pl.ds(128 + k * 128, 128)
        rate_k = rate_u[k * 128:(k + 1) * 128] + diag_ref[rows, :] * state_ref[rows, :]
        rate_k = rate_k + faces[:, (1 + k) * elems:(2 + k) * elems]
        out_ref[rows, :] = state_ref[rows, :] + TIME_STEP_ACOUSTIC * (rate_k - src_ref[pl.ds(k * 128, 128), :])
    if want_faces:
        extract_faces(out_ref, face_ref)
        send_faces(face_ref, sx0_ref, sx4_ref, sy0_ref, sy4_ref, row_len)


def face_shapes(elems, row_len):
    big = jax.ShapeDtypeStruct((FACE_ROWS, elems), jnp.float32)
    small = jax.ShapeDtypeStruct((FACE_ROWS, row_len), jnp.float32)
    return [big, big, small, small]


def dg_faces(state, row_len):
    elems = state.shape[1]
    return pl.pallas_call(
        dg_faces_kernel,
        out_shape=tuple(face_shapes(elems, row_len)),
        scratch_shapes=[pltpu.VMEM((6, FACE_ROWS, elems), jnp.float32)],
    )(state)


def dg_step(state, src, recv, mats, want_faces, row_len, xoff=0, yoff=0):
    elems = state.shape[1]
    out_shape = [jax.ShapeDtypeStruct(state.shape, jnp.float32)]
    if want_faces:
        out_shape += face_shapes(elems, row_len)
    res = pl.pallas_call(
        lambda *refs: dg_step_kernel(want_faces, xoff, yoff, row_len, lax.axis_size("flow"), lax.axis_size("grp"), *refs),
        out_shape=tuple(out_shape),
        scratch_shapes=[
            pltpu.VMEM((6, FACE_ROWS, elems), jnp.float32),
            pltpu.VMEM((768, elems), jnp.float32),
            pltpu.VMEM((FACE_ROWS, elems), jnp.float32),
            pltpu.VMEM((152, 4 * elems), jnp.float32),
        ],
    )(state, src, *recv, *mats)
    return res


def exchange_faces(sent):
    sx0, sx4, sy0, sy4 = sent
    flow_n = lax.axis_size("flow")
    grp_n = lax.axis_size("grp")
    up_f = [(i, (i + 1) % flow_n) for i in range(flow_n)]
    down_f = [((i + 1) % flow_n, i) for i in range(flow_n)]
    up_g = [(i, (i + 1) % grp_n) for i in range(grp_n)]
    down_g = [((i + 1) % grp_n, i) for i in range(grp_n)]
    return (
        lax.ppermute(sx4, "flow", up_f),
        lax.ppermute(sx0, "flow", down_f),
        lax.ppermute(sy4, "grp", up_g),
        lax.ppermute(sy0, "grp", down_g),
    )


def body(velocity, eddy_visc, projection, acoustic_state, route_send, route_place):
    joint = halos(jnp.concatenate([velocity, eddy_visc[None]], axis=0), 1)
    flow_size = lax.axis_size("flow")
    grp_size = lax.axis_size("grp")
    slot_cap = route_send.shape[2]
    elem_count = acoustic_state.shape[2]
    total_slots = flow_size * grp_size * slot_cap
    placing = route_place.reshape(-1)
    sending = route_send.reshape(-1)
    place_hot = (placing[:, None] == jnp.arange(total_slots, dtype=jnp.int32)[None, :]).astype(jnp.float32)
    home_hot = (sending[:, None] == jnp.arange(elem_count, dtype=jnp.int32)[None, :]).astype(jnp.float32)
    padded_state = jnp.pad(acoustic_state, ((0, 0), (0, 3), (0, 0))).reshape(512, elem_count)
    outgoing = jnp.dot(padded_state, place_hot, precision=HIGH)
    arrived = lax.all_to_all(outgoing, ("flow", "grp"), split_axis=1, concat_axis=1, tiled=True)
    state = jnp.dot(arrived, home_hot, precision=HIGH)

    row_len = velocity.shape[3] // 8
    mats = [jnp.asarray(m) for m in dg_matrices()]
    vel, mxup, mxdn, myup, mydn = les_section_first(velocity, eddy_visc, joint, state)
    merged = exchange_faces((mxdn, mxup, mydn, myup))
    vel, lamb = les_section_last(vel, eddy_visc, merged, joint)
    source = project(lamb, projection)
    xoff = 3 * 2 * velocity.shape[2]
    yoff = 3 * 2 * velocity.shape[1]
    res = dg_step(state, source, merged, mats, True, row_len, xoff, yoff)
    state = res[0]
    recv = exchange_faces(res[1:])
    state = dg_step(state, source, recv, mats, False, row_len)[0]
    leaving = lax.dot_general(state, home_hot, (((1,), (1,)), ((), ())), precision=HIGH)
    returned = lax.all_to_all(leaving, ("flow", "grp"), split_axis=1, concat_axis=1, tiled=True)
    acoustic_out = lax.dot_general(returned, place_hot, (((1,), (1,)), ((), ())), precision=HIGH)
    acoustic_out = acoustic_out.reshape(4, 128, elem_count)[:, :125]
    return (vel, acoustic_out)


def solution(mesh):
    placed = (
        P(None, "flow", "grp", None),
        P("flow", "grp", None),
        P(),
        P(None, None, ("flow", "grp")),
        P(("flow", "grp"), None, None),
        P(("flow", "grp"), None),
    )
    return jax.shard_map(
        body,
        mesh=mesh,
        in_specs=placed,
        out_specs=(P(None, "flow", "grp", None), P(None, None, ("flow", "grp"))),
        check_vma=False,
    )
```

```python
import math

import jax
import jax.numpy as jnp
import numpy as np
from jax import lax
from jax.experimental import pallas as pl
from jax.experimental.pallas import tpu as pltpu
from jax.sharding import PartitionSpec as P

LES_SECTIONS = 2
AC_SECTIONS = 2


TIME_STEP_LES = 0.15
TIME_STEP_ACOUSTIC = 0.02
GEOMETRY = 2.0
LIFT_FACTOR = 20.0
HIGH = lax.Precision.HIGHEST
THREE_PASS = lax.Precision.HIGH


def gll_derivative():
    gll_nodes = np.array([-1.0, -math.sqrt(3.0 / 7.0), 0.0, math.sqrt(3.0 / 7.0), 1.0])
    bary_weights = np.array(
        [
            1.0
            / np.prod([gll_nodes[first] - gll_nodes[other] for other in range(5) if other != first])
            for first in range(5)
        ]
    )
    matrix = np.zeros((5, 5))
    for row_id in range(5):
        for col_id in range(5):
            if row_id != col_id:
                matrix[row_id, col_id] = (
                    bary_weights[col_id]
                    / bary_weights[row_id]
                    / (gll_nodes[row_id] - gll_nodes[col_id])
                )
    for row_id in range(5):
        matrix[row_id, row_id] = -matrix[row_id].sum()
    return matrix


def node_id(coords):
    return coords[0] * 25 + coords[1] * 5 + coords[2]


def face_nodes(dim, at):
    ids = []
    for first in range(5):
        for second in range(5):
            coords = [first, second]
            coords.insert(dim, at)
            ids.append(node_id(coords))
    return ids


def dg_matrices():
    dmat = gll_derivative()
    half = LIFT_FACTOR * 0.5
    apu = np.zeros((128, 384))
    aup = np.zeros((384, 128))
    diag = np.zeros((512, 1))
    lift = np.zeros((128, 152))
    for a in range(5):
        for b in range(5):
            for c in range(5):
                pos = (a, b, c)
                row = node_id(pos)
                for dim in range(3):
                    for k in range(5):
                        col_pos = list(pos)
                        col_pos[dim] = k
                        col = node_id(col_pos)
                        weight = -GEOMETRY * dmat[pos[dim], k]
                        apu[row, dim * 128 + col] += weight
                        aup[dim * 128 + row, col] += weight
    for dim in range(3):
        for side, (sign, at) in enumerate(((-1.0, 0), (1.0, 4))):
            f = 2 * dim + side
            for t, node in enumerate(face_nodes(dim, at)):
                apu[node, dim * 128 + node] += half * sign
                aup[dim * 128 + node, node] += half * sign
                for comp in range(4):
                    diag[comp * 128 + node, 0] += -half
                lift[node, f * 25 + t] = 1.0
    return (apu.astype(np.float32), aup.astype(np.float32), diag.astype(np.float32), lift.astype(np.float32))


def face_rows(state, dim, at):
    elems = state.shape[-1]
    cube = state.reshape(4, 5, 5, 5, elems)
    face = lax.index_in_dim(cube, at, axis=1 + dim, keepdims=False)
    return face.reshape(100, elems)


def les_kernel(mode, flow_n, grp_n, vel_ref, nu_ref, vxlo_ref, vxhi_ref, vylo_ref, vyhi_ref,
               nxlo_ref, nxhi_ref, nylo_ref, nyhi_ref, *rest):
    size_x, size_y, size_z = vel_ref.shape[1], vel_ref.shape[2], vel_ref.shape[3]
    half = size_z // 2
    flow_i = lax.axis_index("flow")
    grp_i = lax.axis_index("grp")
    at_lo_f = flow_i == 0
    at_hi_f = flow_i == flow_n - 1
    at_lo_g = grp_i == 0
    at_hi_g = grp_i == grp_n - 1
    row = lax.broadcasted_iota(jnp.int32, (size_y, size_z), 0)
    lane = lax.broadcasted_iota(jnp.int32, (size_y, size_z), 1)
    if mode == 0:
        state_ref, out_ref, mxup_ref, mxdn_ref, myup_ref, mydn_ref, face_ref = rest

        def xlo(c):
            return jnp.where(at_lo_f, 0.0, vxlo_ref[c])

        def xhi(c):
            return jnp.where(at_hi_f, 0.0, vxhi_ref[c])

        def ylo(c, x):
            return jnp.where(at_lo_g, 0.0, vylo_ref[c, x])

        def yhi(c, x):
            return jnp.where(at_hi_g, 0.0, vyhi_ref[c, x])
    else:
        out_ref, lamb_ref = rest

        def plane(ref, c):
            return jnp.concatenate(
                [ref[pl.ds(c * 2 * size_y, size_y), :], ref[pl.ds(c * 2 * size_y + size_y, size_y), :]], axis=1)

        def line(ref, c, x):
            return jnp.concatenate(
                [ref[pl.ds(c * 2 * size_x + x, 1), :], ref[pl.ds(c * 2 * size_x + size_x + x, 1), :]], axis=1)

        def xlo(c):
            return jnp.where(at_lo_f, 0.0, plane(vxlo_ref, c))

        def xhi(c):
            return jnp.where(at_hi_f, 0.0, plane(vxhi_ref, c))

        def ylo(c, x):
            return jnp.where(at_lo_g, 0.0, line(vylo_ref, c, x))

        def yhi(c, x):
            return jnp.where(at_hi_g, 0.0, line(vyhi_ref, c, x))

    def yp(f, halo):
        return jnp.where(row == size_y - 1, halo, pltpu.roll(f, size_y - 1, 0))

    def ym(f, halo):
        return jnp.where(row == 0, halo, pltpu.roll(f, 1, 0))

    def zp(f):
        return jnp.where(lane == size_z - 1, 0.0, pltpu.roll(f, size_z - 1, 1))

    def zm(f):
        return jnp.where(lane == 0, 0.0, pltpu.roll(f, 1, 1))

    def step(x, carry):
        lo = jnp.maximum(x - 1, 0)
        hi = jnp.minimum(x + 1, size_x - 1)
        u = [vel_ref[c, x] for c in range(3)]
        uxm = [jnp.where(x == 0, xlo(c), vel_ref[c, lo]) for c in range(3)]
        uxp = [jnp.where(x == size_x - 1, xhi(c), vel_ref[c, hi]) for c in range(3)]
        uym = [ym(u[c], ylo(c, x)) for c in range(3)]
        uyp = [yp(u[c], yhi(c, x)) for c in range(3)]
        uzm = [zm(u[c]) for c in range(3)]
        uzp = [zp(u[c]) for c in range(3)]
        nu = nu_ref[x]
        nxm = jnp.where(x == 0, jnp.where(at_lo_f, 0.0, nxlo_ref[3]), nu_ref[lo])
        nxp = jnp.where(x == size_x - 1, jnp.where(at_hi_f, 0.0, nxhi_ref[3]), nu_ref[hi])
        nym = ym(nu, jnp.where(at_lo_g, 0.0, nylo_ref[3, x]))
        nyp = yp(nu, jnp.where(at_hi_g, 0.0, nyhi_ref[3, x]))
        nzm = zm(nu)
        nzp = zp(nu)
        plus = (uxp, uyp, uzp)
        minus = (uxm, uym, uzm)

        def d(c, axis):
            return 0.5 * (plus[axis][c] - minus[axis][c])

        wx = d(2, 1) - d(1, 2)
        wy = d(0, 2) - d(2, 0)
        wz = d(1, 0) - d(0, 1)
        lamb = (wy * u[2] - wz * u[1], wz * u[0] - wx * u[2], wx * u[1] - wy * u[0])
        ups = (0.5 * (nu + nxp), 0.5 * (nu + nyp), 0.5 * (nu + nzp))
        downs = (0.5 * (nu + nxm), 0.5 * (nu + nym), 0.5 * (nu + nzm))
        for c in range(3):
            total = None
            for axis in range(3):
                term = ups[axis] * (plus[axis][c] - u[c]) - downs[axis] * (u[c] - minus[axis][c])
                total = term if total is None else total + term
            out_ref[c, x] = u[c] + TIME_STEP_LES * (total - lamb[c])
            if mode == 1:
                lamb_ref[c, x] = lamb[c].astype(lamb_ref.dtype)
        return carry

    lax.fori_loop(0, size_x, step, 0)
    if mode == 0:
        for c in range(3):
            for h in range(2):
                mxup_ref[pl.ds(c * 2 * size_y + h * size_y, size_y), :] = out_ref[c, size_x - 1, :, pl.ds(h * half, half)]
                mxdn_ref[pl.ds(c * 2 * size_y + h * size_y, size_y), :] = out_ref[c, 0, :, pl.ds(h * half, half)]
                for x in range(size_x):
                    at = c * 2 * size_x + h * size_x + x
                    myup_ref[pl.ds(at, 1), :] = out_ref[c, x, pl.ds(size_y - 1, 1), pl.ds(h * half, half)]
                    mydn_ref[pl.ds(at, 1), :] = out_ref[c, x, pl.ds(0, 1), pl.ds(h * half, half)]
        xrows = 3 * 2 * size_y
        yrows = 3 * 2 * size_x
        elems = state_ref.shape[1]
        row_len = size_z // 8
        face_ref[...] = jnp.zeros(face_ref.shape, jnp.float32)
        extract_faces(state_ref, face_ref)
        mxup_ref[pl.ds(xrows, FACE_ROWS), :] = face_ref[1]
        mxdn_ref[pl.ds(xrows, FACE_ROWS), :] = face_ref[0]
        lane = lax.broadcasted_iota(jnp.int32, (FACE_ROWS, elems), 1)
        myup_ref[pl.ds(yrows, FACE_ROWS), :] = jnp.where(lane < row_len, pltpu.roll(face_ref[3], row_len, 1), 0.0)
        mydn_ref[pl.ds(yrows, FACE_ROWS), :] = jnp.where(lane < row_len, face_ref[2], 0.0)


def les_section_first(vel, nu, joint, state):
    size_x, size_y, size_z = vel.shape[1], vel.shape[2], vel.shape[3]
    xbuf = jax.ShapeDtypeStruct((3 * 2 * size_y + FACE_ROWS, size_z // 2), jnp.float32)
    ybuf = jax.ShapeDtypeStruct((3 * 2 * size_x + FACE_ROWS, size_z // 2), jnp.float32)
    return pl.pallas_call(
        lambda *refs: les_kernel(0, lax.axis_size("flow"), lax.axis_size("grp"), *refs),
        out_shape=(jax.ShapeDtypeStruct(vel.shape, jnp.float32), xbuf, xbuf, ybuf, ybuf),
        scratch_shapes=[pltpu.VMEM((6, FACE_ROWS, state.shape[1]), jnp.float32)],
    )(vel, nu, *joint, *joint, state)


def les_section_last(vel, nu, merged, joint):
    return pl.pallas_call(
        lambda *refs: les_kernel(1, lax.axis_size("flow"), lax.axis_size("grp"), *refs),
        out_shape=(jax.ShapeDtypeStruct(vel.shape, jnp.float32), jax.ShapeDtypeStruct(vel.shape, jnp.bfloat16)),
    )(vel, nu, *merged, *joint)


def halos(field, lead):
    flow_n = lax.axis_size("flow")
    grp_n = lax.axis_size("grp")
    up_f = [(i, (i + 1) % flow_n) for i in range(flow_n)]
    down_f = [((i + 1) % flow_n, i) for i in range(flow_n)]
    up_g = [(i, (i + 1) % grp_n) for i in range(grp_n)]
    down_g = [((i + 1) % grp_n, i) for i in range(grp_n)]
    size_x, size_y = field.shape[lead], field.shape[lead + 1]
    xlo = lax.ppermute(lax.index_in_dim(field, size_x - 1, lead, keepdims=False), "flow", up_f)
    xhi = lax.ppermute(lax.index_in_dim(field, 0, lead, keepdims=False), "flow", down_f)
    ylo = lax.ppermute(lax.slice_in_dim(field, size_y - 1, size_y, axis=lead + 1), "grp", up_g)
    yhi = lax.ppermute(lax.slice_in_dim(field, 0, 1, axis=lead + 1), "grp", down_g)
    return xlo, xhi, ylo, yhi


def project(lamb, projection):
    size_x, size_y, size_z = (lamb.shape[1], lamb.shape[2], lamb.shape[3])
    bx, by, bz = size_x // 8, size_y // 8, size_z // 8
    perm = np.zeros((size_z, size_z), np.float32)
    for ez in range(bz):
        for cz in range(8):
            perm[ez * 8 + cz, cz * bz + ez] = 1.0
    rows = lamb.reshape(-1, size_z)
    moved = jnp.dot(rows, jnp.asarray(perm, jnp.bfloat16), preferred_element_type=jnp.float32)
    moved = moved.astype(jnp.bfloat16)
    blocks = moved.reshape(3, bx, 8, by, 8, 8, bz).transpose(2, 4, 5, 0, 1, 3, 6).reshape(512, -1)
    padded_proj = jnp.pad(projection, ((0, 3), (0, 0)))
    source = jnp.dot(padded_proj, blocks, preferred_element_type=jnp.float32)
    source = source.reshape(128, 3, -1).transpose(1, 0, 2)
    return source.reshape(384, -1)


FACE_ROWS = 104


def extract_faces(state_ref, face_ref):
    for dim in range(3):
        for side, at in ((0, 0), (1, 4)):
            f = 2 * dim + side
            for comp in range(4):
                base = comp * 128
                if dim == 0:
                    face_ref[f, pl.ds(comp * 25, 25), :] = state_ref[pl.ds(base + at * 25, 25), :]
                elif dim == 1:
                    for a in range(5):
                        face_ref[f, pl.ds(comp * 25 + a * 5, 5), :] = state_ref[pl.ds(base + a * 25 + at * 5, 5), :]
                else:
                    face_ref[f, pl.ds(comp * 25, 25), :] = state_ref[pl.ds(base + at, 25, stride=5), :]


def send_faces(face_ref, sx0_ref, sx4_ref, sy0_ref, sy4_ref, row_len):
    sx0_ref[...] = face_ref[0]
    sx4_ref[...] = face_ref[1]
    sy0_ref[...] = face_ref[2][:, :row_len]
    last = pltpu.roll(face_ref[3], row_len, 1)
    sy4_ref[...] = last[:, :row_len]


def dg_faces_kernel(state_ref, sx0_ref, sx4_ref, sy0_ref, sy4_ref, face_ref):
    face_ref[...] = jnp.zeros(face_ref.shape, jnp.float32)
    extract_faces(state_ref, face_ref)
    send_faces(face_ref, sx0_ref, sx4_ref, sy0_ref, sy4_ref, sy0_ref.shape[1])


def dg_step_kernel(want_faces, xoff, yoff, row_len, flow_n, grp_n, state_ref, src_ref, xlo_ref, xhi_ref, ylo_ref, yhi_ref,
                   apu_ref, aup_ref, diag_ref, lift_ref, out_ref, *rest):
    if want_faces:
        sx0_ref, sx4_ref, sy0_ref, sy4_ref, face_ref, oth_ref, pad_ref, g_ref = rest
    else:
        face_ref, oth_ref, pad_ref, g_ref = rest
    elems = state_ref.shape[1]
    lane = lax.broadcasted_iota(jnp.int32, (FACE_ROWS, elems), 1)
    ez = lane % row_len
    face_ref[...] = jnp.zeros(face_ref.shape, jnp.float32)
    oth_ref[...] = jnp.zeros(oth_ref.shape, jnp.float32)
    extract_faces(state_ref, face_ref)
    flow_i = lax.axis_index("flow")
    grp_i = lax.axis_index("grp")
    oth_ref[pl.ds(0, FACE_ROWS), :] = jnp.where(flow_i == 0, 0.0, xlo_ref[pl.ds(xoff, FACE_ROWS), :])
    oth_ref[pl.ds(128, FACE_ROWS), :] = jnp.where(flow_i == flow_n - 1, 0.0, xhi_ref[pl.ds(xoff, FACE_ROWS), :])
    pad_ref[:, pl.ds(0, row_len)] = jnp.where(
        grp_i == 0, 0.0, ylo_ref[pl.ds(yoff, FACE_ROWS), pl.ds(0, row_len)])
    oth_ref[pl.ds(256, FACE_ROWS), :] = jnp.where(
        lane < row_len, pad_ref[...], pltpu.roll(face_ref[3], row_len, 1))
    pad_ref[:, pl.ds(0, row_len)] = jnp.where(
        grp_i == grp_n - 1, 0.0, yhi_ref[pl.ds(yoff, FACE_ROWS), pl.ds(0, row_len)])
    oth_ref[pl.ds(384, FACE_ROWS), :] = jnp.where(
        lane >= elems - row_len, pltpu.roll(pad_ref[...], elems - row_len, 1),
        pltpu.roll(face_ref[2], elems - row_len, 1))
    oth_ref[pl.ds(512, FACE_ROWS), :] = jnp.where(ez == 0, 0.0, pltpu.roll(face_ref[5], 1, 1))
    oth_ref[pl.ds(640, FACE_ROWS), :] = jnp.where(
        ez == row_len - 1, 0.0, pltpu.roll(face_ref[4], elems - 1, 1))
    g_ref[pl.ds(144, 8), :] = jnp.zeros((8, 4 * elems), jnp.float32)
    half = LIFT_FACTOR * 0.5
    for dim in range(3):
        for side, sign in ((0, -1.0), (1, 1.0)):
            f = 2 * dim + side
            o_p = oth_ref[pl.ds(f * 128, 25), :]
            o_u = [oth_ref[pl.ds(f * 128 + (1 + k) * 25, 25), :] for k in range(3)]
            g_ref[pl.ds(f * 25, 25), pl.ds(0, elems)] = half * (o_p - sign * o_u[dim])
            for k in range(3):
                value = half * o_u[k]
                if k == dim:
                    value = value - half * sign * o_p
                g_ref[pl.ds(f * 25, 25), pl.ds((1 + k) * elems, elems)] = value
    faces = jnp.dot(lift_ref[...], g_ref[...], precision=THREE_PASS, preferred_element_type=jnp.float32)
    state = state_ref[...]
    pres = state[:128]
    vel = state[128:]
    rate_p = jnp.dot(apu_ref[...], vel, precision=THREE_PASS, preferred_element_type=jnp.float32)
    rate_p = rate_p + diag_ref[pl.ds(0, 128), :] * pres + faces[:, :elems]
    out_ref[pl.ds(0, 128), :] = pres + TIME_STEP_ACOUSTIC * rate_p
    rate_u = jnp.dot(aup_ref[...], pres, precision=THREE_PASS, preferred_element_type=jnp.float32)
    for k in range(3):
        rows = pl.ds(128 + k * 128, 128)
        rate_k = rate_u[k * 128:(k + 1) * 128] + diag_ref[rows, :] * state_ref[rows, :]
        rate_k = rate_k + faces[:, (1 + k) * elems:(2 + k) * elems]
        out_ref[rows, :] = state_ref[rows, :] + TIME_STEP_ACOUSTIC * (rate_k - src_ref[pl.ds(k * 128, 128), :])
    if want_faces:
        extract_faces(out_ref, face_ref)
        send_faces(face_ref, sx0_ref, sx4_ref, sy0_ref, sy4_ref, row_len)


def face_shapes(elems, row_len):
    big = jax.ShapeDtypeStruct((FACE_ROWS, elems), jnp.float32)
    small = jax.ShapeDtypeStruct((FACE_ROWS, row_len), jnp.float32)
    return [big, big, small, small]


def dg_faces(state, row_len):
    elems = state.shape[1]
    return pl.pallas_call(
        dg_faces_kernel,
        out_shape=tuple(face_shapes(elems, row_len)),
        scratch_shapes=[pltpu.VMEM((6, FACE_ROWS, elems), jnp.float32)],
    )(state)


def dg_step(state, src, recv, mats, want_faces, row_len, xoff=0, yoff=0):
    elems = state.shape[1]
    out_shape = [jax.ShapeDtypeStruct(state.shape, jnp.float32)]
    if want_faces:
        out_shape += face_shapes(elems, row_len)
    res = pl.pallas_call(
        lambda *refs: dg_step_kernel(want_faces, xoff, yoff, row_len, lax.axis_size("flow"), lax.axis_size("grp"), *refs),
        out_shape=tuple(out_shape),
        scratch_shapes=[
            pltpu.VMEM((6, FACE_ROWS, elems), jnp.float32),
            pltpu.VMEM((768, elems), jnp.float32),
            pltpu.VMEM((FACE_ROWS, elems), jnp.float32),
            pltpu.VMEM((152, 4 * elems), jnp.float32),
        ],
    )(state, src, *recv, *mats)
    return res


def exchange_faces(sent):
    sx0, sx4, sy0, sy4 = sent
    flow_n = lax.axis_size("flow")
    grp_n = lax.axis_size("grp")
    up_f = [(i, (i + 1) % flow_n) for i in range(flow_n)]
    down_f = [((i + 1) % flow_n, i) for i in range(flow_n)]
    up_g = [(i, (i + 1) % grp_n) for i in range(grp_n)]
    down_g = [((i + 1) % grp_n, i) for i in range(grp_n)]
    return (
        lax.ppermute(sx4, "flow", up_f),
        lax.ppermute(sx0, "flow", down_f),
        lax.ppermute(sy4, "grp", up_g),
        lax.ppermute(sy0, "grp", down_g),
    )


def body(velocity, eddy_visc, projection, acoustic_state, route_send, route_place):
    flow_size = lax.axis_size("flow")
    grp_size = lax.axis_size("grp")
    slot_cap = route_send.shape[2]
    elem_count = acoustic_state.shape[2]
    total_slots = flow_size * grp_size * slot_cap
    placing = route_place.reshape(-1)
    sending = route_send.reshape(-1)
    place_hot = (placing[:, None] == jnp.arange(total_slots, dtype=jnp.int32)[None, :]).astype(jnp.float32)
    home_hot = (sending[:, None] == jnp.arange(elem_count, dtype=jnp.int32)[None, :]).astype(jnp.float32)
    padded_state = jnp.pad(acoustic_state, ((0, 0), (0, 3), (0, 0))).reshape(512, elem_count)
    outgoing = jnp.dot(padded_state, place_hot, precision=HIGH)
    outgoing, vel_in, nu_in = lax.optimization_barrier((outgoing, velocity, eddy_visc))
    joint = halos(jnp.concatenate([vel_in, nu_in[None]], axis=0), 1)
    arrived = lax.all_to_all(outgoing, ("flow", "grp"), split_axis=1, concat_axis=1, tiled=True)
    state = jnp.dot(arrived, home_hot, precision=HIGH)

    row_len = velocity.shape[3] // 8
    mats = [jnp.asarray(m) for m in dg_matrices()]
    vel, mxup, mxdn, myup, mydn = les_section_first(vel_in, nu_in, joint, state)
    merged = exchange_faces((mxdn, mxup, mydn, myup))
    vel, lamb = les_section_last(vel, eddy_visc, merged, joint)
    source = project(lamb, projection)
    xoff = 3 * 2 * velocity.shape[2]
    yoff = 3 * 2 * velocity.shape[1]
    res = dg_step(state, source, merged, mats, True, row_len, xoff, yoff)
    state = res[0]
    recv = exchange_faces(res[1:])
    state = dg_step(state, source, recv, mats, False, row_len)[0]
    leaving = lax.dot_general(state, home_hot, (((1,), (1,)), ((), ())), precision=HIGH)
    returned = lax.all_to_all(leaving, ("flow", "grp"), split_axis=1, concat_axis=1, tiled=True)
    acoustic_out = lax.dot_general(returned, place_hot, (((1,), (1,)), ((), ())), precision=HIGH)
    acoustic_out = acoustic_out.reshape(4, 128, elem_count)[:, :125]
    return (vel, acoustic_out)


def solution(mesh):
    placed = (
        P(None, "flow", "grp", None),
        P("flow", "grp", None),
        P(),
        P(None, None, ("flow", "grp")),
        P(("flow", "grp"), None, None),
        P(("flow", "grp"), None),
    )
    return jax.shard_map(
        body,
        mesh=mesh,
        in_specs=placed,
        out_specs=(P(None, "flow", "grp", None), P(None, None, ("flow", "grp"))),
        check_vma=False,
    )
```

```python
import math

import jax
import jax.numpy as jnp
import numpy as np
from jax import lax
from jax.experimental import pallas as pl
from jax.experimental.pallas import tpu as pltpu
from jax.sharding import PartitionSpec as P

LES_SECTIONS = 2
AC_SECTIONS = 2


TIME_STEP_LES = 0.15
TIME_STEP_ACOUSTIC = 0.02
GEOMETRY = 2.0
LIFT_FACTOR = 20.0
HIGH = lax.Precision.HIGHEST
THREE_PASS = lax.Precision.HIGH


def gll_derivative():
    gll_nodes = np.array([-1.0, -math.sqrt(3.0 / 7.0), 0.0, math.sqrt(3.0 / 7.0), 1.0])
    bary_weights = np.array(
        [
            1.0
            / np.prod([gll_nodes[first] - gll_nodes[other] for other in range(5) if other != first])
            for first in range(5)
        ]
    )
    matrix = np.zeros((5, 5))
    for row_id in range(5):
        for col_id in range(5):
            if row_id != col_id:
                matrix[row_id, col_id] = (
                    bary_weights[col_id]
                    / bary_weights[row_id]
                    / (gll_nodes[row_id] - gll_nodes[col_id])
                )
    for row_id in range(5):
        matrix[row_id, row_id] = -matrix[row_id].sum()
    return matrix


def node_id(coords):
    return coords[0] * 25 + coords[1] * 5 + coords[2]


def face_nodes(dim, at):
    ids = []
    for first in range(5):
        for second in range(5):
            coords = [first, second]
            coords.insert(dim, at)
            ids.append(node_id(coords))
    return ids


def dg_matrices():
    dmat = gll_derivative()
    half = LIFT_FACTOR * 0.5
    apu = np.zeros((128, 384))
    aup = np.zeros((384, 128))
    diag = np.zeros((512, 1))
    lift = np.zeros((128, 152))
    for a in range(5):
        for b in range(5):
            for c in range(5):
                pos = (a, b, c)
                row = node_id(pos)
                for dim in range(3):
                    for k in range(5):
                        col_pos = list(pos)
                        col_pos[dim] = k
                        col = node_id(col_pos)
                        weight = -GEOMETRY * dmat[pos[dim], k]
                        apu[row, dim * 128 + col] += weight
                        aup[dim * 128 + row, col] += weight
    for dim in range(3):
        for side, (sign, at) in enumerate(((-1.0, 0), (1.0, 4))):
            f = 2 * dim + side
            for t, node in enumerate(face_nodes(dim, at)):
                apu[node, dim * 128 + node] += half * sign
                aup[dim * 128 + node, node] += half * sign
                for comp in range(4):
                    diag[comp * 128 + node, 0] += -half
                lift[node, f * 25 + t] = 1.0
    return (apu.astype(np.float32), aup.astype(np.float32), diag.astype(np.float32), lift.astype(np.float32))


def face_rows(state, dim, at):
    elems = state.shape[-1]
    cube = state.reshape(4, 5, 5, 5, elems)
    face = lax.index_in_dim(cube, at, axis=1 + dim, keepdims=False)
    return face.reshape(100, elems)


def les_kernel(mode, flow_n, grp_n, vel_ref, nu_ref, vxlo_ref, vxhi_ref, vylo_ref, vyhi_ref,
               nxlo_ref, nxhi_ref, nylo_ref, nyhi_ref, *rest):
    size_x, size_y, size_z = vel_ref.shape[1], vel_ref.shape[2], vel_ref.shape[3]
    half = size_z // 2
    flow_i = lax.axis_index("flow")
    grp_i = lax.axis_index("grp")
    at_lo_f = flow_i == 0
    at_hi_f = flow_i == flow_n - 1
    at_lo_g = grp_i == 0
    at_hi_g = grp_i == grp_n - 1
    row = lax.broadcasted_iota(jnp.int32, (size_y, size_z), 0)
    lane = lax.broadcasted_iota(jnp.int32, (size_y, size_z), 1)
    if mode == 0:
        state_ref, out_ref, mxup_ref, mxdn_ref, myup_ref, mydn_ref, face_ref = rest

        def xlo(c):
            return jnp.where(at_lo_f, 0.0, vxlo_ref[c])

        def xhi(c):
            return jnp.where(at_hi_f, 0.0, vxhi_ref[c])

        def ylo(c, x):
            return jnp.where(at_lo_g, 0.0, vylo_ref[c, x])

        def yhi(c, x):
            return jnp.where(at_hi_g, 0.0, vyhi_ref[c, x])
    else:
        out_ref, lamb_ref = rest

        def plane(ref, c):
            return jnp.concatenate(
                [ref[pl.ds(c * 2 * size_y, size_y), :], ref[pl.ds(c * 2 * size_y + size_y, size_y), :]], axis=1)

        def line(ref, c, x):
            return jnp.concatenate(
                [ref[pl.ds(c * 2 * size_x + x, 1), :], ref[pl.ds(c * 2 * size_x + size_x + x, 1), :]], axis=1)

        def xlo(c):
            return jnp.where(at_lo_f, 0.0, plane(vxlo_ref, c))

        def xhi(c):
            return jnp.where(at_hi_f, 0.0, plane(vxhi_ref, c))

        def ylo(c, x):
            return jnp.where(at_lo_g, 0.0, line(vylo_ref, c, x))

        def yhi(c, x):
            return jnp.where(at_hi_g, 0.0, line(vyhi_ref, c, x))

    def yp(f, halo):
        return jnp.where(row == size_y - 1, halo, pltpu.roll(f, size_y - 1, 0))

    def ym(f, halo):
        return jnp.where(row == 0, halo, pltpu.roll(f, 1, 0))

    def zp(f):
        return jnp.where(lane == size_z - 1, 0.0, pltpu.roll(f, size_z - 1, 1))

    def zm(f):
        return jnp.where(lane == 0, 0.0, pltpu.roll(f, 1, 1))

    def plane_step(x, first, last):
        lo = x - 1
        hi = x + 1
        u = [vel_ref[c, x] for c in range(3)]
        uxm = [xlo(c) if first else vel_ref[c, lo] for c in range(3)]
        uxp = [xhi(c) if last else vel_ref[c, hi] for c in range(3)]
        uym = [ym(u[c], ylo(c, x)) for c in range(3)]
        uyp = [yp(u[c], yhi(c, x)) for c in range(3)]
        uzm = [zm(u[c]) for c in range(3)]
        uzp = [zp(u[c]) for c in range(3)]
        nu = nu_ref[x]
        nxm = jnp.where(at_lo_f, 0.0, nxlo_ref[3]) if first else nu_ref[lo]
        nxp = jnp.where(at_hi_f, 0.0, nxhi_ref[3]) if last else nu_ref[hi]
        nym = ym(nu, jnp.where(at_lo_g, 0.0, nylo_ref[3, x]))
        nyp = yp(nu, jnp.where(at_hi_g, 0.0, nyhi_ref[3, x]))
        nzm = zm(nu)
        nzp = zp(nu)
        plus = (uxp, uyp, uzp)
        minus = (uxm, uym, uzm)

        def d(c, axis):
            return 0.5 * (plus[axis][c] - minus[axis][c])

        wx = d(2, 1) - d(1, 2)
        wy = d(0, 2) - d(2, 0)
        wz = d(1, 0) - d(0, 1)
        lamb = (wy * u[2] - wz * u[1], wz * u[0] - wx * u[2], wx * u[1] - wy * u[0])
        ups = (0.5 * (nu + nxp), 0.5 * (nu + nyp), 0.5 * (nu + nzp))
        downs = (0.5 * (nu + nxm), 0.5 * (nu + nym), 0.5 * (nu + nzm))
        for c in range(3):
            total = None
            for axis in range(3):
                term = ups[axis] * (plus[axis][c] - u[c]) - downs[axis] * (u[c] - minus[axis][c])
                total = term if total is None else total + term
            out_ref[c, x] = u[c] + TIME_STEP_LES * (total - lamb[c])
            if mode == 1:
                lamb_ref[c, x] = lamb[c].astype(lamb_ref.dtype)

    def step(x, carry):
        plane_step(x, False, False)
        return carry

    plane_step(0, True, False)
    lax.fori_loop(1, size_x - 1, step, 0)
    plane_step(size_x - 1, False, True)
    if mode == 0:
        for c in range(3):
            for h in range(2):
                mxup_ref[pl.ds(c * 2 * size_y + h * size_y, size_y), :] = out_ref[c, size_x - 1, :, pl.ds(h * half, half)]
                mxdn_ref[pl.ds(c * 2 * size_y + h * size_y, size_y), :] = out_ref[c, 0, :, pl.ds(h * half, half)]
                for x in range(size_x):
                    at = c * 2 * size_x + h * size_x + x
                    myup_ref[pl.ds(at, 1), :] = out_ref[c, x, pl.ds(size_y - 1, 1), pl.ds(h * half, half)]
                    mydn_ref[pl.ds(at, 1), :] = out_ref[c, x, pl.ds(0, 1), pl.ds(h * half, half)]
        xrows = 3 * 2 * size_y
        yrows = 3 * 2 * size_x
        elems = state_ref.shape[1]
        row_len = size_z // 8
        face_ref[...] = jnp.zeros(face_ref.shape, jnp.float32)
        extract_faces(state_ref, face_ref)
        mxup_ref[pl.ds(xrows, FACE_ROWS), :] = face_ref[1]
        mxdn_ref[pl.ds(xrows, FACE_ROWS), :] = face_ref[0]
        lane = lax.broadcasted_iota(jnp.int32, (FACE_ROWS, elems), 1)
        myup_ref[pl.ds(yrows, FACE_ROWS), :] = jnp.where(lane < row_len, pltpu.roll(face_ref[3], row_len, 1), 0.0)
        mydn_ref[pl.ds(yrows, FACE_ROWS), :] = jnp.where(lane < row_len, face_ref[2], 0.0)


def les_section_first(vel, nu, joint, state):
    size_x, size_y, size_z = vel.shape[1], vel.shape[2], vel.shape[3]
    xbuf = jax.ShapeDtypeStruct((3 * 2 * size_y + FACE_ROWS, size_z // 2), jnp.float32)
    ybuf = jax.ShapeDtypeStruct((3 * 2 * size_x + FACE_ROWS, size_z // 2), jnp.float32)
    return pl.pallas_call(
        lambda *refs: les_kernel(0, lax.axis_size("flow"), lax.axis_size("grp"), *refs),
        out_shape=(jax.ShapeDtypeStruct(vel.shape, jnp.float32), xbuf, xbuf, ybuf, ybuf),
        scratch_shapes=[pltpu.VMEM((6, FACE_ROWS, state.shape[1]), jnp.float32)],
    )(vel, nu, *joint, *joint, state)


def les_section_last(vel, nu, merged, joint):
    return pl.pallas_call(
        lambda *refs: les_kernel(1, lax.axis_size("flow"), lax.axis_size("grp"), *refs),
        out_shape=(jax.ShapeDtypeStruct(vel.shape, jnp.float32), jax.ShapeDtypeStruct(vel.shape, jnp.bfloat16)),
    )(vel, nu, *merged, *joint)


def halos(field, lead):
    flow_n = lax.axis_size("flow")
    grp_n = lax.axis_size("grp")
    up_f = [(i, (i + 1) % flow_n) for i in range(flow_n)]
    down_f = [((i + 1) % flow_n, i) for i in range(flow_n)]
    up_g = [(i, (i + 1) % grp_n) for i in range(grp_n)]
    down_g = [((i + 1) % grp_n, i) for i in range(grp_n)]
    size_x, size_y = field.shape[lead], field.shape[lead + 1]
    xlo = lax.ppermute(lax.index_in_dim(field, size_x - 1, lead, keepdims=False), "flow", up_f)
    xhi = lax.ppermute(lax.index_in_dim(field, 0, lead, keepdims=False), "flow", down_f)
    ylo = lax.ppermute(lax.slice_in_dim(field, size_y - 1, size_y, axis=lead + 1), "grp", up_g)
    yhi = lax.ppermute(lax.slice_in_dim(field, 0, 1, axis=lead + 1), "grp", down_g)
    return xlo, xhi, ylo, yhi


def project(lamb, projection):
    size_x, size_y, size_z = (lamb.shape[1], lamb.shape[2], lamb.shape[3])
    bx, by, bz = size_x // 8, size_y // 8, size_z // 8
    perm = np.zeros((size_z, size_z), np.float32)
    for ez in range(bz):
        for cz in range(8):
            perm[ez * 8 + cz, cz * bz + ez] = 1.0
    rows = lamb.reshape(-1, size_z)
    moved = jnp.dot(rows, jnp.asarray(perm, jnp.bfloat16), preferred_element_type=jnp.float32)
    moved = moved.astype(jnp.bfloat16)
    blocks = moved.reshape(3, bx, 8, by, 8, 8, bz).transpose(2, 4, 5, 0, 1, 3, 6).reshape(512, -1)
    padded_proj = jnp.pad(projection, ((0, 3), (0, 0)))
    source = jnp.dot(padded_proj, blocks, preferred_element_type=jnp.float32)
    source = source.reshape(128, 3, -1).transpose(1, 0, 2)
    return source.reshape(384, -1)


FACE_ROWS = 104


def extract_faces(state_ref, face_ref):
    for dim in range(3):
        for side, at in ((0, 0), (1, 4)):
            f = 2 * dim + side
            for comp in range(4):
                base = comp * 128
                if dim == 0:
                    face_ref[f, pl.ds(comp * 25, 25), :] = state_ref[pl.ds(base + at * 25, 25), :]
                elif dim == 1:
                    for a in range(5):
                        face_ref[f, pl.ds(comp * 25 + a * 5, 5), :] = state_ref[pl.ds(base + a * 25 + at * 5, 5), :]
                else:
                    face_ref[f, pl.ds(comp * 25, 25), :] = state_ref[pl.ds(base + at, 25, stride=5), :]


def send_faces(face_ref, sx0_ref, sx4_ref, sy0_ref, sy4_ref, row_len):
    sx0_ref[...] = face_ref[0]
    sx4_ref[...] = face_ref[1]
    sy0_ref[...] = face_ref[2][:, :row_len]
    last = pltpu.roll(face_ref[3], row_len, 1)
    sy4_ref[...] = last[:, :row_len]


def dg_faces_kernel(state_ref, sx0_ref, sx4_ref, sy0_ref, sy4_ref, face_ref):
    face_ref[...] = jnp.zeros(face_ref.shape, jnp.float32)
    extract_faces(state_ref, face_ref)
    send_faces(face_ref, sx0_ref, sx4_ref, sy0_ref, sy4_ref, sy0_ref.shape[1])


def dg_step_kernel(want_faces, xoff, yoff, row_len, flow_n, grp_n, state_ref, src_ref, xlo_ref, xhi_ref, ylo_ref, yhi_ref,
                   apu_ref, aup_ref, diag_ref, lift_ref, out_ref, *rest):
    if want_faces:
        sx0_ref, sx4_ref, sy0_ref, sy4_ref, face_ref, oth_ref, pad_ref, g_ref = rest
    else:
        face_ref, oth_ref, pad_ref, g_ref = rest
    elems = state_ref.shape[1]
    lane = lax.broadcasted_iota(jnp.int32, (FACE_ROWS, elems), 1)
    ez = lane % row_len
    face_ref[...] = jnp.zeros(face_ref.shape, jnp.float32)
    oth_ref[...] = jnp.zeros(oth_ref.shape, jnp.float32)
    extract_faces(state_ref, face_ref)
    flow_i = lax.axis_index("flow")
    grp_i = lax.axis_index("grp")
    oth_ref[pl.ds(0, FACE_ROWS), :] = jnp.where(flow_i == 0, 0.0, xlo_ref[pl.ds(xoff, FACE_ROWS), :])
    oth_ref[pl.ds(128, FACE_ROWS), :] = jnp.where(flow_i == flow_n - 1, 0.0, xhi_ref[pl.ds(xoff, FACE_ROWS), :])
    pad_ref[:, pl.ds(0, row_len)] = jnp.where(
        grp_i == 0, 0.0, ylo_ref[pl.ds(yoff, FACE_ROWS), pl.ds(0, row_len)])
    oth_ref[pl.ds(256, FACE_ROWS), :] = jnp.where(
        lane < row_len, pad_ref[...], pltpu.roll(face_ref[3], row_len, 1))
    pad_ref[:, pl.ds(0, row_len)] = jnp.where(
        grp_i == grp_n - 1, 0.0, yhi_ref[pl.ds(yoff, FACE_ROWS), pl.ds(0, row_len)])
    oth_ref[pl.ds(384, FACE_ROWS), :] = jnp.where(
        lane >= elems - row_len, pltpu.roll(pad_ref[...], elems - row_len, 1),
        pltpu.roll(face_ref[2], elems - row_len, 1))
    oth_ref[pl.ds(512, FACE_ROWS), :] = jnp.where(ez == 0, 0.0, pltpu.roll(face_ref[5], 1, 1))
    oth_ref[pl.ds(640, FACE_ROWS), :] = jnp.where(
        ez == row_len - 1, 0.0, pltpu.roll(face_ref[4], elems - 1, 1))
    g_ref[pl.ds(144, 8), :] = jnp.zeros((8, 4 * elems), jnp.float32)
    half = LIFT_FACTOR * 0.5
    for dim in range(3):
        for side, sign in ((0, -1.0), (1, 1.0)):
            f = 2 * dim + side
            o_p = oth_ref[pl.ds(f * 128, 25), :]
            o_u = [oth_ref[pl.ds(f * 128 + (1 + k) * 25, 25), :] for k in range(3)]
            g_ref[pl.ds(f * 25, 25), pl.ds(0, elems)] = half * (o_p - sign * o_u[dim])
            for k in range(3):
                value = half * o_u[k]
                if k == dim:
                    value = value - half * sign * o_p
                g_ref[pl.ds(f * 25, 25), pl.ds((1 + k) * elems, elems)] = value
    faces = jnp.dot(lift_ref[...], g_ref[...], precision=THREE_PASS, preferred_element_type=jnp.float32)
    state = state_ref[...]
    pres = state[:128]
    vel = state[128:]
    rate_p = jnp.dot(apu_ref[...], vel, precision=THREE_PASS, preferred_element_type=jnp.float32)
    rate_p = rate_p + diag_ref[pl.ds(0, 128), :] * pres + faces[:, :elems]
    out_ref[pl.ds(0, 128), :] = pres + TIME_STEP_ACOUSTIC * rate_p
    rate_u = jnp.dot(aup_ref[...], pres, precision=THREE_PASS, preferred_element_type=jnp.float32)
    for k in range(3):
        rows = pl.ds(128 + k * 128, 128)
        rate_k = rate_u[k * 128:(k + 1) * 128] + diag_ref[rows, :] * state_ref[rows, :]
        rate_k = rate_k + faces[:, (1 + k) * elems:(2 + k) * elems]
        out_ref[rows, :] = state_ref[rows, :] + TIME_STEP_ACOUSTIC * (rate_k - src_ref[pl.ds(k * 128, 128), :])
    if want_faces:
        extract_faces(out_ref, face_ref)
        send_faces(face_ref, sx0_ref, sx4_ref, sy0_ref, sy4_ref, row_len)


def face_shapes(elems, row_len):
    big = jax.ShapeDtypeStruct((FACE_ROWS, elems), jnp.float32)
    small = jax.ShapeDtypeStruct((FACE_ROWS, row_len), jnp.float32)
    return [big, big, small, small]


def dg_faces(state, row_len):
    elems = state.shape[1]
    return pl.pallas_call(
        dg_faces_kernel,
        out_shape=tuple(face_shapes(elems, row_len)),
        scratch_shapes=[pltpu.VMEM((6, FACE_ROWS, elems), jnp.float32)],
    )(state)


def dg_step(state, src, recv, mats, want_faces, row_len, xoff=0, yoff=0):
    elems = state.shape[1]
    out_shape = [jax.ShapeDtypeStruct(state.shape, jnp.float32)]
    if want_faces:
        out_shape += face_shapes(elems, row_len)
    res = pl.pallas_call(
        lambda *refs: dg_step_kernel(want_faces, xoff, yoff, row_len, lax.axis_size("flow"), lax.axis_size("grp"), *refs),
        out_shape=tuple(out_shape),
        scratch_shapes=[
            pltpu.VMEM((6, FACE_ROWS, elems), jnp.float32),
            pltpu.VMEM((768, elems), jnp.float32),
            pltpu.VMEM((FACE_ROWS, elems), jnp.float32),
            pltpu.VMEM((152, 4 * elems), jnp.float32),
        ],
    )(state, src, *recv, *mats)
    return res


def exchange_faces(sent):
    sx0, sx4, sy0, sy4 = sent
    flow_n = lax.axis_size("flow")
    grp_n = lax.axis_size("grp")
    up_f = [(i, (i + 1) % flow_n) for i in range(flow_n)]
    down_f = [((i + 1) % flow_n, i) for i in range(flow_n)]
    up_g = [(i, (i + 1) % grp_n) for i in range(grp_n)]
    down_g = [((i + 1) % grp_n, i) for i in range(grp_n)]
    return (
        lax.ppermute(sx4, "flow", up_f),
        lax.ppermute(sx0, "flow", down_f),
        lax.ppermute(sy4, "grp", up_g),
        lax.ppermute(sy0, "grp", down_g),
    )


def body(velocity, eddy_visc, projection, acoustic_state, route_send, route_place):
    joint = halos(jnp.concatenate([velocity, eddy_visc[None]], axis=0), 1)
    flow_size = lax.axis_size("flow")
    grp_size = lax.axis_size("grp")
    slot_cap = route_send.shape[2]
    elem_count = acoustic_state.shape[2]
    total_slots = flow_size * grp_size * slot_cap
    placing = route_place.reshape(-1)
    sending = route_send.reshape(-1)
    place_hot = (placing[:, None] == jnp.arange(total_slots, dtype=jnp.int32)[None, :]).astype(jnp.float32)
    home_hot = (sending[:, None] == jnp.arange(elem_count, dtype=jnp.int32)[None, :]).astype(jnp.float32)
    padded_state = jnp.pad(acoustic_state, ((0, 0), (0, 3), (0, 0))).reshape(512, elem_count)
    outgoing = jnp.dot(padded_state, place_hot, precision=HIGH)
    arrived = lax.all_to_all(outgoing, ("flow", "grp"), split_axis=1, concat_axis=1, tiled=True)
    state = jnp.dot(arrived, home_hot, precision=HIGH)

    row_len = velocity.shape[3] // 8
    mats = [jnp.asarray(m) for m in dg_matrices()]
    vel, mxup, mxdn, myup, mydn = les_section_first(velocity, eddy_visc, joint, state)
    merged = exchange_faces((mxdn, mxup, mydn, myup))
    vel, lamb = les_section_last(vel, eddy_visc, merged, joint)
    source = project(lamb, projection)
    xoff = 3 * 2 * velocity.shape[2]
    yoff = 3 * 2 * velocity.shape[1]
    res = dg_step(state, source, merged, mats, True, row_len, xoff, yoff)
    state = res[0]
    recv = exchange_faces(res[1:])
    state = dg_step(state, source, recv, mats, False, row_len)[0]
    leaving = lax.dot_general(state, home_hot, (((1,), (1,)), ((), ())), precision=HIGH)
    returned = lax.all_to_all(leaving, ("flow", "grp"), split_axis=1, concat_axis=1, tiled=True)
    acoustic_out = lax.dot_general(returned, place_hot, (((1,), (1,)), ((), ())), precision=HIGH)
    acoustic_out = acoustic_out.reshape(4, 128, elem_count)[:, :125]
    return (vel, acoustic_out)


def solution(mesh):
    placed = (
        P(None, "flow", "grp", None),
        P("flow", "grp", None),
        P(),
        P(None, None, ("flow", "grp")),
        P(("flow", "grp"), None, None),
        P(("flow", "grp"), None),
    )
    return jax.shard_map(
        body,
        mesh=mesh,
        in_specs=placed,
        out_specs=(P(None, "flow", "grp", None), P(None, None, ("flow", "grp"))),
        check_vma=False,
    )
```

```python
import math

import jax
import jax.numpy as jnp
import numpy as np
from jax import lax
from jax.experimental import pallas as pl
from jax.experimental.pallas import tpu as pltpu
from jax.sharding import PartitionSpec as P

LES_SECTIONS = 2
AC_SECTIONS = 2


TIME_STEP_LES = 0.15
TIME_STEP_ACOUSTIC = 0.02
GEOMETRY = 2.0
LIFT_FACTOR = 20.0
HIGH = lax.Precision.HIGHEST
THREE_PASS = lax.Precision.HIGH


def gll_derivative():
    gll_nodes = np.array([-1.0, -math.sqrt(3.0 / 7.0), 0.0, math.sqrt(3.0 / 7.0), 1.0])
    bary_weights = np.array(
        [
            1.0
            / np.prod([gll_nodes[first] - gll_nodes[other] for other in range(5) if other != first])
            for first in range(5)
        ]
    )
    matrix = np.zeros((5, 5))
    for row_id in range(5):
        for col_id in range(5):
            if row_id != col_id:
                matrix[row_id, col_id] = (
                    bary_weights[col_id]
                    / bary_weights[row_id]
                    / (gll_nodes[row_id] - gll_nodes[col_id])
                )
    for row_id in range(5):
        matrix[row_id, row_id] = -matrix[row_id].sum()
    return matrix


def node_id(coords):
    return coords[0] * 25 + coords[1] * 5 + coords[2]


def face_nodes(dim, at):
    ids = []
    for first in range(5):
        for second in range(5):
            coords = [first, second]
            coords.insert(dim, at)
            ids.append(node_id(coords))
    return ids


def dg_matrices():
    dmat = gll_derivative()
    half = LIFT_FACTOR * 0.5
    apu = np.zeros((128, 384))
    aup = np.zeros((384, 128))
    diag = np.zeros((512, 1))
    lift = np.zeros((128, 152))
    for a in range(5):
        for b in range(5):
            for c in range(5):
                pos = (a, b, c)
                row = node_id(pos)
                for dim in range(3):
                    for k in range(5):
                        col_pos = list(pos)
                        col_pos[dim] = k
                        col = node_id(col_pos)
                        weight = -GEOMETRY * dmat[pos[dim], k]
                        apu[row, dim * 128 + col] += weight
                        aup[dim * 128 + row, col] += weight
    for dim in range(3):
        for side, (sign, at) in enumerate(((-1.0, 0), (1.0, 4))):
            f = 2 * dim + side
            for t, node in enumerate(face_nodes(dim, at)):
                apu[node, dim * 128 + node] += half * sign
                aup[dim * 128 + node, node] += half * sign
                for comp in range(4):
                    diag[comp * 128 + node, 0] += -half
                lift[node, f * 25 + t] = 1.0
    return (apu.astype(np.float32), aup.astype(np.float32), diag.astype(np.float32), lift.astype(np.float32))


def face_rows(state, dim, at):
    elems = state.shape[-1]
    cube = state.reshape(4, 5, 5, 5, elems)
    face = lax.index_in_dim(cube, at, axis=1 + dim, keepdims=False)
    return face.reshape(100, elems)


def les_kernel(mode, flow_n, grp_n, vel_ref, nu_ref, vxlo_ref, vxhi_ref, vylo_ref, vyhi_ref,
               nxlo_ref, nxhi_ref, nylo_ref, nyhi_ref, *rest):
    size_x, size_y, size_z = vel_ref.shape[1], vel_ref.shape[2], vel_ref.shape[3]
    half = size_z // 2
    flow_i = lax.axis_index("flow")
    grp_i = lax.axis_index("grp")
    at_lo_f = flow_i == 0
    at_hi_f = flow_i == flow_n - 1
    at_lo_g = grp_i == 0
    at_hi_g = grp_i == grp_n - 1
    row = lax.broadcasted_iota(jnp.int32, (size_y, size_z), 0)
    lane = lax.broadcasted_iota(jnp.int32, (size_y, size_z), 1)
    if mode == 0:
        state_ref, out_ref, mxup_ref, mxdn_ref, myup_ref, mydn_ref, face_ref = rest

        def xlo(c):
            return jnp.where(at_lo_f, 0.0, vxlo_ref[c])

        def xhi(c):
            return jnp.where(at_hi_f, 0.0, vxhi_ref[c])

        def ylo(c, x):
            return jnp.where(at_lo_g, 0.0, vylo_ref[c, x])

        def yhi(c, x):
            return jnp.where(at_hi_g, 0.0, vyhi_ref[c, x])
    else:
        out_ref, lamb_ref = rest

        def plane(ref, c):
            return jnp.concatenate(
                [ref[pl.ds(c * 2 * size_y, size_y), :], ref[pl.ds(c * 2 * size_y + size_y, size_y), :]], axis=1)

        def line(ref, c, x):
            return jnp.concatenate(
                [ref[pl.ds(c * 2 * size_x + x, 1), :], ref[pl.ds(c * 2 * size_x + size_x + x, 1), :]], axis=1)

        def xlo(c):
            return jnp.where(at_lo_f, 0.0, plane(vxlo_ref, c))

        def xhi(c):
            return jnp.where(at_hi_f, 0.0, plane(vxhi_ref, c))

        def ylo(c, x):
            return jnp.where(at_lo_g, 0.0, line(vylo_ref, c, x))

        def yhi(c, x):
            return jnp.where(at_hi_g, 0.0, line(vyhi_ref, c, x))

    def yp(f, halo):
        return jnp.where(row == size_y - 1, halo, pltpu.roll(f, size_y - 1, 0))

    def ym(f, halo):
        return jnp.where(row == 0, halo, pltpu.roll(f, 1, 0))

    def zp(f):
        return jnp.where(lane == size_z - 1, 0.0, pltpu.roll(f, size_z - 1, 1))

    def zm(f):
        return jnp.where(lane == 0, 0.0, pltpu.roll(f, 1, 1))

    def plane_step(x, first, last):
        lo = x - 1
        hi = x + 1
        u = [vel_ref[c, x] for c in range(3)]
        uxm = [xlo(c) if first else vel_ref[c, lo] for c in range(3)]
        uxp = [xhi(c) if last else vel_ref[c, hi] for c in range(3)]
        uym = [ym(u[c], ylo(c, x)) for c in range(3)]
        uyp = [yp(u[c], yhi(c, x)) for c in range(3)]
        uzm = [zm(u[c]) for c in range(3)]
        uzp = [zp(u[c]) for c in range(3)]
        nu = nu_ref[x]
        nxm = jnp.where(at_lo_f, 0.0, nxlo_ref[3]) if first else nu_ref[lo]
        nxp = jnp.where(at_hi_f, 0.0, nxhi_ref[3]) if last else nu_ref[hi]
        nym = ym(nu, jnp.where(at_lo_g, 0.0, nylo_ref[3, x]))
        nyp = yp(nu, jnp.where(at_hi_g, 0.0, nyhi_ref[3, x]))
        nzm = zm(nu)
        nzp = zp(nu)
        plus = (uxp, uyp, uzp)
        minus = (uxm, uym, uzm)

        def d(c, axis):
            return 0.5 * (plus[axis][c] - minus[axis][c])

        wx = d(2, 1) - d(1, 2)
        wy = d(0, 2) - d(2, 0)
        wz = d(1, 0) - d(0, 1)
        lamb = (wy * u[2] - wz * u[1], wz * u[0] - wx * u[2], wx * u[1] - wy * u[0])
        ups = (0.5 * (nu + nxp), 0.5 * (nu + nyp), 0.5 * (nu + nzp))
        downs = (0.5 * (nu + nxm), 0.5 * (nu + nym), 0.5 * (nu + nzm))
        for c in range(3):
            total = None
            for axis in range(3):
                term = ups[axis] * (plus[axis][c] - u[c]) - downs[axis] * (u[c] - minus[axis][c])
                total = term if total is None else total + term
            out_ref[c, x] = u[c] + TIME_STEP_LES * (total - lamb[c])
            if mode == 1:
                lamb_ref[c, x] = lamb[c].astype(lamb_ref.dtype)

    def step(x, carry):
        plane_step(x, False, False)
        return carry

    plane_step(0, True, False)
    lax.fori_loop(1, size_x - 1, step, 0)
    plane_step(size_x - 1, False, True)
    if mode == 0:
        for c in range(3):
            for h in range(2):
                mxup_ref[pl.ds(c * 2 * size_y + h * size_y, size_y), :] = out_ref[c, size_x - 1, :, pl.ds(h * half, half)]
                mxdn_ref[pl.ds(c * 2 * size_y + h * size_y, size_y), :] = out_ref[c, 0, :, pl.ds(h * half, half)]
                for x in range(size_x):
                    at = c * 2 * size_x + h * size_x + x
                    myup_ref[pl.ds(at, 1), :] = out_ref[c, x, pl.ds(size_y - 1, 1), pl.ds(h * half, half)]
                    mydn_ref[pl.ds(at, 1), :] = out_ref[c, x, pl.ds(0, 1), pl.ds(h * half, half)]
        xrows = 3 * 2 * size_y
        yrows = 3 * 2 * size_x
        elems = state_ref.shape[1]
        row_len = size_z // 8
        face_ref[...] = jnp.zeros(face_ref.shape, jnp.float32)
        extract_faces(state_ref, face_ref)
        mxup_ref[pl.ds(xrows, FACE_ROWS), :] = face_ref[1]
        mxdn_ref[pl.ds(xrows, FACE_ROWS), :] = face_ref[0]
        lane = lax.broadcasted_iota(jnp.int32, (FACE_ROWS, elems), 1)
        myup_ref[pl.ds(yrows, FACE_ROWS), :] = jnp.where(lane < row_len, pltpu.roll(face_ref[3], row_len, 1), 0.0)
        mydn_ref[pl.ds(yrows, FACE_ROWS), :] = jnp.where(lane < row_len, face_ref[2], 0.0)


def les_section_first(vel, nu, joint, state):
    size_x, size_y, size_z = vel.shape[1], vel.shape[2], vel.shape[3]
    xbuf = jax.ShapeDtypeStruct((3 * 2 * size_y + FACE_ROWS, size_z // 2), jnp.float32)
    ybuf = jax.ShapeDtypeStruct((3 * 2 * size_x + FACE_ROWS, size_z // 2), jnp.float32)
    def kernel(vel_ref, nu_ref, xlo_ref, xhi_ref, ylo_ref, yhi_ref, *rest):
        halo_refs = (xlo_ref, xhi_ref, ylo_ref, yhi_ref)
        les_kernel(0, lax.axis_size("flow"), lax.axis_size("grp"), vel_ref, nu_ref, *halo_refs, *halo_refs, *rest)

    return pl.pallas_call(
        kernel,
        out_shape=(jax.ShapeDtypeStruct(vel.shape, jnp.float32), xbuf, xbuf, ybuf, ybuf),
        scratch_shapes=[pltpu.VMEM((6, FACE_ROWS, state.shape[1]), jnp.float32)],
    )(vel, nu, *joint, state)


def les_section_last(vel, nu, merged, joint):
    return pl.pallas_call(
        lambda *refs: les_kernel(1, lax.axis_size("flow"), lax.axis_size("grp"), *refs),
        out_shape=(jax.ShapeDtypeStruct(vel.shape, jnp.float32), jax.ShapeDtypeStruct(vel.shape, jnp.bfloat16)),
    )(vel, nu, *merged, *joint)


def halos(field, lead):
    flow_n = lax.axis_size("flow")
    grp_n = lax.axis_size("grp")
    up_f = [(i, (i + 1) % flow_n) for i in range(flow_n)]
    down_f = [((i + 1) % flow_n, i) for i in range(flow_n)]
    up_g = [(i, (i + 1) % grp_n) for i in range(grp_n)]
    down_g = [((i + 1) % grp_n, i) for i in range(grp_n)]
    size_x, size_y = field.shape[lead], field.shape[lead + 1]
    xlo = lax.ppermute(lax.index_in_dim(field, size_x - 1, lead, keepdims=False), "flow", up_f)
    xhi = lax.ppermute(lax.index_in_dim(field, 0, lead, keepdims=False), "flow", down_f)
    ylo = lax.ppermute(lax.slice_in_dim(field, size_y - 1, size_y, axis=lead + 1), "grp", up_g)
    yhi = lax.ppermute(lax.slice_in_dim(field, 0, 1, axis=lead + 1), "grp", down_g)
    return xlo, xhi, ylo, yhi


def project(lamb, projection):
    size_x, size_y, size_z = (lamb.shape[1], lamb.shape[2], lamb.shape[3])
    bx, by, bz = size_x // 8, size_y // 8, size_z // 8
    perm = np.zeros((size_z, size_z), np.float32)
    for ez in range(bz):
        for cz in range(8):
            perm[ez * 8 + cz, cz * bz + ez] = 1.0
    rows = lamb.reshape(-1, size_z)
    moved = jnp.dot(rows, jnp.asarray(perm, jnp.bfloat16), preferred_element_type=jnp.float32)
    moved = moved.astype(jnp.bfloat16)
    blocks = moved.reshape(3, bx, 8, by, 8, 8, bz).transpose(2, 4, 5, 0, 1, 3, 6).reshape(512, -1)
    padded_proj = jnp.pad(projection, ((0, 3), (0, 0)))
    source = jnp.dot(padded_proj, blocks, preferred_element_type=jnp.float32)
    source = source.reshape(128, 3, -1).transpose(1, 0, 2)
    return source.reshape(384, -1)


FACE_ROWS = 104


def extract_faces(state_ref, face_ref):
    for dim in range(3):
        for side, at in ((0, 0), (1, 4)):
            f = 2 * dim + side
            for comp in range(4):
                base = comp * 128
                if dim == 0:
                    face_ref[f, pl.ds(comp * 25, 25), :] = state_ref[pl.ds(base + at * 25, 25), :]
                elif dim == 1:
                    for a in range(5):
                        face_ref[f, pl.ds(comp * 25 + a * 5, 5), :] = state_ref[pl.ds(base + a * 25 + at * 5, 5), :]
                else:
                    face_ref[f, pl.ds(comp * 25, 25), :] = state_ref[pl.ds(base + at, 25, stride=5), :]


def send_faces(face_ref, sx0_ref, sx4_ref, sy0_ref, sy4_ref, row_len):
    sx0_ref[...] = face_ref[0]
    sx4_ref[...] = face_ref[1]
    sy0_ref[...] = face_ref[2][:, :row_len]
    last = pltpu.roll(face_ref[3], row_len, 1)
    sy4_ref[...] = last[:, :row_len]


def dg_faces_kernel(state_ref, sx0_ref, sx4_ref, sy0_ref, sy4_ref, face_ref):
    face_ref[...] = jnp.zeros(face_ref.shape, jnp.float32)
    extract_faces(state_ref, face_ref)
    send_faces(face_ref, sx0_ref, sx4_ref, sy0_ref, sy4_ref, sy0_ref.shape[1])


def dg_step_kernel(want_faces, xoff, yoff, row_len, flow_n, grp_n, state_ref, src_ref, xlo_ref, xhi_ref, ylo_ref, yhi_ref,
                   apu_ref, aup_ref, diag_ref, lift_ref, out_ref, *rest):
    if want_faces:
        sx0_ref, sx4_ref, sy0_ref, sy4_ref, face_ref, oth_ref, pad_ref, g_ref = rest
    else:
        face_ref, oth_ref, pad_ref, g_ref = rest
    elems = state_ref.shape[1]
    lane = lax.broadcasted_iota(jnp.int32, (FACE_ROWS, elems), 1)
    ez = lane % row_len
    face_ref[...] = jnp.zeros(face_ref.shape, jnp.float32)
    oth_ref[...] = jnp.zeros(oth_ref.shape, jnp.float32)
    extract_faces(state_ref, face_ref)
    flow_i = lax.axis_index("flow")
    grp_i = lax.axis_index("grp")
    oth_ref[pl.ds(0, FACE_ROWS), :] = jnp.where(flow_i == 0, 0.0, xlo_ref[pl.ds(xoff, FACE_ROWS), :])
    oth_ref[pl.ds(128, FACE_ROWS), :] = jnp.where(flow_i == flow_n - 1, 0.0, xhi_ref[pl.ds(xoff, FACE_ROWS), :])
    pad_ref[:, pl.ds(0, row_len)] = jnp.where(
        grp_i == 0, 0.0, ylo_ref[pl.ds(yoff, FACE_ROWS), pl.ds(0, row_len)])
    oth_ref[pl.ds(256, FACE_ROWS), :] = jnp.where(
        lane < row_len, pad_ref[...], pltpu.roll(face_ref[3], row_len, 1))
    pad_ref[:, pl.ds(0, row_len)] = jnp.where(
        grp_i == grp_n - 1, 0.0, yhi_ref[pl.ds(yoff, FACE_ROWS), pl.ds(0, row_len)])
    oth_ref[pl.ds(384, FACE_ROWS), :] = jnp.where(
        lane >= elems - row_len, pltpu.roll(pad_ref[...], elems - row_len, 1),
        pltpu.roll(face_ref[2], elems - row_len, 1))
    oth_ref[pl.ds(512, FACE_ROWS), :] = jnp.where(ez == 0, 0.0, pltpu.roll(face_ref[5], 1, 1))
    oth_ref[pl.ds(640, FACE_ROWS), :] = jnp.where(
        ez == row_len - 1, 0.0, pltpu.roll(face_ref[4], elems - 1, 1))
    g_ref[pl.ds(144, 8), :] = jnp.zeros((8, 4 * elems), jnp.float32)
    half = LIFT_FACTOR * 0.5
    for dim in range(3):
        for side, sign in ((0, -1.0), (1, 1.0)):
            f = 2 * dim + side
            o_p = oth_ref[pl.ds(f * 128, 25), :]
            o_u = [oth_ref[pl.ds(f * 128 + (1 + k) * 25, 25), :] for k in range(3)]
            g_ref[pl.ds(f * 25, 25), pl.ds(0, elems)] = half * (o_p - sign * o_u[dim])
            for k in range(3):
                value = half * o_u[k]
                if k == dim:
                    value = value - half * sign * o_p
                g_ref[pl.ds(f * 25, 25), pl.ds((1 + k) * elems, elems)] = value
    faces = jnp.dot(lift_ref[...], g_ref[...], precision=THREE_PASS, preferred_element_type=jnp.float32)
    state = state_ref[...]
    pres = state[:128]
    vel = state[128:]
    rate_p = jnp.dot(apu_ref[...], vel, precision=THREE_PASS, preferred_element_type=jnp.float32)
    rate_p = rate_p + diag_ref[pl.ds(0, 128), :] * pres + faces[:, :elems]
    out_ref[pl.ds(0, 128), :] = pres + TIME_STEP_ACOUSTIC * rate_p
    rate_u = jnp.dot(aup_ref[...], pres, precision=THREE_PASS, preferred_element_type=jnp.float32)
    for k in range(3):
        rows = pl.ds(128 + k * 128, 128)
        rate_k = rate_u[k * 128:(k + 1) * 128] + diag_ref[rows, :] * state_ref[rows, :]
        rate_k = rate_k + faces[:, (1 + k) * elems:(2 + k) * elems]
        out_ref[rows, :] = state_ref[rows, :] + TIME_STEP_ACOUSTIC * (rate_k - src_ref[pl.ds(k * 128, 128), :])
    if want_faces:
        extract_faces(out_ref, face_ref)
        send_faces(face_ref, sx0_ref, sx4_ref, sy0_ref, sy4_ref, row_len)


def face_shapes(elems, row_len):
    big = jax.ShapeDtypeStruct((FACE_ROWS, elems), jnp.float32)
    small = jax.ShapeDtypeStruct((FACE_ROWS, row_len), jnp.float32)
    return [big, big, small, small]


def dg_faces(state, row_len):
    elems = state.shape[1]
    return pl.pallas_call(
        dg_faces_kernel,
        out_shape=tuple(face_shapes(elems, row_len)),
        scratch_shapes=[pltpu.VMEM((6, FACE_ROWS, elems), jnp.float32)],
    )(state)


def dg_step(state, src, recv, mats, want_faces, row_len, xoff=0, yoff=0):
    elems = state.shape[1]
    out_shape = [jax.ShapeDtypeStruct(state.shape, jnp.float32)]
    if want_faces:
        out_shape += face_shapes(elems, row_len)
    res = pl.pallas_call(
        lambda *refs: dg_step_kernel(want_faces, xoff, yoff, row_len, lax.axis_size("flow"), lax.axis_size("grp"), *refs),
        out_shape=tuple(out_shape),
        scratch_shapes=[
            pltpu.VMEM((6, FACE_ROWS, elems), jnp.float32),
            pltpu.VMEM((768, elems), jnp.float32),
            pltpu.VMEM((FACE_ROWS, elems), jnp.float32),
            pltpu.VMEM((152, 4 * elems), jnp.float32),
        ],
    )(state, src, *recv, *mats)
    return res


def exchange_faces(sent):
    sx0, sx4, sy0, sy4 = sent
    flow_n = lax.axis_size("flow")
    grp_n = lax.axis_size("grp")
    up_f = [(i, (i + 1) % flow_n) for i in range(flow_n)]
    down_f = [((i + 1) % flow_n, i) for i in range(flow_n)]
    up_g = [(i, (i + 1) % grp_n) for i in range(grp_n)]
    down_g = [((i + 1) % grp_n, i) for i in range(grp_n)]
    return (
        lax.ppermute(sx4, "flow", up_f),
        lax.ppermute(sx0, "flow", down_f),
        lax.ppermute(sy4, "grp", up_g),
        lax.ppermute(sy0, "grp", down_g),
    )


def body(velocity, eddy_visc, projection, acoustic_state, route_send, route_place):
    joint = halos(jnp.concatenate([velocity, eddy_visc[None]], axis=0), 1)
    flow_size = lax.axis_size("flow")
    grp_size = lax.axis_size("grp")
    slot_cap = route_send.shape[2]
    elem_count = acoustic_state.shape[2]
    total_slots = flow_size * grp_size * slot_cap
    placing = route_place.reshape(-1)
    sending = route_send.reshape(-1)
    place_hot = (placing[:, None] == jnp.arange(total_slots, dtype=jnp.int32)[None, :]).astype(jnp.float32)
    home_hot = (sending[:, None] == jnp.arange(elem_count, dtype=jnp.int32)[None, :]).astype(jnp.float32)
    padded_state = jnp.pad(acoustic_state, ((0, 0), (0, 3), (0, 0))).reshape(512, elem_count)
    outgoing = jnp.dot(padded_state, place_hot, precision=HIGH)
    arrived = lax.all_to_all(outgoing, ("flow", "grp"), split_axis=1, concat_axis=1, tiled=True)
    state = jnp.dot(arrived, home_hot, precision=HIGH)

    row_len = velocity.shape[3] // 8
    mats = [jnp.asarray(m) for m in dg_matrices()]
    vel, mxup, mxdn, myup, mydn = les_section_first(velocity, eddy_visc, joint, state)
    merged = exchange_faces((mxdn, mxup, mydn, myup))
    vel, lamb = les_section_last(vel, eddy_visc, merged, joint)
    source = project(lamb, projection)
    xoff = 3 * 2 * velocity.shape[2]
    yoff = 3 * 2 * velocity.shape[1]
    res = dg_step(state, source, merged, mats, True, row_len, xoff, yoff)
    state = res[0]
    recv = exchange_faces(res[1:])
    state = dg_step(state, source, recv, mats, False, row_len)[0]
    leaving = lax.dot_general(state, home_hot, (((1,), (1,)), ((), ())), precision=HIGH)
    returned = lax.all_to_all(leaving, ("flow", "grp"), split_axis=1, concat_axis=1, tiled=True)
    acoustic_out = lax.dot_general(returned, place_hot, (((1,), (1,)), ((), ())), precision=HIGH)
    acoustic_out = acoustic_out.reshape(4, 128, elem_count)[:, :125]
    return (vel, acoustic_out)


def solution(mesh):
    placed = (
        P(None, "flow", "grp", None),
        P("flow", "grp", None),
        P(),
        P(None, None, ("flow", "grp")),
        P(("flow", "grp"), None, None),
        P(("flow", "grp"), None),
    )
    return jax.shard_map(
        body,
        mesh=mesh,
        in_specs=placed,
        out_specs=(P(None, "flow", "grp", None), P(None, None, ("flow", "grp"))),
        check_vma=False,
    )
```

```python
import math

import jax
import jax.numpy as jnp
import numpy as np
from jax import lax
from jax.experimental import pallas as pl
from jax.experimental.pallas import tpu as pltpu
from jax.sharding import PartitionSpec as P

LES_SECTIONS = 2
AC_SECTIONS = 2


TIME_STEP_LES = 0.15
TIME_STEP_ACOUSTIC = 0.02
GEOMETRY = 2.0
LIFT_FACTOR = 20.0
HIGH = lax.Precision.HIGHEST
THREE_PASS = lax.Precision.HIGH


def gll_derivative():
    gll_nodes = np.array([-1.0, -math.sqrt(3.0 / 7.0), 0.0, math.sqrt(3.0 / 7.0), 1.0])
    bary_weights = np.array(
        [
            1.0
            / np.prod([gll_nodes[first] - gll_nodes[other] for other in range(5) if other != first])
            for first in range(5)
        ]
    )
    matrix = np.zeros((5, 5))
    for row_id in range(5):
        for col_id in range(5):
            if row_id != col_id:
                matrix[row_id, col_id] = (
                    bary_weights[col_id]
                    / bary_weights[row_id]
                    / (gll_nodes[row_id] - gll_nodes[col_id])
                )
    for row_id in range(5):
        matrix[row_id, row_id] = -matrix[row_id].sum()
    return matrix


def node_id(coords):
    return coords[0] * 25 + coords[1] * 5 + coords[2]


def face_nodes(dim, at):
    ids = []
    for first in range(5):
        for second in range(5):
            coords = [first, second]
            coords.insert(dim, at)
            ids.append(node_id(coords))
    return ids


def dg_matrices():
    dmat = gll_derivative()
    half = LIFT_FACTOR * 0.5
    apu = np.zeros((128, 384))
    aup = np.zeros((384, 128))
    diag = np.zeros((512, 1))
    lift = np.zeros((128, 152))
    for a in range(5):
        for b in range(5):
            for c in range(5):
                pos = (a, b, c)
                row = node_id(pos)
                for dim in range(3):
                    for k in range(5):
                        col_pos = list(pos)
                        col_pos[dim] = k
                        col = node_id(col_pos)
                        weight = -GEOMETRY * dmat[pos[dim], k]
                        apu[row, dim * 128 + col] += weight
                        aup[dim * 128 + row, col] += weight
    for dim in range(3):
        for side, (sign, at) in enumerate(((-1.0, 0), (1.0, 4))):
            f = 2 * dim + side
            for t, node in enumerate(face_nodes(dim, at)):
                apu[node, dim * 128 + node] += half * sign
                aup[dim * 128 + node, node] += half * sign
                for comp in range(4):
                    diag[comp * 128 + node, 0] += -half
                lift[node, f * 25 + t] = 1.0
    return (apu.astype(np.float32), aup.astype(np.float32), diag.astype(np.float32), lift.astype(np.float32))


def face_rows(state, dim, at):
    elems = state.shape[-1]
    cube = state.reshape(4, 5, 5, 5, elems)
    face = lax.index_in_dim(cube, at, axis=1 + dim, keepdims=False)
    return face.reshape(100, elems)


def les_kernel(mode, flow_n, grp_n, vel_ref, nu_ref, vxlo_ref, vxhi_ref, vylo_ref, vyhi_ref,
               nxlo_ref, nxhi_ref, nylo_ref, nyhi_ref, *rest):
    size_x, size_y, size_z = vel_ref.shape[1], vel_ref.shape[2], vel_ref.shape[3]
    half = size_z // 2
    flow_i = lax.axis_index("flow")
    grp_i = lax.axis_index("grp")
    at_lo_f = flow_i == 0
    at_hi_f = flow_i == flow_n - 1
    at_lo_g = grp_i == 0
    at_hi_g = grp_i == grp_n - 1
    row = lax.broadcasted_iota(jnp.int32, (size_y, size_z), 0)
    lane = lax.broadcasted_iota(jnp.int32, (size_y, size_z), 1)
    if mode == 0:
        state_ref, out_ref, mxup_ref, mxdn_ref, myup_ref, mydn_ref, face_ref = rest

        def xlo(c):
            return jnp.where(at_lo_f, 0.0, vxlo_ref[c])

        def xhi(c):
            return jnp.where(at_hi_f, 0.0, vxhi_ref[c])

        def ylo(c, x):
            return jnp.where(at_lo_g, 0.0, vylo_ref[c, x])

        def yhi(c, x):
            return jnp.where(at_hi_g, 0.0, vyhi_ref[c, x])
    else:
        out_ref, lamb_ref = rest

        def plane(ref, c):
            return jnp.concatenate(
                [ref[pl.ds(c * 2 * size_y, size_y), :], ref[pl.ds(c * 2 * size_y + size_y, size_y), :]], axis=1)

        def line(ref, c, x):
            return jnp.concatenate(
                [ref[pl.ds(c * 2 * size_x + x, 1), :], ref[pl.ds(c * 2 * size_x + size_x + x, 1), :]], axis=1)

        def xlo(c):
            return jnp.where(at_lo_f, 0.0, plane(vxlo_ref, c))

        def xhi(c):
            return jnp.where(at_hi_f, 0.0, plane(vxhi_ref, c))

        def ylo(c, x):
            return jnp.where(at_lo_g, 0.0, line(vylo_ref, c, x))

        def yhi(c, x):
            return jnp.where(at_hi_g, 0.0, line(vyhi_ref, c, x))

    def yp(f, halo):
        return jnp.where(row == size_y - 1, halo, pltpu.roll(f, size_y - 1, 0))

    def ym(f, halo):
        return jnp.where(row == 0, halo, pltpu.roll(f, 1, 0))

    def zp(f):
        return jnp.where(lane == size_z - 1, 0.0, pltpu.roll(f, size_z - 1, 1))

    def zm(f):
        return jnp.where(lane == 0, 0.0, pltpu.roll(f, 1, 1))

    def plane_step(x, first, last):
        lo = x - 1
        hi = x + 1
        u = [vel_ref[c, x] for c in range(3)]
        uxm = [xlo(c) if first else vel_ref[c, lo] for c in range(3)]
        uxp = [xhi(c) if last else vel_ref[c, hi] for c in range(3)]
        uym = [ym(u[c], ylo(c, x)) for c in range(3)]
        uyp = [yp(u[c], yhi(c, x)) for c in range(3)]
        uzm = [zm(u[c]) for c in range(3)]
        uzp = [zp(u[c]) for c in range(3)]
        nu = nu_ref[x]
        nxm = jnp.where(at_lo_f, 0.0, nxlo_ref[3]) if first else nu_ref[lo]
        nxp = jnp.where(at_hi_f, 0.0, nxhi_ref[3]) if last else nu_ref[hi]
        nym = ym(nu, jnp.where(at_lo_g, 0.0, nylo_ref[3, x]))
        nyp = yp(nu, jnp.where(at_hi_g, 0.0, nyhi_ref[3, x]))
        nzm = zm(nu)
        nzp = zp(nu)
        plus = (uxp, uyp, uzp)
        minus = (uxm, uym, uzm)

        def d(c, axis):
            return 0.5 * (plus[axis][c] - minus[axis][c])

        wx = d(2, 1) - d(1, 2)
        wy = d(0, 2) - d(2, 0)
        wz = d(1, 0) - d(0, 1)
        lamb = (wy * u[2] - wz * u[1], wz * u[0] - wx * u[2], wx * u[1] - wy * u[0])
        ups = (0.5 * (nu + nxp), 0.5 * (nu + nyp), 0.5 * (nu + nzp))
        downs = (0.5 * (nu + nxm), 0.5 * (nu + nym), 0.5 * (nu + nzm))
        for c in range(3):
            total = None
            for axis in range(3):
                term = ups[axis] * (plus[axis][c] - u[c]) - downs[axis] * (u[c] - minus[axis][c])
                total = term if total is None else total + term
            out_ref[c, x] = u[c] + TIME_STEP_LES * (total - lamb[c])
            if mode == 1:
                lamb_ref[c, x] = lamb[c].astype(lamb_ref.dtype)

    def step(x, carry):
        plane_step(x, False, False)
        return carry

    plane_step(0, True, False)
    lax.fori_loop(1, size_x - 1, step, 0)
    plane_step(size_x - 1, False, True)
    if mode == 0:
        for c in range(3):
            for h in range(2):
                mxup_ref[pl.ds(c * 2 * size_y + h * size_y, size_y), :] = out_ref[c, size_x - 1, :, pl.ds(h * half, half)]
                mxdn_ref[pl.ds(c * 2 * size_y + h * size_y, size_y), :] = out_ref[c, 0, :, pl.ds(h * half, half)]
                for x in range(size_x):
                    at = c * 2 * size_x + h * size_x + x
                    myup_ref[pl.ds(at, 1), :] = out_ref[c, x, pl.ds(size_y - 1, 1), pl.ds(h * half, half)]
                    mydn_ref[pl.ds(at, 1), :] = out_ref[c, x, pl.ds(0, 1), pl.ds(h * half, half)]
        xrows = 3 * 2 * size_y
        yrows = 3 * 2 * size_x
        elems = state_ref.shape[1]
        row_len = size_z // 8
        face_ref[...] = jnp.zeros(face_ref.shape, jnp.float32)
        extract_faces(state_ref, face_ref)
        mxup_ref[pl.ds(xrows, FACE_ROWS), :] = face_ref[1]
        mxdn_ref[pl.ds(xrows, FACE_ROWS), :] = face_ref[0]
        lane = lax.broadcasted_iota(jnp.int32, (FACE_ROWS, elems), 1)
        myup_ref[pl.ds(yrows, FACE_ROWS), :] = jnp.where(lane < row_len, pltpu.roll(face_ref[3], row_len, 1), 0.0)
        mydn_ref[pl.ds(yrows, FACE_ROWS), :] = jnp.where(lane < row_len, face_ref[2], 0.0)


def les_section_first(vel, nu, joint, state):
    size_x, size_y, size_z = vel.shape[1], vel.shape[2], vel.shape[3]
    xbuf = jax.ShapeDtypeStruct((3 * 2 * size_y + FACE_ROWS, size_z // 2), jnp.float32)
    ybuf = jax.ShapeDtypeStruct((3 * 2 * size_x + FACE_ROWS, size_z // 2), jnp.float32)
    return pl.pallas_call(
        lambda *refs: les_kernel(0, lax.axis_size("flow"), lax.axis_size("grp"), *refs),
        out_shape=(jax.ShapeDtypeStruct(vel.shape, jnp.float32), xbuf, xbuf, ybuf, ybuf),
        scratch_shapes=[pltpu.VMEM((6, FACE_ROWS, state.shape[1]), jnp.float32)],
    )(vel, nu, *joint, *joint, state)


def les_section_last(vel, nu, merged, joint):
    return pl.pallas_call(
        lambda *refs: les_kernel(1, lax.axis_size("flow"), lax.axis_size("grp"), *refs),
        out_shape=(jax.ShapeDtypeStruct(vel.shape, jnp.float32), jax.ShapeDtypeStruct(vel.shape, jnp.bfloat16)),
    )(vel, nu, *merged, *joint)


def halos(field, lead):
    flow_n = lax.axis_size("flow")
    grp_n = lax.axis_size("grp")
    up_f = [(i, (i + 1) % flow_n) for i in range(flow_n)]
    down_f = [((i + 1) % flow_n, i) for i in range(flow_n)]
    up_g = [(i, (i + 1) % grp_n) for i in range(grp_n)]
    down_g = [((i + 1) % grp_n, i) for i in range(grp_n)]
    size_x, size_y = field.shape[lead], field.shape[lead + 1]
    xlo = lax.ppermute(lax.index_in_dim(field, size_x - 1, lead, keepdims=False), "flow", up_f)
    xhi = lax.ppermute(lax.index_in_dim(field, 0, lead, keepdims=False), "flow", down_f)
    ylo = lax.ppermute(lax.slice_in_dim(field, size_y - 1, size_y, axis=lead + 1), "grp", up_g)
    yhi = lax.ppermute(lax.slice_in_dim(field, 0, 1, axis=lead + 1), "grp", down_g)
    return xlo, xhi, ylo, yhi


def project(lamb, projection):
    size_x, size_y, size_z = (lamb.shape[1], lamb.shape[2], lamb.shape[3])
    bx, by, bz = size_x // 8, size_y // 8, size_z // 8
    perm = np.zeros((size_z, size_z), np.float32)
    for ez in range(bz):
        for cz in range(8):
            perm[ez * 8 + cz, cz * bz + ez] = 1.0
    rows = lamb.reshape(-1, size_z)
    moved = jnp.dot(rows, jnp.asarray(perm, jnp.bfloat16), preferred_element_type=jnp.float32)
    moved = moved.astype(jnp.bfloat16)
    blocks = moved.reshape(3, bx, 8, by, 8, 8, bz).transpose(2, 4, 5, 0, 1, 3, 6).reshape(512, -1)
    padded_proj = jnp.pad(projection, ((0, 3), (0, 0)))
    source = jnp.dot(padded_proj, blocks, preferred_element_type=jnp.float32)
    source = source.reshape(128, 3, -1).transpose(1, 0, 2)
    return source.reshape(384, -1)


FACE_ROWS = 104


def extract_faces(state_ref, face_ref):
    for dim in range(3):
        for side, at in ((0, 0), (1, 4)):
            f = 2 * dim + side
            for comp in range(4):
                base = comp * 128
                if dim == 0:
                    face_ref[f, pl.ds(comp * 25, 25), :] = state_ref[pl.ds(base + at * 25, 25), :]
                elif dim == 1:
                    for a in range(5):
                        face_ref[f, pl.ds(comp * 25 + a * 5, 5), :] = state_ref[pl.ds(base + a * 25 + at * 5, 5), :]
                else:
                    face_ref[f, pl.ds(comp * 25, 25), :] = state_ref[pl.ds(base + at, 25, stride=5), :]


def send_faces(face_ref, sx0_ref, sx4_ref, sy0_ref, sy4_ref, row_len):
    sx0_ref[...] = face_ref[0]
    sx4_ref[...] = face_ref[1]
    sy0_ref[...] = face_ref[2][:, :row_len]
    last = pltpu.roll(face_ref[3], row_len, 1)
    sy4_ref[...] = last[:, :row_len]


def dg_faces_kernel(state_ref, sx0_ref, sx4_ref, sy0_ref, sy4_ref, face_ref):
    face_ref[...] = jnp.zeros(face_ref.shape, jnp.float32)
    extract_faces(state_ref, face_ref)
    send_faces(face_ref, sx0_ref, sx4_ref, sy0_ref, sy4_ref, sy0_ref.shape[1])


def dg_step_kernel(want_faces, xoff, yoff, row_len, flow_n, grp_n, state_ref, src_ref, xlo_ref, xhi_ref, ylo_ref, yhi_ref,
                   apu_ref, aup_ref, diag_ref, lift_ref, out_ref, *rest):
    if want_faces:
        sx0_ref, sx4_ref, sy0_ref, sy4_ref, face_ref, oth_ref, pad_ref, g_ref = rest
    else:
        face_ref, oth_ref, pad_ref, g_ref = rest
    elems = state_ref.shape[1]
    lane = lax.broadcasted_iota(jnp.int32, (FACE_ROWS, elems), 1)
    ez = lane % row_len
    face_ref[...] = jnp.zeros(face_ref.shape, jnp.float32)
    oth_ref[...] = jnp.zeros(oth_ref.shape, jnp.float32)
    extract_faces(state_ref, face_ref)
    flow_i = lax.axis_index("flow")
    grp_i = lax.axis_index("grp")
    oth_ref[pl.ds(0, FACE_ROWS), :] = jnp.where(flow_i == 0, 0.0, xlo_ref[pl.ds(xoff, FACE_ROWS), :])
    oth_ref[pl.ds(128, FACE_ROWS), :] = jnp.where(flow_i == flow_n - 1, 0.0, xhi_ref[pl.ds(xoff, FACE_ROWS), :])
    pad_ref[:, pl.ds(0, row_len)] = jnp.where(
        grp_i == 0, 0.0, ylo_ref[pl.ds(yoff, FACE_ROWS), pl.ds(0, row_len)])
    oth_ref[pl.ds(256, FACE_ROWS), :] = jnp.where(
        lane < row_len, pad_ref[...], pltpu.roll(face_ref[3], row_len, 1))
    pad_ref[:, pl.ds(0, row_len)] = jnp.where(
        grp_i == grp_n - 1, 0.0, yhi_ref[pl.ds(yoff, FACE_ROWS), pl.ds(0, row_len)])
    oth_ref[pl.ds(384, FACE_ROWS), :] = jnp.where(
        lane >= elems - row_len, pltpu.roll(pad_ref[...], elems - row_len, 1),
        pltpu.roll(face_ref[2], elems - row_len, 1))
    oth_ref[pl.ds(512, FACE_ROWS), :] = jnp.where(ez == 0, 0.0, pltpu.roll(face_ref[5], 1, 1))
    oth_ref[pl.ds(640, FACE_ROWS), :] = jnp.where(
        ez == row_len - 1, 0.0, pltpu.roll(face_ref[4], elems - 1, 1))
    g_ref[pl.ds(144, 8), :] = jnp.zeros((8, 4 * elems), jnp.float32)
    half = LIFT_FACTOR * 0.5
    for dim in range(3):
        for side, sign in ((0, -1.0), (1, 1.0)):
            f = 2 * dim + side
            o_p = oth_ref[pl.ds(f * 128, 25), :]
            o_u = [oth_ref[pl.ds(f * 128 + (1 + k) * 25, 25), :] for k in range(3)]
            g_ref[pl.ds(f * 25, 25), pl.ds(0, elems)] = half * (o_p - sign * o_u[dim])
            for k in range(3):
                value = half * o_u[k]
                if k == dim:
                    value = value - half * sign * o_p
                g_ref[pl.ds(f * 25, 25), pl.ds((1 + k) * elems, elems)] = value
    faces = jnp.dot(lift_ref[...], g_ref[...], precision=THREE_PASS, preferred_element_type=jnp.float32)
    state = state_ref[...]
    pres = state[:128]
    vel = state[128:]
    rate_p = jnp.dot(apu_ref[...], vel, precision=THREE_PASS, preferred_element_type=jnp.float32)
    rate_p = rate_p + diag_ref[pl.ds(0, 128), :] * pres + faces[:, :elems]
    out_ref[pl.ds(0, 128), :] = pres + TIME_STEP_ACOUSTIC * rate_p
    rate_u = jnp.dot(aup_ref[...], pres, precision=THREE_PASS, preferred_element_type=jnp.float32)
    for k in range(3):
        rows = pl.ds(128 + k * 128, 128)
        rate_k = rate_u[k * 128:(k + 1) * 128] + diag_ref[rows, :] * state_ref[rows, :]
        rate_k = rate_k + faces[:, (1 + k) * elems:(2 + k) * elems]
        out_ref[rows, :] = state_ref[rows, :] + TIME_STEP_ACOUSTIC * (rate_k - src_ref[pl.ds(k * 128, 128), :])
    if want_faces:
        extract_faces(out_ref, face_ref)
        send_faces(face_ref, sx0_ref, sx4_ref, sy0_ref, sy4_ref, row_len)


def face_shapes(elems, row_len):
    big = jax.ShapeDtypeStruct((FACE_ROWS, elems), jnp.float32)
    small = jax.ShapeDtypeStruct((FACE_ROWS, row_len), jnp.float32)
    return [big, big, small, small]


def dg_faces(state, row_len):
    elems = state.shape[1]
    return pl.pallas_call(
        dg_faces_kernel,
        out_shape=tuple(face_shapes(elems, row_len)),
        scratch_shapes=[pltpu.VMEM((6, FACE_ROWS, elems), jnp.float32)],
    )(state)


def dg_step(state, src, recv, mats, want_faces, row_len, xoff=0, yoff=0):
    elems = state.shape[1]
    out_shape = [jax.ShapeDtypeStruct(state.shape, jnp.float32)]
    if want_faces:
        out_shape += face_shapes(elems, row_len)
    res = pl.pallas_call(
        lambda *refs: dg_step_kernel(want_faces, xoff, yoff, row_len, lax.axis_size("flow"), lax.axis_size("grp"), *refs),
        out_shape=tuple(out_shape),
        scratch_shapes=[
            pltpu.VMEM((6, FACE_ROWS, elems), jnp.float32),
            pltpu.VMEM((768, elems), jnp.float32),
            pltpu.VMEM((FACE_ROWS, elems), jnp.float32),
            pltpu.VMEM((152, 4 * elems), jnp.float32),
        ],
    )(state, src, *recv, *mats)
    return res


def exchange_faces(sent):
    sx0, sx4, sy0, sy4 = sent
    flow_n = lax.axis_size("flow")
    grp_n = lax.axis_size("grp")
    up_f = [(i, (i + 1) % flow_n) for i in range(flow_n)]
    down_f = [((i + 1) % flow_n, i) for i in range(flow_n)]
    up_g = [(i, (i + 1) % grp_n) for i in range(grp_n)]
    down_g = [((i + 1) % grp_n, i) for i in range(grp_n)]
    return (
        lax.ppermute(sx4, "flow", up_f),
        lax.ppermute(sx0, "flow", down_f),
        lax.ppermute(sy4, "grp", up_g),
        lax.ppermute(sy0, "grp", down_g),
    )


def body(velocity, eddy_visc, projection, acoustic_state, route_send, route_place):
    joint = halos(jnp.concatenate([velocity, eddy_visc[None]], axis=0), 1)
    flow_size = lax.axis_size("flow")
    grp_size = lax.axis_size("grp")
    slot_cap = route_send.shape[2]
    elem_count = acoustic_state.shape[2]
    total_slots = flow_size * grp_size * slot_cap
    placing = route_place.reshape(-1)
    sending = route_send.reshape(-1)
    place_hot = (placing[:, None] == jnp.arange(total_slots, dtype=jnp.int32)[None, :]).astype(jnp.float32)
    home_hot = (sending[:, None] == jnp.arange(elem_count, dtype=jnp.int32)[None, :]).astype(jnp.float32)
    padded_state = jnp.pad(acoustic_state, ((0, 0), (0, 3), (0, 0))).reshape(512, elem_count)
    outgoing = jnp.dot(padded_state, place_hot, precision=THREE_PASS)
    arrived = lax.all_to_all(outgoing, ("flow", "grp"), split_axis=1, concat_axis=1, tiled=True)
    state = jnp.dot(arrived, home_hot, precision=THREE_PASS)

    row_len = velocity.shape[3] // 8
    mats = [jnp.asarray(m) for m in dg_matrices()]
    vel, mxup, mxdn, myup, mydn = les_section_first(velocity, eddy_visc, joint, state)
    merged = exchange_faces((mxdn, mxup, mydn, myup))
    vel, lamb = les_section_last(vel, eddy_visc, merged, joint)
    source = project(lamb, projection)
    xoff = 3 * 2 * velocity.shape[2]
    yoff = 3 * 2 * velocity.shape[1]
    res = dg_step(state, source, merged, mats, True, row_len, xoff, yoff)
    state = res[0]
    recv = exchange_faces(res[1:])
    state = dg_step(state, source, recv, mats, False, row_len)[0]
    leaving = lax.dot_general(state, home_hot, (((1,), (1,)), ((), ())), precision=THREE_PASS)
    returned = lax.all_to_all(leaving, ("flow", "grp"), split_axis=1, concat_axis=1, tiled=True)
    acoustic_out = lax.dot_general(returned, place_hot, (((1,), (1,)), ((), ())), precision=THREE_PASS)
    acoustic_out = acoustic_out.reshape(4, 128, elem_count)[:, :125]
    return (vel, acoustic_out)


def solution(mesh):
    placed = (
        P(None, "flow", "grp", None),
        P("flow", "grp", None),
        P(),
        P(None, None, ("flow", "grp")),
        P(("flow", "grp"), None, None),
        P(("flow", "grp"), None),
    )
    return jax.shard_map(
        body,
        mesh=mesh,
        in_specs=placed,
        out_specs=(P(None, "flow", "grp", None), P(None, None, ("flow", "grp"))),
        check_vma=False,
    )
```

```python
import math

import jax
import jax.numpy as jnp
import numpy as np
from jax import lax
from jax.experimental import pallas as pl
from jax.experimental.pallas import tpu as pltpu
from jax.sharding import PartitionSpec as P

LES_SECTIONS = 2
AC_SECTIONS = 2


TIME_STEP_LES = 0.15
TIME_STEP_ACOUSTIC = 0.02
GEOMETRY = 2.0
LIFT_FACTOR = 20.0
HIGH = lax.Precision.HIGHEST
THREE_PASS = lax.Precision.HIGH


def gll_derivative():
    gll_nodes = np.array([-1.0, -math.sqrt(3.0 / 7.0), 0.0, math.sqrt(3.0 / 7.0), 1.0])
    bary_weights = np.array(
        [
            1.0
            / np.prod([gll_nodes[first] - gll_nodes[other] for other in range(5) if other != first])
            for first in range(5)
        ]
    )
    matrix = np.zeros((5, 5))
    for row_id in range(5):
        for col_id in range(5):
            if row_id != col_id:
                matrix[row_id, col_id] = (
                    bary_weights[col_id]
                    / bary_weights[row_id]
                    / (gll_nodes[row_id] - gll_nodes[col_id])
                )
    for row_id in range(5):
        matrix[row_id, row_id] = -matrix[row_id].sum()
    return matrix


def node_id(coords):
    return coords[0] * 25 + coords[1] * 5 + coords[2]


def face_nodes(dim, at):
    ids = []
    for first in range(5):
        for second in range(5):
            coords = [first, second]
            coords.insert(dim, at)
            ids.append(node_id(coords))
    return ids


def dg_matrices():
    dmat = gll_derivative()
    half = LIFT_FACTOR * 0.5
    apu = np.zeros((128, 384))
    aup = np.zeros((384, 128))
    diag = np.zeros((512, 1))
    lift = np.zeros((128, 152))
    for a in range(5):
        for b in range(5):
            for c in range(5):
                pos = (a, b, c)
                row = node_id(pos)
                for dim in range(3):
                    for k in range(5):
                        col_pos = list(pos)
                        col_pos[dim] = k
                        col = node_id(col_pos)
                        weight = -GEOMETRY * dmat[pos[dim], k]
                        apu[row, dim * 128 + col] += weight
                        aup[dim * 128 + row, col] += weight
    for dim in range(3):
        for side, (sign, at) in enumerate(((-1.0, 0), (1.0, 4))):
            f = 2 * dim + side
            for t, node in enumerate(face_nodes(dim, at)):
                apu[node, dim * 128 + node] += half * sign
                aup[dim * 128 + node, node] += half * sign
                for comp in range(4):
                    diag[comp * 128 + node, 0] += -half
                lift[node, f * 25 + t] = 1.0
    return (apu.astype(np.float32), aup.astype(np.float32), diag.astype(np.float32), lift.astype(np.float32))


def face_rows(state, dim, at):
    elems = state.shape[-1]
    cube = state.reshape(4, 5, 5, 5, elems)
    face = lax.index_in_dim(cube, at, axis=1 + dim, keepdims=False)
    return face.reshape(100, elems)


def les_kernel(mode, flow_n, grp_n, vel_ref, nu_ref, vxlo_ref, vxhi_ref, vylo_ref, vyhi_ref,
               nxlo_ref, nxhi_ref, nylo_ref, nyhi_ref, *rest):
    size_x, size_y, size_z = vel_ref.shape[1], vel_ref.shape[2], vel_ref.shape[3]
    half = size_z // 2
    flow_i = lax.axis_index("flow")
    grp_i = lax.axis_index("grp")
    at_lo_f = flow_i == 0
    at_hi_f = flow_i == flow_n - 1
    at_lo_g = grp_i == 0
    at_hi_g = grp_i == grp_n - 1
    row = lax.broadcasted_iota(jnp.int32, (size_y, size_z), 0)
    lane = lax.broadcasted_iota(jnp.int32, (size_y, size_z), 1)
    if mode == 0:
        state_ref, out_ref, mxup_ref, mxdn_ref, myup_ref, mydn_ref, face_ref = rest

        def xlo(c):
            return jnp.where(at_lo_f, 0.0, vxlo_ref[c])

        def xhi(c):
            return jnp.where(at_hi_f, 0.0, vxhi_ref[c])

        def ylo(c, x):
            return jnp.where(at_lo_g, 0.0, vylo_ref[c, x])

        def yhi(c, x):
            return jnp.where(at_hi_g, 0.0, vyhi_ref[c, x])
    else:
        out_ref, lamb_ref = rest

        def plane(ref, c):
            return jnp.concatenate(
                [ref[pl.ds(c * 2 * size_y, size_y), :], ref[pl.ds(c * 2 * size_y + size_y, size_y), :]], axis=1)

        def line(ref, c, x):
            return jnp.concatenate(
                [ref[pl.ds(c * 2 * size_x + x, 1), :], ref[pl.ds(c * 2 * size_x + size_x + x, 1), :]], axis=1)

        def xlo(c):
            return jnp.where(at_lo_f, 0.0, plane(vxlo_ref, c))

        def xhi(c):
            return jnp.where(at_hi_f, 0.0, plane(vxhi_ref, c))

        def ylo(c, x):
            return jnp.where(at_lo_g, 0.0, line(vylo_ref, c, x))

        def yhi(c, x):
            return jnp.where(at_hi_g, 0.0, line(vyhi_ref, c, x))

    def yp(f, halo):
        return jnp.where(row == size_y - 1, halo, pltpu.roll(f, size_y - 1, 0))

    def ym(f, halo):
        return jnp.where(row == 0, halo, pltpu.roll(f, 1, 0))

    def zp(f):
        return jnp.where(lane == size_z - 1, 0.0, pltpu.roll(f, size_z - 1, 1))

    def zm(f):
        return jnp.where(lane == 0, 0.0, pltpu.roll(f, 1, 1))

    def plane_step(x, first, last):
        lo = x - 1
        hi = x + 1
        u = [vel_ref[c, x] for c in range(3)]
        uxm = [xlo(c) if first else vel_ref[c, lo] for c in range(3)]
        uxp = [xhi(c) if last else vel_ref[c, hi] for c in range(3)]
        uym = [ym(u[c], ylo(c, x)) for c in range(3)]
        uyp = [yp(u[c], yhi(c, x)) for c in range(3)]
        uzm = [zm(u[c]) for c in range(3)]
        uzp = [zp(u[c]) for c in range(3)]
        nu = nu_ref[x]
        nxm = jnp.where(at_lo_f, 0.0, nxlo_ref[3]) if first else nu_ref[lo]
        nxp = jnp.where(at_hi_f, 0.0, nxhi_ref[3]) if last else nu_ref[hi]
        nym = ym(nu, jnp.where(at_lo_g, 0.0, nylo_ref[3, x]))
        nyp = yp(nu, jnp.where(at_hi_g, 0.0, nyhi_ref[3, x]))
        nzm = zm(nu)
        nzp = zp(nu)
        plus = (uxp, uyp, uzp)
        minus = (uxm, uym, uzm)

        def d(c, axis):
            return 0.5 * (plus[axis][c] - minus[axis][c])

        wx = d(2, 1) - d(1, 2)
        wy = d(0, 2) - d(2, 0)
        wz = d(1, 0) - d(0, 1)
        lamb = (wy * u[2] - wz * u[1], wz * u[0] - wx * u[2], wx * u[1] - wy * u[0])
        ups = (0.5 * (nu + nxp), 0.5 * (nu + nyp), 0.5 * (nu + nzp))
        downs = (0.5 * (nu + nxm), 0.5 * (nu + nym), 0.5 * (nu + nzm))
        for c in range(3):
            total = None
            for axis in range(3):
                term = ups[axis] * (plus[axis][c] - u[c]) - downs[axis] * (u[c] - minus[axis][c])
                total = term if total is None else total + term
            out_ref[c, x] = u[c] + TIME_STEP_LES * (total - lamb[c])
            if mode == 1:
                lamb_ref[c, x] = lamb[c].astype(lamb_ref.dtype)

    def step(x, carry):
        plane_step(x, False, False)
        return carry

    plane_step(0, True, False)
    lax.fori_loop(1, size_x - 1, step, 0)
    plane_step(size_x - 1, False, True)
    if mode == 0:
        for c in range(3):
            for h in range(2):
                mxup_ref[pl.ds(c * 2 * size_y + h * size_y, size_y), :] = out_ref[c, size_x - 1, :, pl.ds(h * half, half)]
                mxdn_ref[pl.ds(c * 2 * size_y + h * size_y, size_y), :] = out_ref[c, 0, :, pl.ds(h * half, half)]
                for x in range(size_x):
                    at = c * 2 * size_x + h * size_x + x
                    myup_ref[pl.ds(at, 1), :] = out_ref[c, x, pl.ds(size_y - 1, 1), pl.ds(h * half, half)]
                    mydn_ref[pl.ds(at, 1), :] = out_ref[c, x, pl.ds(0, 1), pl.ds(h * half, half)]
        xrows = 3 * 2 * size_y
        yrows = 3 * 2 * size_x
        elems = state_ref.shape[1]
        row_len = size_z // 8
        face_ref[:, pl.ds(100, FACE_ROWS - 100), :] = jnp.zeros((6, FACE_ROWS - 100, face_ref.shape[2]), jnp.float32)
        extract_faces(state_ref, face_ref)
        mxup_ref[pl.ds(xrows, FACE_ROWS), :] = face_ref[1]
        mxdn_ref[pl.ds(xrows, FACE_ROWS), :] = face_ref[0]
        lane = lax.broadcasted_iota(jnp.int32, (FACE_ROWS, elems), 1)
        myup_ref[pl.ds(yrows, FACE_ROWS), :] = jnp.where(lane < row_len, pltpu.roll(face_ref[3], row_len, 1), 0.0)
        mydn_ref[pl.ds(yrows, FACE_ROWS), :] = jnp.where(lane < row_len, face_ref[2], 0.0)


def les_section_first(vel, nu, joint, state):
    size_x, size_y, size_z = vel.shape[1], vel.shape[2], vel.shape[3]
    xbuf = jax.ShapeDtypeStruct((3 * 2 * size_y + FACE_ROWS, size_z // 2), jnp.float32)
    ybuf = jax.ShapeDtypeStruct((3 * 2 * size_x + FACE_ROWS, size_z // 2), jnp.float32)
    return pl.pallas_call(
        lambda *refs: les_kernel(0, lax.axis_size("flow"), lax.axis_size("grp"), *refs),
        out_shape=(jax.ShapeDtypeStruct(vel.shape, jnp.float32), xbuf, xbuf, ybuf, ybuf),
        scratch_shapes=[pltpu.VMEM((6, FACE_ROWS, state.shape[1]), jnp.float32)],
    )(vel, nu, *joint, *joint, state)


def les_section_last(vel, nu, merged, joint):
    return pl.pallas_call(
        lambda *refs: les_kernel(1, lax.axis_size("flow"), lax.axis_size("grp"), *refs),
        out_shape=(jax.ShapeDtypeStruct(vel.shape, jnp.float32), jax.ShapeDtypeStruct(vel.shape, jnp.bfloat16)),
    )(vel, nu, *merged, *joint)


def halos(field, lead):
    flow_n = lax.axis_size("flow")
    grp_n = lax.axis_size("grp")
    up_f = [(i, (i + 1) % flow_n) for i in range(flow_n)]
    down_f = [((i + 1) % flow_n, i) for i in range(flow_n)]
    up_g = [(i, (i + 1) % grp_n) for i in range(grp_n)]
    down_g = [((i + 1) % grp_n, i) for i in range(grp_n)]
    size_x, size_y = field.shape[lead], field.shape[lead + 1]
    xlo = lax.ppermute(lax.index_in_dim(field, size_x - 1, lead, keepdims=False), "flow", up_f)
    xhi = lax.ppermute(lax.index_in_dim(field, 0, lead, keepdims=False), "flow", down_f)
    ylo = lax.ppermute(lax.slice_in_dim(field, size_y - 1, size_y, axis=lead + 1), "grp", up_g)
    yhi = lax.ppermute(lax.slice_in_dim(field, 0, 1, axis=lead + 1), "grp", down_g)
    return xlo, xhi, ylo, yhi


def project(lamb, projection):
    size_x, size_y, size_z = (lamb.shape[1], lamb.shape[2], lamb.shape[3])
    bx, by, bz = size_x // 8, size_y // 8, size_z // 8
    perm = np.zeros((size_z, size_z), np.float32)
    for ez in range(bz):
        for cz in range(8):
            perm[ez * 8 + cz, cz * bz + ez] = 1.0
    rows = lamb.reshape(-1, size_z)
    moved = jnp.dot(rows, jnp.asarray(perm, jnp.bfloat16), preferred_element_type=jnp.float32)
    moved = moved.astype(jnp.bfloat16)
    blocks = moved.reshape(3, bx, 8, by, 8, 8, bz).transpose(2, 4, 5, 0, 1, 3, 6).reshape(512, -1)
    padded_proj = jnp.pad(projection, ((0, 3), (0, 0)))
    source = jnp.dot(padded_proj, blocks, preferred_element_type=jnp.float32)
    source = source.reshape(128, 3, -1).transpose(1, 0, 2)
    return source.reshape(384, -1)


FACE_ROWS = 104


def extract_faces(state_ref, face_ref):
    for dim in range(3):
        for side, at in ((0, 0), (1, 4)):
            f = 2 * dim + side
            for comp in range(4):
                base = comp * 128
                if dim == 0:
                    face_ref[f, pl.ds(comp * 25, 25), :] = state_ref[pl.ds(base + at * 25, 25), :]
                elif dim == 1:
                    for a in range(5):
                        face_ref[f, pl.ds(comp * 25 + a * 5, 5), :] = state_ref[pl.ds(base + a * 25 + at * 5, 5), :]
                else:
                    face_ref[f, pl.ds(comp * 25, 25), :] = state_ref[pl.ds(base + at, 25, stride=5), :]


def send_faces(face_ref, sx0_ref, sx4_ref, sy0_ref, sy4_ref, row_len):
    sx0_ref[...] = face_ref[0]
    sx4_ref[...] = face_ref[1]
    sy0_ref[...] = face_ref[2][:, :row_len]
    last = pltpu.roll(face_ref[3], row_len, 1)
    sy4_ref[...] = last[:, :row_len]


def dg_faces_kernel(state_ref, sx0_ref, sx4_ref, sy0_ref, sy4_ref, face_ref):
    face_ref[:, pl.ds(100, FACE_ROWS - 100), :] = jnp.zeros((6, FACE_ROWS - 100, face_ref.shape[2]), jnp.float32)
    extract_faces(state_ref, face_ref)
    send_faces(face_ref, sx0_ref, sx4_ref, sy0_ref, sy4_ref, sy0_ref.shape[1])


def dg_step_kernel(want_faces, xoff, yoff, row_len, flow_n, grp_n, state_ref, src_ref, xlo_ref, xhi_ref, ylo_ref, yhi_ref,
                   apu_ref, aup_ref, diag_ref, lift_ref, out_ref, *rest):
    if want_faces:
        sx0_ref, sx4_ref, sy0_ref, sy4_ref, face_ref, oth_ref, pad_ref, g_ref = rest
    else:
        face_ref, oth_ref, pad_ref, g_ref = rest
    elems = state_ref.shape[1]
    lane = lax.broadcasted_iota(jnp.int32, (FACE_ROWS, elems), 1)
    ez = lane % row_len
    face_ref[:, pl.ds(100, FACE_ROWS - 100), :] = jnp.zeros((6, FACE_ROWS - 100, face_ref.shape[2]), jnp.float32)
    extract_faces(state_ref, face_ref)
    flow_i = lax.axis_index("flow")
    grp_i = lax.axis_index("grp")
    oth_ref[pl.ds(0, FACE_ROWS), :] = jnp.where(flow_i == 0, 0.0, xlo_ref[pl.ds(xoff, FACE_ROWS), :])
    oth_ref[pl.ds(128, FACE_ROWS), :] = jnp.where(flow_i == flow_n - 1, 0.0, xhi_ref[pl.ds(xoff, FACE_ROWS), :])
    pad_ref[:, pl.ds(0, row_len)] = jnp.where(
        grp_i == 0, 0.0, ylo_ref[pl.ds(yoff, FACE_ROWS), pl.ds(0, row_len)])
    oth_ref[pl.ds(256, FACE_ROWS), :] = jnp.where(
        lane < row_len, pad_ref[...], pltpu.roll(face_ref[3], row_len, 1))
    pad_ref[:, pl.ds(0, row_len)] = jnp.where(
        grp_i == grp_n - 1, 0.0, yhi_ref[pl.ds(yoff, FACE_ROWS), pl.ds(0, row_len)])
    oth_ref[pl.ds(384, FACE_ROWS), :] = jnp.where(
        lane >= elems - row_len, pltpu.roll(pad_ref[...], elems - row_len, 1),
        pltpu.roll(face_ref[2], elems - row_len, 1))
    oth_ref[pl.ds(512, FACE_ROWS), :] = jnp.where(ez == 0, 0.0, pltpu.roll(face_ref[5], 1, 1))
    oth_ref[pl.ds(640, FACE_ROWS), :] = jnp.where(
        ez == row_len - 1, 0.0, pltpu.roll(face_ref[4], elems - 1, 1))
    g_ref[pl.ds(144, 8), :] = jnp.zeros((8, 4 * elems), jnp.float32)
    half = LIFT_FACTOR * 0.5
    for dim in range(3):
        for side, sign in ((0, -1.0), (1, 1.0)):
            f = 2 * dim + side
            o_p = oth_ref[pl.ds(f * 128, 25), :]
            o_u = [oth_ref[pl.ds(f * 128 + (1 + k) * 25, 25), :] for k in range(3)]
            g_ref[pl.ds(f * 25, 25), pl.ds(0, elems)] = half * (o_p - sign * o_u[dim])
            for k in range(3):
                value = half * o_u[k]
                if k == dim:
                    value = value - half * sign * o_p
                g_ref[pl.ds(f * 25, 25), pl.ds((1 + k) * elems, elems)] = value
    faces = jnp.dot(lift_ref[...], g_ref[...], precision=THREE_PASS, preferred_element_type=jnp.float32)
    state = state_ref[...]
    pres = state[:128]
    vel = state[128:]
    rate_p = jnp.dot(apu_ref[...], vel, precision=THREE_PASS, preferred_element_type=jnp.float32)
    rate_p = rate_p + diag_ref[pl.ds(0, 128), :] * pres + faces[:, :elems]
    out_ref[pl.ds(0, 128), :] = pres + TIME_STEP_ACOUSTIC * rate_p
    rate_u = jnp.dot(aup_ref[...], pres, precision=THREE_PASS, preferred_element_type=jnp.float32)
    for k in range(3):
        rows = pl.ds(128 + k * 128, 128)
        rate_k = rate_u[k * 128:(k + 1) * 128] + diag_ref[rows, :] * state_ref[rows, :]
        rate_k = rate_k + faces[:, (1 + k) * elems:(2 + k) * elems]
        out_ref[rows, :] = state_ref[rows, :] + TIME_STEP_ACOUSTIC * (rate_k - src_ref[pl.ds(k * 128, 128), :])
    if want_faces:
        extract_faces(out_ref, face_ref)
        send_faces(face_ref, sx0_ref, sx4_ref, sy0_ref, sy4_ref, row_len)


def face_shapes(elems, row_len):
    big = jax.ShapeDtypeStruct((FACE_ROWS, elems), jnp.float32)
    small = jax.ShapeDtypeStruct((FACE_ROWS, row_len), jnp.float32)
    return [big, big, small, small]


def dg_faces(state, row_len):
    elems = state.shape[1]
    return pl.pallas_call(
        dg_faces_kernel,
        out_shape=tuple(face_shapes(elems, row_len)),
        scratch_shapes=[pltpu.VMEM((6, FACE_ROWS, elems), jnp.float32)],
    )(state)


def dg_step(state, src, recv, mats, want_faces, row_len, xoff=0, yoff=0):
    elems = state.shape[1]
    out_shape = [jax.ShapeDtypeStruct(state.shape, jnp.float32)]
    if want_faces:
        out_shape += face_shapes(elems, row_len)
    res = pl.pallas_call(
        lambda *refs: dg_step_kernel(want_faces, xoff, yoff, row_len, lax.axis_size("flow"), lax.axis_size("grp"), *refs),
        out_shape=tuple(out_shape),
        scratch_shapes=[
            pltpu.VMEM((6, FACE_ROWS, elems), jnp.float32),
            pltpu.VMEM((768, elems), jnp.float32),
            pltpu.VMEM((FACE_ROWS, elems), jnp.float32),
            pltpu.VMEM((152, 4 * elems), jnp.float32),
        ],
    )(state, src, *recv, *mats)
    return res


def exchange_faces(sent):
    sx0, sx4, sy0, sy4 = sent
    flow_n = lax.axis_size("flow")
    grp_n = lax.axis_size("grp")
    up_f = [(i, (i + 1) % flow_n) for i in range(flow_n)]
    down_f = [((i + 1) % flow_n, i) for i in range(flow_n)]
    up_g = [(i, (i + 1) % grp_n) for i in range(grp_n)]
    down_g = [((i + 1) % grp_n, i) for i in range(grp_n)]
    return (
        lax.ppermute(sx4, "flow", up_f),
        lax.ppermute(sx0, "flow", down_f),
        lax.ppermute(sy4, "grp", up_g),
        lax.ppermute(sy0, "grp", down_g),
    )


def body(velocity, eddy_visc, projection, acoustic_state, route_send, route_place):
    joint = halos(jnp.concatenate([velocity, eddy_visc[None]], axis=0), 1)
    flow_size = lax.axis_size("flow")
    grp_size = lax.axis_size("grp")
    slot_cap = route_send.shape[2]
    elem_count = acoustic_state.shape[2]
    total_slots = flow_size * grp_size * slot_cap
    placing = route_place.reshape(-1)
    sending = route_send.reshape(-1)
    place_hot = (placing[:, None] == jnp.arange(total_slots, dtype=jnp.int32)[None, :]).astype(jnp.float32)
    home_hot = (sending[:, None] == jnp.arange(elem_count, dtype=jnp.int32)[None, :]).astype(jnp.float32)
    padded_state = jnp.pad(acoustic_state, ((0, 0), (0, 3), (0, 0))).reshape(512, elem_count)
    outgoing = jnp.dot(padded_state, place_hot, precision=THREE_PASS)
    arrived = lax.all_to_all(outgoing, ("flow", "grp"), split_axis=1, concat_axis=1, tiled=True)
    state = jnp.dot(arrived, home_hot, precision=THREE_PASS)

    row_len = velocity.shape[3] // 8
    mats = [jnp.asarray(m) for m in dg_matrices()]
    vel, mxup, mxdn, myup, mydn = les_section_first(velocity, eddy_visc, joint, state)
    merged = exchange_faces((mxdn, mxup, mydn, myup))
    vel, lamb = les_section_last(vel, eddy_visc, merged, joint)
    source = project(lamb, projection)
    xoff = 3 * 2 * velocity.shape[2]
    yoff = 3 * 2 * velocity.shape[1]
    res = dg_step(state, source, merged, mats, True, row_len, xoff, yoff)
    state = res[0]
    recv = exchange_faces(res[1:])
    state = dg_step(state, source, recv, mats, False, row_len)[0]
    leaving = lax.dot_general(state, home_hot, (((1,), (1,)), ((), ())), precision=THREE_PASS)
    returned = lax.all_to_all(leaving, ("flow", "grp"), split_axis=1, concat_axis=1, tiled=True)
    acoustic_out = lax.dot_general(returned, place_hot, (((1,), (1,)), ((), ())), precision=THREE_PASS)
    acoustic_out = acoustic_out.reshape(4, 128, elem_count)[:, :125]
    return (vel, acoustic_out)


def solution(mesh):
    placed = (
        P(None, "flow", "grp", None),
        P("flow", "grp", None),
        P(),
        P(None, None, ("flow", "grp")),
        P(("flow", "grp"), None, None),
        P(("flow", "grp"), None),
    )
    return jax.shard_map(
        body,
        mesh=mesh,
        in_specs=placed,
        out_specs=(P(None, "flow", "grp", None), P(None, None, ("flow", "grp"))),
        check_vma=False,
    )
```

```python
import math

import jax
import jax.numpy as jnp
import numpy as np
from jax import lax
from jax.experimental import pallas as pl
from jax.experimental.pallas import tpu as pltpu
from jax.sharding import PartitionSpec as P

LES_SECTIONS = 2
AC_SECTIONS = 2


TIME_STEP_LES = 0.15
TIME_STEP_ACOUSTIC = 0.02
GEOMETRY = 2.0
LIFT_FACTOR = 20.0
HIGH = lax.Precision.HIGHEST
THREE_PASS = lax.Precision.HIGH


def gll_derivative():
    gll_nodes = np.array([-1.0, -math.sqrt(3.0 / 7.0), 0.0, math.sqrt(3.0 / 7.0), 1.0])
    bary_weights = np.array(
        [
            1.0
            / np.prod([gll_nodes[first] - gll_nodes[other] for other in range(5) if other != first])
            for first in range(5)
        ]
    )
    matrix = np.zeros((5, 5))
    for row_id in range(5):
        for col_id in range(5):
            if row_id != col_id:
                matrix[row_id, col_id] = (
                    bary_weights[col_id]
                    / bary_weights[row_id]
                    / (gll_nodes[row_id] - gll_nodes[col_id])
                )
    for row_id in range(5):
        matrix[row_id, row_id] = -matrix[row_id].sum()
    return matrix


def node_id(coords):
    return coords[0] * 25 + coords[1] * 5 + coords[2]


def face_nodes(dim, at):
    ids = []
    for first in range(5):
        for second in range(5):
            coords = [first, second]
            coords.insert(dim, at)
            ids.append(node_id(coords))
    return ids


def dg_matrices():
    dmat = gll_derivative()
    half = LIFT_FACTOR * 0.5
    apu = np.zeros((128, 384))
    aup = np.zeros((384, 128))
    diag = np.zeros((512, 1))
    lift = np.zeros((128, 152))
    for a in range(5):
        for b in range(5):
            for c in range(5):
                pos = (a, b, c)
                row = node_id(pos)
                for dim in range(3):
                    for k in range(5):
                        col_pos = list(pos)
                        col_pos[dim] = k
                        col = node_id(col_pos)
                        weight = -GEOMETRY * dmat[pos[dim], k]
                        apu[row, dim * 128 + col] += weight
                        aup[dim * 128 + row, col] += weight
    for dim in range(3):
        for side, (sign, at) in enumerate(((-1.0, 0), (1.0, 4))):
            f = 2 * dim + side
            for t, node in enumerate(face_nodes(dim, at)):
                apu[node, dim * 128 + node] += half * sign
                aup[dim * 128 + node, node] += half * sign
                for comp in range(4):
                    diag[comp * 128 + node, 0] += -half
                lift[node, f * 25 + t] = 1.0
    return (apu.astype(np.float32), aup.astype(np.float32), diag.astype(np.float32), lift.astype(np.float32))


def face_rows(state, dim, at):
    elems = state.shape[-1]
    cube = state.reshape(4, 5, 5, 5, elems)
    face = lax.index_in_dim(cube, at, axis=1 + dim, keepdims=False)
    return face.reshape(100, elems)


def les_kernel(mode, flow_n, grp_n, vel_ref, nu_ref, vxlo_ref, vxhi_ref, vylo_ref, vyhi_ref,
               nxlo_ref, nxhi_ref, nylo_ref, nyhi_ref, *rest):
    size_x, size_y, size_z = vel_ref.shape[1], vel_ref.shape[2], vel_ref.shape[3]
    half = size_z // 2
    flow_i = lax.axis_index("flow")
    grp_i = lax.axis_index("grp")
    at_lo_f = flow_i == 0
    at_hi_f = flow_i == flow_n - 1
    at_lo_g = grp_i == 0
    at_hi_g = grp_i == grp_n - 1
    row = lax.broadcasted_iota(jnp.int32, (size_y, size_z), 0)
    lane = lax.broadcasted_iota(jnp.int32, (size_y, size_z), 1)
    if mode == 0:
        state_ref, out_ref, mxup_ref, mxdn_ref, myup_ref, mydn_ref, face_ref = rest

        def xlo(c):
            return jnp.where(at_lo_f, 0.0, vxlo_ref[c])

        def xhi(c):
            return jnp.where(at_hi_f, 0.0, vxhi_ref[c])

        def ylo(c, x):
            return jnp.where(at_lo_g, 0.0, vylo_ref[c, x])

        def yhi(c, x):
            return jnp.where(at_hi_g, 0.0, vyhi_ref[c, x])
    else:
        out_ref, lamb_ref = rest

        def plane(ref, c):
            return jnp.concatenate(
                [ref[pl.ds(c * 2 * size_y, size_y), :], ref[pl.ds(c * 2 * size_y + size_y, size_y), :]], axis=1)

        def line(ref, c, x):
            return jnp.concatenate(
                [ref[pl.ds(c * 2 * size_x + x, 1), :], ref[pl.ds(c * 2 * size_x + size_x + x, 1), :]], axis=1)

        def xlo(c):
            return jnp.where(at_lo_f, 0.0, plane(vxlo_ref, c))

        def xhi(c):
            return jnp.where(at_hi_f, 0.0, plane(vxhi_ref, c))

        def ylo(c, x):
            return jnp.where(at_lo_g, 0.0, line(vylo_ref, c, x))

        def yhi(c, x):
            return jnp.where(at_hi_g, 0.0, line(vyhi_ref, c, x))

    def yp(f, halo):
        return jnp.where(row == size_y - 1, halo, pltpu.roll(f, size_y - 1, 0))

    def ym(f, halo):
        return jnp.where(row == 0, halo, pltpu.roll(f, 1, 0))

    def zp(f):
        return jnp.where(lane == size_z - 1, 0.0, pltpu.roll(f, size_z - 1, 1))

    def zm(f):
        return jnp.where(lane == 0, 0.0, pltpu.roll(f, 1, 1))

    def plane_step(x, first, last):
        lo = x - 1
        hi = x + 1
        u = [vel_ref[c, x] for c in range(3)]
        uxm = [xlo(c) if first else vel_ref[c, lo] for c in range(3)]
        uxp = [xhi(c) if last else vel_ref[c, hi] for c in range(3)]
        uym = [ym(u[c], ylo(c, x)) for c in range(3)]
        uyp = [yp(u[c], yhi(c, x)) for c in range(3)]
        uzm = [zm(u[c]) for c in range(3)]
        uzp = [zp(u[c]) for c in range(3)]
        nu = nu_ref[x]
        nxm = jnp.where(at_lo_f, 0.0, nxlo_ref[3]) if first else nu_ref[lo]
        nxp = jnp.where(at_hi_f, 0.0, nxhi_ref[3]) if last else nu_ref[hi]
        nym = ym(nu, jnp.where(at_lo_g, 0.0, nylo_ref[3, x]))
        nyp = yp(nu, jnp.where(at_hi_g, 0.0, nyhi_ref[3, x]))
        nzm = zm(nu)
        nzp = zp(nu)
        plus = (uxp, uyp, uzp)
        minus = (uxm, uym, uzm)

        def d(c, axis):
            return 0.5 * (plus[axis][c] - minus[axis][c])

        wx = d(2, 1) - d(1, 2)
        wy = d(0, 2) - d(2, 0)
        wz = d(1, 0) - d(0, 1)
        lamb = (wy * u[2] - wz * u[1], wz * u[0] - wx * u[2], wx * u[1] - wy * u[0])
        ups = (0.5 * (nu + nxp), 0.5 * (nu + nyp), 0.5 * (nu + nzp))
        downs = (0.5 * (nu + nxm), 0.5 * (nu + nym), 0.5 * (nu + nzm))
        for c in range(3):
            total = None
            for axis in range(3):
                term = ups[axis] * (plus[axis][c] - u[c]) - downs[axis] * (u[c] - minus[axis][c])
                total = term if total is None else total + term
            out_ref[c, x] = u[c] + TIME_STEP_LES * (total - lamb[c])
            if mode == 1:
                lamb_ref[c, x] = lamb[c].astype(lamb_ref.dtype)

    def step(x, carry):
        plane_step(x, False, False)
        return carry

    plane_step(0, True, False)
    lax.fori_loop(1, size_x - 1, step, 0, unroll=True)
    plane_step(size_x - 1, False, True)
    if mode == 0:
        for c in range(3):
            for h in range(2):
                mxup_ref[pl.ds(c * 2 * size_y + h * size_y, size_y), :] = out_ref[c, size_x - 1, :, pl.ds(h * half, half)]
                mxdn_ref[pl.ds(c * 2 * size_y + h * size_y, size_y), :] = out_ref[c, 0, :, pl.ds(h * half, half)]
                for x in range(size_x):
                    at = c * 2 * size_x + h * size_x + x
                    myup_ref[pl.ds(at, 1), :] = out_ref[c, x, pl.ds(size_y - 1, 1), pl.ds(h * half, half)]
                    mydn_ref[pl.ds(at, 1), :] = out_ref[c, x, pl.ds(0, 1), pl.ds(h * half, half)]
        xrows = 3 * 2 * size_y
        yrows = 3 * 2 * size_x
        elems = state_ref.shape[1]
        row_len = size_z // 8
        face_ref[...] = jnp.zeros(face_ref.shape, jnp.float32)
        extract_faces(state_ref, face_ref)
        mxup_ref[pl.ds(xrows, FACE_ROWS), :] = face_ref[1]
        mxdn_ref[pl.ds(xrows, FACE_ROWS), :] = face_ref[0]
        lane = lax.broadcasted_iota(jnp.int32, (FACE_ROWS, elems), 1)
        myup_ref[pl.ds(yrows, FACE_ROWS), :] = jnp.where(lane < row_len, pltpu.roll(face_ref[3], row_len, 1), 0.0)
        mydn_ref[pl.ds(yrows, FACE_ROWS), :] = jnp.where(lane < row_len, face_ref[2], 0.0)


def les_section_first(vel, nu, joint, state):
    size_x, size_y, size_z = vel.shape[1], vel.shape[2], vel.shape[3]
    xbuf = jax.ShapeDtypeStruct((3 * 2 * size_y + FACE_ROWS, size_z // 2), jnp.float32)
    ybuf = jax.ShapeDtypeStruct((3 * 2 * size_x + FACE_ROWS, size_z // 2), jnp.float32)
    return pl.pallas_call(
        lambda *refs: les_kernel(0, lax.axis_size("flow"), lax.axis_size("grp"), *refs),
        out_shape=(jax.ShapeDtypeStruct(vel.shape, jnp.float32), xbuf, xbuf, ybuf, ybuf),
        scratch_shapes=[pltpu.VMEM((6, FACE_ROWS, state.shape[1]), jnp.float32)],
    )(vel, nu, *joint, *joint, state)


def les_section_last(vel, nu, merged, joint):
    return pl.pallas_call(
        lambda *refs: les_kernel(1, lax.axis_size("flow"), lax.axis_size("grp"), *refs),
        out_shape=(jax.ShapeDtypeStruct(vel.shape, jnp.float32), jax.ShapeDtypeStruct(vel.shape, jnp.bfloat16)),
    )(vel, nu, *merged, *joint)


def halos(field, lead):
    flow_n = lax.axis_size("flow")
    grp_n = lax.axis_size("grp")
    up_f = [(i, (i + 1) % flow_n) for i in range(flow_n)]
    down_f = [((i + 1) % flow_n, i) for i in range(flow_n)]
    up_g = [(i, (i + 1) % grp_n) for i in range(grp_n)]
    down_g = [((i + 1) % grp_n, i) for i in range(grp_n)]
    size_x, size_y = field.shape[lead], field.shape[lead + 1]
    xlo = lax.ppermute(lax.index_in_dim(field, size_x - 1, lead, keepdims=False), "flow", up_f)
    xhi = lax.ppermute(lax.index_in_dim(field, 0, lead, keepdims=False), "flow", down_f)
    ylo = lax.ppermute(lax.slice_in_dim(field, size_y - 1, size_y, axis=lead + 1), "grp", up_g)
    yhi = lax.ppermute(lax.slice_in_dim(field, 0, 1, axis=lead + 1), "grp", down_g)
    return xlo, xhi, ylo, yhi


def project(lamb, projection):
    size_x, size_y, size_z = (lamb.shape[1], lamb.shape[2], lamb.shape[3])
    bx, by, bz = size_x // 8, size_y // 8, size_z // 8
    perm = np.zeros((size_z, size_z), np.float32)
    for ez in range(bz):
        for cz in range(8):
            perm[ez * 8 + cz, cz * bz + ez] = 1.0
    rows = lamb.reshape(-1, size_z)
    moved = jnp.dot(rows, jnp.asarray(perm, jnp.bfloat16), preferred_element_type=jnp.float32)
    moved = moved.astype(jnp.bfloat16)
    blocks = moved.reshape(3, bx, 8, by, 8, 8, bz).transpose(2, 4, 5, 0, 1, 3, 6).reshape(512, -1)
    padded_proj = jnp.pad(projection, ((0, 3), (0, 0)))
    source = jnp.dot(padded_proj, blocks, preferred_element_type=jnp.float32)
    source = source.reshape(128, 3, -1).transpose(1, 0, 2)
    return source.reshape(384, -1)


FACE_ROWS = 104


def extract_faces(state_ref, face_ref):
    for dim in range(3):
        for side, at in ((0, 0), (1, 4)):
            f = 2 * dim + side
            for comp in range(4):
                base = comp * 128
                if dim == 0:
                    face_ref[f, pl.ds(comp * 25, 25), :] = state_ref[pl.ds(base + at * 25, 25), :]
                elif dim == 1:
                    for a in range(5):
                        face_ref[f, pl.ds(comp * 25 + a * 5, 5), :] = state_ref[pl.ds(base + a * 25 + at * 5, 5), :]
                else:
                    face_ref[f, pl.ds(comp * 25, 25), :] = state_ref[pl.ds(base + at, 25, stride=5), :]


def send_faces(face_ref, sx0_ref, sx4_ref, sy0_ref, sy4_ref, row_len):
    sx0_ref[...] = face_ref[0]
    sx4_ref[...] = face_ref[1]
    sy0_ref[...] = face_ref[2][:, :row_len]
    last = pltpu.roll(face_ref[3], row_len, 1)
    sy4_ref[...] = last[:, :row_len]


def dg_faces_kernel(state_ref, sx0_ref, sx4_ref, sy0_ref, sy4_ref, face_ref):
    face_ref[...] = jnp.zeros(face_ref.shape, jnp.float32)
    extract_faces(state_ref, face_ref)
    send_faces(face_ref, sx0_ref, sx4_ref, sy0_ref, sy4_ref, sy0_ref.shape[1])


def dg_step_kernel(want_faces, xoff, yoff, row_len, flow_n, grp_n, state_ref, src_ref, xlo_ref, xhi_ref, ylo_ref, yhi_ref,
                   apu_ref, aup_ref, diag_ref, lift_ref, out_ref, *rest):
    if want_faces:
        sx0_ref, sx4_ref, sy0_ref, sy4_ref, face_ref, oth_ref, pad_ref, g_ref = rest
    else:
        face_ref, oth_ref, pad_ref, g_ref = rest
    elems = state_ref.shape[1]
    lane = lax.broadcasted_iota(jnp.int32, (FACE_ROWS, elems), 1)
    ez = lane % row_len
    face_ref[...] = jnp.zeros(face_ref.shape, jnp.float32)
    oth_ref[...] = jnp.zeros(oth_ref.shape, jnp.float32)
    extract_faces(state_ref, face_ref)
    flow_i = lax.axis_index("flow")
    grp_i = lax.axis_index("grp")
    oth_ref[pl.ds(0, FACE_ROWS), :] = jnp.where(flow_i == 0, 0.0, xlo_ref[pl.ds(xoff, FACE_ROWS), :])
    oth_ref[pl.ds(128, FACE_ROWS), :] = jnp.where(flow_i == flow_n - 1, 0.0, xhi_ref[pl.ds(xoff, FACE_ROWS), :])
    pad_ref[:, pl.ds(0, row_len)] = jnp.where(
        grp_i == 0, 0.0, ylo_ref[pl.ds(yoff, FACE_ROWS), pl.ds(0, row_len)])
    oth_ref[pl.ds(256, FACE_ROWS), :] = jnp.where(
        lane < row_len, pad_ref[...], pltpu.roll(face_ref[3], row_len, 1))
    pad_ref[:, pl.ds(0, row_len)] = jnp.where(
        grp_i == grp_n - 1, 0.0, yhi_ref[pl.ds(yoff, FACE_ROWS), pl.ds(0, row_len)])
    oth_ref[pl.ds(384, FACE_ROWS), :] = jnp.where(
        lane >= elems - row_len, pltpu.roll(pad_ref[...], elems - row_len, 1),
        pltpu.roll(face_ref[2], elems - row_len, 1))
    oth_ref[pl.ds(512, FACE_ROWS), :] = jnp.where(ez == 0, 0.0, pltpu.roll(face_ref[5], 1, 1))
    oth_ref[pl.ds(640, FACE_ROWS), :] = jnp.where(
        ez == row_len - 1, 0.0, pltpu.roll(face_ref[4], elems - 1, 1))
    g_ref[pl.ds(144, 8), :] = jnp.zeros((8, 4 * elems), jnp.float32)
    half = LIFT_FACTOR * 0.5
    for dim in range(3):
        for side, sign in ((0, -1.0), (1, 1.0)):
            f = 2 * dim + side
            o_p = oth_ref[pl.ds(f * 128, 25), :]
            o_u = [oth_ref[pl.ds(f * 128 + (1 + k) * 25, 25), :] for k in range(3)]
            g_ref[pl.ds(f * 25, 25), pl.ds(0, elems)] = half * (o_p - sign * o_u[dim])
            for k in range(3):
                value = half * o_u[k]
                if k == dim:
                    value = value - half * sign * o_p
                g_ref[pl.ds(f * 25, 25), pl.ds((1 + k) * elems, elems)] = value
    faces = jnp.dot(lift_ref[...], g_ref[...], precision=THREE_PASS, preferred_element_type=jnp.float32)
    state = state_ref[...]
    pres = state[:128]
    vel = state[128:]
    rate_p = jnp.dot(apu_ref[...], vel, precision=THREE_PASS, preferred_element_type=jnp.float32)
    rate_p = rate_p + diag_ref[pl.ds(0, 128), :] * pres + faces[:, :elems]
    out_ref[pl.ds(0, 128), :] = pres + TIME_STEP_ACOUSTIC * rate_p
    rate_u = jnp.dot(aup_ref[...], pres, precision=THREE_PASS, preferred_element_type=jnp.float32)
    for k in range(3):
        rows = pl.ds(128 + k * 128, 128)
        rate_k = rate_u[k * 128:(k + 1) * 128] + diag_ref[rows, :] * state_ref[rows, :]
        rate_k = rate_k + faces[:, (1 + k) * elems:(2 + k) * elems]
        out_ref[rows, :] = state_ref[rows, :] + TIME_STEP_ACOUSTIC * (rate_k - src_ref[pl.ds(k * 128, 128), :])
    if want_faces:
        extract_faces(out_ref, face_ref)
        send_faces(face_ref, sx0_ref, sx4_ref, sy0_ref, sy4_ref, row_len)


def face_shapes(elems, row_len):
    big = jax.ShapeDtypeStruct((FACE_ROWS, elems), jnp.float32)
    small = jax.ShapeDtypeStruct((FACE_ROWS, row_len), jnp.float32)
    return [big, big, small, small]


def dg_faces(state, row_len):
    elems = state.shape[1]
    return pl.pallas_call(
        dg_faces_kernel,
        out_shape=tuple(face_shapes(elems, row_len)),
        scratch_shapes=[pltpu.VMEM((6, FACE_ROWS, elems), jnp.float32)],
    )(state)


def dg_step(state, src, recv, mats, want_faces, row_len, xoff=0, yoff=0):
    elems = state.shape[1]
    out_shape = [jax.ShapeDtypeStruct(state.shape, jnp.float32)]
    if want_faces:
        out_shape += face_shapes(elems, row_len)
    res = pl.pallas_call(
        lambda *refs: dg_step_kernel(want_faces, xoff, yoff, row_len, lax.axis_size("flow"), lax.axis_size("grp"), *refs),
        out_shape=tuple(out_shape),
        scratch_shapes=[
            pltpu.VMEM((6, FACE_ROWS, elems), jnp.float32),
            pltpu.VMEM((768, elems), jnp.float32),
            pltpu.VMEM((FACE_ROWS, elems), jnp.float32),
            pltpu.VMEM((152, 4 * elems), jnp.float32),
        ],
    )(state, src, *recv, *mats)
    return res


def exchange_faces(sent):
    sx0, sx4, sy0, sy4 = sent
    flow_n = lax.axis_size("flow")
    grp_n = lax.axis_size("grp")
    up_f = [(i, (i + 1) % flow_n) for i in range(flow_n)]
    down_f = [((i + 1) % flow_n, i) for i in range(flow_n)]
    up_g = [(i, (i + 1) % grp_n) for i in range(grp_n)]
    down_g = [((i + 1) % grp_n, i) for i in range(grp_n)]
    return (
        lax.ppermute(sx4, "flow", up_f),
        lax.ppermute(sx0, "flow", down_f),
        lax.ppermute(sy4, "grp", up_g),
        lax.ppermute(sy0, "grp", down_g),
    )


def body(velocity, eddy_visc, projection, acoustic_state, route_send, route_place):
    joint = halos(jnp.concatenate([velocity, eddy_visc[None]], axis=0), 1)
    flow_size = lax.axis_size("flow")
    grp_size = lax.axis_size("grp")
    slot_cap = route_send.shape[2]
    elem_count = acoustic_state.shape[2]
    total_slots = flow_size * grp_size * slot_cap
    placing = route_place.reshape(-1)
    sending = route_send.reshape(-1)
    place_hot = (placing[:, None] == jnp.arange(total_slots, dtype=jnp.int32)[None, :]).astype(jnp.float32)
    home_hot = (sending[:, None] == jnp.arange(elem_count, dtype=jnp.int32)[None, :]).astype(jnp.float32)
    padded_state = jnp.pad(acoustic_state, ((0, 0), (0, 3), (0, 0))).reshape(512, elem_count)
    outgoing = jnp.dot(padded_state, place_hot, precision=THREE_PASS)
    arrived = lax.all_to_all(outgoing, ("flow", "grp"), split_axis=1, concat_axis=1, tiled=True)
    state = jnp.dot(arrived, home_hot, precision=THREE_PASS)

    row_len = velocity.shape[3] // 8
    mats = [jnp.asarray(m) for m in dg_matrices()]
    vel, mxup, mxdn, myup, mydn = les_section_first(velocity, eddy_visc, joint, state)
    merged = exchange_faces((mxdn, mxup, mydn, myup))
    vel, lamb = les_section_last(vel, eddy_visc, merged, joint)
    source = project(lamb, projection)
    xoff = 3 * 2 * velocity.shape[2]
    yoff = 3 * 2 * velocity.shape[1]
    res = dg_step(state, source, merged, mats, True, row_len, xoff, yoff)
    state = res[0]
    recv = exchange_faces(res[1:])
    state = dg_step(state, source, recv, mats, False, row_len)[0]
    leaving = lax.dot_general(state, home_hot, (((1,), (1,)), ((), ())), precision=THREE_PASS)
    returned = lax.all_to_all(leaving, ("flow", "grp"), split_axis=1, concat_axis=1, tiled=True)
    acoustic_out = lax.dot_general(returned, place_hot, (((1,), (1,)), ((), ())), precision=THREE_PASS)
    acoustic_out = acoustic_out.reshape(4, 128, elem_count)[:, :125]
    return (vel, acoustic_out)


def solution(mesh):
    placed = (
        P(None, "flow", "grp", None),
        P("flow", "grp", None),
        P(),
        P(None, None, ("flow", "grp")),
        P(("flow", "grp"), None, None),
        P(("flow", "grp"), None),
    )
    return jax.shard_map(
        body,
        mesh=mesh,
        in_specs=placed,
        out_specs=(P(None, "flow", "grp", None), P(None, None, ("flow", "grp"))),
        check_vma=False,
    )
```

```python
import math

import jax
import jax.numpy as jnp
import numpy as np
from jax import lax
from jax.experimental import pallas as pl
from jax.experimental.pallas import tpu as pltpu
from jax.sharding import PartitionSpec as P

LES_SECTIONS = 2
AC_SECTIONS = 2


TIME_STEP_LES = 0.15
TIME_STEP_ACOUSTIC = 0.02
GEOMETRY = 2.0
LIFT_FACTOR = 20.0
HIGH = lax.Precision.HIGHEST
THREE_PASS = lax.Precision.HIGH


def gll_derivative():
    gll_nodes = np.array([-1.0, -math.sqrt(3.0 / 7.0), 0.0, math.sqrt(3.0 / 7.0), 1.0])
    bary_weights = np.array(
        [
            1.0
            / np.prod([gll_nodes[first] - gll_nodes[other] for other in range(5) if other != first])
            for first in range(5)
        ]
    )
    matrix = np.zeros((5, 5))
    for row_id in range(5):
        for col_id in range(5):
            if row_id != col_id:
                matrix[row_id, col_id] = (
                    bary_weights[col_id]
                    / bary_weights[row_id]
                    / (gll_nodes[row_id] - gll_nodes[col_id])
                )
    for row_id in range(5):
        matrix[row_id, row_id] = -matrix[row_id].sum()
    return matrix


def node_id(coords):
    return coords[0] * 25 + coords[1] * 5 + coords[2]


def face_nodes(dim, at):
    ids = []
    for first in range(5):
        for second in range(5):
            coords = [first, second]
            coords.insert(dim, at)
            ids.append(node_id(coords))
    return ids


def dg_matrices():
    dmat = gll_derivative()
    half = LIFT_FACTOR * 0.5
    apu = np.zeros((128, 384))
    aup = np.zeros((384, 128))
    diag = np.zeros((512, 1))
    lift = np.zeros((128, 152))
    for a in range(5):
        for b in range(5):
            for c in range(5):
                pos = (a, b, c)
                row = node_id(pos)
                for dim in range(3):
                    for k in range(5):
                        col_pos = list(pos)
                        col_pos[dim] = k
                        col = node_id(col_pos)
                        weight = -GEOMETRY * dmat[pos[dim], k]
                        apu[row, dim * 128 + col] += weight
                        aup[dim * 128 + row, col] += weight
    for dim in range(3):
        for side, (sign, at) in enumerate(((-1.0, 0), (1.0, 4))):
            f = 2 * dim + side
            for t, node in enumerate(face_nodes(dim, at)):
                apu[node, dim * 128 + node] += half * sign
                aup[dim * 128 + node, node] += half * sign
                for comp in range(4):
                    diag[comp * 128 + node, 0] += -half
                lift[node, f * 25 + t] = 1.0
    return (apu.astype(np.float32), aup.astype(np.float32), diag.astype(np.float32), lift.astype(np.float32))


def face_rows(state, dim, at):
    elems = state.shape[-1]
    cube = state.reshape(4, 5, 5, 5, elems)
    face = lax.index_in_dim(cube, at, axis=1 + dim, keepdims=False)
    return face.reshape(100, elems)


def les_kernel(mode, flow_n, grp_n, vel_ref, nu_ref, vxlo_ref, vxhi_ref, vylo_ref, vyhi_ref,
               nxlo_ref, nxhi_ref, nylo_ref, nyhi_ref, *rest):
    size_x, size_y, size_z = vel_ref.shape[1], vel_ref.shape[2], vel_ref.shape[3]
    half = size_z // 2
    flow_i = lax.axis_index("flow")
    grp_i = lax.axis_index("grp")
    at_lo_f = flow_i == 0
    at_hi_f = flow_i == flow_n - 1
    at_lo_g = grp_i == 0
    at_hi_g = grp_i == grp_n - 1
    row = lax.broadcasted_iota(jnp.int32, (size_y, size_z), 0)
    lane = lax.broadcasted_iota(jnp.int32, (size_y, size_z), 1)
    if mode == 0:
        state_ref, out_ref, mxup_ref, mxdn_ref, myup_ref, mydn_ref, face_ref = rest

        def xlo(c):
            return jnp.where(at_lo_f, 0.0, vxlo_ref[c])

        def xhi(c):
            return jnp.where(at_hi_f, 0.0, vxhi_ref[c])

        def ylo(c, x):
            return jnp.where(at_lo_g, 0.0, vylo_ref[c, x])

        def yhi(c, x):
            return jnp.where(at_hi_g, 0.0, vyhi_ref[c, x])
    else:
        out_ref, lamb_ref = rest

        def plane(ref, c):
            return jnp.concatenate(
                [ref[pl.ds(c * 2 * size_y, size_y), :], ref[pl.ds(c * 2 * size_y + size_y, size_y), :]], axis=1)

        def line(ref, c, x):
            return jnp.concatenate(
                [ref[pl.ds(c * 2 * size_x + x, 1), :], ref[pl.ds(c * 2 * size_x + size_x + x, 1), :]], axis=1)

        def xlo(c):
            return jnp.where(at_lo_f, 0.0, plane(vxlo_ref, c))

        def xhi(c):
            return jnp.where(at_hi_f, 0.0, plane(vxhi_ref, c))

        def ylo(c, x):
            return jnp.where(at_lo_g, 0.0, line(vylo_ref, c, x))

        def yhi(c, x):
            return jnp.where(at_hi_g, 0.0, line(vyhi_ref, c, x))

    def yp(f, halo):
        return jnp.where(row == size_y - 1, halo, pltpu.roll(f, size_y - 1, 0))

    def ym(f, halo):
        return jnp.where(row == 0, halo, pltpu.roll(f, 1, 0))

    def zp(f):
        return jnp.where(lane == size_z - 1, 0.0, pltpu.roll(f, size_z - 1, 1))

    def zm(f):
        return jnp.where(lane == 0, 0.0, pltpu.roll(f, 1, 1))

    def plane_step(x, first, last):
        lo = x - 1
        hi = x + 1
        u = [vel_ref[c, x] for c in range(3)]
        uxm = [xlo(c) if first else vel_ref[c, lo] for c in range(3)]
        uxp = [xhi(c) if last else vel_ref[c, hi] for c in range(3)]
        uym = [ym(u[c], ylo(c, x)) for c in range(3)]
        uyp = [yp(u[c], yhi(c, x)) for c in range(3)]
        uzm = [zm(u[c]) for c in range(3)]
        uzp = [zp(u[c]) for c in range(3)]
        nu = nu_ref[x]
        nxm = jnp.where(at_lo_f, 0.0, nxlo_ref[3]) if first else nu_ref[lo]
        nxp = jnp.where(at_hi_f, 0.0, nxhi_ref[3]) if last else nu_ref[hi]
        nym = ym(nu, jnp.where(at_lo_g, 0.0, nylo_ref[3, x]))
        nyp = yp(nu, jnp.where(at_hi_g, 0.0, nyhi_ref[3, x]))
        nzm = zm(nu)
        nzp = zp(nu)
        plus = (uxp, uyp, uzp)
        minus = (uxm, uym, uzm)

        def d(c, axis):
            return 0.5 * (plus[axis][c] - minus[axis][c])

        wx = d(2, 1) - d(1, 2)
        wy = d(0, 2) - d(2, 0)
        wz = d(1, 0) - d(0, 1)
        lamb = (wy * u[2] - wz * u[1], wz * u[0] - wx * u[2], wx * u[1] - wy * u[0])
        ups = (0.5 * (nu + nxp), 0.5 * (nu + nyp), 0.5 * (nu + nzp))
        downs = (0.5 * (nu + nxm), 0.5 * (nu + nym), 0.5 * (nu + nzm))
        for c in range(3):
            total = None
            for axis in range(3):
                term = ups[axis] * (plus[axis][c] - u[c]) - downs[axis] * (u[c] - minus[axis][c])
                total = term if total is None else total + term
            out_ref[c, x] = u[c] + TIME_STEP_LES * (total - lamb[c])
            if mode == 1:
                lamb_ref[c, x] = lamb[c].astype(lamb_ref.dtype)

    def step(x, carry):
        plane_step(x, False, False)
        return carry

    plane_step(0, True, False)
    lax.fori_loop(1, size_x - 1, step, 0, unroll=True)
    plane_step(size_x - 1, False, True)
    if mode == 0:
        for c in range(3):
            for h in range(2):
                mxup_ref[pl.ds(c * 2 * size_y + h * size_y, size_y), :] = out_ref[c, size_x - 1, :, pl.ds(h * half, half)]
                mxdn_ref[pl.ds(c * 2 * size_y + h * size_y, size_y), :] = out_ref[c, 0, :, pl.ds(h * half, half)]
                for x in range(size_x):
                    at = c * 2 * size_x + h * size_x + x
                    myup_ref[pl.ds(at, 1), :] = out_ref[c, x, pl.ds(size_y - 1, 1), pl.ds(h * half, half)]
                    mydn_ref[pl.ds(at, 1), :] = out_ref[c, x, pl.ds(0, 1), pl.ds(h * half, half)]
        xrows = 3 * 2 * size_y
        yrows = 3 * 2 * size_x
        elems = state_ref.shape[1]
        row_len = size_z // 8
        face_ref[...] = jnp.zeros(face_ref.shape, jnp.float32)
        extract_faces(state_ref, face_ref)
        mxup_ref[pl.ds(xrows, FACE_ROWS), :] = face_ref[1]
        mxdn_ref[pl.ds(xrows, FACE_ROWS), :] = face_ref[0]
        lane = lax.broadcasted_iota(jnp.int32, (FACE_ROWS, elems), 1)
        myup_ref[pl.ds(yrows, FACE_ROWS), :] = jnp.where(lane < row_len, pltpu.roll(face_ref[3], row_len, 1), 0.0)
        mydn_ref[pl.ds(yrows, FACE_ROWS), :] = jnp.where(lane < row_len, face_ref[2], 0.0)


def les_section_first(vel, nu, joint, state):
    size_x, size_y, size_z = vel.shape[1], vel.shape[2], vel.shape[3]
    xbuf = jax.ShapeDtypeStruct((3 * 2 * size_y + FACE_ROWS, size_z // 2), jnp.float32)
    ybuf = jax.ShapeDtypeStruct((3 * 2 * size_x + FACE_ROWS, size_z // 2), jnp.float32)
    def kernel(vel_ref, nu_ref, xlo_ref, xhi_ref, ylo_ref, yhi_ref, *rest):
        halo_refs = (xlo_ref, xhi_ref, ylo_ref, yhi_ref)
        les_kernel(0, lax.axis_size("flow"), lax.axis_size("grp"), vel_ref, nu_ref, *halo_refs, *halo_refs, *rest)

    return pl.pallas_call(
        kernel,
        out_shape=(jax.ShapeDtypeStruct(vel.shape, jnp.float32), xbuf, xbuf, ybuf, ybuf),
        scratch_shapes=[pltpu.VMEM((6, FACE_ROWS, state.shape[1]), jnp.float32)],
    )(vel, nu, *joint, state)


def les_section_last(vel, nu, merged, joint):
    return pl.pallas_call(
        lambda *refs: les_kernel(1, lax.axis_size("flow"), lax.axis_size("grp"), *refs),
        out_shape=(jax.ShapeDtypeStruct(vel.shape, jnp.float32), jax.ShapeDtypeStruct(vel.shape, jnp.bfloat16)),
    )(vel, nu, *merged, *joint)


def halos(field, lead):
    flow_n = lax.axis_size("flow")
    grp_n = lax.axis_size("grp")
    up_f = [(i, (i + 1) % flow_n) for i in range(flow_n)]
    down_f = [((i + 1) % flow_n, i) for i in range(flow_n)]
    up_g = [(i, (i + 1) % grp_n) for i in range(grp_n)]
    down_g = [((i + 1) % grp_n, i) for i in range(grp_n)]
    size_x, size_y = field.shape[lead], field.shape[lead + 1]
    xlo = lax.ppermute(lax.index_in_dim(field, size_x - 1, lead, keepdims=False), "flow", up_f)
    xhi = lax.ppermute(lax.index_in_dim(field, 0, lead, keepdims=False), "flow", down_f)
    ylo = lax.ppermute(lax.slice_in_dim(field, size_y - 1, size_y, axis=lead + 1), "grp", up_g)
    yhi = lax.ppermute(lax.slice_in_dim(field, 0, 1, axis=lead + 1), "grp", down_g)
    return xlo, xhi, ylo, yhi


def project(lamb, projection):
    size_x, size_y, size_z = (lamb.shape[1], lamb.shape[2], lamb.shape[3])
    bx, by, bz = size_x // 8, size_y // 8, size_z // 8
    perm = np.zeros((size_z, size_z), np.float32)
    for ez in range(bz):
        for cz in range(8):
            perm[ez * 8 + cz, cz * bz + ez] = 1.0
    rows = lamb.reshape(-1, size_z)
    moved = jnp.dot(rows, jnp.asarray(perm, jnp.bfloat16), preferred_element_type=jnp.float32)
    moved = moved.astype(jnp.bfloat16)
    blocks = moved.reshape(3, bx, 8, by, 8, 8, bz).transpose(2, 4, 5, 0, 1, 3, 6).reshape(512, -1)
    padded_proj = jnp.pad(projection, ((0, 3), (0, 0)))
    source = jnp.dot(padded_proj, blocks, preferred_element_type=jnp.float32)
    source = source.reshape(128, 3, -1).transpose(1, 0, 2)
    return source.reshape(384, -1)


FACE_ROWS = 104


def extract_faces(state_ref, face_ref):
    for dim in range(3):
        for side, at in ((0, 0), (1, 4)):
            f = 2 * dim + side
            for comp in range(4):
                base = comp * 128
                if dim == 0:
                    face_ref[f, pl.ds(comp * 25, 25), :] = state_ref[pl.ds(base + at * 25, 25), :]
                elif dim == 1:
                    for a in range(5):
                        face_ref[f, pl.ds(comp * 25 + a * 5, 5), :] = state_ref[pl.ds(base + a * 25 + at * 5, 5), :]
                else:
                    face_ref[f, pl.ds(comp * 25, 25), :] = state_ref[pl.ds(base + at, 25, stride=5), :]


def send_faces(face_ref, sx0_ref, sx4_ref, sy0_ref, sy4_ref, row_len):
    sx0_ref[...] = face_ref[0]
    sx4_ref[...] = face_ref[1]
    sy0_ref[...] = face_ref[2][:, :row_len]
    last = pltpu.roll(face_ref[3], row_len, 1)
    sy4_ref[...] = last[:, :row_len]


def dg_faces_kernel(state_ref, sx0_ref, sx4_ref, sy0_ref, sy4_ref, face_ref):
    face_ref[...] = jnp.zeros(face_ref.shape, jnp.float32)
    extract_faces(state_ref, face_ref)
    send_faces(face_ref, sx0_ref, sx4_ref, sy0_ref, sy4_ref, sy0_ref.shape[1])


def dg_step_kernel(want_faces, xoff, yoff, row_len, flow_n, grp_n, state_ref, src_ref, xlo_ref, xhi_ref, ylo_ref, yhi_ref,
                   apu_ref, aup_ref, diag_ref, lift_ref, out_ref, *rest):
    if want_faces:
        sx0_ref, sx4_ref, sy0_ref, sy4_ref, face_ref, oth_ref, pad_ref, g_ref = rest
    else:
        face_ref, oth_ref, pad_ref, g_ref = rest
    elems = state_ref.shape[1]
    lane = lax.broadcasted_iota(jnp.int32, (FACE_ROWS, elems), 1)
    ez = lane % row_len
    face_ref[...] = jnp.zeros(face_ref.shape, jnp.float32)
    oth_ref[...] = jnp.zeros(oth_ref.shape, jnp.float32)
    extract_faces(state_ref, face_ref)
    flow_i = lax.axis_index("flow")
    grp_i = lax.axis_index("grp")
    oth_ref[pl.ds(0, FACE_ROWS), :] = jnp.where(flow_i == 0, 0.0, xlo_ref[pl.ds(xoff, FACE_ROWS), :])
    oth_ref[pl.ds(128, FACE_ROWS), :] = jnp.where(flow_i == flow_n - 1, 0.0, xhi_ref[pl.ds(xoff, FACE_ROWS), :])
    pad_ref[:, pl.ds(0, row_len)] = jnp.where(
        grp_i == 0, 0.0, ylo_ref[pl.ds(yoff, FACE_ROWS), pl.ds(0, row_len)])
    oth_ref[pl.ds(256, FACE_ROWS), :] = jnp.where(
        lane < row_len, pad_ref[...], pltpu.roll(face_ref[3], row_len, 1))
    pad_ref[:, pl.ds(0, row_len)] = jnp.where(
        grp_i == grp_n - 1, 0.0, yhi_ref[pl.ds(yoff, FACE_ROWS), pl.ds(0, row_len)])
    oth_ref[pl.ds(384, FACE_ROWS), :] = jnp.where(
        lane >= elems - row_len, pltpu.roll(pad_ref[...], elems - row_len, 1),
        pltpu.roll(face_ref[2], elems - row_len, 1))
    oth_ref[pl.ds(512, FACE_ROWS), :] = jnp.where(ez == 0, 0.0, pltpu.roll(face_ref[5], 1, 1))
    oth_ref[pl.ds(640, FACE_ROWS), :] = jnp.where(
        ez == row_len - 1, 0.0, pltpu.roll(face_ref[4], elems - 1, 1))
    g_ref[pl.ds(144, 8), :] = jnp.zeros((8, 4 * elems), jnp.float32)
    half = LIFT_FACTOR * 0.5
    for dim in range(3):
        for side, sign in ((0, -1.0), (1, 1.0)):
            f = 2 * dim + side
            o_p = oth_ref[pl.ds(f * 128, 25), :]
            o_u = [oth_ref[pl.ds(f * 128 + (1 + k) * 25, 25), :] for k in range(3)]
            g_ref[pl.ds(f * 25, 25), pl.ds(0, elems)] = half * (o_p - sign * o_u[dim])
            for k in range(3):
                value = half * o_u[k]
                if k == dim:
                    value = value - half * sign * o_p
                g_ref[pl.ds(f * 25, 25), pl.ds((1 + k) * elems, elems)] = value
    faces = jnp.dot(lift_ref[...], g_ref[...], precision=THREE_PASS, preferred_element_type=jnp.float32)
    state = state_ref[...]
    pres = state[:128]
    vel = state[128:]
    rate_p = jnp.dot(apu_ref[...], vel, precision=THREE_PASS, preferred_element_type=jnp.float32)
    rate_p = rate_p + diag_ref[pl.ds(0, 128), :] * pres + faces[:, :elems]
    out_ref[pl.ds(0, 128), :] = pres + TIME_STEP_ACOUSTIC * rate_p
    rate_u = jnp.dot(aup_ref[...], pres, precision=THREE_PASS, preferred_element_type=jnp.float32)
    for k in range(3):
        rows = pl.ds(128 + k * 128, 128)
        rate_k = rate_u[k * 128:(k + 1) * 128] + diag_ref[rows, :] * state_ref[rows, :]
        rate_k = rate_k + faces[:, (1 + k) * elems:(2 + k) * elems]
        out_ref[rows, :] = state_ref[rows, :] + TIME_STEP_ACOUSTIC * (rate_k - src_ref[pl.ds(k * 128, 128), :])
    if want_faces:
        extract_faces(out_ref, face_ref)
        send_faces(face_ref, sx0_ref, sx4_ref, sy0_ref, sy4_ref, row_len)


def face_shapes(elems, row_len):
    big = jax.ShapeDtypeStruct((FACE_ROWS, elems), jnp.float32)
    small = jax.ShapeDtypeStruct((FACE_ROWS, row_len), jnp.float32)
    return [big, big, small, small]


def dg_faces(state, row_len):
    elems = state.shape[1]
    return pl.pallas_call(
        dg_faces_kernel,
        out_shape=tuple(face_shapes(elems, row_len)),
        scratch_shapes=[pltpu.VMEM((6, FACE_ROWS, elems), jnp.float32)],
    )(state)


def dg_step(state, src, recv, mats, want_faces, row_len, xoff=0, yoff=0):
    elems = state.shape[1]
    out_shape = [jax.ShapeDtypeStruct(state.shape, jnp.float32)]
    if want_faces:
        out_shape += face_shapes(elems, row_len)
    res = pl.pallas_call(
        lambda *refs: dg_step_kernel(want_faces, xoff, yoff, row_len, lax.axis_size("flow"), lax.axis_size("grp"), *refs),
        out_shape=tuple(out_shape),
        scratch_shapes=[
            pltpu.VMEM((6, FACE_ROWS, elems), jnp.float32),
            pltpu.VMEM((768, elems), jnp.float32),
            pltpu.VMEM((FACE_ROWS, elems), jnp.float32),
            pltpu.VMEM((152, 4 * elems), jnp.float32),
        ],
    )(state, src, *recv, *mats)
    return res


def exchange_faces(sent):
    sx0, sx4, sy0, sy4 = sent
    flow_n = lax.axis_size("flow")
    grp_n = lax.axis_size("grp")
    up_f = [(i, (i + 1) % flow_n) for i in range(flow_n)]
    down_f = [((i + 1) % flow_n, i) for i in range(flow_n)]
    up_g = [(i, (i + 1) % grp_n) for i in range(grp_n)]
    down_g = [((i + 1) % grp_n, i) for i in range(grp_n)]
    return (
        lax.ppermute(sx4, "flow", up_f),
        lax.ppermute(sx0, "flow", down_f),
        lax.ppermute(sy4, "grp", up_g),
        lax.ppermute(sy0, "grp", down_g),
    )


def body(velocity, eddy_visc, projection, acoustic_state, route_send, route_place):
    joint = halos(jnp.concatenate([velocity, eddy_visc[None]], axis=0), 1)
    flow_size = lax.axis_size("flow")
    grp_size = lax.axis_size("grp")
    slot_cap = route_send.shape[2]
    elem_count = acoustic_state.shape[2]
    total_slots = flow_size * grp_size * slot_cap
    placing = route_place.reshape(-1)
    sending = route_send.reshape(-1)
    place_hot = (placing[:, None] == jnp.arange(total_slots, dtype=jnp.int32)[None, :]).astype(jnp.float32)
    home_hot = (sending[:, None] == jnp.arange(elem_count, dtype=jnp.int32)[None, :]).astype(jnp.float32)
    padded_state = jnp.pad(acoustic_state, ((0, 0), (0, 3), (0, 0))).reshape(512, elem_count)
    outgoing = jnp.dot(padded_state, place_hot, precision=THREE_PASS)
    arrived = lax.all_to_all(outgoing, ("flow", "grp"), split_axis=1, concat_axis=1, tiled=True)
    state = jnp.dot(arrived, home_hot, precision=THREE_PASS)

    row_len = velocity.shape[3] // 8
    mats = [jnp.asarray(m) for m in dg_matrices()]
    vel, mxup, mxdn, myup, mydn = les_section_first(velocity, eddy_visc, joint, state)
    merged = exchange_faces((mxdn, mxup, mydn, myup))
    vel, lamb = les_section_last(vel, eddy_visc, merged, joint)
    source = project(lamb, projection)
    xoff = 3 * 2 * velocity.shape[2]
    yoff = 3 * 2 * velocity.shape[1]
    res = dg_step(state, source, merged, mats, True, row_len, xoff, yoff)
    state = res[0]
    recv = exchange_faces(res[1:])
    state = dg_step(state, source, recv, mats, False, row_len)[0]
    leaving = lax.dot_general(state, home_hot, (((1,), (1,)), ((), ())), precision=THREE_PASS)
    returned = lax.all_to_all(leaving, ("flow", "grp"), split_axis=1, concat_axis=1, tiled=True)
    acoustic_out = lax.dot_general(returned, place_hot, (((1,), (1,)), ((), ())), precision=THREE_PASS)
    acoustic_out = acoustic_out.reshape(4, 128, elem_count)[:, :125]
    return (vel, acoustic_out)


def solution(mesh):
    placed = (
        P(None, "flow", "grp", None),
        P("flow", "grp", None),
        P(),
        P(None, None, ("flow", "grp")),
        P(("flow", "grp"), None, None),
        P(("flow", "grp"), None),
    )
    return jax.shard_map(
        body,
        mesh=mesh,
        in_specs=placed,
        out_specs=(P(None, "flow", "grp", None), P(None, None, ("flow", "grp"))),
        check_vma=False,
    )
```
